32 devices in a mesh: real: 2 (over y), gx: 4 (over z), gy: 2 (over x), gz: 2 (over core).
Axes of the slice: x: 2, y: 2, z: 4, core: 2. Of those that a mesh axis runs over, the one named last changes fastest.
Arguments:
- log_noise: float32 [64, 128, 256], P(('real', 'gz'), 'gx', 'gy'), parts along dimension 0, may hold values from -3 to 3
- facies: int32 [64, 128, 256], P(('real', 'gz'), 'gx', 'gy'), parts along dimension 0, may hold values from 0 to 3
- facies_table: float32 [3, 4], replicated, may hold values from -1 to 1
- pressure_old: float32 [8, 4, 8], P(('real', 'gz'), 'gx', 'gy'), parts along dimension 0, may hold values from -6 to 6
- accumulation: float32 [8, 4, 8], P(('real', 'gz'), 'gx', 'gy'), parts along dimension 0, may hold values from 100 to 1000
- source: float32 [8, 4, 8], P(('real', 'gz'), 'gx', 'gy'), parts along dimension 0, may hold values from -600 to 600
Outputs:
- coarse_pressure: float32 [8, 4, 8], P(('real', 'gz'), 'gx', 'gy'), parts along dimension 0
- upscaled: float32 [3, 8, 4, 8], P(None, ('real', 'gz'), 'gx', 'gy'), parts along dimension 1
The draws below stay inside these ranges and needn't reach their ends.
There are 2 independent parts, one for each index of `real`. The reference program is written for one: setup_inputs(seed, part) draws one part's arguments, and reference() takes and returns one part's arrays. A program takes and returns all parts, laid end to end along the dimension named above; an argument that names none is the same for every part. Nothing has to cross between parts.
All inputs are finite; a program needn't handle non-finite values.
Results may differ from the reference program's by a relative error of at most 0.0003.
Values sent between devices are 32-bit elements; how exact they have to be, the bound alone decides.
No kernel may reach another device: no remote copies, remote signals or barrier semaphores. Data moves between devices by JAX's collectives and lax.ppermute only.
A program may use at most 64 MiB of HBM per device.

```python
import math
import jax
import jax.numpy as jnp
from jax import lax

NFAC = 4
CCX = 32
CCY = 32
CCZ = 8
RIM = 4
SWEEPS = 3
CSWEEPS = 2
NX = 128
NY = 256
NZ = 32
NCX = 4
NCY = 8
NCZ = 4


def place_ends(values, own_key, least, high):
    longest = values.shape.index(max(values.shape))
    spots = []
    for shift in (0, 1):
        where = [jax.random.randint(jax.random.fold_in(own_key, axis), (), 0, length) for axis, length in enumerate(values.shape)]
        where[longest] = (where[longest] + shift) % values.shape[longest]
        spots.append(tuple(where))
    return values.at[spots[0]].set(least).at[spots[1]].set(high)


def block_scale(stream_key, shape, cuts, low, largest):
    loudness = 1.0
    for axis_at, parts in cuts:
        steps = jax.random.uniform(jax.random.fold_in(jax.random.fold_in(stream_key, 6), axis_at), (parts,), jnp.float32, low / len(cuts), largest / len(cuts))
        loudness = loudness * jnp.repeat(jnp.exp(steps), shape[axis_at] // parts).reshape((-1,) + (1,) * (len(shape) - 1 - axis_at))
    return loudness


def centred(stream_key, dims, spread, reach, shards=(), kind=jnp.bfloat16):
    level = block_scale(stream_key, dims, shards, -0.22, 0.18) if shards else 1.0
    result = jax.random.normal(stream_key, dims, jnp.float32) * spread * level
    return jnp.minimum(jnp.maximum(result, -reach), reach).astype(kind)


def setup_inputs(seed: int = 0, part: int = 0) -> dict:
    streams_of = jax.random.split(jax.random.key(seed), 7)
    part_keys = jax.random.split(jax.random.fold_in(streams_of[6], part), 7)
    log_noise = centred(part_keys[0], (NZ, NX, NY), 0.5, 3.0, ((0, 2), (1, 4), (2, 2)), jnp.float32)
    facies = place_ends(jax.random.randint(part_keys[1], (NZ, NX, NY), 0, NFAC), jax.random.fold_in(part_keys[1], 1), 0, NFAC - 1).astype(jnp.int32)
    facies_table = jnp.clip(jax.random.uniform(streams_of[2], (3, NFAC), jnp.float32, -1.0, 1.0), -1.0, 1.0)
    pressure_old = centred(part_keys[3], (NCZ, NCX, NCY), 1.0, 6.0, ((0, 2), (1, 4), (2, 2)), jnp.float32)
    accumulation = jnp.clip(jnp.exp(math.log(1000.0) - 2.3025851 * jax.random.uniform(part_keys[4], (NCZ, NCX, NCY), jnp.float32) ** block_scale(part_keys[4], (NCZ, NCX, NCY), ((0, 2), (1, 4), (2, 2)), -0.2, 0.2)), 100.0, 1000.0)
    source = centred(part_keys[5], (NCZ, NCX, NCY), 100.0, 600.0, ((0, 2), (1, 4), (2, 2)), jnp.float32)
    return {"log_noise": log_noise, "facies": facies, "facies_table": facies_table, "pressure_old": pressure_old, "accumulation": accumulation, "source": source}


BOUND_MID = 1.0
BOUND_HALF = 0.9


def raise_flat(values, offset):
    zeros_block = jnp.zeros(values.shape[:-1] + (offset,), values.dtype)
    return jnp.concatenate([values[..., offset:], zeros_block], axis=-1)


def lower_flat(values, offset):
    zeros_block = jnp.zeros(values.shape[:-1] + (offset,), values.dtype)
    return jnp.concatenate([zeros_block, values[..., :-offset]], axis=-1)


def raise_depth(values):
    zeros_block = jnp.zeros(values.shape[:1] + (1,) + values.shape[2:], values.dtype)
    return jnp.concatenate([values[:, 1:], zeros_block], axis=1)


def lower_depth(values):
    zeros_block = jnp.zeros(values.shape[:1] + (1,) + values.shape[2:], values.dtype)
    return jnp.concatenate([zeros_block, values[:, :-1]], axis=1)


def log_fields(log_noise, facies, facies_table):
    base_log = log_noise
    extra_y = jnp.zeros_like(log_noise)
    extra_z = jnp.zeros_like(log_noise)
    for code_value in range(NFAC):
        matched = facies == code_value
        base_log = base_log + jnp.where(matched, facies_table[0, code_value], jnp.float32(0.0))
        extra_y = extra_y + jnp.where(matched, facies_table[1, code_value], jnp.float32(0.0))
        extra_z = extra_z + jnp.where(matched, facies_table[2, code_value], jnp.float32(0.0))
    return base_log, base_log + extra_y, base_log + extra_z


def upscale(perm_logs, inside):
    span_z = CCZ + 2 * RIM
    span_x = CCX + 2 * RIM
    span_y = CCY + 2 * RIM
    depth_pos = lax.broadcasted_iota(jnp.int32, (1, span_z, 1), 1)
    flat_pos = lax.broadcasted_iota(jnp.int32, (1, 1, span_x * span_y), 2)
    column_pos = flat_pos // span_y
    row_pos = flat_pos % span_y
    perm_x = jnp.exp(perm_logs[0])
    perm_y = jnp.exp(perm_logs[1])
    perm_z = jnp.exp(perm_logs[2])

    def links(perm, other_perm, other_inside):
        return inside * other_inside * 2.0 * perm * other_perm / (perm + other_perm)

    link_x = links(perm_x, raise_flat(perm_x, span_y), raise_flat(inside, span_y))
    link_y = links(perm_y, raise_flat(perm_y, 1), raise_flat(inside, 1)) * (row_pos < span_y - 1).astype(jnp.float32)
    link_z = links(perm_z, raise_depth(perm_z), raise_depth(inside))
    diagonal = link_x + lower_flat(link_x, span_y) + link_y + lower_flat(link_y, 1) + link_z + lower_depth(link_z)

    def apply_operator(field):
        beside = link_x * raise_flat(field, span_y) + lower_flat(link_x * field, span_y)
        beside = beside + link_y * raise_flat(field, 1) + lower_flat(link_y * field, 1)
        beside = beside + link_z * raise_depth(field) + lower_depth(link_z * field)
        return diagonal * field - beside

    interior = (depth_pos >= 1) & (depth_pos <= span_z - 2) & (column_pos >= 1) & (column_pos <= span_x - 2) & (row_pos >= 1) & (row_pos <= span_y - 2)
    unknown = inside * interior.astype(jnp.float32)
    scaling = unknown / (diagonal + 1.0 - unknown)
    core_z = (depth_pos >= RIM) & (depth_pos < RIM + CCZ)
    core_x = (column_pos >= RIM) & (column_pos < RIM + CCX)
    core_y = (row_pos >= RIM) & (row_pos < RIM + CCY)
    face_x = (((column_pos == RIM - 1) | (column_pos == RIM + CCX - 1)) & core_z & core_y).astype(jnp.float32)
    face_y = (((row_pos == RIM - 1) | (row_pos == RIM + CCY - 1)) & core_z & core_x).astype(jnp.float32)
    face_z = (((depth_pos == RIM - 1) | (depth_pos == RIM + CCZ - 1)) & core_x & core_y).astype(jnp.float32)
    ramp_x = ((span_x - 1) / 2.0 - column_pos).astype(jnp.float32)
    ramp_y = ((span_y - 1) / 2.0 - row_pos).astype(jnp.float32)
    ramp_z = ((span_z - 1) / 2.0 - depth_pos).astype(jnp.float32)
    cheb_ratio = BOUND_MID / BOUND_HALF
    results = []
    cases = ((ramp_x, link_x, face_x, CCY * CCZ, 0), (ramp_y, link_y, face_y, CCX * CCZ, 1), (ramp_z, link_z, face_z, CCX * CCY, 2))
    for ramp, link, face, area, direction in cases:
        ramp_full = jnp.broadcast_to(ramp, inside.shape)
        source_term = -unknown * apply_operator(ramp_full)
        update = scaling * source_term / BOUND_MID
        solution = update
        rho_old = 1.0 / cheb_ratio
        for sweep_index in range(SWEEPS - 1):
            residual = source_term - apply_operator(solution)
            rho_new = 1.0 / (2.0 * cheb_ratio - rho_old)
            update = rho_new * rho_old * update + (2.0 * rho_new / BOUND_HALF) * (scaling * residual)
            solution = solution + update
            rho_old = rho_new
        pressure = ramp_full + solution
        if direction == 0:
            upper = raise_flat(pressure, span_y)
        elif direction == 1:
            upper = raise_flat(pressure, 1)
        else:
            upper = raise_depth(pressure)
        flux = link * (pressure - upper) * face
        results.append(jnp.sum(flux, axis=(1, 2)) * (0.5 / area))
    return jnp.stack(results)


def coarse_sweep(perm_pad, press_pad, inside_pad, accumulation, fixed):
    centre = (slice(1, -1), slice(1, -1), slice(1, -1))
    factors = (CCY * CCZ / CCX, CCX * CCZ / CCY, CCX * CCY / CCZ)
    numer = fixed
    denom = accumulation
    for component, axis_dim in ((0, 1), (1, 2), (2, 0)):
        for offset in (-1, 1):
            window_slice = [slice(1, -1), slice(1, -1), slice(1, -1)]
            window_slice[axis_dim] = slice(1 + offset, press_pad.shape[axis_dim] - 1 + offset)
            beside = tuple(window_slice)
            link = factors[component] * 0.5 * (perm_pad[component][centre] + perm_pad[component][beside]) * inside_pad[beside]
            numer = numer + link * press_pad[beside]
            denom = denom + jnp.abs(link)
    return numer / denom


def reference(log_noise, facies, facies_table, pressure_old, accumulation, source):
    log_x, log_y, log_z = log_fields(log_noise, facies, facies_table)
    padded_logs = [jnp.pad(field, RIM) for field in (log_x, log_y, log_z)]
    inside_all = jnp.pad(jnp.ones(log_x.shape, jnp.float32), RIM)
    fields = padded_logs + [inside_all]
    count_z, count_x, count_y = NZ // CCZ, NX // CCX, NY // CCY
    span_z = CCZ + 2 * RIM
    span_x = CCX + 2 * RIM
    span_y = CCY + 2 * RIM

    def one_row(row_index):
        coarse_z = row_index // count_x
        coarse_x = row_index % count_x

        def window(field, coarse_y):
            start = (coarse_z * CCZ, coarse_x * CCX, coarse_y * CCY)
            piece = lax.dynamic_slice(field, tuple(jnp.asarray(s).astype(jnp.int32) for s in start), (span_z, span_x, span_y))
            return piece.reshape(span_z, span_x * span_y)

        columns = jnp.arange(count_y, dtype=jnp.int32)
        cut = [jax.vmap(partial_window(window, field))(columns) for field in fields]
        return upscale(tuple(cut[:3]), cut[3])

    rows = lax.map(one_row, jnp.arange(count_z * count_x, dtype=jnp.int32))
    upscaled = rows.transpose(1, 0, 2).reshape(3, count_z, count_x, count_y)
    perm_pad = jnp.pad(upscaled, ((0, 0), (1, 1), (1, 1), (1, 1)))
    inside_pad = jnp.pad(jnp.ones(pressure_old.shape, jnp.float32), 1)
    fixed = accumulation * pressure_old + source
    pressure = pressure_old
    for sweep_index in range(CSWEEPS):
        pressure = coarse_sweep(perm_pad, jnp.pad(pressure, 1), inside_pad, accumulation, fixed)
    return pressure, upscaled


def partial_window(window, field):
    def apply_window(coarse_y):
        return window(field, coarse_y)
    return apply_window
```

```python
import jax
import jax.numpy as jnp
from jax import lax
from jax.sharding import PartitionSpec as P

NFAC = 4
CCX = 32
CCY = 32
CCZ = 8
RIM = 4
SWEEPS = 3


BOUND_MID = 1.0
BOUND_HALF = 0.9


def extended(cells, sides, width):
    for axis, dim in sides:
        count = lax.axis_size(axis)
        ends = count - 1
        head = lax.slice_in_dim(cells, 0, width, axis=dim)
        tail = lax.slice_in_dim(cells, cells.shape[dim] - width, cells.shape[dim], axis=dim)
        cells = jnp.concatenate(
            [
                lax.ppermute(tail, axis, [(i, (i + 1) % count) for i in range(ends)]),
                cells,
                lax.ppermute(head, axis, [((i + 1) % count, i) for i in range(ends)]),
            ],
            axis=dim,
        )
    return cells


def raise_flat(values, offset):
    zeros_block = jnp.zeros(values.shape[:-1] + (offset,), values.dtype)
    return jnp.concatenate([values[..., offset:], zeros_block], axis=-1)


def lower_flat(values, offset):
    zeros_block = jnp.zeros(values.shape[:-1] + (offset,), values.dtype)
    return jnp.concatenate([zeros_block, values[..., :-offset]], axis=-1)


def raise_depth(values):
    zeros_block = jnp.zeros(values.shape[:1] + (1,) + values.shape[2:], values.dtype)
    return jnp.concatenate([values[:, 1:], zeros_block], axis=1)


def lower_depth(values):
    zeros_block = jnp.zeros(values.shape[:1] + (1,) + values.shape[2:], values.dtype)
    return jnp.concatenate([zeros_block, values[:, :-1]], axis=1)


def log_fields(log_noise, facies, facies_table):
    base_log = log_noise
    extra_y = jnp.zeros_like(log_noise)
    extra_z = jnp.zeros_like(log_noise)
    for code_value in range(NFAC):
        matched = facies == code_value
        base_log = base_log + jnp.where(matched, facies_table[0, code_value], jnp.float32(0.0))
        extra_y = extra_y + jnp.where(matched, facies_table[1, code_value], jnp.float32(0.0))
        extra_z = extra_z + jnp.where(matched, facies_table[2, code_value], jnp.float32(0.0))
    return (base_log, base_log + extra_y, base_log + extra_z)


def upscale(perm_logs, inside):
    span_z = CCZ + 2 * RIM
    span_x = CCX + 2 * RIM
    span_y = CCY + 2 * RIM
    depth_pos = lax.broadcasted_iota(jnp.int32, (1, span_z, 1), 1)
    flat_pos = lax.broadcasted_iota(jnp.int32, (1, 1, span_x * span_y), 2)
    column_pos = flat_pos // span_y
    row_pos = flat_pos % span_y
    perm_x = jnp.exp(perm_logs[0])
    perm_y = jnp.exp(perm_logs[1])
    perm_z = jnp.exp(perm_logs[2])

    def links(perm, other_perm, other_inside):
        return inside * other_inside * 2.0 * perm * other_perm / (perm + other_perm)

    link_x = links(perm_x, raise_flat(perm_x, span_y), raise_flat(inside, span_y))
    link_y = links(perm_y, raise_flat(perm_y, 1), raise_flat(inside, 1)) * (
        row_pos < span_y - 1
    ).astype(jnp.float32)
    link_z = links(perm_z, raise_depth(perm_z), raise_depth(inside))
    diagonal = (
        link_x
        + lower_flat(link_x, span_y)
        + link_y
        + lower_flat(link_y, 1)
        + link_z
        + lower_depth(link_z)
    )

    def apply_operator(field):
        beside = link_x * raise_flat(field, span_y) + lower_flat(link_x * field, span_y)
        beside = beside + link_y * raise_flat(field, 1) + lower_flat(link_y * field, 1)
        beside = beside + link_z * raise_depth(field) + lower_depth(link_z * field)
        return diagonal * field - beside

    interior = (
        (depth_pos >= 1)
        & (depth_pos <= span_z - 2)
        & (column_pos >= 1)
        & (column_pos <= span_x - 2)
        & (row_pos >= 1)
        & (row_pos <= span_y - 2)
    )
    unknown = inside * interior.astype(jnp.float32)
    scaling = unknown / (diagonal + 1.0 - unknown)
    core_z = (depth_pos >= RIM) & (depth_pos < RIM + CCZ)
    core_x = (column_pos >= RIM) & (column_pos < RIM + CCX)
    core_y = (row_pos >= RIM) & (row_pos < RIM + CCY)
    face_x = (((column_pos == RIM - 1) | (column_pos == RIM + CCX - 1)) & core_z & core_y).astype(
        jnp.float32
    )
    face_y = (((row_pos == RIM - 1) | (row_pos == RIM + CCY - 1)) & core_z & core_x).astype(
        jnp.float32
    )
    face_z = (((depth_pos == RIM - 1) | (depth_pos == RIM + CCZ - 1)) & core_x & core_y).astype(
        jnp.float32
    )
    ramp_x = ((span_x - 1) / 2.0 - column_pos).astype(jnp.float32)
    ramp_y = ((span_y - 1) / 2.0 - row_pos).astype(jnp.float32)
    ramp_z = ((span_z - 1) / 2.0 - depth_pos).astype(jnp.float32)
    cheb_ratio = BOUND_MID / BOUND_HALF
    results = []
    cases = (
        (ramp_x, link_x, face_x, CCY * CCZ, 0),
        (ramp_y, link_y, face_y, CCX * CCZ, 1),
        (ramp_z, link_z, face_z, CCX * CCY, 2),
    )
    for ramp, link, face, area, direction in cases:
        ramp_full = jnp.broadcast_to(ramp, inside.shape)
        source_term = -unknown * apply_operator(ramp_full)
        update = scaling * source_term / BOUND_MID
        solution = update
        rho_old = 1.0 / cheb_ratio
        for sweep_index in range(SWEEPS - 1):
            residual = source_term - apply_operator(solution)
            rho_new = 1.0 / (2.0 * cheb_ratio - rho_old)
            update = rho_new * rho_old * update + 2.0 * rho_new / BOUND_HALF * (scaling * residual)
            solution = solution + update
            rho_old = rho_new
        pressure = ramp_full + solution
        if direction == 0:
            upper = raise_flat(pressure, span_y)
        elif direction == 1:
            upper = raise_flat(pressure, 1)
        else:
            upper = raise_depth(pressure)
        flux = link * (pressure - upper) * face
        results.append(jnp.sum(flux, axis=(1, 2)) * (0.5 / area))
    return jnp.stack(results)


def coarse_sweep(perm_pad, press_pad, inside_pad, accumulation, fixed):
    centre = (slice(1, -1), slice(1, -1), slice(1, -1))
    factors = (CCY * CCZ / CCX, CCX * CCZ / CCY, CCX * CCY / CCZ)
    numer = fixed
    denom = accumulation
    for component, axis_dim in ((0, 1), (1, 2), (2, 0)):
        for offset in (-1, 1):
            window_slice = [slice(1, -1), slice(1, -1), slice(1, -1)]
            window_slice[axis_dim] = slice(1 + offset, press_pad.shape[axis_dim] - 1 + offset)
            beside = tuple(window_slice)
            link = (
                factors[component]
                * 0.5
                * (perm_pad[component][centre] + perm_pad[component][beside])
                * inside_pad[beside]
            )
            numer = numer + link * press_pad[beside]
            denom = denom + jnp.abs(link)
    return numer / denom


def span_mask(anchor, length, total, margin):
    coords = anchor - margin + jnp.arange(length + 2 * margin, dtype=jnp.int32)
    return ((coords >= 0) & (coords < total)).astype(jnp.float32)


def cut_windows(fields):
    span_z = CCZ + 2 * RIM
    span_x = CCX + 2 * RIM
    span_y = CCY + 2 * RIM
    count_z = (fields[0].shape[0] - 2 * RIM) // CCZ
    count_x = (fields[0].shape[1] - 2 * RIM) // CCX
    count_y = (fields[0].shape[2] - 2 * RIM) // CCY
    stacks = []
    for field in fields:
        pieces = []
        for block_z in range(count_z):
            for block_y in range(count_y):
                piece = field[
                    block_z * CCZ : block_z * CCZ + span_z,
                    0:span_x,
                    block_y * CCY : block_y * CCY + span_y,
                ]
                pieces.append(piece.reshape(span_z, span_x * span_y))
        stacks.append(jnp.stack(pieces))
    return (stacks, (count_z, count_x, count_y))


def faces(block, sides):
    got = []
    for axis, dim in sides:
        count = lax.axis_size(axis)
        ends = count - 1
        head = lax.slice_in_dim(block, 0, 1, axis=dim)
        tail = lax.slice_in_dim(block, block.shape[dim] - 1, block.shape[dim], axis=dim)
        lower = lax.ppermute(tail, axis, [(i, i + 1) for i in range(ends)])
        upper = lax.ppermute(head, axis, [(i + 1, i) for i in range(ends)])
        got.append((lower, upper))
    return got


def neighbour_views(block, got, dim_of):
    views = []
    for (lower, upper), dim in zip(got, dim_of):
        size = block.shape[dim]
        below = jnp.concatenate([lower, lax.slice_in_dim(block, 0, size - 1, axis=dim)], axis=dim)
        above = jnp.concatenate([lax.slice_in_dim(block, 1, size, axis=dim), upper], axis=dim)
        views.append((below, above))
    return views


def coarse_step(upscaled, views, inside_views, pressure, accumulation, fixed):
    factors = (CCY * CCZ / CCX, CCX * CCZ / CCY, CCX * CCY / CCZ)
    numer = fixed
    denom = accumulation
    for component in range(3):
        for side in range(2):
            beside = views[component][side]
            link = factors[component] * 0.5 * (upscaled[component] + beside[component]) * inside_views[component][side]
            numer = numer + link * pressure[component][side]
            denom = denom + jnp.abs(link)
    return numer / denom


def local(log_noise, facies, facies_table, pressure_old, accumulation, source):
    depth_len, rows_len, cols_len = log_noise.shape
    size_z = lax.axis_size("gz")
    size_x = lax.axis_size("gx")
    size_y = lax.axis_size("gy")
    index_z = lax.axis_index("gz")
    index_x = lax.axis_index("gx")
    index_y = lax.axis_index("gy")
    raw = jnp.stack([log_noise, facies.astype(jnp.float32)])
    raw = extended(raw, (("gx", 2), ("gy", 3), ("gz", 1)), RIM)
    log_x, log_y, log_z = log_fields(raw[0], raw[1], facies_table)
    anchor_z = index_z * depth_len
    anchor_y = index_y * cols_len
    anchor_x = index_x * rows_len
    mask_z = span_mask(anchor_z, log_x.shape[0] - 2 * RIM, depth_len * size_z, RIM)
    mask_x = span_mask(anchor_x, log_x.shape[1] - 2 * RIM, rows_len * size_x, RIM)
    mask_y = span_mask(anchor_y, log_x.shape[2] - 2 * RIM, cols_len * size_y, RIM)
    inside = mask_z[:, None, None] * mask_x[None, :, None] * mask_y[None, None, :]
    stacks, counts = cut_windows((log_x, log_y, log_z, inside))
    upscaled = upscale((stacks[0], stacks[1], stacks[2]), stacks[3]).reshape((3,) + counts)
    fixed = accumulation * pressure_old + source
    ones = jnp.ones_like(pressure_old)
    bundle = jnp.stack([upscaled[0], upscaled[1], upscaled[2], pressure_old, ones])
    sides = (("gx", 2), ("gy", 3), ("gz", 1))
    dim_of = (2, 3, 1)
    views = neighbour_views(bundle, faces(bundle, sides), dim_of)
    inside_views = [(below[4], above[4]) for below, above in views]
    perm_views = [(below[:3], above[:3]) for below, above in views]
    press_views = [(below[3], above[3]) for below, above in views]
    pressure = coarse_step(upscaled, perm_views, inside_views, press_views, accumulation, fixed)
    got = faces(pressure, (("gx", 1), ("gy", 2), ("gz", 0)))
    press_views = neighbour_views(pressure, got, (1, 2, 0))
    pressure = coarse_step(upscaled, perm_views, inside_views, press_views, accumulation, fixed)
    return (pressure, upscaled)


def solution(mesh):
    placed = (
        P(("real", "gz"), "gx", "gy"),
        P(("real", "gz"), "gx", "gy"),
        P(),
        P(("real", "gz"), "gx", "gy"),
        P(("real", "gz"), "gx", "gy"),
        P(("real", "gz"), "gx", "gy"),
    )
    return jax.shard_map(
        local,
        mesh=mesh,
        in_specs=placed,
        out_specs=(P(("real", "gz"), "gx", "gy"), P(None, ("real", "gz"), "gx", "gy")),
        check_vma=False,
    )
```

```python
import jax
import jax.numpy as jnp
from jax import lax
from jax.sharding import PartitionSpec as P
from jax.experimental import pallas as pl
from jax.experimental.pallas import tpu as pltpu

NFAC = 4
CCX = 32
CCY = 32
CCZ = 8
RIM = 4
SWEEPS = 3


BOUND_MID = 1.0
BOUND_HALF = 0.9


def extended(cells, sides, width):
    for axis, dim in sides:
        count = lax.axis_size(axis)
        ends = count - 1
        head = lax.slice_in_dim(cells, 0, width, axis=dim)
        tail = lax.slice_in_dim(cells, cells.shape[dim] - width, cells.shape[dim], axis=dim)
        cells = jnp.concatenate(
            [
                lax.ppermute(tail, axis, [(i, (i + 1) % count) for i in range(ends)]),
                cells,
                lax.ppermute(head, axis, [((i + 1) % count, i) for i in range(ends)]),
            ],
            axis=dim,
        )
    return cells


def raise_flat(values, offset):
    zeros_block = jnp.zeros(values.shape[:-1] + (offset,), values.dtype)
    return jnp.concatenate([values[..., offset:], zeros_block], axis=-1)


def lower_flat(values, offset):
    zeros_block = jnp.zeros(values.shape[:-1] + (offset,), values.dtype)
    return jnp.concatenate([zeros_block, values[..., :-offset]], axis=-1)


def raise_depth(values):
    zeros_block = jnp.zeros(values.shape[:1] + (1,) + values.shape[2:], values.dtype)
    return jnp.concatenate([values[:, 1:], zeros_block], axis=1)


def lower_depth(values):
    zeros_block = jnp.zeros(values.shape[:1] + (1,) + values.shape[2:], values.dtype)
    return jnp.concatenate([zeros_block, values[:, :-1]], axis=1)


def log_fields(log_noise, facies, facies_table):
    base_log = log_noise
    extra_y = jnp.zeros_like(log_noise)
    extra_z = jnp.zeros_like(log_noise)
    for code_value in range(NFAC):
        matched = facies == code_value
        base_log = base_log + jnp.where(matched, facies_table[0, code_value], jnp.float32(0.0))
        extra_y = extra_y + jnp.where(matched, facies_table[1, code_value], jnp.float32(0.0))
        extra_z = extra_z + jnp.where(matched, facies_table[2, code_value], jnp.float32(0.0))
    return (base_log, base_log + extra_y, base_log + extra_z)


def upscale(perm_logs, inside):
    span_z = CCZ + 2 * RIM
    span_x = CCX + 2 * RIM
    span_y = CCY + 2 * RIM
    depth_pos = lax.broadcasted_iota(jnp.int32, (1, span_z, 1), 1)
    flat_pos = lax.broadcasted_iota(jnp.int32, (1, 1, span_x * span_y), 2)
    column_pos = flat_pos // span_y
    row_pos = flat_pos % span_y
    perm_x = jnp.exp(perm_logs[0])
    perm_y = jnp.exp(perm_logs[1])
    perm_z = jnp.exp(perm_logs[2])

    def links(perm, other_perm, other_inside):
        return inside * other_inside * 2.0 * perm * other_perm / (perm + other_perm)

    link_x = links(perm_x, raise_flat(perm_x, span_y), raise_flat(inside, span_y))
    link_y = links(perm_y, raise_flat(perm_y, 1), raise_flat(inside, 1)) * (
        row_pos < span_y - 1
    ).astype(jnp.float32)
    link_z = links(perm_z, raise_depth(perm_z), raise_depth(inside))
    diagonal = (
        link_x
        + lower_flat(link_x, span_y)
        + link_y
        + lower_flat(link_y, 1)
        + link_z
        + lower_depth(link_z)
    )

    def apply_operator(field):
        beside = link_x * raise_flat(field, span_y) + lower_flat(link_x * field, span_y)
        beside = beside + link_y * raise_flat(field, 1) + lower_flat(link_y * field, 1)
        beside = beside + link_z * raise_depth(field) + lower_depth(link_z * field)
        return diagonal * field - beside

    interior = (
        (depth_pos >= 1)
        & (depth_pos <= span_z - 2)
        & (column_pos >= 1)
        & (column_pos <= span_x - 2)
        & (row_pos >= 1)
        & (row_pos <= span_y - 2)
    )
    unknown = inside * interior.astype(jnp.float32)
    scaling = unknown / (diagonal + 1.0 - unknown)
    core_z = (depth_pos >= RIM) & (depth_pos < RIM + CCZ)
    core_x = (column_pos >= RIM) & (column_pos < RIM + CCX)
    core_y = (row_pos >= RIM) & (row_pos < RIM + CCY)
    face_x = (((column_pos == RIM - 1) | (column_pos == RIM + CCX - 1)) & core_z & core_y).astype(
        jnp.float32
    )
    face_y = (((row_pos == RIM - 1) | (row_pos == RIM + CCY - 1)) & core_z & core_x).astype(
        jnp.float32
    )
    face_z = (((depth_pos == RIM - 1) | (depth_pos == RIM + CCZ - 1)) & core_x & core_y).astype(
        jnp.float32
    )
    ramp_x = ((span_x - 1) / 2.0 - column_pos).astype(jnp.float32)
    ramp_y = ((span_y - 1) / 2.0 - row_pos).astype(jnp.float32)
    ramp_z = ((span_z - 1) / 2.0 - depth_pos).astype(jnp.float32)
    cheb_ratio = BOUND_MID / BOUND_HALF
    results = []
    cases = (
        (ramp_x, link_x, face_x, CCY * CCZ, 0),
        (ramp_y, link_y, face_y, CCX * CCZ, 1),
        (ramp_z, link_z, face_z, CCX * CCY, 2),
    )
    for ramp, link, face, area, direction in cases:
        ramp_full = jnp.broadcast_to(ramp, inside.shape)
        source_term = -unknown * apply_operator(ramp_full)
        update = scaling * source_term / BOUND_MID
        solution = update
        rho_old = 1.0 / cheb_ratio
        for sweep_index in range(SWEEPS - 1):
            residual = source_term - apply_operator(solution)
            rho_new = 1.0 / (2.0 * cheb_ratio - rho_old)
            update = rho_new * rho_old * update + 2.0 * rho_new / BOUND_HALF * (scaling * residual)
            solution = solution + update
            rho_old = rho_new
        pressure = ramp_full + solution
        if direction == 0:
            upper = raise_flat(pressure, span_y)
        elif direction == 1:
            upper = raise_flat(pressure, 1)
        else:
            upper = raise_depth(pressure)
        flux = link * (pressure - upper) * face
        results.append(jnp.sum(flux, axis=(1, 2)) * (0.5 / area))
    return jnp.stack(results)


LANES = 128


def window_kernel(w_ref, o_ref):
    span_z = CCZ + 2 * RIM
    span_x = CCX + 2 * RIM
    span_y = CCY + 2 * RIM
    shape = (span_z, span_x, LANES)
    log_x = w_ref[0, 0]
    log_y = w_ref[0, 1]
    log_z = w_ref[0, 2]
    inside = w_ref[0, 3]
    depth_pos = lax.broadcasted_iota(jnp.int32, shape, 0)
    column_pos = lax.broadcasted_iota(jnp.int32, shape, 1)
    row_pos = lax.broadcasted_iota(jnp.int32, shape, 2)
    perm_x = jnp.exp(log_x)
    perm_y = jnp.exp(log_y)
    perm_z = jnp.exp(log_z)

    def up_x(v):
        return pltpu.roll(v, span_x - 1, 1)

    def down_x(v):
        return pltpu.roll(v, 1, 1)

    def up_y(v):
        return pltpu.roll(v, LANES - 1, 2)

    def down_y(v):
        return pltpu.roll(v, 1, 2)

    def up_z(v):
        return jnp.concatenate([v[1:], v[:1]], axis=0)

    def down_z(v):
        return jnp.concatenate([v[-1:], v[:-1]], axis=0)

    def links(perm, other_perm, other_inside, valid):
        value = inside * other_inside * 2.0 * perm * other_perm / (perm + other_perm)
        return jnp.where(valid, value, 0.0)

    link_x = links(perm_x, up_x(perm_x), up_x(inside), column_pos < span_x - 1)
    link_y = links(perm_y, up_y(perm_y), up_y(inside), row_pos < span_y - 1)
    link_z = links(perm_z, up_z(perm_z), up_z(inside), depth_pos < span_z - 1)
    diagonal = link_x + down_x(link_x) + link_y + down_y(link_y) + link_z + down_z(link_z)

    def apply_operator(field):
        beside = link_x * up_x(field) + down_x(link_x * field)
        beside = beside + link_y * up_y(field) + down_y(link_y * field)
        beside = beside + link_z * up_z(field) + down_z(link_z * field)
        return diagonal * field - beside

    interior = (
        (depth_pos >= 1)
        & (depth_pos <= span_z - 2)
        & (column_pos >= 1)
        & (column_pos <= span_x - 2)
        & (row_pos >= 1)
        & (row_pos <= span_y - 2)
    )
    unknown = jnp.where(interior, inside, 0.0)
    scaling = unknown / (diagonal + 1.0 - unknown)
    core_z = (depth_pos >= RIM) & (depth_pos < RIM + CCZ)
    core_x = (column_pos >= RIM) & (column_pos < RIM + CCX)
    core_y = (row_pos >= RIM) & (row_pos < RIM + CCY)
    face_x = ((column_pos == RIM - 1) | (column_pos == RIM + CCX - 1)) & core_z & core_y
    face_y = ((row_pos == RIM - 1) | (row_pos == RIM + CCY - 1)) & core_z & core_x
    face_z = ((depth_pos == RIM - 1) | (depth_pos == RIM + CCZ - 1)) & core_x & core_y
    ramp_x = ((span_x - 1) / 2.0 - column_pos).astype(jnp.float32)
    ramp_y = ((span_y - 1) / 2.0 - row_pos).astype(jnp.float32)
    ramp_z = ((span_z - 1) / 2.0 - depth_pos).astype(jnp.float32)
    cheb_ratio = BOUND_MID / BOUND_HALF
    cases = (
        (ramp_x, link_x, face_x, CCY * CCZ, up_x),
        (ramp_y, link_y, face_y, CCX * CCZ, up_y),
        (ramp_z, link_z, face_z, CCX * CCY, up_z),
    )
    rows = []
    for ramp, link, face, area, upper_of in cases:
        source_term = -unknown * apply_operator(ramp)
        update = scaling * source_term / BOUND_MID
        solution = update
        rho_old = 1.0 / cheb_ratio
        for sweep_index in range(SWEEPS - 1):
            residual = source_term - apply_operator(solution)
            rho_new = 1.0 / (2.0 * cheb_ratio - rho_old)
            update = rho_new * rho_old * update + 2.0 * rho_new / BOUND_HALF * (scaling * residual)
            solution = solution + update
            rho_old = rho_new
        pressure = ramp + solution
        flux = jnp.where(face, link * (pressure - upper_of(pressure)), 0.0)
        total = jnp.sum(flux, axis=0)
        total = jnp.sum(total, axis=0, keepdims=True)
        total = jnp.sum(total, axis=1, keepdims=True)
        rows.append(jnp.broadcast_to(total * (0.5 / area), (1, LANES)))
    rows.append(jnp.zeros((8 - len(rows), LANES), jnp.float32))
    o_ref[0] = jnp.concatenate(rows, axis=0)


def upscale_windows(fields):
    span_z = CCZ + 2 * RIM
    span_x = CCX + 2 * RIM
    span_y = CCY + 2 * RIM
    count_z = (fields.shape[1] - 2 * RIM) // CCZ
    count_x = (fields.shape[2] - 2 * RIM) // CCX
    count_y = (fields.shape[3] - 2 * RIM) // CCY
    pieces = []
    for block_z in range(count_z):
        for block_x in range(count_x):
            for block_y in range(count_y):
                piece = fields[
                    :,
                    block_z * CCZ : block_z * CCZ + span_z,
                    block_x * CCX : block_x * CCX + span_x,
                    block_y * CCY : block_y * CCY + span_y,
                ]
                pieces.append(piece)
    windows = jnp.stack(pieces)
    windows = jnp.pad(windows, ((0, 0),) * 4 + ((0, LANES - span_y),))
    count = windows.shape[0]
    sums = pl.pallas_call(
        window_kernel,
        grid=(count,),
        in_specs=[pl.BlockSpec((1, 4, span_z, span_x, LANES), lambda i: (i, 0, 0, 0, 0))],
        out_specs=pl.BlockSpec((1, 8, LANES), lambda i: (i, 0, 0)),
        out_shape=jax.ShapeDtypeStruct((count, 8, LANES), jnp.float32),
    )(windows)
    return sums[:, :3, 0].T.reshape((3, count_z, count_x, count_y))


def coarse_sweep(perm_pad, press_pad, inside_pad, accumulation, fixed):
    centre = (slice(1, -1), slice(1, -1), slice(1, -1))
    factors = (CCY * CCZ / CCX, CCX * CCZ / CCY, CCX * CCY / CCZ)
    numer = fixed
    denom = accumulation
    for component, axis_dim in ((0, 1), (1, 2), (2, 0)):
        for offset in (-1, 1):
            window_slice = [slice(1, -1), slice(1, -1), slice(1, -1)]
            window_slice[axis_dim] = slice(1 + offset, press_pad.shape[axis_dim] - 1 + offset)
            beside = tuple(window_slice)
            link = (
                factors[component]
                * 0.5
                * (perm_pad[component][centre] + perm_pad[component][beside])
                * inside_pad[beside]
            )
            numer = numer + link * press_pad[beside]
            denom = denom + jnp.abs(link)
    return numer / denom


def span_mask(anchor, length, total, margin):
    coords = anchor - margin + jnp.arange(length + 2 * margin, dtype=jnp.int32)
    return ((coords >= 0) & (coords < total)).astype(jnp.float32)


def cut_windows(fields):
    span_z = CCZ + 2 * RIM
    span_x = CCX + 2 * RIM
    span_y = CCY + 2 * RIM
    count_z = (fields[0].shape[0] - 2 * RIM) // CCZ
    count_x = (fields[0].shape[1] - 2 * RIM) // CCX
    count_y = (fields[0].shape[2] - 2 * RIM) // CCY
    stacks = []
    for field in fields:
        pieces = []
        for block_z in range(count_z):
            for block_y in range(count_y):
                piece = field[
                    block_z * CCZ : block_z * CCZ + span_z,
                    0:span_x,
                    block_y * CCY : block_y * CCY + span_y,
                ]
                pieces.append(piece.reshape(span_z, span_x * span_y))
        stacks.append(jnp.stack(pieces))
    return (stacks, (count_z, count_x, count_y))


def faces(block, sides):
    got = []
    for axis, dim in sides:
        count = lax.axis_size(axis)
        ends = count - 1
        head = lax.slice_in_dim(block, 0, 1, axis=dim)
        tail = lax.slice_in_dim(block, block.shape[dim] - 1, block.shape[dim], axis=dim)
        lower = lax.ppermute(tail, axis, [(i, i + 1) for i in range(ends)])
        upper = lax.ppermute(head, axis, [(i + 1, i) for i in range(ends)])
        got.append((lower, upper))
    return got


def neighbour_views(block, got, dim_of):
    views = []
    for (lower, upper), dim in zip(got, dim_of):
        size = block.shape[dim]
        below = jnp.concatenate([lower, lax.slice_in_dim(block, 0, size - 1, axis=dim)], axis=dim)
        above = jnp.concatenate([lax.slice_in_dim(block, 1, size, axis=dim), upper], axis=dim)
        views.append((below, above))
    return views


def coarse_step(upscaled, views, inside_views, pressure, accumulation, fixed):
    factors = (CCY * CCZ / CCX, CCX * CCZ / CCY, CCX * CCY / CCZ)
    numer = fixed
    denom = accumulation
    for component in range(3):
        for side in range(2):
            beside = views[component][side]
            link = factors[component] * 0.5 * (upscaled[component] + beside[component]) * inside_views[component][side]
            numer = numer + link * pressure[component][side]
            denom = denom + jnp.abs(link)
    return numer / denom


def local(log_noise, facies, facies_table, pressure_old, accumulation, source):
    depth_len, rows_len, cols_len = log_noise.shape
    size_z = lax.axis_size("gz")
    size_x = lax.axis_size("gx")
    size_y = lax.axis_size("gy")
    index_z = lax.axis_index("gz")
    index_x = lax.axis_index("gx")
    index_y = lax.axis_index("gy")
    raw = jnp.stack([log_noise, facies.astype(jnp.float32)])
    raw = extended(raw, (("gx", 2), ("gy", 3), ("gz", 1)), RIM)
    log_x, log_y, log_z = log_fields(raw[0], raw[1], facies_table)
    anchor_z = index_z * depth_len
    anchor_y = index_y * cols_len
    anchor_x = index_x * rows_len
    mask_z = span_mask(anchor_z, log_x.shape[0] - 2 * RIM, depth_len * size_z, RIM)
    mask_x = span_mask(anchor_x, log_x.shape[1] - 2 * RIM, rows_len * size_x, RIM)
    mask_y = span_mask(anchor_y, log_x.shape[2] - 2 * RIM, cols_len * size_y, RIM)
    inside = mask_z[:, None, None] * mask_x[None, :, None] * mask_y[None, None, :]
    upscaled = upscale_windows(jnp.stack([log_x, log_y, log_z, inside]))
    fixed = accumulation * pressure_old + source
    ones = jnp.ones_like(pressure_old)
    bundle = jnp.stack([upscaled[0], upscaled[1], upscaled[2], pressure_old, ones])
    sides = (("gx", 2), ("gy", 3), ("gz", 1))
    dim_of = (2, 3, 1)
    views = neighbour_views(bundle, faces(bundle, sides), dim_of)
    inside_views = [(below[4], above[4]) for below, above in views]
    perm_views = [(below[:3], above[:3]) for below, above in views]
    press_views = [(below[3], above[3]) for below, above in views]
    pressure = coarse_step(upscaled, perm_views, inside_views, press_views, accumulation, fixed)
    got = faces(pressure, (("gx", 1), ("gy", 2), ("gz", 0)))
    press_views = neighbour_views(pressure, got, (1, 2, 0))
    pressure = coarse_step(upscaled, perm_views, inside_views, press_views, accumulation, fixed)
    return (pressure, upscaled)


def solution(mesh):
    placed = (
        P(("real", "gz"), "gx", "gy"),
        P(("real", "gz"), "gx", "gy"),
        P(),
        P(("real", "gz"), "gx", "gy"),
        P(("real", "gz"), "gx", "gy"),
        P(("real", "gz"), "gx", "gy"),
    )
    return jax.shard_map(
        local,
        mesh=mesh,
        in_specs=placed,
        out_specs=(P(("real", "gz"), "gx", "gy"), P(None, ("real", "gz"), "gx", "gy")),
        check_vma=False,
    )
```

```python
import jax
import jax.numpy as jnp
from jax import lax
from jax.sharding import PartitionSpec as P
from jax.experimental import pallas as pl
from jax.experimental.pallas import tpu as pltpu

NFAC = 4
CCX = 32
CCY = 32
CCZ = 8
RIM = 4
SWEEPS = 3


BOUND_MID = 1.0
BOUND_HALF = 0.9


def extended(cells, sides, width):
    for axis, dim in sides:
        count = lax.axis_size(axis)
        ends = count - 1
        head = lax.slice_in_dim(cells, 0, width, axis=dim)
        tail = lax.slice_in_dim(cells, cells.shape[dim] - width, cells.shape[dim], axis=dim)
        cells = jnp.concatenate(
            [
                lax.ppermute(tail, axis, [(i, (i + 1) % count) for i in range(ends)]),
                cells,
                lax.ppermute(head, axis, [((i + 1) % count, i) for i in range(ends)]),
            ],
            axis=dim,
        )
    return cells


def raise_flat(values, offset):
    zeros_block = jnp.zeros(values.shape[:-1] + (offset,), values.dtype)
    return jnp.concatenate([values[..., offset:], zeros_block], axis=-1)


def lower_flat(values, offset):
    zeros_block = jnp.zeros(values.shape[:-1] + (offset,), values.dtype)
    return jnp.concatenate([zeros_block, values[..., :-offset]], axis=-1)


def raise_depth(values):
    zeros_block = jnp.zeros(values.shape[:1] + (1,) + values.shape[2:], values.dtype)
    return jnp.concatenate([values[:, 1:], zeros_block], axis=1)


def lower_depth(values):
    zeros_block = jnp.zeros(values.shape[:1] + (1,) + values.shape[2:], values.dtype)
    return jnp.concatenate([zeros_block, values[:, :-1]], axis=1)


def log_fields(log_noise, facies, facies_table):
    base_log = log_noise
    extra_y = jnp.zeros_like(log_noise)
    extra_z = jnp.zeros_like(log_noise)
    for code_value in range(NFAC):
        matched = facies == code_value
        base_log = base_log + jnp.where(matched, facies_table[0, code_value], jnp.float32(0.0))
        extra_y = extra_y + jnp.where(matched, facies_table[1, code_value], jnp.float32(0.0))
        extra_z = extra_z + jnp.where(matched, facies_table[2, code_value], jnp.float32(0.0))
    return (base_log, base_log + extra_y, base_log + extra_z)


def upscale(perm_logs, inside):
    span_z = CCZ + 2 * RIM
    span_x = CCX + 2 * RIM
    span_y = CCY + 2 * RIM
    depth_pos = lax.broadcasted_iota(jnp.int32, (1, span_z, 1), 1)
    flat_pos = lax.broadcasted_iota(jnp.int32, (1, 1, span_x * span_y), 2)
    column_pos = flat_pos // span_y
    row_pos = flat_pos % span_y
    perm_x = jnp.exp(perm_logs[0])
    perm_y = jnp.exp(perm_logs[1])
    perm_z = jnp.exp(perm_logs[2])

    def links(perm, other_perm, other_inside):
        return inside * other_inside * 2.0 * perm * other_perm / (perm + other_perm)

    link_x = links(perm_x, raise_flat(perm_x, span_y), raise_flat(inside, span_y))
    link_y = links(perm_y, raise_flat(perm_y, 1), raise_flat(inside, 1)) * (
        row_pos < span_y - 1
    ).astype(jnp.float32)
    link_z = links(perm_z, raise_depth(perm_z), raise_depth(inside))
    diagonal = (
        link_x
        + lower_flat(link_x, span_y)
        + link_y
        + lower_flat(link_y, 1)
        + link_z
        + lower_depth(link_z)
    )

    def apply_operator(field):
        beside = link_x * raise_flat(field, span_y) + lower_flat(link_x * field, span_y)
        beside = beside + link_y * raise_flat(field, 1) + lower_flat(link_y * field, 1)
        beside = beside + link_z * raise_depth(field) + lower_depth(link_z * field)
        return diagonal * field - beside

    interior = (
        (depth_pos >= 1)
        & (depth_pos <= span_z - 2)
        & (column_pos >= 1)
        & (column_pos <= span_x - 2)
        & (row_pos >= 1)
        & (row_pos <= span_y - 2)
    )
    unknown = inside * interior.astype(jnp.float32)
    scaling = unknown / (diagonal + 1.0 - unknown)
    core_z = (depth_pos >= RIM) & (depth_pos < RIM + CCZ)
    core_x = (column_pos >= RIM) & (column_pos < RIM + CCX)
    core_y = (row_pos >= RIM) & (row_pos < RIM + CCY)
    face_x = (((column_pos == RIM - 1) | (column_pos == RIM + CCX - 1)) & core_z & core_y).astype(
        jnp.float32
    )
    face_y = (((row_pos == RIM - 1) | (row_pos == RIM + CCY - 1)) & core_z & core_x).astype(
        jnp.float32
    )
    face_z = (((depth_pos == RIM - 1) | (depth_pos == RIM + CCZ - 1)) & core_x & core_y).astype(
        jnp.float32
    )
    ramp_x = ((span_x - 1) / 2.0 - column_pos).astype(jnp.float32)
    ramp_y = ((span_y - 1) / 2.0 - row_pos).astype(jnp.float32)
    ramp_z = ((span_z - 1) / 2.0 - depth_pos).astype(jnp.float32)
    cheb_ratio = BOUND_MID / BOUND_HALF
    results = []
    cases = (
        (ramp_x, link_x, face_x, CCY * CCZ, 0),
        (ramp_y, link_y, face_y, CCX * CCZ, 1),
        (ramp_z, link_z, face_z, CCX * CCY, 2),
    )
    for ramp, link, face, area, direction in cases:
        ramp_full = jnp.broadcast_to(ramp, inside.shape)
        source_term = -unknown * apply_operator(ramp_full)
        update = scaling * source_term / BOUND_MID
        solution = update
        rho_old = 1.0 / cheb_ratio
        for sweep_index in range(SWEEPS - 1):
            residual = source_term - apply_operator(solution)
            rho_new = 1.0 / (2.0 * cheb_ratio - rho_old)
            update = rho_new * rho_old * update + 2.0 * rho_new / BOUND_HALF * (scaling * residual)
            solution = solution + update
            rho_old = rho_new
        pressure = ramp_full + solution
        if direction == 0:
            upper = raise_flat(pressure, span_y)
        elif direction == 1:
            upper = raise_flat(pressure, 1)
        else:
            upper = raise_depth(pressure)
        flux = link * (pressure - upper) * face
        results.append(jnp.sum(flux, axis=(1, 2)) * (0.5 / area))
    return jnp.stack(results)


LANES = 128


def window_kernel(w_ref, o_ref):
    span_z = CCZ + 2 * RIM
    span_x = CCX + 2 * RIM
    span_y = CCY + 2 * RIM
    shape = (span_z, span_x, LANES)
    log_x = w_ref[0, 0]
    log_y = w_ref[0, 1]
    log_z = w_ref[0, 2]
    inside = w_ref[0, 3]
    depth_pos = lax.broadcasted_iota(jnp.int32, shape, 0)
    column_pos = lax.broadcasted_iota(jnp.int32, shape, 1)
    row_pos = lax.broadcasted_iota(jnp.int32, shape, 2)
    perm_x = jnp.exp(log_x)
    perm_y = jnp.exp(log_y)
    perm_z = jnp.exp(log_z)

    def up_x(v):
        return pltpu.roll(v, span_x - 1, 1)

    def down_x(v):
        return pltpu.roll(v, 1, 1)

    def up_y(v):
        return pltpu.roll(v, LANES - 1, 2)

    def down_y(v):
        return pltpu.roll(v, 1, 2)

    def up_z(v):
        return jnp.concatenate([v[1:], v[:1]], axis=0)

    def down_z(v):
        return jnp.concatenate([v[-1:], v[:-1]], axis=0)

    def links(perm, other_perm, other_inside, valid):
        value = inside * other_inside * 2.0 * perm * other_perm / (perm + other_perm)
        return jnp.where(valid, value, 0.0)

    link_x = links(perm_x, up_x(perm_x), up_x(inside), column_pos < span_x - 1)
    link_y = links(perm_y, up_y(perm_y), up_y(inside), row_pos < span_y - 1)
    link_z = links(perm_z, up_z(perm_z), up_z(inside), depth_pos < span_z - 1)
    diagonal = link_x + down_x(link_x) + link_y + down_y(link_y) + link_z + down_z(link_z)

    def apply_operator(field):
        beside = link_x * up_x(field) + down_x(link_x * field)
        beside = beside + link_y * up_y(field) + down_y(link_y * field)
        beside = beside + link_z * up_z(field) + down_z(link_z * field)
        return diagonal * field - beside

    interior = (
        (depth_pos >= 1)
        & (depth_pos <= span_z - 2)
        & (column_pos >= 1)
        & (column_pos <= span_x - 2)
        & (row_pos >= 1)
        & (row_pos <= span_y - 2)
    )
    unknown = jnp.where(interior, inside, 0.0)
    scaling = unknown / (diagonal + 1.0 - unknown)
    core_z = (depth_pos >= RIM) & (depth_pos < RIM + CCZ)
    core_x = (column_pos >= RIM) & (column_pos < RIM + CCX)
    core_y = (row_pos >= RIM) & (row_pos < RIM + CCY)
    face_x = ((column_pos == RIM - 1) | (column_pos == RIM + CCX - 1)) & core_z & core_y
    face_y = ((row_pos == RIM - 1) | (row_pos == RIM + CCY - 1)) & core_z & core_x
    face_z = ((depth_pos == RIM - 1) | (depth_pos == RIM + CCZ - 1)) & core_x & core_y
    ramp_x = ((span_x - 1) / 2.0 - column_pos).astype(jnp.float32)
    ramp_y = ((span_y - 1) / 2.0 - row_pos).astype(jnp.float32)
    ramp_z = ((span_z - 1) / 2.0 - depth_pos).astype(jnp.float32)
    cheb_ratio = BOUND_MID / BOUND_HALF
    cases = (
        (ramp_x, link_x, face_x, CCY * CCZ, up_x),
        (ramp_y, link_y, face_y, CCX * CCZ, up_y),
        (ramp_z, link_z, face_z, CCX * CCY, up_z),
    )
    rows = []
    for ramp, link, face, area, upper_of in cases:
        source_term = -unknown * apply_operator(ramp)
        update = scaling * source_term / BOUND_MID
        solution = update
        rho_old = 1.0 / cheb_ratio
        for sweep_index in range(SWEEPS - 1):
            residual = source_term - apply_operator(solution)
            rho_new = 1.0 / (2.0 * cheb_ratio - rho_old)
            update = rho_new * rho_old * update + 2.0 * rho_new / BOUND_HALF * (scaling * residual)
            solution = solution + update
            rho_old = rho_new
        pressure = ramp + solution
        flux = jnp.where(face, link * (pressure - upper_of(pressure)), 0.0)
        total = jnp.sum(flux, axis=0)
        total = jnp.sum(total, axis=0, keepdims=True)
        total = jnp.sum(total, axis=1, keepdims=True)
        rows.append(jnp.broadcast_to(total * (0.5 / area), (1, LANES)))
    rows.append(jnp.zeros((8 - len(rows), LANES), jnp.float32))
    o_ref[0] = jnp.concatenate(rows, axis=0)


def upscale_windows(fields):
    span_z = CCZ + 2 * RIM
    span_x = CCX + 2 * RIM
    span_y = CCY + 2 * RIM
    count_z = (fields.shape[1] - 2 * RIM) // CCZ
    count_x = (fields.shape[2] - 2 * RIM) // CCX
    count_y = (fields.shape[3] - 2 * RIM) // CCY
    pieces = []
    for block_z in range(count_z):
        for block_x in range(count_x):
            for block_y in range(count_y):
                piece = fields[
                    :,
                    block_z * CCZ : block_z * CCZ + span_z,
                    block_x * CCX : block_x * CCX + span_x,
                    block_y * CCY : block_y * CCY + span_y,
                ]
                pieces.append(piece)
    windows = jnp.stack(pieces)
    windows = jnp.pad(windows, ((0, 0),) * 4 + ((0, LANES - span_y),))
    count = windows.shape[0]
    sums = pl.pallas_call(
        window_kernel,
        grid=(count,),
        in_specs=[pl.BlockSpec((1, 4, span_z, span_x, LANES), lambda i: (i, 0, 0, 0, 0))],
        out_specs=pl.BlockSpec((1, 8, LANES), lambda i: (i, 0, 0)),
        out_shape=jax.ShapeDtypeStruct((count, 8, LANES), jnp.float32),
    )(windows)
    return sums[:, :3, 0].T.reshape((3, count_z, count_x, count_y))


def coarse_sweep(perm_pad, press_pad, inside_pad, accumulation, fixed):
    centre = (slice(1, -1), slice(1, -1), slice(1, -1))
    factors = (CCY * CCZ / CCX, CCX * CCZ / CCY, CCX * CCY / CCZ)
    numer = fixed
    denom = accumulation
    for component, axis_dim in ((0, 1), (1, 2), (2, 0)):
        for offset in (-1, 1):
            window_slice = [slice(1, -1), slice(1, -1), slice(1, -1)]
            window_slice[axis_dim] = slice(1 + offset, press_pad.shape[axis_dim] - 1 + offset)
            beside = tuple(window_slice)
            link = (
                factors[component]
                * 0.5
                * (perm_pad[component][centre] + perm_pad[component][beside])
                * inside_pad[beside]
            )
            numer = numer + link * press_pad[beside]
            denom = denom + jnp.abs(link)
    return numer / denom


def span_mask(anchor, length, total, margin):
    coords = anchor - margin + jnp.arange(length + 2 * margin, dtype=jnp.int32)
    return ((coords >= 0) & (coords < total)).astype(jnp.float32)


def cut_windows(fields):
    span_z = CCZ + 2 * RIM
    span_x = CCX + 2 * RIM
    span_y = CCY + 2 * RIM
    count_z = (fields[0].shape[0] - 2 * RIM) // CCZ
    count_x = (fields[0].shape[1] - 2 * RIM) // CCX
    count_y = (fields[0].shape[2] - 2 * RIM) // CCY
    stacks = []
    for field in fields:
        pieces = []
        for block_z in range(count_z):
            for block_y in range(count_y):
                piece = field[
                    block_z * CCZ : block_z * CCZ + span_z,
                    0:span_x,
                    block_y * CCY : block_y * CCY + span_y,
                ]
                pieces.append(piece.reshape(span_z, span_x * span_y))
        stacks.append(jnp.stack(pieces))
    return (stacks, (count_z, count_x, count_y))


def faces(block, sides):
    got = []
    for axis, dim in sides:
        count = lax.axis_size(axis)
        ends = count - 1
        head = lax.slice_in_dim(block, 0, 1, axis=dim)
        tail = lax.slice_in_dim(block, block.shape[dim] - 1, block.shape[dim], axis=dim)
        lower = lax.ppermute(tail, axis, [(i, i + 1) for i in range(ends)])
        upper = lax.ppermute(head, axis, [(i + 1, i) for i in range(ends)])
        got.append((lower, upper))
    return got


def neighbour_views(block, got, dim_of):
    views = []
    for (lower, upper), dim in zip(got, dim_of):
        size = block.shape[dim]
        below = jnp.concatenate([lower, lax.slice_in_dim(block, 0, size - 1, axis=dim)], axis=dim)
        above = jnp.concatenate([lax.slice_in_dim(block, 1, size, axis=dim), upper], axis=dim)
        views.append((below, above))
    return views


def coarse_step(upscaled, views, inside_views, pressure, accumulation, fixed):
    factors = (CCY * CCZ / CCX, CCX * CCZ / CCY, CCX * CCY / CCZ)
    numer = fixed
    denom = accumulation
    for component in range(3):
        for side in range(2):
            beside = views[component][side]
            link = factors[component] * 0.5 * (upscaled[component] + beside[component]) * inside_views[component][side]
            numer = numer + link * pressure[component][side]
            denom = denom + jnp.abs(link)
    return numer / denom


def local(log_noise, facies, facies_table, pressure_old, accumulation, source):
    depth_len, rows_len, cols_len = log_noise.shape
    size_z = lax.axis_size("gz")
    size_x = lax.axis_size("gx")
    size_y = lax.axis_size("gy")
    index_z = lax.axis_index("gz")
    index_x = lax.axis_index("gx")
    index_y = lax.axis_index("gy")
    raw = jnp.stack([log_noise, facies.astype(jnp.float32)])
    raw = extended(raw, (("gx", 2), ("gy", 3), ("gz", 1)), RIM)
    log_x, log_y, log_z = log_fields(raw[0], raw[1], facies_table)
    anchor_z = index_z * depth_len
    anchor_y = index_y * cols_len
    anchor_x = index_x * rows_len
    mask_z = span_mask(anchor_z, log_x.shape[0] - 2 * RIM, depth_len * size_z, RIM)
    mask_x = span_mask(anchor_x, log_x.shape[1] - 2 * RIM, rows_len * size_x, RIM)
    mask_y = span_mask(anchor_y, log_x.shape[2] - 2 * RIM, cols_len * size_y, RIM)
    inside = mask_z[:, None, None] * mask_x[None, :, None] * mask_y[None, None, :]
    upscaled = upscale_windows(jnp.stack([log_x, log_y, log_z, inside]))
    coarse_z, coarse_x, coarse_y = pressure_old.shape
    bundle = jnp.stack([upscaled[0], upscaled[1], upscaled[2], pressure_old, accumulation, source])
    every = lax.all_gather(bundle, ("gz", "gx", "gy"), axis=0, tiled=False)
    every = every.reshape((size_z, size_x, size_y) + bundle.shape)
    every = every.transpose(3, 0, 4, 1, 5, 2, 6).reshape(
        (bundle.shape[0], size_z * coarse_z, size_x * coarse_x, size_y * coarse_y)
    )
    perm_pad = jnp.pad(every[:3], ((0, 0), (1, 1), (1, 1), (1, 1)))
    old_all = every[3]
    acc_all = every[4]
    fixed_all = acc_all * old_all + every[5]
    inside_pad = jnp.pad(jnp.ones(old_all.shape, jnp.float32), 1)
    pressure = old_all
    for sweep_index in range(2):
        pressure = coarse_sweep(perm_pad, jnp.pad(pressure, 1), inside_pad, acc_all, fixed_all)
    pressure = lax.dynamic_slice(
        pressure, (index_z * coarse_z, index_x * coarse_x, index_y * coarse_y), (coarse_z, coarse_x, coarse_y)
    )
    return (pressure, upscaled)


def solution(mesh):
    placed = (
        P(("real", "gz"), "gx", "gy"),
        P(("real", "gz"), "gx", "gy"),
        P(),
        P(("real", "gz"), "gx", "gy"),
        P(("real", "gz"), "gx", "gy"),
        P(("real", "gz"), "gx", "gy"),
    )
    return jax.shard_map(
        local,
        mesh=mesh,
        in_specs=placed,
        out_specs=(P(("real", "gz"), "gx", "gy"), P(None, ("real", "gz"), "gx", "gy")),
        check_vma=False,
    )
```

```python
import jax
import jax.numpy as jnp
from jax import lax
from jax.sharding import PartitionSpec as P
from jax.experimental import pallas as pl
from jax.experimental.pallas import tpu as pltpu

NFAC = 4
CCX = 32
CCY = 32
CCZ = 8
RIM = 4
SWEEPS = 3


BOUND_MID = 1.0
BOUND_HALF = 0.9


def extended(cells, sides, width):
    for axis, dim in sides:
        count = lax.axis_size(axis)
        ends = count - 1
        head = lax.slice_in_dim(cells, 0, width, axis=dim)
        tail = lax.slice_in_dim(cells, cells.shape[dim] - width, cells.shape[dim], axis=dim)
        cells = jnp.concatenate(
            [
                lax.ppermute(tail, axis, [(i, (i + 1) % count) for i in range(ends)]),
                cells,
                lax.ppermute(head, axis, [((i + 1) % count, i) for i in range(ends)]),
            ],
            axis=dim,
        )
    return cells


def raise_flat(values, offset):
    zeros_block = jnp.zeros(values.shape[:-1] + (offset,), values.dtype)
    return jnp.concatenate([values[..., offset:], zeros_block], axis=-1)


def lower_flat(values, offset):
    zeros_block = jnp.zeros(values.shape[:-1] + (offset,), values.dtype)
    return jnp.concatenate([zeros_block, values[..., :-offset]], axis=-1)


def raise_depth(values):
    zeros_block = jnp.zeros(values.shape[:1] + (1,) + values.shape[2:], values.dtype)
    return jnp.concatenate([values[:, 1:], zeros_block], axis=1)


def lower_depth(values):
    zeros_block = jnp.zeros(values.shape[:1] + (1,) + values.shape[2:], values.dtype)
    return jnp.concatenate([zeros_block, values[:, :-1]], axis=1)


def log_fields(log_noise, facies, facies_table):
    base_log = log_noise
    extra_y = jnp.zeros_like(log_noise)
    extra_z = jnp.zeros_like(log_noise)
    for code_value in range(NFAC):
        matched = facies == code_value
        base_log = base_log + jnp.where(matched, facies_table[0, code_value], jnp.float32(0.0))
        extra_y = extra_y + jnp.where(matched, facies_table[1, code_value], jnp.float32(0.0))
        extra_z = extra_z + jnp.where(matched, facies_table[2, code_value], jnp.float32(0.0))
    return (base_log, base_log + extra_y, base_log + extra_z)


def upscale(perm_logs, inside):
    span_z = CCZ + 2 * RIM
    span_x = CCX + 2 * RIM
    span_y = CCY + 2 * RIM
    depth_pos = lax.broadcasted_iota(jnp.int32, (1, span_z, 1), 1)
    flat_pos = lax.broadcasted_iota(jnp.int32, (1, 1, span_x * span_y), 2)
    column_pos = flat_pos // span_y
    row_pos = flat_pos % span_y
    perm_x = jnp.exp(perm_logs[0])
    perm_y = jnp.exp(perm_logs[1])
    perm_z = jnp.exp(perm_logs[2])

    def links(perm, other_perm, other_inside):
        return inside * other_inside * 2.0 * perm * other_perm / (perm + other_perm)

    link_x = links(perm_x, raise_flat(perm_x, span_y), raise_flat(inside, span_y))
    link_y = links(perm_y, raise_flat(perm_y, 1), raise_flat(inside, 1)) * (
        row_pos < span_y - 1
    ).astype(jnp.float32)
    link_z = links(perm_z, raise_depth(perm_z), raise_depth(inside))
    diagonal = (
        link_x
        + lower_flat(link_x, span_y)
        + link_y
        + lower_flat(link_y, 1)
        + link_z
        + lower_depth(link_z)
    )

    def apply_operator(field):
        beside = link_x * raise_flat(field, span_y) + lower_flat(link_x * field, span_y)
        beside = beside + link_y * raise_flat(field, 1) + lower_flat(link_y * field, 1)
        beside = beside + link_z * raise_depth(field) + lower_depth(link_z * field)
        return diagonal * field - beside

    interior = (
        (depth_pos >= 1)
        & (depth_pos <= span_z - 2)
        & (column_pos >= 1)
        & (column_pos <= span_x - 2)
        & (row_pos >= 1)
        & (row_pos <= span_y - 2)
    )
    unknown = inside * interior.astype(jnp.float32)
    scaling = unknown / (diagonal + 1.0 - unknown)
    core_z = (depth_pos >= RIM) & (depth_pos < RIM + CCZ)
    core_x = (column_pos >= RIM) & (column_pos < RIM + CCX)
    core_y = (row_pos >= RIM) & (row_pos < RIM + CCY)
    face_x = (((column_pos == RIM - 1) | (column_pos == RIM + CCX - 1)) & core_z & core_y).astype(
        jnp.float32
    )
    face_y = (((row_pos == RIM - 1) | (row_pos == RIM + CCY - 1)) & core_z & core_x).astype(
        jnp.float32
    )
    face_z = (((depth_pos == RIM - 1) | (depth_pos == RIM + CCZ - 1)) & core_x & core_y).astype(
        jnp.float32
    )
    ramp_x = ((span_x - 1) / 2.0 - column_pos).astype(jnp.float32)
    ramp_y = ((span_y - 1) / 2.0 - row_pos).astype(jnp.float32)
    ramp_z = ((span_z - 1) / 2.0 - depth_pos).astype(jnp.float32)
    cheb_ratio = BOUND_MID / BOUND_HALF
    results = []
    cases = (
        (ramp_x, link_x, face_x, CCY * CCZ, 0),
        (ramp_y, link_y, face_y, CCX * CCZ, 1),
        (ramp_z, link_z, face_z, CCX * CCY, 2),
    )
    for ramp, link, face, area, direction in cases:
        ramp_full = jnp.broadcast_to(ramp, inside.shape)
        source_term = -unknown * apply_operator(ramp_full)
        update = scaling * source_term / BOUND_MID
        solution = update
        rho_old = 1.0 / cheb_ratio
        for sweep_index in range(SWEEPS - 1):
            residual = source_term - apply_operator(solution)
            rho_new = 1.0 / (2.0 * cheb_ratio - rho_old)
            update = rho_new * rho_old * update + 2.0 * rho_new / BOUND_HALF * (scaling * residual)
            solution = solution + update
            rho_old = rho_new
        pressure = ramp_full + solution
        if direction == 0:
            upper = raise_flat(pressure, span_y)
        elif direction == 1:
            upper = raise_flat(pressure, 1)
        else:
            upper = raise_depth(pressure)
        flux = link * (pressure - upper) * face
        results.append(jnp.sum(flux, axis=(1, 2)) * (0.5 / area))
    return jnp.stack(results)


LANES = 128


def window_kernel(w_ref, o_ref):
    span_z = CCZ + 2 * RIM
    span_x = CCX + 2 * RIM
    span_y = CCY + 2 * RIM
    shape = (span_z, span_x, LANES)
    log_x = w_ref[0, 0]
    log_y = w_ref[0, 1]
    log_z = w_ref[0, 2]
    inside = w_ref[0, 3]
    depth_pos = lax.broadcasted_iota(jnp.int32, shape, 0)
    column_pos = lax.broadcasted_iota(jnp.int32, shape, 1)
    row_pos = lax.broadcasted_iota(jnp.int32, shape, 2)
    perm_x = jnp.exp(log_x)
    perm_y = jnp.exp(log_y)
    perm_z = jnp.exp(log_z)

    def up_x(v):
        return pltpu.roll(v, span_x - 1, 1)

    def down_x(v):
        return pltpu.roll(v, 1, 1)

    def up_y(v):
        return pltpu.roll(v, LANES - 1, 2)

    def down_y(v):
        return pltpu.roll(v, 1, 2)

    def up_z(v):
        return jnp.concatenate([v[1:], v[:1]], axis=0)

    def down_z(v):
        return jnp.concatenate([v[-1:], v[:-1]], axis=0)

    def links(perm, other_perm, other_inside, valid):
        value = inside * other_inside * 2.0 * perm * other_perm / (perm + other_perm)
        return jnp.where(valid, value, 0.0)

    link_x = links(perm_x, up_x(perm_x), up_x(inside), column_pos < span_x - 1)
    link_y = links(perm_y, up_y(perm_y), up_y(inside), row_pos < span_y - 1)
    link_z = links(perm_z, up_z(perm_z), up_z(inside), depth_pos < span_z - 1)
    diagonal = link_x + down_x(link_x) + link_y + down_y(link_y) + link_z + down_z(link_z)

    def apply_operator(field):
        beside = link_x * up_x(field) + down_x(link_x * field)
        beside = beside + link_y * up_y(field) + down_y(link_y * field)
        beside = beside + link_z * up_z(field) + down_z(link_z * field)
        return diagonal * field - beside

    interior = (
        (depth_pos >= 1)
        & (depth_pos <= span_z - 2)
        & (column_pos >= 1)
        & (column_pos <= span_x - 2)
        & (row_pos >= 1)
        & (row_pos <= span_y - 2)
    )
    unknown = jnp.where(interior, inside, 0.0)
    scaling = unknown / (diagonal + 1.0 - unknown)
    core_z = (depth_pos >= RIM) & (depth_pos < RIM + CCZ)
    core_x = (column_pos >= RIM) & (column_pos < RIM + CCX)
    core_y = (row_pos >= RIM) & (row_pos < RIM + CCY)
    face_x = ((column_pos == RIM - 1) | (column_pos == RIM + CCX - 1)) & core_z & core_y
    face_y = ((row_pos == RIM - 1) | (row_pos == RIM + CCY - 1)) & core_z & core_x
    face_z = ((depth_pos == RIM - 1) | (depth_pos == RIM + CCZ - 1)) & core_x & core_y
    ramp_x = ((span_x - 1) / 2.0 - column_pos).astype(jnp.float32)
    ramp_y = ((span_y - 1) / 2.0 - row_pos).astype(jnp.float32)
    ramp_z = ((span_z - 1) / 2.0 - depth_pos).astype(jnp.float32)
    cheb_ratio = BOUND_MID / BOUND_HALF
    cases = (
        (ramp_x, link_x, face_x, CCY * CCZ, up_x),
        (ramp_y, link_y, face_y, CCX * CCZ, up_y),
        (ramp_z, link_z, face_z, CCX * CCY, up_z),
    )
    rows = []
    for ramp, link, face, area, upper_of in cases:
        source_term = -unknown * apply_operator(ramp)
        update = scaling * source_term / BOUND_MID
        solution = update
        rho_old = 1.0 / cheb_ratio
        for sweep_index in range(SWEEPS - 1):
            residual = source_term - apply_operator(solution)
            rho_new = 1.0 / (2.0 * cheb_ratio - rho_old)
            update = rho_new * rho_old * update + 2.0 * rho_new / BOUND_HALF * (scaling * residual)
            solution = solution + update
            rho_old = rho_new
        pressure = ramp + solution
        flux = jnp.where(face, link * (pressure - upper_of(pressure)), 0.0)
        total = jnp.sum(flux, axis=0)
        total = jnp.sum(total, axis=0, keepdims=True)
        total = jnp.sum(total, axis=1, keepdims=True)
        rows.append(jnp.broadcast_to(total * (0.5 / area), (1, LANES)))
    rows.append(jnp.zeros((8 - len(rows), LANES), jnp.float32))
    o_ref[0] = jnp.concatenate(rows, axis=0)


def upscale_windows(fields):
    span_z = CCZ + 2 * RIM
    span_x = CCX + 2 * RIM
    span_y = CCY + 2 * RIM
    count_z = (fields.shape[1] - 2 * RIM) // CCZ
    count_x = (fields.shape[2] - 2 * RIM) // CCX
    count_y = (fields.shape[3] - 2 * RIM) // CCY
    pieces = []
    for block_z in range(count_z):
        for block_x in range(count_x):
            for block_y in range(count_y):
                piece = fields[
                    :,
                    block_z * CCZ : block_z * CCZ + span_z,
                    block_x * CCX : block_x * CCX + span_x,
                    block_y * CCY : block_y * CCY + span_y,
                ]
                pieces.append(piece)
    windows = jnp.stack(pieces)
    windows = jnp.pad(windows, ((0, 0),) * 4 + ((0, LANES - span_y),))
    count = windows.shape[0]
    sums = pl.pallas_call(
        window_kernel,
        grid=(count,),
        in_specs=[pl.BlockSpec((1, 4, span_z, span_x, LANES), lambda i: (i, 0, 0, 0, 0))],
        out_specs=pl.BlockSpec((1, 8, LANES), lambda i: (i, 0, 0)),
        out_shape=jax.ShapeDtypeStruct((count, 8, LANES), jnp.float32),
    )(windows)
    return sums[:, :3, 0].T.reshape((3, count_z, count_x, count_y))


def coarse_sweep(perm_pad, press_pad, inside_pad, accumulation, fixed):
    centre = (slice(1, -1), slice(1, -1), slice(1, -1))
    factors = (CCY * CCZ / CCX, CCX * CCZ / CCY, CCX * CCY / CCZ)
    numer = fixed
    denom = accumulation
    for component, axis_dim in ((0, 1), (1, 2), (2, 0)):
        for offset in (-1, 1):
            window_slice = [slice(1, -1), slice(1, -1), slice(1, -1)]
            window_slice[axis_dim] = slice(1 + offset, press_pad.shape[axis_dim] - 1 + offset)
            beside = tuple(window_slice)
            link = (
                factors[component]
                * 0.5
                * (perm_pad[component][centre] + perm_pad[component][beside])
                * inside_pad[beside]
            )
            numer = numer + link * press_pad[beside]
            denom = denom + jnp.abs(link)
    return numer / denom


def span_mask(anchor, length, total, margin):
    coords = anchor - margin + jnp.arange(length + 2 * margin, dtype=jnp.int32)
    return ((coords >= 0) & (coords < total)).astype(jnp.float32)


def cut_windows(fields):
    span_z = CCZ + 2 * RIM
    span_x = CCX + 2 * RIM
    span_y = CCY + 2 * RIM
    count_z = (fields[0].shape[0] - 2 * RIM) // CCZ
    count_x = (fields[0].shape[1] - 2 * RIM) // CCX
    count_y = (fields[0].shape[2] - 2 * RIM) // CCY
    stacks = []
    for field in fields:
        pieces = []
        for block_z in range(count_z):
            for block_y in range(count_y):
                piece = field[
                    block_z * CCZ : block_z * CCZ + span_z,
                    0:span_x,
                    block_y * CCY : block_y * CCY + span_y,
                ]
                pieces.append(piece.reshape(span_z, span_x * span_y))
        stacks.append(jnp.stack(pieces))
    return (stacks, (count_z, count_x, count_y))


def faces(block, sides):
    got = []
    for axis, dim in sides:
        count = lax.axis_size(axis)
        ends = count - 1
        head = lax.slice_in_dim(block, 0, 1, axis=dim)
        tail = lax.slice_in_dim(block, block.shape[dim] - 1, block.shape[dim], axis=dim)
        lower = lax.ppermute(tail, axis, [(i, i + 1) for i in range(ends)])
        upper = lax.ppermute(head, axis, [(i + 1, i) for i in range(ends)])
        got.append((lower, upper))
    return got


def neighbour_views(block, got, dim_of):
    views = []
    for (lower, upper), dim in zip(got, dim_of):
        size = block.shape[dim]
        below = jnp.concatenate([lower, lax.slice_in_dim(block, 0, size - 1, axis=dim)], axis=dim)
        above = jnp.concatenate([lax.slice_in_dim(block, 1, size, axis=dim), upper], axis=dim)
        views.append((below, above))
    return views


def coarse_step(upscaled, views, inside_views, pressure, accumulation, fixed):
    factors = (CCY * CCZ / CCX, CCX * CCZ / CCY, CCX * CCY / CCZ)
    numer = fixed
    denom = accumulation
    for component in range(3):
        for side in range(2):
            beside = views[component][side]
            link = factors[component] * 0.5 * (upscaled[component] + beside[component]) * inside_views[component][side]
            numer = numer + link * pressure[component][side]
            denom = denom + jnp.abs(link)
    return numer / denom


def local(log_noise, facies, facies_table, pressure_old, accumulation, source):
    depth_len, rows_len, cols_len = log_noise.shape
    size_z = lax.axis_size("gz")
    size_x = lax.axis_size("gx")
    size_y = lax.axis_size("gy")
    index_z = lax.axis_index("gz")
    index_x = lax.axis_index("gx")
    index_y = lax.axis_index("gy")
    raw = jnp.stack([log_noise, facies.astype(jnp.float32)])
    raw = extended(raw, (("gx", 2), ("gy", 3), ("gz", 1)), RIM)
    log_x, log_y, log_z = log_fields(raw[0], raw[1], facies_table)
    anchor_z = index_z * depth_len
    anchor_y = index_y * cols_len
    anchor_x = index_x * rows_len
    mask_z = span_mask(anchor_z, log_x.shape[0] - 2 * RIM, depth_len * size_z, RIM)
    mask_x = span_mask(anchor_x, log_x.shape[1] - 2 * RIM, rows_len * size_x, RIM)
    mask_y = span_mask(anchor_y, log_x.shape[2] - 2 * RIM, cols_len * size_y, RIM)
    inside = mask_z[:, None, None] * mask_x[None, :, None] * mask_y[None, None, :]
    upscaled = upscale_windows(jnp.stack([log_x, log_y, log_z, inside]))
    coarse_z, coarse_x, coarse_y = pressure_old.shape
    bundle = jnp.stack([upscaled[0], upscaled[1], upscaled[2], pressure_old, accumulation, source])
    every = lax.all_gather(bundle, "gy", axis=3, tiled=True)
    every = lax.all_gather(every, "gx", axis=2, tiled=True)
    every = lax.all_gather(every, "gz", axis=1, tiled=True)
    perm_pad = jnp.pad(every[:3], ((0, 0), (1, 1), (1, 1), (1, 1)))
    old_all = every[3]
    acc_all = every[4]
    fixed_all = acc_all * old_all + every[5]
    inside_pad = jnp.pad(jnp.ones(old_all.shape, jnp.float32), 1)
    pressure = old_all
    for sweep_index in range(2):
        pressure = coarse_sweep(perm_pad, jnp.pad(pressure, 1), inside_pad, acc_all, fixed_all)
    pressure = lax.dynamic_slice(
        pressure, (index_z * coarse_z, index_x * coarse_x, index_y * coarse_y), (coarse_z, coarse_x, coarse_y)
    )
    return (pressure, upscaled)


def solution(mesh):
    placed = (
        P(("real", "gz"), "gx", "gy"),
        P(("real", "gz"), "gx", "gy"),
        P(),
        P(("real", "gz"), "gx", "gy"),
        P(("real", "gz"), "gx", "gy"),
        P(("real", "gz"), "gx", "gy"),
    )
    return jax.shard_map(
        local,
        mesh=mesh,
        in_specs=placed,
        out_specs=(P(("real", "gz"), "gx", "gy"), P(None, ("real", "gz"), "gx", "gy")),
        check_vma=False,
    )
```

```python
import jax
import jax.numpy as jnp
from jax import lax
from jax.sharding import PartitionSpec as P
from jax.experimental import pallas as pl
from jax.experimental.pallas import tpu as pltpu

NFAC = 4
CCX = 32
CCY = 32
CCZ = 8
RIM = 4
SWEEPS = 3


BOUND_MID = 1.0
BOUND_HALF = 0.9


def extended(cells, sides, width):
    for axis, dim in sides:
        count = lax.axis_size(axis)
        ends = count - 1
        head = lax.slice_in_dim(cells, 0, width, axis=dim)
        tail = lax.slice_in_dim(cells, cells.shape[dim] - width, cells.shape[dim], axis=dim)
        cells = jnp.concatenate(
            [
                lax.ppermute(tail, axis, [(i, (i + 1) % count) for i in range(ends)]),
                cells,
                lax.ppermute(head, axis, [((i + 1) % count, i) for i in range(ends)]),
            ],
            axis=dim,
        )
    return cells


def raise_flat(values, offset):
    zeros_block = jnp.zeros(values.shape[:-1] + (offset,), values.dtype)
    return jnp.concatenate([values[..., offset:], zeros_block], axis=-1)


def lower_flat(values, offset):
    zeros_block = jnp.zeros(values.shape[:-1] + (offset,), values.dtype)
    return jnp.concatenate([zeros_block, values[..., :-offset]], axis=-1)


def raise_depth(values):
    zeros_block = jnp.zeros(values.shape[:1] + (1,) + values.shape[2:], values.dtype)
    return jnp.concatenate([values[:, 1:], zeros_block], axis=1)


def lower_depth(values):
    zeros_block = jnp.zeros(values.shape[:1] + (1,) + values.shape[2:], values.dtype)
    return jnp.concatenate([zeros_block, values[:, :-1]], axis=1)


def log_fields(log_noise, facies, facies_table):
    base_log = log_noise
    extra_y = jnp.zeros_like(log_noise)
    extra_z = jnp.zeros_like(log_noise)
    for code_value in range(NFAC):
        matched = facies == code_value
        base_log = base_log + jnp.where(matched, facies_table[0, code_value], jnp.float32(0.0))
        extra_y = extra_y + jnp.where(matched, facies_table[1, code_value], jnp.float32(0.0))
        extra_z = extra_z + jnp.where(matched, facies_table[2, code_value], jnp.float32(0.0))
    return (base_log, base_log + extra_y, base_log + extra_z)


def upscale(perm_logs, inside):
    span_z = CCZ + 2 * RIM
    span_x = CCX + 2 * RIM
    span_y = CCY + 2 * RIM
    depth_pos = lax.broadcasted_iota(jnp.int32, (1, span_z, 1), 1)
    flat_pos = lax.broadcasted_iota(jnp.int32, (1, 1, span_x * span_y), 2)
    column_pos = flat_pos // span_y
    row_pos = flat_pos % span_y
    perm_x = jnp.exp(perm_logs[0])
    perm_y = jnp.exp(perm_logs[1])
    perm_z = jnp.exp(perm_logs[2])

    def links(perm, other_perm, other_inside):
        return inside * other_inside * 2.0 * perm * other_perm / (perm + other_perm)

    link_x = links(perm_x, raise_flat(perm_x, span_y), raise_flat(inside, span_y))
    link_y = links(perm_y, raise_flat(perm_y, 1), raise_flat(inside, 1)) * (
        row_pos < span_y - 1
    ).astype(jnp.float32)
    link_z = links(perm_z, raise_depth(perm_z), raise_depth(inside))
    diagonal = (
        link_x
        + lower_flat(link_x, span_y)
        + link_y
        + lower_flat(link_y, 1)
        + link_z
        + lower_depth(link_z)
    )

    def apply_operator(field):
        beside = link_x * raise_flat(field, span_y) + lower_flat(link_x * field, span_y)
        beside = beside + link_y * raise_flat(field, 1) + lower_flat(link_y * field, 1)
        beside = beside + link_z * raise_depth(field) + lower_depth(link_z * field)
        return diagonal * field - beside

    interior = (
        (depth_pos >= 1)
        & (depth_pos <= span_z - 2)
        & (column_pos >= 1)
        & (column_pos <= span_x - 2)
        & (row_pos >= 1)
        & (row_pos <= span_y - 2)
    )
    unknown = inside * interior.astype(jnp.float32)
    scaling = unknown / (diagonal + 1.0 - unknown)
    core_z = (depth_pos >= RIM) & (depth_pos < RIM + CCZ)
    core_x = (column_pos >= RIM) & (column_pos < RIM + CCX)
    core_y = (row_pos >= RIM) & (row_pos < RIM + CCY)
    face_x = (((column_pos == RIM - 1) | (column_pos == RIM + CCX - 1)) & core_z & core_y).astype(
        jnp.float32
    )
    face_y = (((row_pos == RIM - 1) | (row_pos == RIM + CCY - 1)) & core_z & core_x).astype(
        jnp.float32
    )
    face_z = (((depth_pos == RIM - 1) | (depth_pos == RIM + CCZ - 1)) & core_x & core_y).astype(
        jnp.float32
    )
    ramp_x = ((span_x - 1) / 2.0 - column_pos).astype(jnp.float32)
    ramp_y = ((span_y - 1) / 2.0 - row_pos).astype(jnp.float32)
    ramp_z = ((span_z - 1) / 2.0 - depth_pos).astype(jnp.float32)
    cheb_ratio = BOUND_MID / BOUND_HALF
    results = []
    cases = (
        (ramp_x, link_x, face_x, CCY * CCZ, 0),
        (ramp_y, link_y, face_y, CCX * CCZ, 1),
        (ramp_z, link_z, face_z, CCX * CCY, 2),
    )
    for ramp, link, face, area, direction in cases:
        ramp_full = jnp.broadcast_to(ramp, inside.shape)
        source_term = -unknown * apply_operator(ramp_full)
        update = scaling * source_term / BOUND_MID
        solution = update
        rho_old = 1.0 / cheb_ratio
        for sweep_index in range(SWEEPS - 1):
            residual = source_term - apply_operator(solution)
            rho_new = 1.0 / (2.0 * cheb_ratio - rho_old)
            update = rho_new * rho_old * update + 2.0 * rho_new / BOUND_HALF * (scaling * residual)
            solution = solution + update
            rho_old = rho_new
        pressure = ramp_full + solution
        if direction == 0:
            upper = raise_flat(pressure, span_y)
        elif direction == 1:
            upper = raise_flat(pressure, 1)
        else:
            upper = raise_depth(pressure)
        flux = link * (pressure - upper) * face
        results.append(jnp.sum(flux, axis=(1, 2)) * (0.5 / area))
    return jnp.stack(results)


LANES = 128


def window_kernel(table_ref, raw_ref, o_ref):
    span_z = CCZ + 2 * RIM
    span_x = CCX + 2 * RIM
    span_y = CCY + 2 * RIM
    shape = (span_z, span_x, LANES)
    block_z = pl.program_id(0)
    block_x = pl.program_id(1)
    block_y = pl.program_id(2)
    wide = raw_ref.shape[-1]
    shift = (wide - block_y * CCY) % wide

    def cut(field):
        slab = raw_ref[field, pl.ds(block_z * CCZ, span_z), pl.ds(block_x * CCX, span_x), :]
        return pltpu.roll(slab, shift, 2)[:, :, :LANES]

    noise = cut(0)
    codes = cut(1)
    depth_pos = lax.broadcasted_iota(jnp.int32, shape, 0)
    column_pos = lax.broadcasted_iota(jnp.int32, shape, 1)
    row_pos = lax.broadcasted_iota(jnp.int32, shape, 2)
    inside = jnp.where(row_pos < span_y, cut(2), 0.0)

    def lookup(row):
        value = jnp.zeros(shape, jnp.float32)
        for code_value in range(NFAC):
            value = jnp.where(codes == code_value, table_ref[row, code_value], value)
        return value

    log_x = noise + lookup(0)
    log_y = log_x + lookup(1)
    log_z = log_x + lookup(2)
    perm_x = jnp.exp(log_x)
    perm_y = jnp.exp(log_y)
    perm_z = jnp.exp(log_z)

    def up_x(v):
        return pltpu.roll(v, span_x - 1, 1)

    def down_x(v):
        return pltpu.roll(v, 1, 1)

    def up_y(v):
        return pltpu.roll(v, LANES - 1, 2)

    def down_y(v):
        return pltpu.roll(v, 1, 2)

    def up_z(v):
        return jnp.concatenate([v[1:], v[:1]], axis=0)

    def down_z(v):
        return jnp.concatenate([v[-1:], v[:-1]], axis=0)

    def links(perm, other_perm, other_inside, valid):
        value = inside * other_inside * 2.0 * perm * other_perm / (perm + other_perm)
        return jnp.where(valid, value, 0.0)

    link_x = links(perm_x, up_x(perm_x), up_x(inside), column_pos < span_x - 1)
    link_y = links(perm_y, up_y(perm_y), up_y(inside), row_pos < span_y - 1)
    link_z = links(perm_z, up_z(perm_z), up_z(inside), depth_pos < span_z - 1)
    diagonal = link_x + down_x(link_x) + link_y + down_y(link_y) + link_z + down_z(link_z)

    def apply_operator(field):
        beside = link_x * up_x(field) + down_x(link_x * field)
        beside = beside + link_y * up_y(field) + down_y(link_y * field)
        beside = beside + link_z * up_z(field) + down_z(link_z * field)
        return diagonal * field - beside

    interior = (
        (depth_pos >= 1)
        & (depth_pos <= span_z - 2)
        & (column_pos >= 1)
        & (column_pos <= span_x - 2)
        & (row_pos >= 1)
        & (row_pos <= span_y - 2)
    )
    unknown = jnp.where(interior, inside, 0.0)
    scaling = unknown / (diagonal + 1.0 - unknown)
    core_z = (depth_pos >= RIM) & (depth_pos < RIM + CCZ)
    core_x = (column_pos >= RIM) & (column_pos < RIM + CCX)
    core_y = (row_pos >= RIM) & (row_pos < RIM + CCY)
    face_x = ((column_pos == RIM - 1) | (column_pos == RIM + CCX - 1)) & core_z & core_y
    face_y = ((row_pos == RIM - 1) | (row_pos == RIM + CCY - 1)) & core_z & core_x
    face_z = ((depth_pos == RIM - 1) | (depth_pos == RIM + CCZ - 1)) & core_x & core_y
    ramp_x = ((span_x - 1) / 2.0 - column_pos).astype(jnp.float32)
    ramp_y = ((span_y - 1) / 2.0 - row_pos).astype(jnp.float32)
    ramp_z = ((span_z - 1) / 2.0 - depth_pos).astype(jnp.float32)
    cheb_ratio = BOUND_MID / BOUND_HALF
    cases = (
        (ramp_x, link_x, face_x, CCY * CCZ, up_x),
        (ramp_y, link_y, face_y, CCX * CCZ, up_y),
        (ramp_z, link_z, face_z, CCX * CCY, up_z),
    )
    rows = []
    for ramp, link, face, area, upper_of in cases:
        source_term = -unknown * apply_operator(ramp)
        update = scaling * source_term / BOUND_MID
        solution = update
        rho_old = 1.0 / cheb_ratio
        for sweep_index in range(SWEEPS - 1):
            residual = source_term - apply_operator(solution)
            rho_new = 1.0 / (2.0 * cheb_ratio - rho_old)
            update = rho_new * rho_old * update + 2.0 * rho_new / BOUND_HALF * (scaling * residual)
            solution = solution + update
            rho_old = rho_new
        pressure = ramp + solution
        flux = jnp.where(face, link * (pressure - upper_of(pressure)), 0.0)
        total = jnp.sum(flux, axis=0)
        total = jnp.sum(total, axis=0, keepdims=True)
        total = jnp.sum(total, axis=1, keepdims=True)
        rows.append(jnp.broadcast_to(total * (0.5 / area), (1, LANES)))
    rows.append(jnp.zeros((8 - len(rows), LANES), jnp.float32))
    o_ref[0] = jnp.concatenate(rows, axis=0)


def upscale_windows(raw, facies_table):
    span_y = CCY + 2 * RIM
    count_z = (raw.shape[1] - 2 * RIM) // CCZ
    count_x = (raw.shape[2] - 2 * RIM) // CCX
    count_y = (raw.shape[3] - 2 * RIM) // CCY
    wide = -(-(raw.shape[3] + LANES) // LANES) * LANES
    raw = jnp.pad(raw, ((0, 0),) * 3 + ((0, wide - raw.shape[3]),))
    count = count_z * count_x * count_y
    sums = pl.pallas_call(
        window_kernel,
        grid=(count_z, count_x, count_y),
        in_specs=[
            pl.BlockSpec(memory_space=pltpu.SMEM),
            pl.BlockSpec(raw.shape, lambda z, x, y: (0, 0, 0, 0)),
        ],
        out_specs=pl.BlockSpec(
            (1, 8, LANES), lambda z, x, y: (z * count_x * count_y + x * count_y + y, 0, 0)
        ),
        out_shape=jax.ShapeDtypeStruct((count, 8, LANES), jnp.float32),
    )(facies_table, raw)
    return sums[:, :3, 0].T.reshape((3, count_z, count_x, count_y))


def coarse_sweep(perm_pad, press_pad, inside_pad, accumulation, fixed):
    centre = (slice(1, -1), slice(1, -1), slice(1, -1))
    factors = (CCY * CCZ / CCX, CCX * CCZ / CCY, CCX * CCY / CCZ)
    numer = fixed
    denom = accumulation
    for component, axis_dim in ((0, 1), (1, 2), (2, 0)):
        for offset in (-1, 1):
            window_slice = [slice(1, -1), slice(1, -1), slice(1, -1)]
            window_slice[axis_dim] = slice(1 + offset, press_pad.shape[axis_dim] - 1 + offset)
            beside = tuple(window_slice)
            link = (
                factors[component]
                * 0.5
                * (perm_pad[component][centre] + perm_pad[component][beside])
                * inside_pad[beside]
            )
            numer = numer + link * press_pad[beside]
            denom = denom + jnp.abs(link)
    return numer / denom


def span_mask(anchor, length, total, margin):
    coords = anchor - margin + jnp.arange(length + 2 * margin, dtype=jnp.int32)
    return ((coords >= 0) & (coords < total)).astype(jnp.float32)


def cut_windows(fields):
    span_z = CCZ + 2 * RIM
    span_x = CCX + 2 * RIM
    span_y = CCY + 2 * RIM
    count_z = (fields[0].shape[0] - 2 * RIM) // CCZ
    count_x = (fields[0].shape[1] - 2 * RIM) // CCX
    count_y = (fields[0].shape[2] - 2 * RIM) // CCY
    stacks = []
    for field in fields:
        pieces = []
        for block_z in range(count_z):
            for block_y in range(count_y):
                piece = field[
                    block_z * CCZ : block_z * CCZ + span_z,
                    0:span_x,
                    block_y * CCY : block_y * CCY + span_y,
                ]
                pieces.append(piece.reshape(span_z, span_x * span_y))
        stacks.append(jnp.stack(pieces))
    return (stacks, (count_z, count_x, count_y))


def faces(block, sides):
    got = []
    for axis, dim in sides:
        count = lax.axis_size(axis)
        ends = count - 1
        head = lax.slice_in_dim(block, 0, 1, axis=dim)
        tail = lax.slice_in_dim(block, block.shape[dim] - 1, block.shape[dim], axis=dim)
        lower = lax.ppermute(tail, axis, [(i, i + 1) for i in range(ends)])
        upper = lax.ppermute(head, axis, [(i + 1, i) for i in range(ends)])
        got.append((lower, upper))
    return got


def neighbour_views(block, got, dim_of):
    views = []
    for (lower, upper), dim in zip(got, dim_of):
        size = block.shape[dim]
        below = jnp.concatenate([lower, lax.slice_in_dim(block, 0, size - 1, axis=dim)], axis=dim)
        above = jnp.concatenate([lax.slice_in_dim(block, 1, size, axis=dim), upper], axis=dim)
        views.append((below, above))
    return views


def coarse_step(upscaled, views, inside_views, pressure, accumulation, fixed):
    factors = (CCY * CCZ / CCX, CCX * CCZ / CCY, CCX * CCY / CCZ)
    numer = fixed
    denom = accumulation
    for component in range(3):
        for side in range(2):
            beside = views[component][side]
            link = factors[component] * 0.5 * (upscaled[component] + beside[component]) * inside_views[component][side]
            numer = numer + link * pressure[component][side]
            denom = denom + jnp.abs(link)
    return numer / denom


def local(log_noise, facies, facies_table, pressure_old, accumulation, source):
    depth_len, rows_len, cols_len = log_noise.shape
    size_z = lax.axis_size("gz")
    size_x = lax.axis_size("gx")
    size_y = lax.axis_size("gy")
    index_z = lax.axis_index("gz")
    index_x = lax.axis_index("gx")
    index_y = lax.axis_index("gy")
    raw = jnp.stack([log_noise, facies.astype(jnp.float32)])
    raw = extended(raw, (("gx", 2), ("gy", 3), ("gz", 1)), RIM)
    anchor_z = index_z * depth_len
    anchor_y = index_y * cols_len
    anchor_x = index_x * rows_len
    mask_z = span_mask(anchor_z, depth_len, depth_len * size_z, RIM)
    mask_x = span_mask(anchor_x, rows_len, rows_len * size_x, RIM)
    mask_y = span_mask(anchor_y, cols_len, cols_len * size_y, RIM)
    inside = mask_z[:, None, None] * mask_x[None, :, None] * mask_y[None, None, :]
    upscaled = upscale_windows(jnp.concatenate([raw, inside[None]]), facies_table)
    coarse_z, coarse_x, coarse_y = pressure_old.shape
    bundle = jnp.stack([upscaled[0], upscaled[1], upscaled[2], pressure_old, accumulation, source])
    every = lax.all_gather(bundle, "gy", axis=3, tiled=True)
    every = lax.all_gather(every, "gx", axis=2, tiled=True)
    every = lax.all_gather(every, "gz", axis=1, tiled=True)
    perm_pad = jnp.pad(every[:3], ((0, 0), (1, 1), (1, 1), (1, 1)))
    old_all = every[3]
    acc_all = every[4]
    fixed_all = acc_all * old_all + every[5]
    inside_pad = jnp.pad(jnp.ones(old_all.shape, jnp.float32), 1)
    pressure = old_all
    for sweep_index in range(2):
        pressure = coarse_sweep(perm_pad, jnp.pad(pressure, 1), inside_pad, acc_all, fixed_all)
    pressure = lax.dynamic_slice(
        pressure, (index_z * coarse_z, index_x * coarse_x, index_y * coarse_y), (coarse_z, coarse_x, coarse_y)
    )
    return (pressure, upscaled)


def solution(mesh):
    placed = (
        P(("real", "gz"), "gx", "gy"),
        P(("real", "gz"), "gx", "gy"),
        P(),
        P(("real", "gz"), "gx", "gy"),
        P(("real", "gz"), "gx", "gy"),
        P(("real", "gz"), "gx", "gy"),
    )
    return jax.shard_map(
        local,
        mesh=mesh,
        in_specs=placed,
        out_specs=(P(("real", "gz"), "gx", "gy"), P(None, ("real", "gz"), "gx", "gy")),
        check_vma=False,
    )
```

```python
import functools

import jax
import jax.numpy as jnp
from jax import lax
from jax.sharding import PartitionSpec as P
from jax.experimental import pallas as pl
from jax.experimental.pallas import tpu as pltpu

NFAC = 4
CCX = 32
CCY = 32
CCZ = 8
RIM = 4
SWEEPS = 3


BOUND_MID = 1.0
BOUND_HALF = 0.9


def extended(cells, sides, width):
    for axis, dim in sides:
        count = lax.axis_size(axis)
        ends = count - 1
        head = lax.slice_in_dim(cells, 0, width, axis=dim)
        tail = lax.slice_in_dim(cells, cells.shape[dim] - width, cells.shape[dim], axis=dim)
        cells = jnp.concatenate(
            [
                lax.ppermute(tail, axis, [(i, (i + 1) % count) for i in range(ends)]),
                cells,
                lax.ppermute(head, axis, [((i + 1) % count, i) for i in range(ends)]),
            ],
            axis=dim,
        )
    return cells


def raise_flat(values, offset):
    zeros_block = jnp.zeros(values.shape[:-1] + (offset,), values.dtype)
    return jnp.concatenate([values[..., offset:], zeros_block], axis=-1)


def lower_flat(values, offset):
    zeros_block = jnp.zeros(values.shape[:-1] + (offset,), values.dtype)
    return jnp.concatenate([zeros_block, values[..., :-offset]], axis=-1)


def raise_depth(values):
    zeros_block = jnp.zeros(values.shape[:1] + (1,) + values.shape[2:], values.dtype)
    return jnp.concatenate([values[:, 1:], zeros_block], axis=1)


def lower_depth(values):
    zeros_block = jnp.zeros(values.shape[:1] + (1,) + values.shape[2:], values.dtype)
    return jnp.concatenate([zeros_block, values[:, :-1]], axis=1)


def log_fields(log_noise, facies, facies_table):
    base_log = log_noise
    extra_y = jnp.zeros_like(log_noise)
    extra_z = jnp.zeros_like(log_noise)
    for code_value in range(NFAC):
        matched = facies == code_value
        base_log = base_log + jnp.where(matched, facies_table[0, code_value], jnp.float32(0.0))
        extra_y = extra_y + jnp.where(matched, facies_table[1, code_value], jnp.float32(0.0))
        extra_z = extra_z + jnp.where(matched, facies_table[2, code_value], jnp.float32(0.0))
    return (base_log, base_log + extra_y, base_log + extra_z)


def upscale(perm_logs, inside):
    span_z = CCZ + 2 * RIM
    span_x = CCX + 2 * RIM
    span_y = CCY + 2 * RIM
    depth_pos = lax.broadcasted_iota(jnp.int32, (1, span_z, 1), 1)
    flat_pos = lax.broadcasted_iota(jnp.int32, (1, 1, span_x * span_y), 2)
    column_pos = flat_pos // span_y
    row_pos = flat_pos % span_y
    perm_x = jnp.exp(perm_logs[0])
    perm_y = jnp.exp(perm_logs[1])
    perm_z = jnp.exp(perm_logs[2])

    def links(perm, other_perm, other_inside):
        return inside * other_inside * 2.0 * perm * other_perm / (perm + other_perm)

    link_x = links(perm_x, raise_flat(perm_x, span_y), raise_flat(inside, span_y))
    link_y = links(perm_y, raise_flat(perm_y, 1), raise_flat(inside, 1)) * (
        row_pos < span_y - 1
    ).astype(jnp.float32)
    link_z = links(perm_z, raise_depth(perm_z), raise_depth(inside))
    diagonal = (
        link_x
        + lower_flat(link_x, span_y)
        + link_y
        + lower_flat(link_y, 1)
        + link_z
        + lower_depth(link_z)
    )

    def apply_operator(field):
        beside = link_x * raise_flat(field, span_y) + lower_flat(link_x * field, span_y)
        beside = beside + link_y * raise_flat(field, 1) + lower_flat(link_y * field, 1)
        beside = beside + link_z * raise_depth(field) + lower_depth(link_z * field)
        return diagonal * field - beside

    interior = (
        (depth_pos >= 1)
        & (depth_pos <= span_z - 2)
        & (column_pos >= 1)
        & (column_pos <= span_x - 2)
        & (row_pos >= 1)
        & (row_pos <= span_y - 2)
    )
    unknown = inside * interior.astype(jnp.float32)
    scaling = unknown / (diagonal + 1.0 - unknown)
    core_z = (depth_pos >= RIM) & (depth_pos < RIM + CCZ)
    core_x = (column_pos >= RIM) & (column_pos < RIM + CCX)
    core_y = (row_pos >= RIM) & (row_pos < RIM + CCY)
    face_x = (((column_pos == RIM - 1) | (column_pos == RIM + CCX - 1)) & core_z & core_y).astype(
        jnp.float32
    )
    face_y = (((row_pos == RIM - 1) | (row_pos == RIM + CCY - 1)) & core_z & core_x).astype(
        jnp.float32
    )
    face_z = (((depth_pos == RIM - 1) | (depth_pos == RIM + CCZ - 1)) & core_x & core_y).astype(
        jnp.float32
    )
    ramp_x = ((span_x - 1) / 2.0 - column_pos).astype(jnp.float32)
    ramp_y = ((span_y - 1) / 2.0 - row_pos).astype(jnp.float32)
    ramp_z = ((span_z - 1) / 2.0 - depth_pos).astype(jnp.float32)
    cheb_ratio = BOUND_MID / BOUND_HALF
    results = []
    cases = (
        (ramp_x, link_x, face_x, CCY * CCZ, 0),
        (ramp_y, link_y, face_y, CCX * CCZ, 1),
        (ramp_z, link_z, face_z, CCX * CCY, 2),
    )
    for ramp, link, face, area, direction in cases:
        ramp_full = jnp.broadcast_to(ramp, inside.shape)
        source_term = -unknown * apply_operator(ramp_full)
        update = scaling * source_term / BOUND_MID
        solution = update
        rho_old = 1.0 / cheb_ratio
        for sweep_index in range(SWEEPS - 1):
            residual = source_term - apply_operator(solution)
            rho_new = 1.0 / (2.0 * cheb_ratio - rho_old)
            update = rho_new * rho_old * update + 2.0 * rho_new / BOUND_HALF * (scaling * residual)
            solution = solution + update
            rho_old = rho_new
        pressure = ramp_full + solution
        if direction == 0:
            upper = raise_flat(pressure, span_y)
        elif direction == 1:
            upper = raise_flat(pressure, 1)
        else:
            upper = raise_depth(pressure)
        flux = link * (pressure - upper) * face
        results.append(jnp.sum(flux, axis=(1, 2)) * (0.5 / area))
    return jnp.stack(results)


LANES = 128


def window_kernel(table_ref, raw_ref, o_ref, *, count_x, count_y, count):
    span_z = CCZ + 2 * RIM
    span_x = CCX + 2 * RIM
    span_y = CCY + 2 * RIM
    segments = LANES // span_y
    shape = (span_z, span_x, LANES)
    pack = pl.program_id(0)
    wide = raw_ref.shape[-1]
    depth_pos = lax.broadcasted_iota(jnp.int32, shape, 0)
    column_pos = lax.broadcasted_iota(jnp.int32, shape, 1)
    lane = lax.broadcasted_iota(jnp.int32, shape, 2)
    segment = jnp.zeros(shape, jnp.int32)
    for bound in range(1, segments + 1):
        segment = segment + (lane >= bound * span_y).astype(jnp.int32)
    row_pos = lane - span_y * segment
    noise = jnp.zeros(shape, jnp.float32)
    codes = jnp.zeros(shape, jnp.float32)
    inside = jnp.zeros(shape, jnp.float32)
    for slot in range(segments):
        window = pack * segments + slot
        valid = window < count
        window = jnp.minimum(window, count - 1)
        block_z = window // (count_x * count_y)
        block_x = (window // count_y) % count_x
        block_y = window % count_y
        shift = (slot * span_y - block_y * CCY + wide) % wide
        here = segment == slot

        def cut(field):
            slab = raw_ref[field, pl.ds(block_z * CCZ, span_z), pl.ds(block_x * CCX, span_x), :]
            return pltpu.roll(slab, shift, 2)[:, :, :LANES]

        noise = jnp.where(here, cut(0), noise)
        codes = jnp.where(here, cut(1), codes)
        inside = jnp.where(here & valid, cut(2), inside)

    def lookup(row):
        value = jnp.zeros(shape, jnp.float32)
        for code_value in range(NFAC):
            value = jnp.where(codes == code_value, table_ref[row, code_value], value)
        return value

    log_x = noise + lookup(0)
    log_y = log_x + lookup(1)
    log_z = log_x + lookup(2)
    perm_x = jnp.exp(log_x)
    perm_y = jnp.exp(log_y)
    perm_z = jnp.exp(log_z)

    def up_x(v):
        return pltpu.roll(v, span_x - 1, 1)

    def down_x(v):
        return pltpu.roll(v, 1, 1)

    def up_y(v):
        return pltpu.roll(v, LANES - 1, 2)

    def down_y(v):
        return pltpu.roll(v, 1, 2)

    def up_z(v):
        return jnp.concatenate([v[1:], v[:1]], axis=0)

    def down_z(v):
        return jnp.concatenate([v[-1:], v[:-1]], axis=0)

    def links(perm, other_perm, other_inside, valid):
        value = inside * other_inside * 2.0 * perm * other_perm / (perm + other_perm)
        return jnp.where(valid, value, 0.0)

    link_x = links(perm_x, up_x(perm_x), up_x(inside), column_pos < span_x - 1)
    link_y = links(perm_y, up_y(perm_y), up_y(inside), row_pos < span_y - 1)
    link_z = links(perm_z, up_z(perm_z), up_z(inside), depth_pos < span_z - 1)
    diagonal = link_x + down_x(link_x) + link_y + down_y(link_y) + link_z + down_z(link_z)

    def apply_operator(field):
        beside = link_x * up_x(field) + down_x(link_x * field)
        beside = beside + link_y * up_y(field) + down_y(link_y * field)
        beside = beside + link_z * up_z(field) + down_z(link_z * field)
        return diagonal * field - beside

    interior = (
        (depth_pos >= 1)
        & (depth_pos <= span_z - 2)
        & (column_pos >= 1)
        & (column_pos <= span_x - 2)
        & (row_pos >= 1)
        & (row_pos <= span_y - 2)
    )
    unknown = jnp.where(interior, inside, 0.0)
    scaling = unknown / (diagonal + 1.0 - unknown)
    core_z = (depth_pos >= RIM) & (depth_pos < RIM + CCZ)
    core_x = (column_pos >= RIM) & (column_pos < RIM + CCX)
    core_y = (row_pos >= RIM) & (row_pos < RIM + CCY)
    face_x = ((column_pos == RIM - 1) | (column_pos == RIM + CCX - 1)) & core_z & core_y
    face_y = ((row_pos == RIM - 1) | (row_pos == RIM + CCY - 1)) & core_z & core_x
    face_z = ((depth_pos == RIM - 1) | (depth_pos == RIM + CCZ - 1)) & core_x & core_y
    ramp_x = ((span_x - 1) / 2.0 - column_pos).astype(jnp.float32)
    ramp_y = ((span_y - 1) / 2.0 - row_pos).astype(jnp.float32)
    ramp_z = ((span_z - 1) / 2.0 - depth_pos).astype(jnp.float32)
    cheb_ratio = BOUND_MID / BOUND_HALF
    cases = (
        (ramp_x, link_x, face_x, CCY * CCZ, up_x, down_x),
        (ramp_y, link_y, face_y, CCX * CCZ, up_y, down_y),
        (ramp_z, link_z, face_z, CCX * CCY, up_z, down_z),
    )
    rows = []
    for ramp, link, face, area, upper_of, lower_of in cases:
        source_term = -unknown * (link - lower_of(link))
        update = scaling * source_term / BOUND_MID
        solution = update
        rho_old = 1.0 / cheb_ratio
        for sweep_index in range(SWEEPS - 1):
            residual = source_term - apply_operator(solution)
            rho_new = 1.0 / (2.0 * cheb_ratio - rho_old)
            update = rho_new * rho_old * update + 2.0 * rho_new / BOUND_HALF * (scaling * residual)
            solution = solution + update
            rho_old = rho_new
        pressure = ramp + solution
        flux = jnp.where(face, link * (pressure - upper_of(pressure)), 0.0)
        total = jnp.sum(flux, axis=0)
        total = jnp.sum(total, axis=0, keepdims=True)
        rows.append(total * (0.5 / area))
    rows.append(jnp.zeros((8 - len(rows), LANES), jnp.float32))
    o_ref[0] = jnp.concatenate(rows, axis=0)


def upscale_windows(raw, facies_table):
    span_y = CCY + 2 * RIM
    count_z = (raw.shape[1] - 2 * RIM) // CCZ
    count_x = (raw.shape[2] - 2 * RIM) // CCX
    count_y = (raw.shape[3] - 2 * RIM) // CCY
    wide = -(-(raw.shape[3] + LANES) // LANES) * LANES
    raw = jnp.pad(raw, ((0, 0),) * 3 + ((0, wide - raw.shape[3]),))
    count = count_z * count_x * count_y
    segments = LANES // span_y
    packs = -(-count // segments)
    kernel = functools.partial(window_kernel, count_x=count_x, count_y=count_y, count=count)
    sums = pl.pallas_call(
        kernel,
        grid=(packs,),
        in_specs=[
            pl.BlockSpec(memory_space=pltpu.SMEM),
            pl.BlockSpec(raw.shape, lambda p: (0, 0, 0, 0)),
        ],
        out_specs=pl.BlockSpec((1, 8, LANES), lambda p: (p, 0, 0)),
        out_shape=jax.ShapeDtypeStruct((packs, 8, LANES), jnp.float32),
    )(facies_table, raw)
    sums = sums[:, :3, : segments * span_y].reshape(packs, 3, segments, span_y).sum(axis=3)
    sums = sums.transpose(1, 0, 2).reshape(3, packs * segments)[:, :count]
    return sums.reshape((3, count_z, count_x, count_y))


def coarse_sweep(perm_pad, press_pad, inside_pad, accumulation, fixed):
    centre = (slice(1, -1), slice(1, -1), slice(1, -1))
    factors = (CCY * CCZ / CCX, CCX * CCZ / CCY, CCX * CCY / CCZ)
    numer = fixed
    denom = accumulation
    for component, axis_dim in ((0, 1), (1, 2), (2, 0)):
        for offset in (-1, 1):
            window_slice = [slice(1, -1), slice(1, -1), slice(1, -1)]
            window_slice[axis_dim] = slice(1 + offset, press_pad.shape[axis_dim] - 1 + offset)
            beside = tuple(window_slice)
            link = (
                factors[component]
                * 0.5
                * (perm_pad[component][centre] + perm_pad[component][beside])
                * inside_pad[beside]
            )
            numer = numer + link * press_pad[beside]
            denom = denom + jnp.abs(link)
    return numer / denom


def span_mask(anchor, length, total, margin):
    coords = anchor - margin + jnp.arange(length + 2 * margin, dtype=jnp.int32)
    return ((coords >= 0) & (coords < total)).astype(jnp.float32)


def cut_windows(fields):
    span_z = CCZ + 2 * RIM
    span_x = CCX + 2 * RIM
    span_y = CCY + 2 * RIM
    count_z = (fields[0].shape[0] - 2 * RIM) // CCZ
    count_x = (fields[0].shape[1] - 2 * RIM) // CCX
    count_y = (fields[0].shape[2] - 2 * RIM) // CCY
    stacks = []
    for field in fields:
        pieces = []
        for block_z in range(count_z):
            for block_y in range(count_y):
                piece = field[
                    block_z * CCZ : block_z * CCZ + span_z,
                    0:span_x,
                    block_y * CCY : block_y * CCY + span_y,
                ]
                pieces.append(piece.reshape(span_z, span_x * span_y))
        stacks.append(jnp.stack(pieces))
    return (stacks, (count_z, count_x, count_y))


def faces(block, sides):
    got = []
    for axis, dim in sides:
        count = lax.axis_size(axis)
        ends = count - 1
        head = lax.slice_in_dim(block, 0, 1, axis=dim)
        tail = lax.slice_in_dim(block, block.shape[dim] - 1, block.shape[dim], axis=dim)
        lower = lax.ppermute(tail, axis, [(i, i + 1) for i in range(ends)])
        upper = lax.ppermute(head, axis, [(i + 1, i) for i in range(ends)])
        got.append((lower, upper))
    return got


def neighbour_views(block, got, dim_of):
    views = []
    for (lower, upper), dim in zip(got, dim_of):
        size = block.shape[dim]
        below = jnp.concatenate([lower, lax.slice_in_dim(block, 0, size - 1, axis=dim)], axis=dim)
        above = jnp.concatenate([lax.slice_in_dim(block, 1, size, axis=dim), upper], axis=dim)
        views.append((below, above))
    return views


def coarse_step(upscaled, views, inside_views, pressure, accumulation, fixed):
    factors = (CCY * CCZ / CCX, CCX * CCZ / CCY, CCX * CCY / CCZ)
    numer = fixed
    denom = accumulation
    for component in range(3):
        for side in range(2):
            beside = views[component][side]
            link = factors[component] * 0.5 * (upscaled[component] + beside[component]) * inside_views[component][side]
            numer = numer + link * pressure[component][side]
            denom = denom + jnp.abs(link)
    return numer / denom


def local(log_noise, facies, facies_table, pressure_old, accumulation, source):
    depth_len, rows_len, cols_len = log_noise.shape
    size_z = lax.axis_size("gz")
    size_x = lax.axis_size("gx")
    size_y = lax.axis_size("gy")
    index_z = lax.axis_index("gz")
    index_x = lax.axis_index("gx")
    index_y = lax.axis_index("gy")
    raw = jnp.stack([log_noise, facies.astype(jnp.float32)])
    raw = extended(raw, (("gx", 2), ("gy", 3), ("gz", 1)), RIM)
    anchor_z = index_z * depth_len
    anchor_y = index_y * cols_len
    anchor_x = index_x * rows_len
    mask_z = span_mask(anchor_z, depth_len, depth_len * size_z, RIM)
    mask_x = span_mask(anchor_x, rows_len, rows_len * size_x, RIM)
    mask_y = span_mask(anchor_y, cols_len, cols_len * size_y, RIM)
    inside = mask_z[:, None, None] * mask_x[None, :, None] * mask_y[None, None, :]
    upscaled = upscale_windows(jnp.concatenate([raw, inside[None]]), facies_table)
    coarse_z, coarse_x, coarse_y = pressure_old.shape
    bundle = jnp.stack([upscaled[0], upscaled[1], upscaled[2], pressure_old, accumulation, source])
    every = lax.all_gather(bundle, "gy", axis=3, tiled=True)
    every = lax.all_gather(every, "gx", axis=2, tiled=True)
    every = lax.all_gather(every, "gz", axis=1, tiled=True)
    perm_pad = jnp.pad(every[:3], ((0, 0), (1, 1), (1, 1), (1, 1)))
    old_all = every[3]
    acc_all = every[4]
    fixed_all = acc_all * old_all + every[5]
    inside_pad = jnp.pad(jnp.ones(old_all.shape, jnp.float32), 1)
    pressure = old_all
    for sweep_index in range(2):
        pressure = coarse_sweep(perm_pad, jnp.pad(pressure, 1), inside_pad, acc_all, fixed_all)
    pressure = lax.dynamic_slice(
        pressure, (index_z * coarse_z, index_x * coarse_x, index_y * coarse_y), (coarse_z, coarse_x, coarse_y)
    )
    return (pressure, upscaled)


def solution(mesh):
    placed = (
        P(("real", "gz"), "gx", "gy"),
        P(("real", "gz"), "gx", "gy"),
        P(),
        P(("real", "gz"), "gx", "gy"),
        P(("real", "gz"), "gx", "gy"),
        P(("real", "gz"), "gx", "gy"),
    )
    return jax.shard_map(
        local,
        mesh=mesh,
        in_specs=placed,
        out_specs=(P(("real", "gz"), "gx", "gy"), P(None, ("real", "gz"), "gx", "gy")),
        check_vma=False,
    )
```

```python
import functools
import itertools

import jax
import jax.numpy as jnp
from jax import lax
from jax.sharding import PartitionSpec as P
from jax.experimental import pallas as pl
from jax.experimental.pallas import tpu as pltpu

NFAC = 4
CCX = 32
CCY = 32
CCZ = 8
RIM = 4
SWEEPS = 3


BOUND_MID = 1.0
BOUND_HALF = 0.9


def extended(cells, sides, width):
    for axis, dim in sides:
        count = lax.axis_size(axis)
        ends = count - 1
        head = lax.slice_in_dim(cells, 0, width, axis=dim)
        tail = lax.slice_in_dim(cells, cells.shape[dim] - width, cells.shape[dim], axis=dim)
        cells = jnp.concatenate(
            [
                lax.ppermute(tail, axis, [(i, (i + 1) % count) for i in range(ends)]),
                cells,
                lax.ppermute(head, axis, [((i + 1) % count, i) for i in range(ends)]),
            ],
            axis=dim,
        )
    return cells


def halo_all(block, width):
    names = ("gx", "gy", "gz")
    dims = (2, 3, 1)
    sizes = [lax.axis_size(name) for name in names]
    coords = [lax.axis_index(name) for name in names]

    def linear(point):
        return (point[0] * sizes[1] + point[1]) * sizes[2] + point[2]

    def region(values, dim, offset, lower_first):
        length = values.shape[dim]
        first = lax.slice_in_dim(values, 0, width, axis=dim)
        last = lax.slice_in_dim(values, length - width, length, axis=dim)
        if offset == "P":
            return jnp.where(lower_first, last, first)
        return last if offset == -1 else first

    received = {}

    def fetch(key):
        if key in received:
            return received[key]
        slab = block
        for axis in range(3):
            if key[axis] != 0:
                slab = region(slab, dims[axis], key[axis], coords[axis] == 0)
        pairs = []
        for source in itertools.product(*[range(size) for size in sizes]):
            target = []
            for axis in range(3):
                if key[axis] == "P":
                    target.append(1 - source[axis])
                else:
                    target.append(source[axis] - key[axis])
            if all(0 <= target[axis] < sizes[axis] for axis in range(3)):
                pairs.append((linear(source), linear(target)))
        received[key] = lax.ppermute(slab, names, pairs) if pairs else jnp.zeros_like(slab)
        return received[key]

    pieces = {}
    for offset in itertools.product((-1, 0, 1), repeat=3):
        if offset == (0, 0, 0):
            pieces[offset] = block
            continue
        key = []
        keep = jnp.bool_(True)
        for axis in range(3):
            if offset[axis] != 0 and sizes[axis] == 2:
                key.append("P")
                keep = keep & (coords[axis] == (1 if offset[axis] == -1 else 0))
            else:
                key.append(offset[axis])
        if any(abs(offset[axis]) == 1 and sizes[axis] == 1 for axis in range(3)):
            slab = block
            for axis in range(3):
                if offset[axis] != 0:
                    slab = lax.slice_in_dim(slab, 0, width, axis=dims[axis])
            pieces[offset] = jnp.zeros_like(slab)
            continue
        got = fetch(tuple(key))
        pieces[offset] = jnp.where(keep, got, 0.0)
    planes = []
    for oz in (-1, 0, 1):
        rows = []
        for ox in (-1, 0, 1):
            rows.append(jnp.concatenate([pieces[(ox, oy, oz)] for oy in (-1, 0, 1)], axis=3))
        planes.append(jnp.concatenate(rows, axis=2))
    return jnp.concatenate(planes, axis=1)


def raise_flat(values, offset):
    zeros_block = jnp.zeros(values.shape[:-1] + (offset,), values.dtype)
    return jnp.concatenate([values[..., offset:], zeros_block], axis=-1)


def lower_flat(values, offset):
    zeros_block = jnp.zeros(values.shape[:-1] + (offset,), values.dtype)
    return jnp.concatenate([zeros_block, values[..., :-offset]], axis=-1)


def raise_depth(values):
    zeros_block = jnp.zeros(values.shape[:1] + (1,) + values.shape[2:], values.dtype)
    return jnp.concatenate([values[:, 1:], zeros_block], axis=1)


def lower_depth(values):
    zeros_block = jnp.zeros(values.shape[:1] + (1,) + values.shape[2:], values.dtype)
    return jnp.concatenate([zeros_block, values[:, :-1]], axis=1)


def log_fields(log_noise, facies, facies_table):
    base_log = log_noise
    extra_y = jnp.zeros_like(log_noise)
    extra_z = jnp.zeros_like(log_noise)
    for code_value in range(NFAC):
        matched = facies == code_value
        base_log = base_log + jnp.where(matched, facies_table[0, code_value], jnp.float32(0.0))
        extra_y = extra_y + jnp.where(matched, facies_table[1, code_value], jnp.float32(0.0))
        extra_z = extra_z + jnp.where(matched, facies_table[2, code_value], jnp.float32(0.0))
    return (base_log, base_log + extra_y, base_log + extra_z)


def upscale(perm_logs, inside):
    span_z = CCZ + 2 * RIM
    span_x = CCX + 2 * RIM
    span_y = CCY + 2 * RIM
    depth_pos = lax.broadcasted_iota(jnp.int32, (1, span_z, 1), 1)
    flat_pos = lax.broadcasted_iota(jnp.int32, (1, 1, span_x * span_y), 2)
    column_pos = flat_pos // span_y
    row_pos = flat_pos % span_y
    perm_x = jnp.exp(perm_logs[0])
    perm_y = jnp.exp(perm_logs[1])
    perm_z = jnp.exp(perm_logs[2])

    def links(perm, other_perm, other_inside):
        return inside * other_inside * 2.0 * perm * other_perm / (perm + other_perm)

    link_x = links(perm_x, raise_flat(perm_x, span_y), raise_flat(inside, span_y))
    link_y = links(perm_y, raise_flat(perm_y, 1), raise_flat(inside, 1)) * (
        row_pos < span_y - 1
    ).astype(jnp.float32)
    link_z = links(perm_z, raise_depth(perm_z), raise_depth(inside))
    diagonal = (
        link_x
        + lower_flat(link_x, span_y)
        + link_y
        + lower_flat(link_y, 1)
        + link_z
        + lower_depth(link_z)
    )

    def apply_operator(field):
        beside = link_x * raise_flat(field, span_y) + lower_flat(link_x * field, span_y)
        beside = beside + link_y * raise_flat(field, 1) + lower_flat(link_y * field, 1)
        beside = beside + link_z * raise_depth(field) + lower_depth(link_z * field)
        return diagonal * field - beside

    interior = (
        (depth_pos >= 1)
        & (depth_pos <= span_z - 2)
        & (column_pos >= 1)
        & (column_pos <= span_x - 2)
        & (row_pos >= 1)
        & (row_pos <= span_y - 2)
    )
    unknown = inside * interior.astype(jnp.float32)
    scaling = unknown / (diagonal + 1.0 - unknown)
    core_z = (depth_pos >= RIM) & (depth_pos < RIM + CCZ)
    core_x = (column_pos >= RIM) & (column_pos < RIM + CCX)
    core_y = (row_pos >= RIM) & (row_pos < RIM + CCY)
    face_x = (((column_pos == RIM - 1) | (column_pos == RIM + CCX - 1)) & core_z & core_y).astype(
        jnp.float32
    )
    face_y = (((row_pos == RIM - 1) | (row_pos == RIM + CCY - 1)) & core_z & core_x).astype(
        jnp.float32
    )
    face_z = (((depth_pos == RIM - 1) | (depth_pos == RIM + CCZ - 1)) & core_x & core_y).astype(
        jnp.float32
    )
    ramp_x = ((span_x - 1) / 2.0 - column_pos).astype(jnp.float32)
    ramp_y = ((span_y - 1) / 2.0 - row_pos).astype(jnp.float32)
    ramp_z = ((span_z - 1) / 2.0 - depth_pos).astype(jnp.float32)
    cheb_ratio = BOUND_MID / BOUND_HALF
    results = []
    cases = (
        (ramp_x, link_x, face_x, CCY * CCZ, 0),
        (ramp_y, link_y, face_y, CCX * CCZ, 1),
        (ramp_z, link_z, face_z, CCX * CCY, 2),
    )
    for ramp, link, face, area, direction in cases:
        ramp_full = jnp.broadcast_to(ramp, inside.shape)
        source_term = -unknown * apply_operator(ramp_full)
        update = scaling * source_term / BOUND_MID
        solution = update
        rho_old = 1.0 / cheb_ratio
        for sweep_index in range(SWEEPS - 1):
            residual = source_term - apply_operator(solution)
            rho_new = 1.0 / (2.0 * cheb_ratio - rho_old)
            update = rho_new * rho_old * update + 2.0 * rho_new / BOUND_HALF * (scaling * residual)
            solution = solution + update
            rho_old = rho_new
        pressure = ramp_full + solution
        if direction == 0:
            upper = raise_flat(pressure, span_y)
        elif direction == 1:
            upper = raise_flat(pressure, 1)
        else:
            upper = raise_depth(pressure)
        flux = link * (pressure - upper) * face
        results.append(jnp.sum(flux, axis=(1, 2)) * (0.5 / area))
    return jnp.stack(results)


LANES = 128


def window_kernel(table_ref, raw_ref, o_ref, *, count_x, count_y, count):
    span_z = CCZ + 2 * RIM
    span_x = CCX + 2 * RIM
    span_y = CCY + 2 * RIM
    segments = LANES // span_y
    shape = (span_z, span_x, LANES)
    pack = pl.program_id(0)
    wide = raw_ref.shape[-1]
    depth_pos = lax.broadcasted_iota(jnp.int32, shape, 0)
    column_pos = lax.broadcasted_iota(jnp.int32, shape, 1)
    lane = lax.broadcasted_iota(jnp.int32, shape, 2)
    segment = jnp.zeros(shape, jnp.int32)
    for bound in range(1, segments + 1):
        segment = segment + (lane >= bound * span_y).astype(jnp.int32)
    row_pos = lane - span_y * segment
    noise = jnp.zeros(shape, jnp.float32)
    codes = jnp.zeros(shape, jnp.float32)
    inside = jnp.zeros(shape, jnp.float32)
    for slot in range(segments):
        window = pack * segments + slot
        valid = window < count
        window = jnp.minimum(window, count - 1)
        block_z = window // (count_x * count_y)
        block_x = (window // count_y) % count_x
        block_y = window % count_y
        shift = (slot * span_y - block_y * CCY + wide) % wide
        here = segment == slot

        def cut(field):
            slab = raw_ref[field, pl.ds(block_z * CCZ, span_z), pl.ds(block_x * CCX, span_x), :]
            return pltpu.roll(slab, shift, 2)[:, :, :LANES]

        noise = jnp.where(here, cut(0), noise)
        codes = jnp.where(here, cut(1), codes)
        inside = jnp.where(here & valid, cut(2), inside)

    def lookup(row):
        value = jnp.zeros(shape, jnp.float32)
        for code_value in range(NFAC):
            value = jnp.where(codes == code_value, table_ref[row, code_value], value)
        return value

    log_x = noise + lookup(0)
    log_y = log_x + lookup(1)
    log_z = log_x + lookup(2)
    perm_x = jnp.exp(log_x)
    perm_y = jnp.exp(log_y)
    perm_z = jnp.exp(log_z)

    def up_x(v):
        return pltpu.roll(v, span_x - 1, 1)

    def down_x(v):
        return pltpu.roll(v, 1, 1)

    def up_y(v):
        return pltpu.roll(v, LANES - 1, 2)

    def down_y(v):
        return pltpu.roll(v, 1, 2)

    def up_z(v):
        return jnp.concatenate([v[1:], v[:1]], axis=0)

    def down_z(v):
        return jnp.concatenate([v[-1:], v[:-1]], axis=0)

    def links(perm, other_perm, other_inside, valid):
        value = inside * other_inside * 2.0 * perm * other_perm / (perm + other_perm)
        return jnp.where(valid, value, 0.0)

    link_x = links(perm_x, up_x(perm_x), up_x(inside), column_pos < span_x - 1)
    link_y = links(perm_y, up_y(perm_y), up_y(inside), row_pos < span_y - 1)
    link_z = links(perm_z, up_z(perm_z), up_z(inside), depth_pos < span_z - 1)
    diagonal = link_x + down_x(link_x) + link_y + down_y(link_y) + link_z + down_z(link_z)

    def apply_operator(field):
        beside = link_x * up_x(field) + down_x(link_x * field)
        beside = beside + link_y * up_y(field) + down_y(link_y * field)
        beside = beside + link_z * up_z(field) + down_z(link_z * field)
        return diagonal * field - beside

    interior = (
        (depth_pos >= 1)
        & (depth_pos <= span_z - 2)
        & (column_pos >= 1)
        & (column_pos <= span_x - 2)
        & (row_pos >= 1)
        & (row_pos <= span_y - 2)
    )
    unknown = jnp.where(interior, inside, 0.0)
    scaling = unknown / (diagonal + 1.0 - unknown)
    core_z = (depth_pos >= RIM) & (depth_pos < RIM + CCZ)
    core_x = (column_pos >= RIM) & (column_pos < RIM + CCX)
    core_y = (row_pos >= RIM) & (row_pos < RIM + CCY)
    face_x = ((column_pos == RIM - 1) | (column_pos == RIM + CCX - 1)) & core_z & core_y
    face_y = ((row_pos == RIM - 1) | (row_pos == RIM + CCY - 1)) & core_z & core_x
    face_z = ((depth_pos == RIM - 1) | (depth_pos == RIM + CCZ - 1)) & core_x & core_y
    ramp_x = ((span_x - 1) / 2.0 - column_pos).astype(jnp.float32)
    ramp_y = ((span_y - 1) / 2.0 - row_pos).astype(jnp.float32)
    ramp_z = ((span_z - 1) / 2.0 - depth_pos).astype(jnp.float32)
    cheb_ratio = BOUND_MID / BOUND_HALF
    cases = (
        (ramp_x, link_x, face_x, CCY * CCZ, up_x, down_x),
        (ramp_y, link_y, face_y, CCX * CCZ, up_y, down_y),
        (ramp_z, link_z, face_z, CCX * CCY, up_z, down_z),
    )
    rows = []
    for ramp, link, face, area, upper_of, lower_of in cases:
        source_term = -unknown * (link - lower_of(link))
        update = scaling * source_term / BOUND_MID
        solution = update
        rho_old = 1.0 / cheb_ratio
        for sweep_index in range(SWEEPS - 1):
            residual = source_term - apply_operator(solution)
            rho_new = 1.0 / (2.0 * cheb_ratio - rho_old)
            update = rho_new * rho_old * update + 2.0 * rho_new / BOUND_HALF * (scaling * residual)
            solution = solution + update
            rho_old = rho_new
        pressure = ramp + solution
        flux = jnp.where(face, link * (pressure - upper_of(pressure)), 0.0)
        total = jnp.sum(flux, axis=0)
        total = jnp.sum(total, axis=0, keepdims=True)
        rows.append(total * (0.5 / area))
    rows.append(jnp.zeros((8 - len(rows), LANES), jnp.float32))
    o_ref[0] = jnp.concatenate(rows, axis=0)


def upscale_windows(raw, facies_table):
    span_y = CCY + 2 * RIM
    count_z = (raw.shape[1] - 2 * RIM) // CCZ
    count_x = (raw.shape[2] - 2 * RIM) // CCX
    count_y = (raw.shape[3] - 2 * RIM) // CCY
    wide = -(-(raw.shape[3] + LANES) // LANES) * LANES
    raw = jnp.pad(raw, ((0, 0),) * 3 + ((0, wide - raw.shape[3]),))
    count = count_z * count_x * count_y
    segments = LANES // span_y
    packs = -(-count // segments)
    kernel = functools.partial(window_kernel, count_x=count_x, count_y=count_y, count=count)
    sums = pl.pallas_call(
        kernel,
        grid=(packs,),
        in_specs=[
            pl.BlockSpec(memory_space=pltpu.SMEM),
            pl.BlockSpec(raw.shape, lambda p: (0, 0, 0, 0)),
        ],
        out_specs=pl.BlockSpec((1, 8, LANES), lambda p: (p, 0, 0)),
        out_shape=jax.ShapeDtypeStruct((packs, 8, LANES), jnp.float32),
    )(facies_table, raw)
    sums = sums[:, :3, : segments * span_y].reshape(packs, 3, segments, span_y).sum(axis=3)
    sums = sums.transpose(1, 0, 2).reshape(3, packs * segments)[:, :count]
    return sums.reshape((3, count_z, count_x, count_y))


def coarse_sweep(perm_pad, press_pad, inside_pad, accumulation, fixed):
    centre = (slice(1, -1), slice(1, -1), slice(1, -1))
    factors = (CCY * CCZ / CCX, CCX * CCZ / CCY, CCX * CCY / CCZ)
    numer = fixed
    denom = accumulation
    for component, axis_dim in ((0, 1), (1, 2), (2, 0)):
        for offset in (-1, 1):
            window_slice = [slice(1, -1), slice(1, -1), slice(1, -1)]
            window_slice[axis_dim] = slice(1 + offset, press_pad.shape[axis_dim] - 1 + offset)
            beside = tuple(window_slice)
            link = (
                factors[component]
                * 0.5
                * (perm_pad[component][centre] + perm_pad[component][beside])
                * inside_pad[beside]
            )
            numer = numer + link * press_pad[beside]
            denom = denom + jnp.abs(link)
    return numer / denom


def span_mask(anchor, length, total, margin):
    coords = anchor - margin + jnp.arange(length + 2 * margin, dtype=jnp.int32)
    return ((coords >= 0) & (coords < total)).astype(jnp.float32)


def cut_windows(fields):
    span_z = CCZ + 2 * RIM
    span_x = CCX + 2 * RIM
    span_y = CCY + 2 * RIM
    count_z = (fields[0].shape[0] - 2 * RIM) // CCZ
    count_x = (fields[0].shape[1] - 2 * RIM) // CCX
    count_y = (fields[0].shape[2] - 2 * RIM) // CCY
    stacks = []
    for field in fields:
        pieces = []
        for block_z in range(count_z):
            for block_y in range(count_y):
                piece = field[
                    block_z * CCZ : block_z * CCZ + span_z,
                    0:span_x,
                    block_y * CCY : block_y * CCY + span_y,
                ]
                pieces.append(piece.reshape(span_z, span_x * span_y))
        stacks.append(jnp.stack(pieces))
    return (stacks, (count_z, count_x, count_y))


def faces(block, sides):
    got = []
    for axis, dim in sides:
        count = lax.axis_size(axis)
        ends = count - 1
        head = lax.slice_in_dim(block, 0, 1, axis=dim)
        tail = lax.slice_in_dim(block, block.shape[dim] - 1, block.shape[dim], axis=dim)
        lower = lax.ppermute(tail, axis, [(i, i + 1) for i in range(ends)])
        upper = lax.ppermute(head, axis, [(i + 1, i) for i in range(ends)])
        got.append((lower, upper))
    return got


def neighbour_views(block, got, dim_of):
    views = []
    for (lower, upper), dim in zip(got, dim_of):
        size = block.shape[dim]
        below = jnp.concatenate([lower, lax.slice_in_dim(block, 0, size - 1, axis=dim)], axis=dim)
        above = jnp.concatenate([lax.slice_in_dim(block, 1, size, axis=dim), upper], axis=dim)
        views.append((below, above))
    return views


def coarse_step(upscaled, views, inside_views, pressure, accumulation, fixed):
    factors = (CCY * CCZ / CCX, CCX * CCZ / CCY, CCX * CCY / CCZ)
    numer = fixed
    denom = accumulation
    for component in range(3):
        for side in range(2):
            beside = views[component][side]
            link = factors[component] * 0.5 * (upscaled[component] + beside[component]) * inside_views[component][side]
            numer = numer + link * pressure[component][side]
            denom = denom + jnp.abs(link)
    return numer / denom


def local(log_noise, facies, facies_table, pressure_old, accumulation, source):
    depth_len, rows_len, cols_len = log_noise.shape
    size_z = lax.axis_size("gz")
    size_x = lax.axis_size("gx")
    size_y = lax.axis_size("gy")
    index_z = lax.axis_index("gz")
    index_x = lax.axis_index("gx")
    index_y = lax.axis_index("gy")
    raw = jnp.stack([log_noise, facies.astype(jnp.float32)])
    raw = halo_all(raw, RIM)
    anchor_z = index_z * depth_len
    anchor_y = index_y * cols_len
    anchor_x = index_x * rows_len
    mask_z = span_mask(anchor_z, depth_len, depth_len * size_z, RIM)
    mask_x = span_mask(anchor_x, rows_len, rows_len * size_x, RIM)
    mask_y = span_mask(anchor_y, cols_len, cols_len * size_y, RIM)
    inside = mask_z[:, None, None] * mask_x[None, :, None] * mask_y[None, None, :]
    upscaled = upscale_windows(jnp.concatenate([raw, inside[None]]), facies_table)
    coarse_z, coarse_x, coarse_y = pressure_old.shape
    bundle = jnp.stack([upscaled[0], upscaled[1], upscaled[2], pressure_old, accumulation, source])
    every = lax.all_gather(bundle, "gy", axis=3, tiled=True)
    every = lax.all_gather(every, "gx", axis=2, tiled=True)
    every = lax.all_gather(every, "gz", axis=1, tiled=True)
    perm_pad = jnp.pad(every[:3], ((0, 0), (1, 1), (1, 1), (1, 1)))
    old_all = every[3]
    acc_all = every[4]
    fixed_all = acc_all * old_all + every[5]
    inside_pad = jnp.pad(jnp.ones(old_all.shape, jnp.float32), 1)
    pressure = old_all
    for sweep_index in range(2):
        pressure = coarse_sweep(perm_pad, jnp.pad(pressure, 1), inside_pad, acc_all, fixed_all)
    pressure = lax.dynamic_slice(
        pressure, (index_z * coarse_z, index_x * coarse_x, index_y * coarse_y), (coarse_z, coarse_x, coarse_y)
    )
    return (pressure, upscaled)


def solution(mesh):
    placed = (
        P(("real", "gz"), "gx", "gy"),
        P(("real", "gz"), "gx", "gy"),
        P(),
        P(("real", "gz"), "gx", "gy"),
        P(("real", "gz"), "gx", "gy"),
        P(("real", "gz"), "gx", "gy"),
    )
    return jax.shard_map(
        local,
        mesh=mesh,
        in_specs=placed,
        out_specs=(P(("real", "gz"), "gx", "gy"), P(None, ("real", "gz"), "gx", "gy")),
        check_vma=False,
    )
```

```python
import functools

import jax
import jax.numpy as jnp
from jax import lax
from jax.sharding import PartitionSpec as P
from jax.experimental import pallas as pl
from jax.experimental.pallas import tpu as pltpu

NFAC = 4
CCX = 32
CCY = 32
CCZ = 8
RIM = 4
SWEEPS = 3


BOUND_MID = 1.0
BOUND_HALF = 0.9


def extended(cells, sides, width):
    for axis, dim in sides:
        count = lax.axis_size(axis)
        ends = count - 1
        head = lax.slice_in_dim(cells, 0, width, axis=dim)
        tail = lax.slice_in_dim(cells, cells.shape[dim] - width, cells.shape[dim], axis=dim)
        if count == 2:
            lower_side = lax.axis_index(axis) == 0
            got = lax.ppermute(jnp.where(lower_side, tail, head), axis, [(0, 1), (1, 0)])
            below = jnp.where(lower_side, 0.0, got)
            above = jnp.where(lower_side, got, 0.0)
        else:
            below = lax.ppermute(tail, axis, [(i, (i + 1) % count) for i in range(ends)])
            above = lax.ppermute(head, axis, [((i + 1) % count, i) for i in range(ends)])
        cells = jnp.concatenate([below, cells, above], axis=dim)
    return cells


def raise_flat(values, offset):
    zeros_block = jnp.zeros(values.shape[:-1] + (offset,), values.dtype)
    return jnp.concatenate([values[..., offset:], zeros_block], axis=-1)


def lower_flat(values, offset):
    zeros_block = jnp.zeros(values.shape[:-1] + (offset,), values.dtype)
    return jnp.concatenate([zeros_block, values[..., :-offset]], axis=-1)


def raise_depth(values):
    zeros_block = jnp.zeros(values.shape[:1] + (1,) + values.shape[2:], values.dtype)
    return jnp.concatenate([values[:, 1:], zeros_block], axis=1)


def lower_depth(values):
    zeros_block = jnp.zeros(values.shape[:1] + (1,) + values.shape[2:], values.dtype)
    return jnp.concatenate([zeros_block, values[:, :-1]], axis=1)


def log_fields(log_noise, facies, facies_table):
    base_log = log_noise
    extra_y = jnp.zeros_like(log_noise)
    extra_z = jnp.zeros_like(log_noise)
    for code_value in range(NFAC):
        matched = facies == code_value
        base_log = base_log + jnp.where(matched, facies_table[0, code_value], jnp.float32(0.0))
        extra_y = extra_y + jnp.where(matched, facies_table[1, code_value], jnp.float32(0.0))
        extra_z = extra_z + jnp.where(matched, facies_table[2, code_value], jnp.float32(0.0))
    return (base_log, base_log + extra_y, base_log + extra_z)


def upscale(perm_logs, inside):
    span_z = CCZ + 2 * RIM
    span_x = CCX + 2 * RIM
    span_y = CCY + 2 * RIM
    depth_pos = lax.broadcasted_iota(jnp.int32, (1, span_z, 1), 1)
    flat_pos = lax.broadcasted_iota(jnp.int32, (1, 1, span_x * span_y), 2)
    column_pos = flat_pos // span_y
    row_pos = flat_pos % span_y
    perm_x = jnp.exp(perm_logs[0])
    perm_y = jnp.exp(perm_logs[1])
    perm_z = jnp.exp(perm_logs[2])

    def links(perm, other_perm, other_inside):
        return inside * other_inside * 2.0 * perm * other_perm / (perm + other_perm)

    link_x = links(perm_x, raise_flat(perm_x, span_y), raise_flat(inside, span_y))
    link_y = links(perm_y, raise_flat(perm_y, 1), raise_flat(inside, 1)) * (
        row_pos < span_y - 1
    ).astype(jnp.float32)
    link_z = links(perm_z, raise_depth(perm_z), raise_depth(inside))
    diagonal = (
        link_x
        + lower_flat(link_x, span_y)
        + link_y
        + lower_flat(link_y, 1)
        + link_z
        + lower_depth(link_z)
    )

    def apply_operator(field):
        beside = link_x * raise_flat(field, span_y) + lower_flat(link_x * field, span_y)
        beside = beside + link_y * raise_flat(field, 1) + lower_flat(link_y * field, 1)
        beside = beside + link_z * raise_depth(field) + lower_depth(link_z * field)
        return diagonal * field - beside

    interior = (
        (depth_pos >= 1)
        & (depth_pos <= span_z - 2)
        & (column_pos >= 1)
        & (column_pos <= span_x - 2)
        & (row_pos >= 1)
        & (row_pos <= span_y - 2)
    )
    unknown = inside * interior.astype(jnp.float32)
    scaling = unknown / (diagonal + 1.0 - unknown)
    core_z = (depth_pos >= RIM) & (depth_pos < RIM + CCZ)
    core_x = (column_pos >= RIM) & (column_pos < RIM + CCX)
    core_y = (row_pos >= RIM) & (row_pos < RIM + CCY)
    face_x = (((column_pos == RIM - 1) | (column_pos == RIM + CCX - 1)) & core_z & core_y).astype(
        jnp.float32
    )
    face_y = (((row_pos == RIM - 1) | (row_pos == RIM + CCY - 1)) & core_z & core_x).astype(
        jnp.float32
    )
    face_z = (((depth_pos == RIM - 1) | (depth_pos == RIM + CCZ - 1)) & core_x & core_y).astype(
        jnp.float32
    )
    ramp_x = ((span_x - 1) / 2.0 - column_pos).astype(jnp.float32)
    ramp_y = ((span_y - 1) / 2.0 - row_pos).astype(jnp.float32)
    ramp_z = ((span_z - 1) / 2.0 - depth_pos).astype(jnp.float32)
    cheb_ratio = BOUND_MID / BOUND_HALF
    results = []
    cases = (
        (ramp_x, link_x, face_x, CCY * CCZ, 0),
        (ramp_y, link_y, face_y, CCX * CCZ, 1),
        (ramp_z, link_z, face_z, CCX * CCY, 2),
    )
    for ramp, link, face, area, direction in cases:
        ramp_full = jnp.broadcast_to(ramp, inside.shape)
        source_term = -unknown * apply_operator(ramp_full)
        update = scaling * source_term / BOUND_MID
        solution = update
        rho_old = 1.0 / cheb_ratio
        for sweep_index in range(SWEEPS - 1):
            residual = source_term - apply_operator(solution)
            rho_new = 1.0 / (2.0 * cheb_ratio - rho_old)
            update = rho_new * rho_old * update + 2.0 * rho_new / BOUND_HALF * (scaling * residual)
            solution = solution + update
            rho_old = rho_new
        pressure = ramp_full + solution
        if direction == 0:
            upper = raise_flat(pressure, span_y)
        elif direction == 1:
            upper = raise_flat(pressure, 1)
        else:
            upper = raise_depth(pressure)
        flux = link * (pressure - upper) * face
        results.append(jnp.sum(flux, axis=(1, 2)) * (0.5 / area))
    return jnp.stack(results)


LANES = 128


def window_kernel(table_ref, raw_ref, o_ref, *, count_x, count_y, count):
    span_z = CCZ + 2 * RIM
    span_x = CCX + 2 * RIM
    span_y = CCY + 2 * RIM
    segments = LANES // span_y
    shape = (span_z, span_x, LANES)
    pack = pl.program_id(0)
    wide = raw_ref.shape[-1]
    depth_pos = lax.broadcasted_iota(jnp.int32, shape, 0)
    column_pos = lax.broadcasted_iota(jnp.int32, shape, 1)
    lane = lax.broadcasted_iota(jnp.int32, shape, 2)
    segment = jnp.zeros(shape, jnp.int32)
    for bound in range(1, segments + 1):
        segment = segment + (lane >= bound * span_y).astype(jnp.int32)
    row_pos = lane - span_y * segment
    noise = jnp.zeros(shape, jnp.float32)
    codes = jnp.zeros(shape, jnp.float32)
    inside = jnp.zeros(shape, jnp.float32)
    for slot in range(segments):
        window = pack * segments + slot
        valid = window < count
        window = jnp.minimum(window, count - 1)
        block_z = window // (count_x * count_y)
        block_x = (window // count_y) % count_x
        block_y = window % count_y
        shift = (slot * span_y - block_y * CCY + wide) % wide
        here = segment == slot

        def cut(field):
            slab = raw_ref[field, pl.ds(block_z * CCZ, span_z), pl.ds(block_x * CCX, span_x), :]
            return pltpu.roll(slab, shift, 2)[:, :, :LANES]

        noise = jnp.where(here, cut(0), noise)
        codes = jnp.where(here, cut(1), codes)
        inside = jnp.where(here & valid, cut(2), inside)

    def lookup(row):
        value = jnp.zeros(shape, jnp.float32)
        for code_value in range(NFAC):
            value = jnp.where(codes == code_value, table_ref[row, code_value], value)
        return value

    log_x = noise + lookup(0)
    log_y = log_x + lookup(1)
    log_z = log_x + lookup(2)
    perm_x = jnp.exp(log_x)
    perm_y = jnp.exp(log_y)
    perm_z = jnp.exp(log_z)

    def up_x(v):
        return pltpu.roll(v, span_x - 1, 1)

    def down_x(v):
        return pltpu.roll(v, 1, 1)

    def up_y(v):
        return pltpu.roll(v, LANES - 1, 2)

    def down_y(v):
        return pltpu.roll(v, 1, 2)

    def up_z(v):
        return jnp.concatenate([v[1:], v[:1]], axis=0)

    def down_z(v):
        return jnp.concatenate([v[-1:], v[:-1]], axis=0)

    def links(perm, other_perm, other_inside, valid):
        value = inside * other_inside * 2.0 * perm * other_perm / (perm + other_perm)
        return jnp.where(valid, value, 0.0)

    link_x = links(perm_x, up_x(perm_x), up_x(inside), column_pos < span_x - 1)
    link_y = links(perm_y, up_y(perm_y), up_y(inside), row_pos < span_y - 1)
    link_z = links(perm_z, up_z(perm_z), up_z(inside), depth_pos < span_z - 1)
    diagonal = link_x + down_x(link_x) + link_y + down_y(link_y) + link_z + down_z(link_z)

    def apply_operator(field):
        beside = link_x * up_x(field) + down_x(link_x * field)
        beside = beside + link_y * up_y(field) + down_y(link_y * field)
        beside = beside + link_z * up_z(field) + down_z(link_z * field)
        return diagonal * field - beside

    interior = (
        (depth_pos >= 1)
        & (depth_pos <= span_z - 2)
        & (column_pos >= 1)
        & (column_pos <= span_x - 2)
        & (row_pos >= 1)
        & (row_pos <= span_y - 2)
    )
    unknown = jnp.where(interior, inside, 0.0)
    scaling = unknown / (diagonal + 1.0 - unknown)
    core_z = (depth_pos >= RIM) & (depth_pos < RIM + CCZ)
    core_x = (column_pos >= RIM) & (column_pos < RIM + CCX)
    core_y = (row_pos >= RIM) & (row_pos < RIM + CCY)
    face_x = ((column_pos == RIM - 1) | (column_pos == RIM + CCX - 1)) & core_z & core_y
    face_y = ((row_pos == RIM - 1) | (row_pos == RIM + CCY - 1)) & core_z & core_x
    face_z = ((depth_pos == RIM - 1) | (depth_pos == RIM + CCZ - 1)) & core_x & core_y
    ramp_x = ((span_x - 1) / 2.0 - column_pos).astype(jnp.float32)
    ramp_y = ((span_y - 1) / 2.0 - row_pos).astype(jnp.float32)
    ramp_z = ((span_z - 1) / 2.0 - depth_pos).astype(jnp.float32)
    cheb_ratio = BOUND_MID / BOUND_HALF
    cases = (
        (ramp_x, link_x, face_x, CCY * CCZ, up_x, down_x),
        (ramp_y, link_y, face_y, CCX * CCZ, up_y, down_y),
        (ramp_z, link_z, face_z, CCX * CCY, up_z, down_z),
    )
    rows = []
    for ramp, link, face, area, upper_of, lower_of in cases:
        source_term = -unknown * (link - lower_of(link))
        update = scaling * source_term / BOUND_MID
        solution = update
        rho_old = 1.0 / cheb_ratio
        for sweep_index in range(SWEEPS - 1):
            residual = source_term - apply_operator(solution)
            rho_new = 1.0 / (2.0 * cheb_ratio - rho_old)
            update = rho_new * rho_old * update + 2.0 * rho_new / BOUND_HALF * (scaling * residual)
            solution = solution + update
            rho_old = rho_new
        pressure = ramp + solution
        flux = jnp.where(face, link * (pressure - upper_of(pressure)), 0.0)
        total = jnp.sum(flux, axis=0)
        total = jnp.sum(total, axis=0, keepdims=True)
        rows.append(total * (0.5 / area))
    rows.append(jnp.zeros((8 - len(rows), LANES), jnp.float32))
    o_ref[0] = jnp.concatenate(rows, axis=0)


def upscale_windows(raw, facies_table):
    span_y = CCY + 2 * RIM
    count_z = (raw.shape[1] - 2 * RIM) // CCZ
    count_x = (raw.shape[2] - 2 * RIM) // CCX
    count_y = (raw.shape[3] - 2 * RIM) // CCY
    wide = -(-(raw.shape[3] + LANES) // LANES) * LANES
    raw = jnp.pad(raw, ((0, 0),) * 3 + ((0, wide - raw.shape[3]),))
    count = count_z * count_x * count_y
    segments = LANES // span_y
    packs = -(-count // segments)
    kernel = functools.partial(window_kernel, count_x=count_x, count_y=count_y, count=count)
    sums = pl.pallas_call(
        kernel,
        grid=(packs,),
        in_specs=[
            pl.BlockSpec(memory_space=pltpu.SMEM),
            pl.BlockSpec(raw.shape, lambda p: (0, 0, 0, 0)),
        ],
        out_specs=pl.BlockSpec((1, 8, LANES), lambda p: (p, 0, 0)),
        out_shape=jax.ShapeDtypeStruct((packs, 8, LANES), jnp.float32),
    )(facies_table, raw)
    sums = sums[:, :3, : segments * span_y].reshape(packs, 3, segments, span_y).sum(axis=3)
    sums = sums.transpose(1, 0, 2).reshape(3, packs * segments)[:, :count]
    return sums.reshape((3, count_z, count_x, count_y))


def coarse_sweep(perm_pad, press_pad, inside_pad, accumulation, fixed):
    centre = (slice(1, -1), slice(1, -1), slice(1, -1))
    factors = (CCY * CCZ / CCX, CCX * CCZ / CCY, CCX * CCY / CCZ)
    numer = fixed
    denom = accumulation
    for component, axis_dim in ((0, 1), (1, 2), (2, 0)):
        for offset in (-1, 1):
            window_slice = [slice(1, -1), slice(1, -1), slice(1, -1)]
            window_slice[axis_dim] = slice(1 + offset, press_pad.shape[axis_dim] - 1 + offset)
            beside = tuple(window_slice)
            link = (
                factors[component]
                * 0.5
                * (perm_pad[component][centre] + perm_pad[component][beside])
                * inside_pad[beside]
            )
            numer = numer + link * press_pad[beside]
            denom = denom + jnp.abs(link)
    return numer / denom


def span_mask(anchor, length, total, margin):
    coords = anchor - margin + jnp.arange(length + 2 * margin, dtype=jnp.int32)
    return ((coords >= 0) & (coords < total)).astype(jnp.float32)


def cut_windows(fields):
    span_z = CCZ + 2 * RIM
    span_x = CCX + 2 * RIM
    span_y = CCY + 2 * RIM
    count_z = (fields[0].shape[0] - 2 * RIM) // CCZ
    count_x = (fields[0].shape[1] - 2 * RIM) // CCX
    count_y = (fields[0].shape[2] - 2 * RIM) // CCY
    stacks = []
    for field in fields:
        pieces = []
        for block_z in range(count_z):
            for block_y in range(count_y):
                piece = field[
                    block_z * CCZ : block_z * CCZ + span_z,
                    0:span_x,
                    block_y * CCY : block_y * CCY + span_y,
                ]
                pieces.append(piece.reshape(span_z, span_x * span_y))
        stacks.append(jnp.stack(pieces))
    return (stacks, (count_z, count_x, count_y))


def faces(block, sides):
    got = []
    for axis, dim in sides:
        count = lax.axis_size(axis)
        ends = count - 1
        head = lax.slice_in_dim(block, 0, 1, axis=dim)
        tail = lax.slice_in_dim(block, block.shape[dim] - 1, block.shape[dim], axis=dim)
        lower = lax.ppermute(tail, axis, [(i, i + 1) for i in range(ends)])
        upper = lax.ppermute(head, axis, [(i + 1, i) for i in range(ends)])
        got.append((lower, upper))
    return got


def neighbour_views(block, got, dim_of):
    views = []
    for (lower, upper), dim in zip(got, dim_of):
        size = block.shape[dim]
        below = jnp.concatenate([lower, lax.slice_in_dim(block, 0, size - 1, axis=dim)], axis=dim)
        above = jnp.concatenate([lax.slice_in_dim(block, 1, size, axis=dim), upper], axis=dim)
        views.append((below, above))
    return views


def coarse_step(upscaled, views, inside_views, pressure, accumulation, fixed):
    factors = (CCY * CCZ / CCX, CCX * CCZ / CCY, CCX * CCY / CCZ)
    numer = fixed
    denom = accumulation
    for component in range(3):
        for side in range(2):
            beside = views[component][side]
            link = factors[component] * 0.5 * (upscaled[component] + beside[component]) * inside_views[component][side]
            numer = numer + link * pressure[component][side]
            denom = denom + jnp.abs(link)
    return numer / denom


def local(log_noise, facies, facies_table, pressure_old, accumulation, source):
    depth_len, rows_len, cols_len = log_noise.shape
    size_z = lax.axis_size("gz")
    size_x = lax.axis_size("gx")
    size_y = lax.axis_size("gy")
    index_z = lax.axis_index("gz")
    index_x = lax.axis_index("gx")
    index_y = lax.axis_index("gy")
    raw = jnp.stack([log_noise, facies.astype(jnp.float32)])
    raw = extended(raw, (("gx", 2), ("gy", 3), ("gz", 1)), RIM)
    anchor_z = index_z * depth_len
    anchor_y = index_y * cols_len
    anchor_x = index_x * rows_len
    mask_z = span_mask(anchor_z, depth_len, depth_len * size_z, RIM)
    mask_x = span_mask(anchor_x, rows_len, rows_len * size_x, RIM)
    mask_y = span_mask(anchor_y, cols_len, cols_len * size_y, RIM)
    inside = mask_z[:, None, None] * mask_x[None, :, None] * mask_y[None, None, :]
    upscaled = upscale_windows(jnp.concatenate([raw, inside[None]]), facies_table)
    coarse_z, coarse_x, coarse_y = pressure_old.shape
    bundle = jnp.stack([upscaled[0], upscaled[1], upscaled[2], pressure_old, accumulation, source])
    every = lax.all_gather(bundle, "gy", axis=3, tiled=True)
    every = lax.all_gather(every, "gx", axis=2, tiled=True)
    every = lax.all_gather(every, "gz", axis=1, tiled=True)
    perm_pad = jnp.pad(every[:3], ((0, 0), (1, 1), (1, 1), (1, 1)))
    old_all = every[3]
    acc_all = every[4]
    fixed_all = acc_all * old_all + every[5]
    inside_pad = jnp.pad(jnp.ones(old_all.shape, jnp.float32), 1)
    pressure = old_all
    for sweep_index in range(2):
        pressure = coarse_sweep(perm_pad, jnp.pad(pressure, 1), inside_pad, acc_all, fixed_all)
    pressure = lax.dynamic_slice(
        pressure, (index_z * coarse_z, index_x * coarse_x, index_y * coarse_y), (coarse_z, coarse_x, coarse_y)
    )
    return (pressure, upscaled)


def solution(mesh):
    placed = (
        P(("real", "gz"), "gx", "gy"),
        P(("real", "gz"), "gx", "gy"),
        P(),
        P(("real", "gz"), "gx", "gy"),
        P(("real", "gz"), "gx", "gy"),
        P(("real", "gz"), "gx", "gy"),
    )
    return jax.shard_map(
        local,
        mesh=mesh,
        in_specs=placed,
        out_specs=(P(("real", "gz"), "gx", "gy"), P(None, ("real", "gz"), "gx", "gy")),
        check_vma=False,
    )
```

```python
import functools

import jax
import jax.numpy as jnp
from jax import lax
from jax.sharding import PartitionSpec as P
from jax.experimental import pallas as pl
from jax.experimental.pallas import tpu as pltpu

NFAC = 4
CCX = 32
CCY = 32
CCZ = 8
RIM = 4
SWEEPS = 3


BOUND_MID = 1.0
BOUND_HALF = 0.9


def extended(cells, sides, width, lanes=None):
    for axis, dim in sides:
        count = lax.axis_size(axis)
        ends = count - 1
        head = lax.slice_in_dim(cells, 0, width, axis=dim)
        tail = lax.slice_in_dim(cells, cells.shape[dim] - width, cells.shape[dim], axis=dim)
        if count == 2:
            lower_side = lax.axis_index(axis) == 0
            got = lax.ppermute(jnp.where(lower_side, tail, head), axis, [(0, 1), (1, 0)])
            below = jnp.where(lower_side, 0.0, got)
            above = jnp.where(lower_side, got, 0.0)
        else:
            below = lax.ppermute(tail, axis, [(i, (i + 1) % count) for i in range(ends)])
            above = lax.ppermute(head, axis, [((i + 1) % count, i) for i in range(ends)])
        parts = [below, cells, above]
        if lanes is not None and dim == cells.ndim - 1:
            extra = lanes - (cells.shape[dim] + 2 * width)
            parts.append(jnp.zeros(cells.shape[:-1] + (extra,), cells.dtype))
        cells = jnp.concatenate(parts, axis=dim)
    return cells


def raise_flat(values, offset):
    zeros_block = jnp.zeros(values.shape[:-1] + (offset,), values.dtype)
    return jnp.concatenate([values[..., offset:], zeros_block], axis=-1)


def lower_flat(values, offset):
    zeros_block = jnp.zeros(values.shape[:-1] + (offset,), values.dtype)
    return jnp.concatenate([zeros_block, values[..., :-offset]], axis=-1)


def raise_depth(values):
    zeros_block = jnp.zeros(values.shape[:1] + (1,) + values.shape[2:], values.dtype)
    return jnp.concatenate([values[:, 1:], zeros_block], axis=1)


def lower_depth(values):
    zeros_block = jnp.zeros(values.shape[:1] + (1,) + values.shape[2:], values.dtype)
    return jnp.concatenate([zeros_block, values[:, :-1]], axis=1)


def log_fields(log_noise, facies, facies_table):
    base_log = log_noise
    extra_y = jnp.zeros_like(log_noise)
    extra_z = jnp.zeros_like(log_noise)
    for code_value in range(NFAC):
        matched = facies == code_value
        base_log = base_log + jnp.where(matched, facies_table[0, code_value], jnp.float32(0.0))
        extra_y = extra_y + jnp.where(matched, facies_table[1, code_value], jnp.float32(0.0))
        extra_z = extra_z + jnp.where(matched, facies_table[2, code_value], jnp.float32(0.0))
    return (base_log, base_log + extra_y, base_log + extra_z)


def upscale(perm_logs, inside):
    span_z = CCZ + 2 * RIM
    span_x = CCX + 2 * RIM
    span_y = CCY + 2 * RIM
    depth_pos = lax.broadcasted_iota(jnp.int32, (1, span_z, 1), 1)
    flat_pos = lax.broadcasted_iota(jnp.int32, (1, 1, span_x * span_y), 2)
    column_pos = flat_pos // span_y
    row_pos = flat_pos % span_y
    perm_x = jnp.exp(perm_logs[0])
    perm_y = jnp.exp(perm_logs[1])
    perm_z = jnp.exp(perm_logs[2])

    def links(perm, other_perm, other_inside):
        return inside * other_inside * 2.0 * perm * other_perm / (perm + other_perm)

    link_x = links(perm_x, raise_flat(perm_x, span_y), raise_flat(inside, span_y))
    link_y = links(perm_y, raise_flat(perm_y, 1), raise_flat(inside, 1)) * (
        row_pos < span_y - 1
    ).astype(jnp.float32)
    link_z = links(perm_z, raise_depth(perm_z), raise_depth(inside))
    diagonal = (
        link_x
        + lower_flat(link_x, span_y)
        + link_y
        + lower_flat(link_y, 1)
        + link_z
        + lower_depth(link_z)
    )

    def apply_operator(field):
        beside = link_x * raise_flat(field, span_y) + lower_flat(link_x * field, span_y)
        beside = beside + link_y * raise_flat(field, 1) + lower_flat(link_y * field, 1)
        beside = beside + link_z * raise_depth(field) + lower_depth(link_z * field)
        return diagonal * field - beside

    interior = (
        (depth_pos >= 1)
        & (depth_pos <= span_z - 2)
        & (column_pos >= 1)
        & (column_pos <= span_x - 2)
        & (row_pos >= 1)
        & (row_pos <= span_y - 2)
    )
    unknown = inside * interior.astype(jnp.float32)
    scaling = unknown / (diagonal + 1.0 - unknown)
    core_z = (depth_pos >= RIM) & (depth_pos < RIM + CCZ)
    core_x = (column_pos >= RIM) & (column_pos < RIM + CCX)
    core_y = (row_pos >= RIM) & (row_pos < RIM + CCY)
    face_x = (((column_pos == RIM - 1) | (column_pos == RIM + CCX - 1)) & core_z & core_y).astype(
        jnp.float32
    )
    face_y = (((row_pos == RIM - 1) | (row_pos == RIM + CCY - 1)) & core_z & core_x).astype(
        jnp.float32
    )
    face_z = (((depth_pos == RIM - 1) | (depth_pos == RIM + CCZ - 1)) & core_x & core_y).astype(
        jnp.float32
    )
    ramp_x = ((span_x - 1) / 2.0 - column_pos).astype(jnp.float32)
    ramp_y = ((span_y - 1) / 2.0 - row_pos).astype(jnp.float32)
    ramp_z = ((span_z - 1) / 2.0 - depth_pos).astype(jnp.float32)
    cheb_ratio = BOUND_MID / BOUND_HALF
    results = []
    cases = (
        (ramp_x, link_x, face_x, CCY * CCZ, 0),
        (ramp_y, link_y, face_y, CCX * CCZ, 1),
        (ramp_z, link_z, face_z, CCX * CCY, 2),
    )
    for ramp, link, face, area, direction in cases:
        ramp_full = jnp.broadcast_to(ramp, inside.shape)
        source_term = -unknown * apply_operator(ramp_full)
        update = scaling * source_term / BOUND_MID
        solution = update
        rho_old = 1.0 / cheb_ratio
        for sweep_index in range(SWEEPS - 1):
            residual = source_term - apply_operator(solution)
            rho_new = 1.0 / (2.0 * cheb_ratio - rho_old)
            update = rho_new * rho_old * update + 2.0 * rho_new / BOUND_HALF * (scaling * residual)
            solution = solution + update
            rho_old = rho_new
        pressure = ramp_full + solution
        if direction == 0:
            upper = raise_flat(pressure, span_y)
        elif direction == 1:
            upper = raise_flat(pressure, 1)
        else:
            upper = raise_depth(pressure)
        flux = link * (pressure - upper) * face
        results.append(jnp.sum(flux, axis=(1, 2)) * (0.5 / area))
    return jnp.stack(results)


LANES = 128


def window_kernel(table_ref, bounds_ref, raw_ref, o_ref, *, count_x, count_y, count):
    span_z = CCZ + 2 * RIM
    span_x = CCX + 2 * RIM
    span_y = CCY + 2 * RIM
    segments = LANES // span_y
    shape = (span_z, span_x, LANES)
    pack = pl.program_id(0)
    wide = raw_ref.shape[-1]
    depth_pos = lax.broadcasted_iota(jnp.int32, shape, 0)
    column_pos = lax.broadcasted_iota(jnp.int32, shape, 1)
    lane = lax.broadcasted_iota(jnp.int32, shape, 2)
    segment = jnp.zeros(shape, jnp.int32)
    for bound in range(1, segments + 1):
        segment = segment + (lane >= bound * span_y).astype(jnp.int32)
    row_pos = lane - span_y * segment
    noise = jnp.zeros(shape, jnp.float32)
    codes = jnp.zeros(shape, jnp.float32)
    inside = jnp.zeros(shape, jnp.float32)
    for slot in range(segments):
        window = pack * segments + slot
        valid = window < count
        window = jnp.minimum(window, count - 1)
        block_z = window // (count_x * count_y)
        block_x = (window // count_y) % count_x
        block_y = window % count_y
        shift = (slot * span_y - block_y * CCY + wide) % wide
        here = segment == slot

        def cut(field):
            slab = raw_ref[field, pl.ds(block_z * CCZ, span_z), pl.ds(block_x * CCX, span_x), :]
            return pltpu.roll(slab, shift, 2)[:, :, :LANES]

        depth_at = depth_pos + block_z * CCZ
        column_at = column_pos + block_x * CCX
        row_at = row_pos + block_y * CCY
        held = (
            (depth_at >= bounds_ref[0])
            & (depth_at < bounds_ref[1])
            & (column_at >= bounds_ref[2])
            & (column_at < bounds_ref[3])
            & (row_at >= bounds_ref[4])
            & (row_at < bounds_ref[5])
        )
        noise = jnp.where(here, cut(0), noise)
        codes = jnp.where(here, cut(1), codes)
        inside = jnp.where(here & valid & held, 1.0, inside)

    def lookup(row):
        value = jnp.zeros(shape, jnp.float32)
        for code_value in range(NFAC):
            value = jnp.where(codes == code_value, table_ref[row, code_value], value)
        return value

    log_x = noise + lookup(0)
    log_y = log_x + lookup(1)
    log_z = log_x + lookup(2)
    perm_x = jnp.exp(log_x)
    perm_y = jnp.exp(log_y)
    perm_z = jnp.exp(log_z)

    def up_x(v):
        return pltpu.roll(v, span_x - 1, 1)

    def down_x(v):
        return pltpu.roll(v, 1, 1)

    def up_y(v):
        return pltpu.roll(v, LANES - 1, 2)

    def down_y(v):
        return pltpu.roll(v, 1, 2)

    def up_z(v):
        return jnp.concatenate([v[1:], v[:1]], axis=0)

    def down_z(v):
        return jnp.concatenate([v[-1:], v[:-1]], axis=0)

    def links(perm, other_perm, other_inside, valid):
        value = inside * other_inside * 2.0 * perm * other_perm / (perm + other_perm)
        return jnp.where(valid, value, 0.0)

    link_x = links(perm_x, up_x(perm_x), up_x(inside), column_pos < span_x - 1)
    link_y = links(perm_y, up_y(perm_y), up_y(inside), row_pos < span_y - 1)
    link_z = links(perm_z, up_z(perm_z), up_z(inside), depth_pos < span_z - 1)
    diagonal = link_x + down_x(link_x) + link_y + down_y(link_y) + link_z + down_z(link_z)

    def apply_operator(field):
        beside = link_x * up_x(field) + down_x(link_x * field)
        beside = beside + link_y * up_y(field) + down_y(link_y * field)
        beside = beside + link_z * up_z(field) + down_z(link_z * field)
        return diagonal * field - beside

    interior = (
        (depth_pos >= 1)
        & (depth_pos <= span_z - 2)
        & (column_pos >= 1)
        & (column_pos <= span_x - 2)
        & (row_pos >= 1)
        & (row_pos <= span_y - 2)
    )
    unknown = jnp.where(interior, inside, 0.0)
    scaling = unknown / (diagonal + 1.0 - unknown)
    core_z = (depth_pos >= RIM) & (depth_pos < RIM + CCZ)
    core_x = (column_pos >= RIM) & (column_pos < RIM + CCX)
    core_y = (row_pos >= RIM) & (row_pos < RIM + CCY)
    face_x = ((column_pos == RIM - 1) | (column_pos == RIM + CCX - 1)) & core_z & core_y
    face_y = ((row_pos == RIM - 1) | (row_pos == RIM + CCY - 1)) & core_z & core_x
    face_z = ((depth_pos == RIM - 1) | (depth_pos == RIM + CCZ - 1)) & core_x & core_y
    ramp_x = ((span_x - 1) / 2.0 - column_pos).astype(jnp.float32)
    ramp_y = ((span_y - 1) / 2.0 - row_pos).astype(jnp.float32)
    ramp_z = ((span_z - 1) / 2.0 - depth_pos).astype(jnp.float32)
    cheb_ratio = BOUND_MID / BOUND_HALF
    cases = (
        (ramp_x, link_x, face_x, CCY * CCZ, up_x, down_x),
        (ramp_y, link_y, face_y, CCX * CCZ, up_y, down_y),
        (ramp_z, link_z, face_z, CCX * CCY, up_z, down_z),
    )
    rows = []
    for ramp, link, face, area, upper_of, lower_of in cases:
        source_term = -unknown * (link - lower_of(link))
        update = scaling * source_term / BOUND_MID
        solution = update
        rho_old = 1.0 / cheb_ratio
        for sweep_index in range(SWEEPS - 1):
            residual = source_term - apply_operator(solution)
            rho_new = 1.0 / (2.0 * cheb_ratio - rho_old)
            update = rho_new * rho_old * update + 2.0 * rho_new / BOUND_HALF * (scaling * residual)
            solution = solution + update
            rho_old = rho_new
        pressure = ramp + solution
        flux = jnp.where(face, link * (pressure - upper_of(pressure)), 0.0)
        total = jnp.sum(flux, axis=0)
        total = jnp.sum(total, axis=0, keepdims=True)
        rows.append(total * (0.5 / area))
    rows.append(jnp.zeros((8 - len(rows), LANES), jnp.float32))
    o_ref[0] = jnp.concatenate(rows, axis=0)


def upscale_windows(raw, facies_table, bounds, cols_len):
    span_y = CCY + 2 * RIM
    count_z = (raw.shape[1] - 2 * RIM) // CCZ
    count_x = (raw.shape[2] - 2 * RIM) // CCX
    count_y = cols_len // CCY
    count = count_z * count_x * count_y
    segments = LANES // span_y
    packs = -(-count // segments)
    kernel = functools.partial(window_kernel, count_x=count_x, count_y=count_y, count=count)
    sums = pl.pallas_call(
        kernel,
        grid=(packs,),
        in_specs=[
            pl.BlockSpec(memory_space=pltpu.SMEM),
            pl.BlockSpec(memory_space=pltpu.SMEM),
            pl.BlockSpec(raw.shape, lambda p: (0, 0, 0, 0)),
        ],
        out_specs=pl.BlockSpec((1, 8, LANES), lambda p: (p, 0, 0)),
        out_shape=jax.ShapeDtypeStruct((packs, 8, LANES), jnp.float32),
    )(facies_table, bounds, raw)
    sums = sums[:, :3, : segments * span_y].reshape(packs, 3, segments, span_y).sum(axis=3)
    sums = sums.transpose(1, 0, 2).reshape(3, packs * segments)[:, :count]
    return sums.reshape((3, count_z, count_x, count_y))


def coarse_sweep(perm_pad, press_pad, inside_pad, accumulation, fixed):
    centre = (slice(1, -1), slice(1, -1), slice(1, -1))
    factors = (CCY * CCZ / CCX, CCX * CCZ / CCY, CCX * CCY / CCZ)
    numer = fixed
    denom = accumulation
    for component, axis_dim in ((0, 1), (1, 2), (2, 0)):
        for offset in (-1, 1):
            window_slice = [slice(1, -1), slice(1, -1), slice(1, -1)]
            window_slice[axis_dim] = slice(1 + offset, press_pad.shape[axis_dim] - 1 + offset)
            beside = tuple(window_slice)
            link = (
                factors[component]
                * 0.5
                * (perm_pad[component][centre] + perm_pad[component][beside])
                * inside_pad[beside]
            )
            numer = numer + link * press_pad[beside]
            denom = denom + jnp.abs(link)
    return numer / denom


def span_mask(anchor, length, total, margin):
    coords = anchor - margin + jnp.arange(length + 2 * margin, dtype=jnp.int32)
    return ((coords >= 0) & (coords < total)).astype(jnp.float32)


def cut_windows(fields):
    span_z = CCZ + 2 * RIM
    span_x = CCX + 2 * RIM
    span_y = CCY + 2 * RIM
    count_z = (fields[0].shape[0] - 2 * RIM) // CCZ
    count_x = (fields[0].shape[1] - 2 * RIM) // CCX
    count_y = (fields[0].shape[2] - 2 * RIM) // CCY
    stacks = []
    for field in fields:
        pieces = []
        for block_z in range(count_z):
            for block_y in range(count_y):
                piece = field[
                    block_z * CCZ : block_z * CCZ + span_z,
                    0:span_x,
                    block_y * CCY : block_y * CCY + span_y,
                ]
                pieces.append(piece.reshape(span_z, span_x * span_y))
        stacks.append(jnp.stack(pieces))
    return (stacks, (count_z, count_x, count_y))


def faces(block, sides):
    got = []
    for axis, dim in sides:
        count = lax.axis_size(axis)
        ends = count - 1
        head = lax.slice_in_dim(block, 0, 1, axis=dim)
        tail = lax.slice_in_dim(block, block.shape[dim] - 1, block.shape[dim], axis=dim)
        lower = lax.ppermute(tail, axis, [(i, i + 1) for i in range(ends)])
        upper = lax.ppermute(head, axis, [(i + 1, i) for i in range(ends)])
        got.append((lower, upper))
    return got


def neighbour_views(block, got, dim_of):
    views = []
    for (lower, upper), dim in zip(got, dim_of):
        size = block.shape[dim]
        below = jnp.concatenate([lower, lax.slice_in_dim(block, 0, size - 1, axis=dim)], axis=dim)
        above = jnp.concatenate([lax.slice_in_dim(block, 1, size, axis=dim), upper], axis=dim)
        views.append((below, above))
    return views


def coarse_step(upscaled, views, inside_views, pressure, accumulation, fixed):
    factors = (CCY * CCZ / CCX, CCX * CCZ / CCY, CCX * CCY / CCZ)
    numer = fixed
    denom = accumulation
    for component in range(3):
        for side in range(2):
            beside = views[component][side]
            link = factors[component] * 0.5 * (upscaled[component] + beside[component]) * inside_views[component][side]
            numer = numer + link * pressure[component][side]
            denom = denom + jnp.abs(link)
    return numer / denom


def local(log_noise, facies, facies_table, pressure_old, accumulation, source):
    depth_len, rows_len, cols_len = log_noise.shape
    size_z = lax.axis_size("gz")
    size_x = lax.axis_size("gx")
    size_y = lax.axis_size("gy")
    index_z = lax.axis_index("gz")
    index_x = lax.axis_index("gx")
    index_y = lax.axis_index("gy")
    raw = jnp.stack([log_noise, facies.astype(jnp.float32)])
    wide = -(-(cols_len + 2 * RIM) // LANES) * LANES
    raw = extended(raw, (("gx", 2), ("gz", 1), ("gy", 3)), RIM, wide)
    anchor_z = index_z * depth_len
    anchor_y = index_y * cols_len
    anchor_x = index_x * rows_len
    bounds = jnp.stack(
        [
            RIM - anchor_z,
            depth_len * size_z + RIM - anchor_z,
            RIM - anchor_x,
            rows_len * size_x + RIM - anchor_x,
            RIM - anchor_y,
            cols_len * size_y + RIM - anchor_y,
        ]
    ).astype(jnp.int32)
    upscaled = upscale_windows(raw, facies_table, bounds, cols_len)
    coarse_z, coarse_x, coarse_y = pressure_old.shape
    bundle = jnp.stack([upscaled[0], upscaled[1], upscaled[2], pressure_old, accumulation, source])
    every = lax.all_gather(bundle, "gy", axis=3, tiled=True)
    every = lax.all_gather(every, "gx", axis=2, tiled=True)
    every = lax.all_gather(every, "gz", axis=1, tiled=True)
    perm_pad = jnp.pad(every[:3], ((0, 0), (1, 1), (1, 1), (1, 1)))
    old_all = every[3]
    acc_all = every[4]
    fixed_all = acc_all * old_all + every[5]
    inside_pad = jnp.pad(jnp.ones(old_all.shape, jnp.float32), 1)
    pressure = old_all
    for sweep_index in range(2):
        pressure = coarse_sweep(perm_pad, jnp.pad(pressure, 1), inside_pad, acc_all, fixed_all)
    pressure = lax.dynamic_slice(
        pressure, (index_z * coarse_z, index_x * coarse_x, index_y * coarse_y), (coarse_z, coarse_x, coarse_y)
    )
    return (pressure, upscaled)


def solution(mesh):
    placed = (
        P(("real", "gz"), "gx", "gy"),
        P(("real", "gz"), "gx", "gy"),
        P(),
        P(("real", "gz"), "gx", "gy"),
        P(("real", "gz"), "gx", "gy"),
        P(("real", "gz"), "gx", "gy"),
    )
    return jax.shard_map(
        local,
        mesh=mesh,
        in_specs=placed,
        out_specs=(P(("real", "gz"), "gx", "gy"), P(None, ("real", "gz"), "gx", "gy")),
        check_vma=False,
    )
```

```python
import functools

import jax
import jax.numpy as jnp
from jax import lax
from jax.sharding import PartitionSpec as P
from jax.experimental import pallas as pl
from jax.experimental.pallas import tpu as pltpu

NFAC = 4
CCX = 32
CCY = 32
CCZ = 8
RIM = 4
SWEEPS = 3


BOUND_MID = 1.0
BOUND_HALF = 0.9


def extended(cells, sides, width, lanes=None):
    for axis, dim in sides:
        count = lax.axis_size(axis)
        ends = count - 1
        head = lax.slice_in_dim(cells, 0, width, axis=dim)
        tail = lax.slice_in_dim(cells, cells.shape[dim] - width, cells.shape[dim], axis=dim)
        if count == 2:
            lower_side = lax.axis_index(axis) == 0
            got = lax.ppermute(jnp.where(lower_side, tail, head), axis, [(0, 1), (1, 0)])
            below = jnp.where(lower_side, 0.0, got)
            above = jnp.where(lower_side, got, 0.0)
        else:
            below = lax.ppermute(tail, axis, [(i, (i + 1) % count) for i in range(ends)])
            above = lax.ppermute(head, axis, [((i + 1) % count, i) for i in range(ends)])
        parts = [below, cells, above]
        if lanes is not None and dim == cells.ndim - 1:
            extra = lanes - (cells.shape[dim] + 2 * width)
            parts.append(jnp.zeros(cells.shape[:-1] + (extra,), cells.dtype))
        cells = jnp.concatenate(parts, axis=dim)
    return cells


def raise_flat(values, offset):
    zeros_block = jnp.zeros(values.shape[:-1] + (offset,), values.dtype)
    return jnp.concatenate([values[..., offset:], zeros_block], axis=-1)


def lower_flat(values, offset):
    zeros_block = jnp.zeros(values.shape[:-1] + (offset,), values.dtype)
    return jnp.concatenate([zeros_block, values[..., :-offset]], axis=-1)


def raise_depth(values):
    zeros_block = jnp.zeros(values.shape[:1] + (1,) + values.shape[2:], values.dtype)
    return jnp.concatenate([values[:, 1:], zeros_block], axis=1)


def lower_depth(values):
    zeros_block = jnp.zeros(values.shape[:1] + (1,) + values.shape[2:], values.dtype)
    return jnp.concatenate([zeros_block, values[:, :-1]], axis=1)


def log_fields(log_noise, facies, facies_table):
    base_log = log_noise
    extra_y = jnp.zeros_like(log_noise)
    extra_z = jnp.zeros_like(log_noise)
    for code_value in range(NFAC):
        matched = facies == code_value
        base_log = base_log + jnp.where(matched, facies_table[0, code_value], jnp.float32(0.0))
        extra_y = extra_y + jnp.where(matched, facies_table[1, code_value], jnp.float32(0.0))
        extra_z = extra_z + jnp.where(matched, facies_table[2, code_value], jnp.float32(0.0))
    return (base_log, base_log + extra_y, base_log + extra_z)


def upscale(perm_logs, inside):
    span_z = CCZ + 2 * RIM
    span_x = CCX + 2 * RIM
    span_y = CCY + 2 * RIM
    depth_pos = lax.broadcasted_iota(jnp.int32, (1, span_z, 1), 1)
    flat_pos = lax.broadcasted_iota(jnp.int32, (1, 1, span_x * span_y), 2)
    column_pos = flat_pos // span_y
    row_pos = flat_pos % span_y
    perm_x = jnp.exp(perm_logs[0])
    perm_y = jnp.exp(perm_logs[1])
    perm_z = jnp.exp(perm_logs[2])

    def links(perm, other_perm, other_inside):
        return inside * other_inside * 2.0 * perm * other_perm / (perm + other_perm)

    link_x = links(perm_x, raise_flat(perm_x, span_y), raise_flat(inside, span_y))
    link_y = links(perm_y, raise_flat(perm_y, 1), raise_flat(inside, 1)) * (
        row_pos < span_y - 1
    ).astype(jnp.float32)
    link_z = links(perm_z, raise_depth(perm_z), raise_depth(inside))
    diagonal = (
        link_x
        + lower_flat(link_x, span_y)
        + link_y
        + lower_flat(link_y, 1)
        + link_z
        + lower_depth(link_z)
    )

    def apply_operator(field):
        beside = link_x * raise_flat(field, span_y) + lower_flat(link_x * field, span_y)
        beside = beside + link_y * raise_flat(field, 1) + lower_flat(link_y * field, 1)
        beside = beside + link_z * raise_depth(field) + lower_depth(link_z * field)
        return diagonal * field - beside

    interior = (
        (depth_pos >= 1)
        & (depth_pos <= span_z - 2)
        & (column_pos >= 1)
        & (column_pos <= span_x - 2)
        & (row_pos >= 1)
        & (row_pos <= span_y - 2)
    )
    unknown = inside * interior.astype(jnp.float32)
    scaling = unknown / (diagonal + 1.0 - unknown)
    core_z = (depth_pos >= RIM) & (depth_pos < RIM + CCZ)
    core_x = (column_pos >= RIM) & (column_pos < RIM + CCX)
    core_y = (row_pos >= RIM) & (row_pos < RIM + CCY)
    face_x = (((column_pos == RIM - 1) | (column_pos == RIM + CCX - 1)) & core_z & core_y).astype(
        jnp.float32
    )
    face_y = (((row_pos == RIM - 1) | (row_pos == RIM + CCY - 1)) & core_z & core_x).astype(
        jnp.float32
    )
    face_z = (((depth_pos == RIM - 1) | (depth_pos == RIM + CCZ - 1)) & core_x & core_y).astype(
        jnp.float32
    )
    ramp_x = ((span_x - 1) / 2.0 - column_pos).astype(jnp.float32)
    ramp_y = ((span_y - 1) / 2.0 - row_pos).astype(jnp.float32)
    ramp_z = ((span_z - 1) / 2.0 - depth_pos).astype(jnp.float32)
    cheb_ratio = BOUND_MID / BOUND_HALF
    results = []
    cases = (
        (ramp_x, link_x, face_x, CCY * CCZ, 0),
        (ramp_y, link_y, face_y, CCX * CCZ, 1),
        (ramp_z, link_z, face_z, CCX * CCY, 2),
    )
    for ramp, link, face, area, direction in cases:
        ramp_full = jnp.broadcast_to(ramp, inside.shape)
        source_term = -unknown * apply_operator(ramp_full)
        update = scaling * source_term / BOUND_MID
        solution = update
        rho_old = 1.0 / cheb_ratio
        for sweep_index in range(SWEEPS - 1):
            residual = source_term - apply_operator(solution)
            rho_new = 1.0 / (2.0 * cheb_ratio - rho_old)
            update = rho_new * rho_old * update + 2.0 * rho_new / BOUND_HALF * (scaling * residual)
            solution = solution + update
            rho_old = rho_new
        pressure = ramp_full + solution
        if direction == 0:
            upper = raise_flat(pressure, span_y)
        elif direction == 1:
            upper = raise_flat(pressure, 1)
        else:
            upper = raise_depth(pressure)
        flux = link * (pressure - upper) * face
        results.append(jnp.sum(flux, axis=(1, 2)) * (0.5 / area))
    return jnp.stack(results)


LANES = 128


def window_kernel(table_ref, bounds_ref, raw_ref, o_ref, *, count_x, count_y, count):
    span_z = CCZ + 2 * RIM
    span_x = CCX + 2 * RIM
    span_y = CCY + 2 * RIM
    segments = LANES // span_y
    shape = (span_z, span_x, LANES)
    pack = pl.program_id(0)
    wide = raw_ref.shape[-1]
    depth_pos = lax.broadcasted_iota(jnp.int32, shape, 0)
    column_pos = lax.broadcasted_iota(jnp.int32, shape, 1)
    lane = lax.broadcasted_iota(jnp.int32, shape, 2)
    segment = jnp.zeros(shape, jnp.int32)
    for bound in range(1, segments + 1):
        segment = segment + (lane >= bound * span_y).astype(jnp.int32)
    row_pos = lane - span_y * segment
    noise = jnp.zeros(shape, jnp.float32)
    codes = jnp.zeros(shape, jnp.float32)
    inside = jnp.zeros(shape, jnp.float32)
    for slot in range(segments):
        window = pack * segments + slot
        valid = window < count
        window = jnp.minimum(window, count - 1)
        block_z = window // (count_x * count_y)
        block_x = (window // count_y) % count_x
        block_y = window % count_y
        shift = (slot * span_y - block_y * CCY + wide) % wide
        here = segment == slot

        def cut(field):
            slab = raw_ref[field, pl.ds(block_z * CCZ, span_z), pl.ds(block_x * CCX, span_x), :]
            return pltpu.roll(slab, shift, 2)[:, :, :LANES]

        depth_at = depth_pos + block_z * CCZ
        column_at = column_pos + block_x * CCX
        row_at = row_pos + block_y * CCY
        held = (
            (depth_at >= bounds_ref[0])
            & (depth_at < bounds_ref[1])
            & (column_at >= bounds_ref[2])
            & (column_at < bounds_ref[3])
            & (row_at >= bounds_ref[4])
            & (row_at < bounds_ref[5])
        )
        noise = jnp.where(here, cut(0), noise)
        codes = jnp.where(here, cut(1), codes)
        inside = jnp.where(here & valid & held, 1.0, inside)

    matches = [codes == code_value for code_value in range(NFAC)]

    def lookup(row):
        value = jnp.zeros(shape, jnp.float32)
        for code_value in range(NFAC):
            value = jnp.where(matches[code_value], table_ref[row, code_value], value)
        return value

    log_x = noise + lookup(0)
    log_y = log_x + lookup(1)
    log_z = log_x + lookup(2)
    perm_x = jnp.exp(log_x)
    perm_y = jnp.exp(log_y)
    perm_z = jnp.exp(log_z)

    def up_x(v):
        return pltpu.roll(v, span_x - 1, 1)

    def down_x(v):
        return pltpu.roll(v, 1, 1)

    def up_y(v):
        return pltpu.roll(v, LANES - 1, 2)

    def down_y(v):
        return pltpu.roll(v, 1, 2)

    def up_z(v):
        return jnp.concatenate([v[1:], v[:1]], axis=0)

    def down_z(v):
        return jnp.concatenate([v[-1:], v[:-1]], axis=0)

    def links(perm, other_perm, other_inside, valid):
        value = inside * other_inside * 2.0 * perm * other_perm / (perm + other_perm)
        return jnp.where(valid, value, 0.0)

    link_x = links(perm_x, up_x(perm_x), up_x(inside), column_pos < span_x - 1)
    link_y = links(perm_y, up_y(perm_y), up_y(inside), row_pos < span_y - 1)
    link_z = links(perm_z, up_z(perm_z), up_z(inside), depth_pos < span_z - 1)
    diagonal = link_x + down_x(link_x) + link_y + down_y(link_y) + link_z + down_z(link_z)

    def apply_operator(field):
        beside = link_x * up_x(field) + down_x(link_x * field)
        beside = beside + link_y * up_y(field) + down_y(link_y * field)
        beside = beside + link_z * up_z(field) + down_z(link_z * field)
        return diagonal * field - beside

    interior = (
        (depth_pos >= 1)
        & (depth_pos <= span_z - 2)
        & (column_pos >= 1)
        & (column_pos <= span_x - 2)
        & (row_pos >= 1)
        & (row_pos <= span_y - 2)
    )
    unknown = jnp.where(interior, inside, 0.0)
    scaling = unknown / (diagonal + 1.0 - unknown)
    core_z = (depth_pos >= RIM) & (depth_pos < RIM + CCZ)
    core_x = (column_pos >= RIM) & (column_pos < RIM + CCX)
    core_y = (row_pos >= RIM) & (row_pos < RIM + CCY)
    face_x = ((column_pos == RIM - 1) | (column_pos == RIM + CCX - 1)) & core_z & core_y
    face_y = ((row_pos == RIM - 1) | (row_pos == RIM + CCY - 1)) & core_z & core_x
    face_z = ((depth_pos == RIM - 1) | (depth_pos == RIM + CCZ - 1)) & core_x & core_y
    ramp_x = ((span_x - 1) / 2.0 - column_pos).astype(jnp.float32)
    ramp_y = ((span_y - 1) / 2.0 - row_pos).astype(jnp.float32)
    ramp_z = ((span_z - 1) / 2.0 - depth_pos).astype(jnp.float32)
    cheb_ratio = BOUND_MID / BOUND_HALF
    cases = (
        (ramp_x, link_x, face_x, CCY * CCZ, up_x, down_x),
        (ramp_y, link_y, face_y, CCX * CCZ, up_y, down_y),
        (ramp_z, link_z, face_z, CCX * CCY, up_z, down_z),
    )
    rows = []
    for ramp, link, face, area, upper_of, lower_of in cases:
        source_term = -unknown * (link - lower_of(link))
        update = scaling * source_term / BOUND_MID
        solution = update
        rho_old = 1.0 / cheb_ratio
        for sweep_index in range(SWEEPS - 1):
            residual = source_term - apply_operator(solution)
            rho_new = 1.0 / (2.0 * cheb_ratio - rho_old)
            update = rho_new * rho_old * update + 2.0 * rho_new / BOUND_HALF * (scaling * residual)
            solution = solution + update
            rho_old = rho_new
        pressure = ramp + solution
        flux = jnp.where(face, link * (pressure - upper_of(pressure)), 0.0)
        total = jnp.sum(flux, axis=0)
        total = jnp.sum(total, axis=0, keepdims=True)
        rows.append(total * (0.5 / area))
    rows.append(jnp.zeros((8 - len(rows), LANES), jnp.float32))
    o_ref[0] = jnp.concatenate(rows, axis=0)


def upscale_windows(raw, facies_table, bounds, cols_len):
    span_y = CCY + 2 * RIM
    count_z = (raw.shape[1] - 2 * RIM) // CCZ
    count_x = (raw.shape[2] - 2 * RIM) // CCX
    count_y = cols_len // CCY
    count = count_z * count_x * count_y
    segments = LANES // span_y
    packs = -(-count // segments)
    kernel = functools.partial(window_kernel, count_x=count_x, count_y=count_y, count=count)
    sums = pl.pallas_call(
        kernel,
        grid=(packs,),
        in_specs=[
            pl.BlockSpec(memory_space=pltpu.SMEM),
            pl.BlockSpec(memory_space=pltpu.SMEM),
            pl.BlockSpec(raw.shape, lambda p: (0, 0, 0, 0)),
        ],
        out_specs=pl.BlockSpec((1, 8, LANES), lambda p: (p, 0, 0)),
        out_shape=jax.ShapeDtypeStruct((packs, 8, LANES), jnp.float32),
    )(facies_table, bounds, raw)
    sums = sums[:, :3, : segments * span_y].reshape(packs, 3, segments, span_y).sum(axis=3)
    sums = sums.transpose(1, 0, 2).reshape(3, packs * segments)[:, :count]
    return sums.reshape((3, count_z, count_x, count_y))


def coarse_sweep(perm_pad, press_pad, inside_pad, accumulation, fixed):
    centre = (slice(1, -1), slice(1, -1), slice(1, -1))
    factors = (CCY * CCZ / CCX, CCX * CCZ / CCY, CCX * CCY / CCZ)
    numer = fixed
    denom = accumulation
    for component, axis_dim in ((0, 1), (1, 2), (2, 0)):
        for offset in (-1, 1):
            window_slice = [slice(1, -1), slice(1, -1), slice(1, -1)]
            window_slice[axis_dim] = slice(1 + offset, press_pad.shape[axis_dim] - 1 + offset)
            beside = tuple(window_slice)
            link = (
                factors[component]
                * 0.5
                * (perm_pad[component][centre] + perm_pad[component][beside])
                * inside_pad[beside]
            )
            numer = numer + link * press_pad[beside]
            denom = denom + jnp.abs(link)
    return numer / denom


def span_mask(anchor, length, total, margin):
    coords = anchor - margin + jnp.arange(length + 2 * margin, dtype=jnp.int32)
    return ((coords >= 0) & (coords < total)).astype(jnp.float32)


def cut_windows(fields):
    span_z = CCZ + 2 * RIM
    span_x = CCX + 2 * RIM
    span_y = CCY + 2 * RIM
    count_z = (fields[0].shape[0] - 2 * RIM) // CCZ
    count_x = (fields[0].shape[1] - 2 * RIM) // CCX
    count_y = (fields[0].shape[2] - 2 * RIM) // CCY
    stacks = []
    for field in fields:
        pieces = []
        for block_z in range(count_z):
            for block_y in range(count_y):
                piece = field[
                    block_z * CCZ : block_z * CCZ + span_z,
                    0:span_x,
                    block_y * CCY : block_y * CCY + span_y,
                ]
                pieces.append(piece.reshape(span_z, span_x * span_y))
        stacks.append(jnp.stack(pieces))
    return (stacks, (count_z, count_x, count_y))


def faces(block, sides):
    got = []
    for axis, dim in sides:
        count = lax.axis_size(axis)
        ends = count - 1
        head = lax.slice_in_dim(block, 0, 1, axis=dim)
        tail = lax.slice_in_dim(block, block.shape[dim] - 1, block.shape[dim], axis=dim)
        lower = lax.ppermute(tail, axis, [(i, i + 1) for i in range(ends)])
        upper = lax.ppermute(head, axis, [(i + 1, i) for i in range(ends)])
        got.append((lower, upper))
    return got


def neighbour_views(block, got, dim_of):
    views = []
    for (lower, upper), dim in zip(got, dim_of):
        size = block.shape[dim]
        below = jnp.concatenate([lower, lax.slice_in_dim(block, 0, size - 1, axis=dim)], axis=dim)
        above = jnp.concatenate([lax.slice_in_dim(block, 1, size, axis=dim), upper], axis=dim)
        views.append((below, above))
    return views


def coarse_step(upscaled, views, inside_views, pressure, accumulation, fixed):
    factors = (CCY * CCZ / CCX, CCX * CCZ / CCY, CCX * CCY / CCZ)
    numer = fixed
    denom = accumulation
    for component in range(3):
        for side in range(2):
            beside = views[component][side]
            link = factors[component] * 0.5 * (upscaled[component] + beside[component]) * inside_views[component][side]
            numer = numer + link * pressure[component][side]
            denom = denom + jnp.abs(link)
    return numer / denom


def local(log_noise, facies, facies_table, pressure_old, accumulation, source):
    depth_len, rows_len, cols_len = log_noise.shape
    size_z = lax.axis_size("gz")
    size_x = lax.axis_size("gx")
    size_y = lax.axis_size("gy")
    index_z = lax.axis_index("gz")
    index_x = lax.axis_index("gx")
    index_y = lax.axis_index("gy")
    raw = jnp.stack([log_noise, facies.astype(jnp.float32)])
    wide = -(-(cols_len + 2 * RIM) // LANES) * LANES
    raw = extended(raw, (("gx", 2), ("gz", 1), ("gy", 3)), RIM, wide)
    anchor_z = index_z * depth_len
    anchor_y = index_y * cols_len
    anchor_x = index_x * rows_len
    bounds = jnp.stack(
        [
            RIM - anchor_z,
            depth_len * size_z + RIM - anchor_z,
            RIM - anchor_x,
            rows_len * size_x + RIM - anchor_x,
            RIM - anchor_y,
            cols_len * size_y + RIM - anchor_y,
        ]
    ).astype(jnp.int32)
    upscaled = upscale_windows(raw, facies_table, bounds, cols_len)
    coarse_z, coarse_x, coarse_y = pressure_old.shape
    bundle = jnp.stack([upscaled[0], upscaled[1], upscaled[2], pressure_old, accumulation, source])
    fields = bundle.shape[0]
    every = lax.all_gather(bundle, ("gy", "gz"), axis=0, tiled=False)
    every = every.reshape((size_y, size_z) + bundle.shape).transpose(2, 1, 3, 4, 0, 5)
    every = every.reshape((fields, size_z * coarse_z, coarse_x, size_y * coarse_y))
    every = lax.all_gather(every, "gx", axis=2, tiled=True)
    perm_pad = jnp.pad(every[:3], ((0, 0), (1, 1), (1, 1), (1, 1)))
    old_all = every[3]
    acc_all = every[4]
    fixed_all = acc_all * old_all + every[5]
    inside_pad = jnp.pad(jnp.ones(old_all.shape, jnp.float32), 1)
    pressure = old_all
    for sweep_index in range(2):
        pressure = coarse_sweep(perm_pad, jnp.pad(pressure, 1), inside_pad, acc_all, fixed_all)
    pressure = lax.dynamic_slice(
        pressure, (index_z * coarse_z, index_x * coarse_x, index_y * coarse_y), (coarse_z, coarse_x, coarse_y)
    )
    return (pressure, upscaled)


def solution(mesh):
    placed = (
        P(("real", "gz"), "gx", "gy"),
        P(("real", "gz"), "gx", "gy"),
        P(),
        P(("real", "gz"), "gx", "gy"),
        P(("real", "gz"), "gx", "gy"),
        P(("real", "gz"), "gx", "gy"),
    )
    return jax.shard_map(
        local,
        mesh=mesh,
        in_specs=placed,
        out_specs=(P(("real", "gz"), "gx", "gy"), P(None, ("real", "gz"), "gx", "gy")),
        check_vma=False,
    )
```

```python
import functools

import jax
import jax.numpy as jnp
from jax import lax
from jax.sharding import PartitionSpec as P
from jax.experimental import pallas as pl
from jax.experimental.pallas import tpu as pltpu

NFAC = 4
CCX = 32
CCY = 32
CCZ = 8
RIM = 4
SWEEPS = 3


BOUND_MID = 1.0
BOUND_HALF = 0.9


def extended(cells, sides, width, lanes=None, edges=None):
    for axis, dim in sides:
        count = lax.axis_size(axis)
        ends = count - 1
        if edges is not None:
            head, tail = edges
            edges = None
        else:
            head = lax.slice_in_dim(cells, 0, width, axis=dim)
            tail = lax.slice_in_dim(cells, cells.shape[dim] - width, cells.shape[dim], axis=dim)
        if count == 2:
            lower_side = lax.axis_index(axis) == 0
            got = lax.ppermute(jnp.where(lower_side, tail, head), axis, [(0, 1), (1, 0)])
            below = jnp.where(lower_side, 0.0, got)
            above = jnp.where(lower_side, got, 0.0)
        else:
            below = lax.ppermute(tail, axis, [(i, (i + 1) % count) for i in range(ends)])
            above = lax.ppermute(head, axis, [((i + 1) % count, i) for i in range(ends)])
        parts = [below, cells, above]
        if lanes is not None and dim == cells.ndim - 1:
            extra = lanes - (cells.shape[dim] + 2 * width)
            parts.append(jnp.zeros(cells.shape[:-1] + (extra,), cells.dtype))
        cells = jnp.concatenate(parts, axis=dim)
    return cells


def raise_flat(values, offset):
    zeros_block = jnp.zeros(values.shape[:-1] + (offset,), values.dtype)
    return jnp.concatenate([values[..., offset:], zeros_block], axis=-1)


def lower_flat(values, offset):
    zeros_block = jnp.zeros(values.shape[:-1] + (offset,), values.dtype)
    return jnp.concatenate([zeros_block, values[..., :-offset]], axis=-1)


def raise_depth(values):
    zeros_block = jnp.zeros(values.shape[:1] + (1,) + values.shape[2:], values.dtype)
    return jnp.concatenate([values[:, 1:], zeros_block], axis=1)


def lower_depth(values):
    zeros_block = jnp.zeros(values.shape[:1] + (1,) + values.shape[2:], values.dtype)
    return jnp.concatenate([zeros_block, values[:, :-1]], axis=1)


def log_fields(log_noise, facies, facies_table):
    base_log = log_noise
    extra_y = jnp.zeros_like(log_noise)
    extra_z = jnp.zeros_like(log_noise)
    for code_value in range(NFAC):
        matched = facies == code_value
        base_log = base_log + jnp.where(matched, facies_table[0, code_value], jnp.float32(0.0))
        extra_y = extra_y + jnp.where(matched, facies_table[1, code_value], jnp.float32(0.0))
        extra_z = extra_z + jnp.where(matched, facies_table[2, code_value], jnp.float32(0.0))
    return (base_log, base_log + extra_y, base_log + extra_z)


def upscale(perm_logs, inside):
    span_z = CCZ + 2 * RIM
    span_x = CCX + 2 * RIM
    span_y = CCY + 2 * RIM
    depth_pos = lax.broadcasted_iota(jnp.int32, (1, span_z, 1), 1)
    flat_pos = lax.broadcasted_iota(jnp.int32, (1, 1, span_x * span_y), 2)
    column_pos = flat_pos // span_y
    row_pos = flat_pos % span_y
    perm_x = jnp.exp(perm_logs[0])
    perm_y = jnp.exp(perm_logs[1])
    perm_z = jnp.exp(perm_logs[2])

    def links(perm, other_perm, other_inside):
        return inside * other_inside * 2.0 * perm * other_perm / (perm + other_perm)

    link_x = links(perm_x, raise_flat(perm_x, span_y), raise_flat(inside, span_y))
    link_y = links(perm_y, raise_flat(perm_y, 1), raise_flat(inside, 1)) * (
        row_pos < span_y - 1
    ).astype(jnp.float32)
    link_z = links(perm_z, raise_depth(perm_z), raise_depth(inside))
    diagonal = (
        link_x
        + lower_flat(link_x, span_y)
        + link_y
        + lower_flat(link_y, 1)
        + link_z
        + lower_depth(link_z)
    )

    def apply_operator(field):
        beside = link_x * raise_flat(field, span_y) + lower_flat(link_x * field, span_y)
        beside = beside + link_y * raise_flat(field, 1) + lower_flat(link_y * field, 1)
        beside = beside + link_z * raise_depth(field) + lower_depth(link_z * field)
        return diagonal * field - beside

    interior = (
        (depth_pos >= 1)
        & (depth_pos <= span_z - 2)
        & (column_pos >= 1)
        & (column_pos <= span_x - 2)
        & (row_pos >= 1)
        & (row_pos <= span_y - 2)
    )
    unknown = inside * interior.astype(jnp.float32)
    scaling = unknown / (diagonal + 1.0 - unknown)
    core_z = (depth_pos >= RIM) & (depth_pos < RIM + CCZ)
    core_x = (column_pos >= RIM) & (column_pos < RIM + CCX)
    core_y = (row_pos >= RIM) & (row_pos < RIM + CCY)
    face_x = (((column_pos == RIM - 1) | (column_pos == RIM + CCX - 1)) & core_z & core_y).astype(
        jnp.float32
    )
    face_y = (((row_pos == RIM - 1) | (row_pos == RIM + CCY - 1)) & core_z & core_x).astype(
        jnp.float32
    )
    face_z = (((depth_pos == RIM - 1) | (depth_pos == RIM + CCZ - 1)) & core_x & core_y).astype(
        jnp.float32
    )
    ramp_x = ((span_x - 1) / 2.0 - column_pos).astype(jnp.float32)
    ramp_y = ((span_y - 1) / 2.0 - row_pos).astype(jnp.float32)
    ramp_z = ((span_z - 1) / 2.0 - depth_pos).astype(jnp.float32)
    cheb_ratio = BOUND_MID / BOUND_HALF
    results = []
    cases = (
        (ramp_x, link_x, face_x, CCY * CCZ, 0),
        (ramp_y, link_y, face_y, CCX * CCZ, 1),
        (ramp_z, link_z, face_z, CCX * CCY, 2),
    )
    for ramp, link, face, area, direction in cases:
        ramp_full = jnp.broadcast_to(ramp, inside.shape)
        source_term = -unknown * apply_operator(ramp_full)
        update = scaling * source_term / BOUND_MID
        solution = update
        rho_old = 1.0 / cheb_ratio
        for sweep_index in range(SWEEPS - 1):
            residual = source_term - apply_operator(solution)
            rho_new = 1.0 / (2.0 * cheb_ratio - rho_old)
            update = rho_new * rho_old * update + 2.0 * rho_new / BOUND_HALF * (scaling * residual)
            solution = solution + update
            rho_old = rho_new
        pressure = ramp_full + solution
        if direction == 0:
            upper = raise_flat(pressure, span_y)
        elif direction == 1:
            upper = raise_flat(pressure, 1)
        else:
            upper = raise_depth(pressure)
        flux = link * (pressure - upper) * face
        results.append(jnp.sum(flux, axis=(1, 2)) * (0.5 / area))
    return jnp.stack(results)


LANES = 128


def window_kernel(table_ref, bounds_ref, raw_ref, o_ref, *, count_x, count_y, count):
    span_z = CCZ + 2 * RIM
    span_x = CCX + 2 * RIM
    span_y = CCY + 2 * RIM
    segments = LANES // span_y
    shape = (span_z, span_x, LANES)
    pack = pl.program_id(0)
    wide = raw_ref.shape[-1]
    depth_pos = lax.broadcasted_iota(jnp.int32, shape, 0)
    column_pos = lax.broadcasted_iota(jnp.int32, shape, 1)
    lane = lax.broadcasted_iota(jnp.int32, shape, 2)
    segment = jnp.zeros(shape, jnp.int32)
    for bound in range(1, segments + 1):
        segment = segment + (lane >= bound * span_y).astype(jnp.int32)
    row_pos = lane - span_y * segment
    noise = jnp.zeros(shape, jnp.float32)
    codes = jnp.zeros(shape, jnp.float32)
    inside = jnp.zeros(shape, jnp.float32)
    for slot in range(segments):
        window = pack * segments + slot
        valid = window < count
        window = jnp.minimum(window, count - 1)
        block_z = window // (count_x * count_y)
        block_x = (window // count_y) % count_x
        block_y = window % count_y
        shift = (slot * span_y - block_y * CCY + wide) % wide
        here = segment == slot

        def cut(field):
            slab = raw_ref[field, pl.ds(block_z * CCZ, span_z), pl.ds(block_x * CCX, span_x), :]
            return pltpu.roll(slab, shift, 2)[:, :, :LANES]

        depth_at = depth_pos + block_z * CCZ
        column_at = column_pos + block_x * CCX
        row_at = row_pos + block_y * CCY
        held = (
            (depth_at >= bounds_ref[0])
            & (depth_at < bounds_ref[1])
            & (column_at >= bounds_ref[2])
            & (column_at < bounds_ref[3])
            & (row_at >= bounds_ref[4])
            & (row_at < bounds_ref[5])
        )
        noise = jnp.where(here, cut(0), noise)
        codes = jnp.where(here, cut(1), codes)
        inside = jnp.where(here & valid & held, 1.0, inside)

    def lookup(row):
        value = jnp.zeros(shape, jnp.float32)
        for code_value in range(NFAC):
            value = jnp.where(codes == code_value, table_ref[row, code_value], value)
        return value

    log_x = noise + lookup(0)
    log_y = log_x + lookup(1)
    log_z = log_x + lookup(2)
    perm_x = jnp.exp(log_x)
    perm_y = jnp.exp(log_y)
    perm_z = jnp.exp(log_z)

    def up_x(v):
        return pltpu.roll(v, span_x - 1, 1)

    def down_x(v):
        return pltpu.roll(v, 1, 1)

    def up_y(v):
        return pltpu.roll(v, LANES - 1, 2)

    def down_y(v):
        return pltpu.roll(v, 1, 2)

    def up_z(v):
        return jnp.concatenate([v[1:], v[:1]], axis=0)

    def down_z(v):
        return jnp.concatenate([v[-1:], v[:-1]], axis=0)

    def links(perm, other_perm, other_inside, valid):
        value = inside * other_inside * 2.0 * perm * other_perm / (perm + other_perm)
        return jnp.where(valid, value, 0.0)

    link_x = links(perm_x, up_x(perm_x), up_x(inside), column_pos < span_x - 1)
    link_y = links(perm_y, up_y(perm_y), up_y(inside), row_pos < span_y - 1)
    link_z = links(perm_z, up_z(perm_z), up_z(inside), depth_pos < span_z - 1)
    diagonal = link_x + down_x(link_x) + link_y + down_y(link_y) + link_z + down_z(link_z)

    def apply_operator(field):
        beside = link_x * up_x(field) + down_x(link_x * field)
        beside = beside + link_y * up_y(field) + down_y(link_y * field)
        beside = beside + link_z * up_z(field) + down_z(link_z * field)
        return diagonal * field - beside

    interior = (
        (depth_pos >= 1)
        & (depth_pos <= span_z - 2)
        & (column_pos >= 1)
        & (column_pos <= span_x - 2)
        & (row_pos >= 1)
        & (row_pos <= span_y - 2)
    )
    unknown = jnp.where(interior, inside, 0.0)
    scaling = unknown / (diagonal + 1.0 - unknown)
    core_z = (depth_pos >= RIM) & (depth_pos < RIM + CCZ)
    core_x = (column_pos >= RIM) & (column_pos < RIM + CCX)
    core_y = (row_pos >= RIM) & (row_pos < RIM + CCY)
    face_x = ((column_pos == RIM - 1) | (column_pos == RIM + CCX - 1)) & core_z & core_y
    face_y = ((row_pos == RIM - 1) | (row_pos == RIM + CCY - 1)) & core_z & core_x
    face_z = ((depth_pos == RIM - 1) | (depth_pos == RIM + CCZ - 1)) & core_x & core_y
    ramp_x = ((span_x - 1) / 2.0 - column_pos).astype(jnp.float32)
    ramp_y = ((span_y - 1) / 2.0 - row_pos).astype(jnp.float32)
    ramp_z = ((span_z - 1) / 2.0 - depth_pos).astype(jnp.float32)
    cheb_ratio = BOUND_MID / BOUND_HALF
    cases = (
        (ramp_x, link_x, face_x, CCY * CCZ, up_x, down_x),
        (ramp_y, link_y, face_y, CCX * CCZ, up_y, down_y),
        (ramp_z, link_z, face_z, CCX * CCY, up_z, down_z),
    )
    rows = []
    for ramp, link, face, area, upper_of, lower_of in cases:
        source_term = -unknown * (link - lower_of(link))
        update = scaling * source_term / BOUND_MID
        solution = update
        rho_old = 1.0 / cheb_ratio
        for sweep_index in range(SWEEPS - 1):
            residual = source_term - apply_operator(solution)
            rho_new = 1.0 / (2.0 * cheb_ratio - rho_old)
            update = rho_new * rho_old * update + 2.0 * rho_new / BOUND_HALF * (scaling * residual)
            solution = solution + update
            rho_old = rho_new
        pressure = ramp + solution
        flux = jnp.where(face, link * (pressure - upper_of(pressure)), 0.0)
        total = jnp.sum(flux, axis=0)
        total = jnp.sum(total, axis=0, keepdims=True)
        rows.append(total * (0.5 / area))
    rows.append(jnp.zeros((8 - len(rows), LANES), jnp.float32))
    o_ref[0] = jnp.concatenate(rows, axis=0)


def upscale_windows(raw, facies_table, bounds, cols_len):
    span_y = CCY + 2 * RIM
    count_z = (raw.shape[1] - 2 * RIM) // CCZ
    count_x = (raw.shape[2] - 2 * RIM) // CCX
    count_y = cols_len // CCY
    count = count_z * count_x * count_y
    segments = LANES // span_y
    packs = -(-count // segments)
    kernel = functools.partial(window_kernel, count_x=count_x, count_y=count_y, count=count)
    sums = pl.pallas_call(
        kernel,
        grid=(packs,),
        in_specs=[
            pl.BlockSpec(memory_space=pltpu.SMEM),
            pl.BlockSpec(memory_space=pltpu.SMEM),
            pl.BlockSpec(raw.shape, lambda p: (0, 0, 0, 0)),
        ],
        out_specs=pl.BlockSpec((1, 8, LANES), lambda p: (p, 0, 0)),
        out_shape=jax.ShapeDtypeStruct((packs, 8, LANES), jnp.float32),
    )(facies_table, bounds, raw)
    sums = sums[:, :3, : segments * span_y].reshape(packs, 3, segments, span_y).sum(axis=3)
    sums = sums.transpose(1, 0, 2).reshape(3, packs * segments)[:, :count]
    return sums.reshape((3, count_z, count_x, count_y))


def coarse_sweep(perm_pad, press_pad, inside_pad, accumulation, fixed):
    centre = (slice(1, -1), slice(1, -1), slice(1, -1))
    factors = (CCY * CCZ / CCX, CCX * CCZ / CCY, CCX * CCY / CCZ)
    numer = fixed
    denom = accumulation
    for component, axis_dim in ((0, 1), (1, 2), (2, 0)):
        for offset in (-1, 1):
            window_slice = [slice(1, -1), slice(1, -1), slice(1, -1)]
            window_slice[axis_dim] = slice(1 + offset, press_pad.shape[axis_dim] - 1 + offset)
            beside = tuple(window_slice)
            link = (
                factors[component]
                * 0.5
                * (perm_pad[component][centre] + perm_pad[component][beside])
                * inside_pad[beside]
            )
            numer = numer + link * press_pad[beside]
            denom = denom + jnp.abs(link)
    return numer / denom


def span_mask(anchor, length, total, margin):
    coords = anchor - margin + jnp.arange(length + 2 * margin, dtype=jnp.int32)
    return ((coords >= 0) & (coords < total)).astype(jnp.float32)


def cut_windows(fields):
    span_z = CCZ + 2 * RIM
    span_x = CCX + 2 * RIM
    span_y = CCY + 2 * RIM
    count_z = (fields[0].shape[0] - 2 * RIM) // CCZ
    count_x = (fields[0].shape[1] - 2 * RIM) // CCX
    count_y = (fields[0].shape[2] - 2 * RIM) // CCY
    stacks = []
    for field in fields:
        pieces = []
        for block_z in range(count_z):
            for block_y in range(count_y):
                piece = field[
                    block_z * CCZ : block_z * CCZ + span_z,
                    0:span_x,
                    block_y * CCY : block_y * CCY + span_y,
                ]
                pieces.append(piece.reshape(span_z, span_x * span_y))
        stacks.append(jnp.stack(pieces))
    return (stacks, (count_z, count_x, count_y))


def faces(block, sides):
    got = []
    for axis, dim in sides:
        count = lax.axis_size(axis)
        ends = count - 1
        head = lax.slice_in_dim(block, 0, 1, axis=dim)
        tail = lax.slice_in_dim(block, block.shape[dim] - 1, block.shape[dim], axis=dim)
        lower = lax.ppermute(tail, axis, [(i, i + 1) for i in range(ends)])
        upper = lax.ppermute(head, axis, [(i + 1, i) for i in range(ends)])
        got.append((lower, upper))
    return got


def neighbour_views(block, got, dim_of):
    views = []
    for (lower, upper), dim in zip(got, dim_of):
        size = block.shape[dim]
        below = jnp.concatenate([lower, lax.slice_in_dim(block, 0, size - 1, axis=dim)], axis=dim)
        above = jnp.concatenate([lax.slice_in_dim(block, 1, size, axis=dim), upper], axis=dim)
        views.append((below, above))
    return views


def coarse_step(upscaled, views, inside_views, pressure, accumulation, fixed):
    factors = (CCY * CCZ / CCX, CCX * CCZ / CCY, CCX * CCY / CCZ)
    numer = fixed
    denom = accumulation
    for component in range(3):
        for side in range(2):
            beside = views[component][side]
            link = factors[component] * 0.5 * (upscaled[component] + beside[component]) * inside_views[component][side]
            numer = numer + link * pressure[component][side]
            denom = denom + jnp.abs(link)
    return numer / denom


def local(log_noise, facies, facies_table, pressure_old, accumulation, source):
    depth_len, rows_len, cols_len = log_noise.shape
    size_z = lax.axis_size("gz")
    size_x = lax.axis_size("gx")
    size_y = lax.axis_size("gy")
    index_z = lax.axis_index("gz")
    index_x = lax.axis_index("gx")
    index_y = lax.axis_index("gy")
    sources = (log_noise, facies.astype(jnp.float32))
    edges = (
        jnp.stack([field[:, :RIM] for field in sources]),
        jnp.stack([field[:, rows_len - RIM :] for field in sources]),
    )
    raw = jnp.stack(sources)
    wide = -(-(cols_len + 2 * RIM) // LANES) * LANES
    raw = extended(raw, (("gx", 2), ("gz", 1), ("gy", 3)), RIM, wide, edges)
    anchor_z = index_z * depth_len
    anchor_y = index_y * cols_len
    anchor_x = index_x * rows_len
    bounds = jnp.stack(
        [
            RIM - anchor_z,
            depth_len * size_z + RIM - anchor_z,
            RIM - anchor_x,
            rows_len * size_x + RIM - anchor_x,
            RIM - anchor_y,
            cols_len * size_y + RIM - anchor_y,
        ]
    ).astype(jnp.int32)
    upscaled = upscale_windows(raw, facies_table, bounds, cols_len)
    coarse_z, coarse_x, coarse_y = pressure_old.shape
    bundle = jnp.stack([upscaled[0], upscaled[1], upscaled[2], pressure_old, accumulation, source])
    every = lax.all_gather(bundle, "gy", axis=3, tiled=True)
    every = lax.all_gather(every, "gx", axis=2, tiled=True)
    every = lax.all_gather(every, "gz", axis=1, tiled=True)
    perm_pad = jnp.pad(every[:3], ((0, 0), (1, 1), (1, 1), (1, 1)))
    old_all = every[3]
    acc_all = every[4]
    fixed_all = acc_all * old_all + every[5]
    inside_pad = jnp.pad(jnp.ones(old_all.shape, jnp.float32), 1)
    pressure = old_all
    for sweep_index in range(2):
        pressure = coarse_sweep(perm_pad, jnp.pad(pressure, 1), inside_pad, acc_all, fixed_all)
    pressure = lax.dynamic_slice(
        pressure, (index_z * coarse_z, index_x * coarse_x, index_y * coarse_y), (coarse_z, coarse_x, coarse_y)
    )
    return (pressure, upscaled)


def solution(mesh):
    placed = (
        P(("real", "gz"), "gx", "gy"),
        P(("real", "gz"), "gx", "gy"),
        P(),
        P(("real", "gz"), "gx", "gy"),
        P(("real", "gz"), "gx", "gy"),
        P(("real", "gz"), "gx", "gy"),
    )
    return jax.shard_map(
        local,
        mesh=mesh,
        in_specs=placed,
        out_specs=(P(("real", "gz"), "gx", "gy"), P(None, ("real", "gz"), "gx", "gy")),
        check_vma=False,
    )
```

```python
import functools

import jax
import jax.numpy as jnp
from jax import lax
from jax.sharding import PartitionSpec as P
from jax.experimental import pallas as pl
from jax.experimental.pallas import tpu as pltpu

NFAC = 4
CCX = 32
CCY = 32
CCZ = 8
RIM = 4
SWEEPS = 3


BOUND_MID = 1.0
BOUND_HALF = 0.9


def extended(cells, sides, width, lanes=None):
    for axis, dim in sides:
        count = lax.axis_size(axis)
        ends = count - 1
        head = lax.slice_in_dim(cells, 0, width, axis=dim)
        tail = lax.slice_in_dim(cells, cells.shape[dim] - width, cells.shape[dim], axis=dim)
        if count == 2:
            lower_side = lax.axis_index(axis) == 0
            got = lax.ppermute(jnp.where(lower_side, tail, head), axis, [(0, 1), (1, 0)])
            below = jnp.where(lower_side, 0.0, got)
            above = jnp.where(lower_side, got, 0.0)
        else:
            below = lax.ppermute(tail, axis, [(i, (i + 1) % count) for i in range(ends)])
            above = lax.ppermute(head, axis, [((i + 1) % count, i) for i in range(ends)])
        parts = [below, cells, above]
        if lanes is not None and dim == cells.ndim - 1:
            extra = lanes - (cells.shape[dim] + 2 * width)
            parts.append(jnp.zeros(cells.shape[:-1] + (extra,), cells.dtype))
        cells = jnp.concatenate(parts, axis=dim)
    return cells


def raise_flat(values, offset):
    zeros_block = jnp.zeros(values.shape[:-1] + (offset,), values.dtype)
    return jnp.concatenate([values[..., offset:], zeros_block], axis=-1)


def lower_flat(values, offset):
    zeros_block = jnp.zeros(values.shape[:-1] + (offset,), values.dtype)
    return jnp.concatenate([zeros_block, values[..., :-offset]], axis=-1)


def raise_depth(values):
    zeros_block = jnp.zeros(values.shape[:1] + (1,) + values.shape[2:], values.dtype)
    return jnp.concatenate([values[:, 1:], zeros_block], axis=1)


def lower_depth(values):
    zeros_block = jnp.zeros(values.shape[:1] + (1,) + values.shape[2:], values.dtype)
    return jnp.concatenate([zeros_block, values[:, :-1]], axis=1)


def log_fields(log_noise, facies, facies_table):
    base_log = log_noise
    extra_y = jnp.zeros_like(log_noise)
    extra_z = jnp.zeros_like(log_noise)
    for code_value in range(NFAC):
        matched = facies == code_value
        base_log = base_log + jnp.where(matched, facies_table[0, code_value], jnp.float32(0.0))
        extra_y = extra_y + jnp.where(matched, facies_table[1, code_value], jnp.float32(0.0))
        extra_z = extra_z + jnp.where(matched, facies_table[2, code_value], jnp.float32(0.0))
    return (base_log, base_log + extra_y, base_log + extra_z)


def upscale(perm_logs, inside):
    span_z = CCZ + 2 * RIM
    span_x = CCX + 2 * RIM
    span_y = CCY + 2 * RIM
    depth_pos = lax.broadcasted_iota(jnp.int32, (1, span_z, 1), 1)
    flat_pos = lax.broadcasted_iota(jnp.int32, (1, 1, span_x * span_y), 2)
    column_pos = flat_pos // span_y
    row_pos = flat_pos % span_y
    perm_x = jnp.exp(perm_logs[0])
    perm_y = jnp.exp(perm_logs[1])
    perm_z = jnp.exp(perm_logs[2])

    def links(perm, other_perm, other_inside):
        return inside * other_inside * 2.0 * perm * other_perm / (perm + other_perm)

    link_x = links(perm_x, raise_flat(perm_x, span_y), raise_flat(inside, span_y))
    link_y = links(perm_y, raise_flat(perm_y, 1), raise_flat(inside, 1)) * (
        row_pos < span_y - 1
    ).astype(jnp.float32)
    link_z = links(perm_z, raise_depth(perm_z), raise_depth(inside))
    diagonal = (
        link_x
        + lower_flat(link_x, span_y)
        + link_y
        + lower_flat(link_y, 1)
        + link_z
        + lower_depth(link_z)
    )

    def apply_operator(field):
        beside = link_x * raise_flat(field, span_y) + lower_flat(link_x * field, span_y)
        beside = beside + link_y * raise_flat(field, 1) + lower_flat(link_y * field, 1)
        beside = beside + link_z * raise_depth(field) + lower_depth(link_z * field)
        return diagonal * field - beside

    interior = (
        (depth_pos >= 1)
        & (depth_pos <= span_z - 2)
        & (column_pos >= 1)
        & (column_pos <= span_x - 2)
        & (row_pos >= 1)
        & (row_pos <= span_y - 2)
    )
    unknown = inside * interior.astype(jnp.float32)
    scaling = unknown / (diagonal + 1.0 - unknown)
    core_z = (depth_pos >= RIM) & (depth_pos < RIM + CCZ)
    core_x = (column_pos >= RIM) & (column_pos < RIM + CCX)
    core_y = (row_pos >= RIM) & (row_pos < RIM + CCY)
    face_x = (((column_pos == RIM - 1) | (column_pos == RIM + CCX - 1)) & core_z & core_y).astype(
        jnp.float32
    )
    face_y = (((row_pos == RIM - 1) | (row_pos == RIM + CCY - 1)) & core_z & core_x).astype(
        jnp.float32
    )
    face_z = (((depth_pos == RIM - 1) | (depth_pos == RIM + CCZ - 1)) & core_x & core_y).astype(
        jnp.float32
    )
    ramp_x = ((span_x - 1) / 2.0 - column_pos).astype(jnp.float32)
    ramp_y = ((span_y - 1) / 2.0 - row_pos).astype(jnp.float32)
    ramp_z = ((span_z - 1) / 2.0 - depth_pos).astype(jnp.float32)
    cheb_ratio = BOUND_MID / BOUND_HALF
    results = []
    cases = (
        (ramp_x, link_x, face_x, CCY * CCZ, 0),
        (ramp_y, link_y, face_y, CCX * CCZ, 1),
        (ramp_z, link_z, face_z, CCX * CCY, 2),
    )
    for ramp, link, face, area, direction in cases:
        ramp_full = jnp.broadcast_to(ramp, inside.shape)
        source_term = -unknown * apply_operator(ramp_full)
        update = scaling * source_term / BOUND_MID
        solution = update
        rho_old = 1.0 / cheb_ratio
        for sweep_index in range(SWEEPS - 1):
            residual = source_term - apply_operator(solution)
            rho_new = 1.0 / (2.0 * cheb_ratio - rho_old)
            update = rho_new * rho_old * update + 2.0 * rho_new / BOUND_HALF * (scaling * residual)
            solution = solution + update
            rho_old = rho_new
        pressure = ramp_full + solution
        if direction == 0:
            upper = raise_flat(pressure, span_y)
        elif direction == 1:
            upper = raise_flat(pressure, 1)
        else:
            upper = raise_depth(pressure)
        flux = link * (pressure - upper) * face
        results.append(jnp.sum(flux, axis=(1, 2)) * (0.5 / area))
    return jnp.stack(results)


LANES = 128


def window_kernel(table_ref, bounds_ref, raw_ref, o_ref, *, count_x, count_y, count):
    span_z = CCZ + 2 * RIM
    span_x = CCX + 2 * RIM
    span_y = CCY + 2 * RIM
    segments = LANES // span_y
    shape = (span_z, span_x, LANES)
    pack = pl.program_id(0)
    wide = raw_ref.shape[-1]
    plane = (span_x, LANES)
    column_pos = lax.broadcasted_iota(jnp.int32, plane, 0)
    lane = lax.broadcasted_iota(jnp.int32, plane, 1)
    segment = jnp.zeros(plane, jnp.int32)
    for bound in range(1, segments + 1):
        segment = segment + (lane >= bound * span_y).astype(jnp.int32)
    row_pos = lane - span_y * segment
    zero_plane = jnp.zeros(plane, jnp.float32)
    one_plane = jnp.ones(plane, jnp.float32)

    def deep(make):
        return jnp.stack([make(depth) for depth in range(span_z)])

    def flat(values):
        return jnp.broadcast_to(values[None], shape)

    def as_float(mask):
        return mask.astype(jnp.float32)

    noise = jnp.zeros(shape, jnp.float32)
    codes = jnp.zeros(shape, jnp.float32)
    inside = jnp.zeros(shape, jnp.float32)
    for slot in range(segments):
        window = pack * segments + slot
        valid = window < count
        window = jnp.minimum(window, count - 1)
        block_z = window // (count_x * count_y)
        block_x = (window // count_y) % count_x
        block_y = window % count_y
        shift = (slot * span_y - block_y * CCY + wide) % wide
        here = segment == slot

        def cut(field):
            slab = raw_ref[field, pl.ds(block_z * CCZ, span_z), pl.ds(block_x * CCX, span_x), :]
            return pltpu.roll(slab, shift, 2)[:, :, :LANES]

        column_at = column_pos + block_x * CCX
        row_at = row_pos + block_y * CCY
        held = as_float(
            here
            & (column_at >= bounds_ref[2])
            & (column_at < bounds_ref[3])
            & (row_at >= bounds_ref[4])
            & (row_at < bounds_ref[5])
        ) * jnp.where(valid, 1.0, 0.0)

        def layer(depth):
            depth_at = depth + block_z * CCZ
            keep = (depth_at >= bounds_ref[0]) & (depth_at < bounds_ref[1])
            return held * jnp.where(keep, 1.0, 0.0)

        noise = jnp.where(here[None], cut(0), noise)
        codes = jnp.where(here[None], cut(1), codes)
        inside = inside + deep(layer)

    def lookup(row):
        value = jnp.zeros(shape, jnp.float32)
        for code_value in range(NFAC):
            value = jnp.where(codes == code_value, table_ref[row, code_value], value)
        return value

    log_x = noise + lookup(0)
    log_y = log_x + lookup(1)
    log_z = log_x + lookup(2)
    perm_x = jnp.exp(log_x)
    perm_y = jnp.exp(log_y)
    perm_z = jnp.exp(log_z)

    def up_x(v):
        return pltpu.roll(v, span_x - 1, 1)

    def down_x(v):
        return pltpu.roll(v, 1, 1)

    def up_y(v):
        return pltpu.roll(v, LANES - 1, 2)

    def down_y(v):
        return pltpu.roll(v, 1, 2)

    def up_z(v):
        return jnp.concatenate([v[1:], v[:1]], axis=0)

    def down_z(v):
        return jnp.concatenate([v[-1:], v[:-1]], axis=0)

    def links(perm, other_perm, other_inside, valid):
        return inside * other_inside * 2.0 * perm * other_perm / (perm + other_perm) * valid

    link_x = links(perm_x, up_x(perm_x), up_x(inside), flat(as_float(column_pos < span_x - 1)))
    link_y = links(perm_y, up_y(perm_y), up_y(inside), flat(as_float(row_pos < span_y - 1)))
    link_z = links(
        perm_z, up_z(perm_z), up_z(inside), deep(lambda depth: one_plane if depth < span_z - 1 else zero_plane)
    )
    diagonal = link_x + down_x(link_x) + link_y + down_y(link_y) + link_z + down_z(link_z)

    def apply_operator(field):
        beside = link_x * up_x(field) + down_x(link_x * field)
        beside = beside + link_y * up_y(field) + down_y(link_y * field)
        beside = beside + link_z * up_z(field) + down_z(link_z * field)
        return diagonal * field - beside

    interior_plane = as_float(
        (column_pos >= 1) & (column_pos <= span_x - 2) & (row_pos >= 1) & (row_pos <= span_y - 2)
    )
    unknown = inside * deep(lambda depth: interior_plane if 1 <= depth <= span_z - 2 else zero_plane)
    scaling = unknown / (diagonal + 1.0 - unknown)
    core_x = (column_pos >= RIM) & (column_pos < RIM + CCX)
    core_y = (row_pos >= RIM) & (row_pos < RIM + CCY)
    face_x_plane = as_float(((column_pos == RIM - 1) | (column_pos == RIM + CCX - 1)) & core_y)
    face_y_plane = as_float(((row_pos == RIM - 1) | (row_pos == RIM + CCY - 1)) & core_x)
    face_z_plane = as_float(core_x & core_y)
    face_x = deep(lambda depth: face_x_plane if RIM <= depth < RIM + CCZ else zero_plane)
    face_y = deep(lambda depth: face_y_plane if RIM <= depth < RIM + CCZ else zero_plane)
    face_z = deep(lambda depth: face_z_plane if depth in (RIM - 1, RIM + CCZ - 1) else zero_plane)
    ramp_x = flat(((span_x - 1) / 2.0 - column_pos).astype(jnp.float32))
    ramp_y = flat(((span_y - 1) / 2.0 - row_pos).astype(jnp.float32))
    ramp_z = deep(lambda depth: jnp.full(plane, (span_z - 1) / 2.0 - depth, jnp.float32))
    cheb_ratio = BOUND_MID / BOUND_HALF
    cases = (
        (ramp_x, link_x, face_x, CCY * CCZ, up_x, down_x),
        (ramp_y, link_y, face_y, CCX * CCZ, up_y, down_y),
        (ramp_z, link_z, face_z, CCX * CCY, up_z, down_z),
    )
    rows = []
    for ramp, link, face, area, upper_of, lower_of in cases:
        source_term = -unknown * (link - lower_of(link))
        update = scaling * source_term / BOUND_MID
        solution = update
        rho_old = 1.0 / cheb_ratio
        for sweep_index in range(SWEEPS - 1):
            residual = source_term - apply_operator(solution)
            rho_new = 1.0 / (2.0 * cheb_ratio - rho_old)
            update = rho_new * rho_old * update + 2.0 * rho_new / BOUND_HALF * (scaling * residual)
            solution = solution + update
            rho_old = rho_new
        pressure = ramp + solution
        flux = link * (pressure - upper_of(pressure)) * face
        total = jnp.sum(flux, axis=0)
        total = jnp.sum(total, axis=0, keepdims=True)
        rows.append(total * (0.5 / area))
    rows.append(jnp.zeros((8 - len(rows), LANES), jnp.float32))
    o_ref[0] = jnp.concatenate(rows, axis=0)


def upscale_windows(raw, facies_table, bounds, cols_len):
    span_y = CCY + 2 * RIM
    count_z = (raw.shape[1] - 2 * RIM) // CCZ
    count_x = (raw.shape[2] - 2 * RIM) // CCX
    count_y = cols_len // CCY
    count = count_z * count_x * count_y
    segments = LANES // span_y
    packs = -(-count // segments)
    kernel = functools.partial(window_kernel, count_x=count_x, count_y=count_y, count=count)
    sums = pl.pallas_call(
        kernel,
        grid=(packs,),
        in_specs=[
            pl.BlockSpec(memory_space=pltpu.SMEM),
            pl.BlockSpec(memory_space=pltpu.SMEM),
            pl.BlockSpec(raw.shape, lambda p: (0, 0, 0, 0)),
        ],
        out_specs=pl.BlockSpec((1, 8, LANES), lambda p: (p, 0, 0)),
        out_shape=jax.ShapeDtypeStruct((packs, 8, LANES), jnp.float32),
    )(facies_table, bounds, raw)
    sums = sums[:, :3, : segments * span_y].reshape(packs, 3, segments, span_y).sum(axis=3)
    sums = sums.transpose(1, 0, 2).reshape(3, packs * segments)[:, :count]
    return sums.reshape((3, count_z, count_x, count_y))


def coarse_sweep(perm_pad, press_pad, inside_pad, accumulation, fixed):
    centre = (slice(1, -1), slice(1, -1), slice(1, -1))
    factors = (CCY * CCZ / CCX, CCX * CCZ / CCY, CCX * CCY / CCZ)
    numer = fixed
    denom = accumulation
    for component, axis_dim in ((0, 1), (1, 2), (2, 0)):
        for offset in (-1, 1):
            window_slice = [slice(1, -1), slice(1, -1), slice(1, -1)]
            window_slice[axis_dim] = slice(1 + offset, press_pad.shape[axis_dim] - 1 + offset)
            beside = tuple(window_slice)
            link = (
                factors[component]
                * 0.5
                * (perm_pad[component][centre] + perm_pad[component][beside])
                * inside_pad[beside]
            )
            numer = numer + link * press_pad[beside]
            denom = denom + jnp.abs(link)
    return numer / denom


def span_mask(anchor, length, total, margin):
    coords = anchor - margin + jnp.arange(length + 2 * margin, dtype=jnp.int32)
    return ((coords >= 0) & (coords < total)).astype(jnp.float32)


def cut_windows(fields):
    span_z = CCZ + 2 * RIM
    span_x = CCX + 2 * RIM
    span_y = CCY + 2 * RIM
    count_z = (fields[0].shape[0] - 2 * RIM) // CCZ
    count_x = (fields[0].shape[1] - 2 * RIM) // CCX
    count_y = (fields[0].shape[2] - 2 * RIM) // CCY
    stacks = []
    for field in fields:
        pieces = []
        for block_z in range(count_z):
            for block_y in range(count_y):
                piece = field[
                    block_z * CCZ : block_z * CCZ + span_z,
                    0:span_x,
                    block_y * CCY : block_y * CCY + span_y,
                ]
                pieces.append(piece.reshape(span_z, span_x * span_y))
        stacks.append(jnp.stack(pieces))
    return (stacks, (count_z, count_x, count_y))


def faces(block, sides):
    got = []
    for axis, dim in sides:
        count = lax.axis_size(axis)
        ends = count - 1
        head = lax.slice_in_dim(block, 0, 1, axis=dim)
        tail = lax.slice_in_dim(block, block.shape[dim] - 1, block.shape[dim], axis=dim)
        lower = lax.ppermute(tail, axis, [(i, i + 1) for i in range(ends)])
        upper = lax.ppermute(head, axis, [(i + 1, i) for i in range(ends)])
        got.append((lower, upper))
    return got


def neighbour_views(block, got, dim_of):
    views = []
    for (lower, upper), dim in zip(got, dim_of):
        size = block.shape[dim]
        below = jnp.concatenate([lower, lax.slice_in_dim(block, 0, size - 1, axis=dim)], axis=dim)
        above = jnp.concatenate([lax.slice_in_dim(block, 1, size, axis=dim), upper], axis=dim)
        views.append((below, above))
    return views


def coarse_step(upscaled, views, inside_views, pressure, accumulation, fixed):
    factors = (CCY * CCZ / CCX, CCX * CCZ / CCY, CCX * CCY / CCZ)
    numer = fixed
    denom = accumulation
    for component in range(3):
        for side in range(2):
            beside = views[component][side]
            link = factors[component] * 0.5 * (upscaled[component] + beside[component]) * inside_views[component][side]
            numer = numer + link * pressure[component][side]
            denom = denom + jnp.abs(link)
    return numer / denom


def local(log_noise, facies, facies_table, pressure_old, accumulation, source):
    depth_len, rows_len, cols_len = log_noise.shape
    size_z = lax.axis_size("gz")
    size_x = lax.axis_size("gx")
    size_y = lax.axis_size("gy")
    index_z = lax.axis_index("gz")
    index_x = lax.axis_index("gx")
    index_y = lax.axis_index("gy")
    raw = jnp.stack([log_noise, facies.astype(jnp.float32)])
    wide = -(-(cols_len + 2 * RIM) // LANES) * LANES
    raw = extended(raw, (("gx", 2), ("gz", 1), ("gy", 3)), RIM, wide)
    anchor_z = index_z * depth_len
    anchor_y = index_y * cols_len
    anchor_x = index_x * rows_len
    bounds = jnp.stack(
        [
            RIM - anchor_z,
            depth_len * size_z + RIM - anchor_z,
            RIM - anchor_x,
            rows_len * size_x + RIM - anchor_x,
            RIM - anchor_y,
            cols_len * size_y + RIM - anchor_y,
        ]
    ).astype(jnp.int32)
    upscaled = upscale_windows(raw, facies_table, bounds, cols_len)
    coarse_z, coarse_x, coarse_y = pressure_old.shape
    bundle = jnp.stack([upscaled[0], upscaled[1], upscaled[2], pressure_old, accumulation, source])
    every = lax.all_gather(bundle, "gy", axis=3, tiled=True)
    every = lax.all_gather(every, "gx", axis=2, tiled=True)
    every = lax.all_gather(every, "gz", axis=1, tiled=True)
    perm_pad = jnp.pad(every[:3], ((0, 0), (1, 1), (1, 1), (1, 1)))
    old_all = every[3]
    acc_all = every[4]
    fixed_all = acc_all * old_all + every[5]
    inside_pad = jnp.pad(jnp.ones(old_all.shape, jnp.float32), 1)
    pressure = old_all
    for sweep_index in range(2):
        pressure = coarse_sweep(perm_pad, jnp.pad(pressure, 1), inside_pad, acc_all, fixed_all)
    pressure = lax.dynamic_slice(
        pressure, (index_z * coarse_z, index_x * coarse_x, index_y * coarse_y), (coarse_z, coarse_x, coarse_y)
    )
    return (pressure, upscaled)


def solution(mesh):
    placed = (
        P(("real", "gz"), "gx", "gy"),
        P(("real", "gz"), "gx", "gy"),
        P(),
        P(("real", "gz"), "gx", "gy"),
        P(("real", "gz"), "gx", "gy"),
        P(("real", "gz"), "gx", "gy"),
    )
    return jax.shard_map(
        local,
        mesh=mesh,
        in_specs=placed,
        out_specs=(P(("real", "gz"), "gx", "gy"), P(None, ("real", "gz"), "gx", "gy")),
        check_vma=False,
    )
```

```python
import functools

import jax
import jax.numpy as jnp
from jax import lax
from jax.sharding import PartitionSpec as P
from jax.experimental import pallas as pl
from jax.experimental.pallas import tpu as pltpu

NFAC = 4
CCX = 32
CCY = 32
CCZ = 8
RIM = 4
SWEEPS = 3


BOUND_MID = 1.0
BOUND_HALF = 0.9


def extended(cells, sides, width, lanes=None):
    for axis, dim in sides:
        count = lax.axis_size(axis)
        ends = count - 1
        head = lax.slice_in_dim(cells, 0, width, axis=dim)
        tail = lax.slice_in_dim(cells, cells.shape[dim] - width, cells.shape[dim], axis=dim)
        if count == 2:
            lower_side = lax.axis_index(axis) == 0
            got = lax.ppermute(jnp.where(lower_side, tail, head), axis, [(0, 1), (1, 0)])
            below = jnp.where(lower_side, 0.0, got)
            above = jnp.where(lower_side, got, 0.0)
        else:
            below = lax.ppermute(tail, axis, [(i, (i + 1) % count) for i in range(ends)])
            above = lax.ppermute(head, axis, [((i + 1) % count, i) for i in range(ends)])
        if lanes is not None and dim == cells.ndim - 1:
            extra = lanes - (cells.shape[dim] + 2 * width)
            parts = [cells, above, jnp.zeros(cells.shape[:-1] + (extra,), cells.dtype), below]
        else:
            parts = [below, cells, above]
        cells = jnp.concatenate(parts, axis=dim)
    return cells


def raise_flat(values, offset):
    zeros_block = jnp.zeros(values.shape[:-1] + (offset,), values.dtype)
    return jnp.concatenate([values[..., offset:], zeros_block], axis=-1)


def lower_flat(values, offset):
    zeros_block = jnp.zeros(values.shape[:-1] + (offset,), values.dtype)
    return jnp.concatenate([zeros_block, values[..., :-offset]], axis=-1)


def raise_depth(values):
    zeros_block = jnp.zeros(values.shape[:1] + (1,) + values.shape[2:], values.dtype)
    return jnp.concatenate([values[:, 1:], zeros_block], axis=1)


def lower_depth(values):
    zeros_block = jnp.zeros(values.shape[:1] + (1,) + values.shape[2:], values.dtype)
    return jnp.concatenate([zeros_block, values[:, :-1]], axis=1)


def log_fields(log_noise, facies, facies_table):
    base_log = log_noise
    extra_y = jnp.zeros_like(log_noise)
    extra_z = jnp.zeros_like(log_noise)
    for code_value in range(NFAC):
        matched = facies == code_value
        base_log = base_log + jnp.where(matched, facies_table[0, code_value], jnp.float32(0.0))
        extra_y = extra_y + jnp.where(matched, facies_table[1, code_value], jnp.float32(0.0))
        extra_z = extra_z + jnp.where(matched, facies_table[2, code_value], jnp.float32(0.0))
    return (base_log, base_log + extra_y, base_log + extra_z)


def upscale(perm_logs, inside):
    span_z = CCZ + 2 * RIM
    span_x = CCX + 2 * RIM
    span_y = CCY + 2 * RIM
    depth_pos = lax.broadcasted_iota(jnp.int32, (1, span_z, 1), 1)
    flat_pos = lax.broadcasted_iota(jnp.int32, (1, 1, span_x * span_y), 2)
    column_pos = flat_pos // span_y
    row_pos = flat_pos % span_y
    perm_x = jnp.exp(perm_logs[0])
    perm_y = jnp.exp(perm_logs[1])
    perm_z = jnp.exp(perm_logs[2])

    def links(perm, other_perm, other_inside):
        return inside * other_inside * 2.0 * perm * other_perm / (perm + other_perm)

    link_x = links(perm_x, raise_flat(perm_x, span_y), raise_flat(inside, span_y))
    link_y = links(perm_y, raise_flat(perm_y, 1), raise_flat(inside, 1)) * (
        row_pos < span_y - 1
    ).astype(jnp.float32)
    link_z = links(perm_z, raise_depth(perm_z), raise_depth(inside))
    diagonal = (
        link_x
        + lower_flat(link_x, span_y)
        + link_y
        + lower_flat(link_y, 1)
        + link_z
        + lower_depth(link_z)
    )

    def apply_operator(field):
        beside = link_x * raise_flat(field, span_y) + lower_flat(link_x * field, span_y)
        beside = beside + link_y * raise_flat(field, 1) + lower_flat(link_y * field, 1)
        beside = beside + link_z * raise_depth(field) + lower_depth(link_z * field)
        return diagonal * field - beside

    interior = (
        (depth_pos >= 1)
        & (depth_pos <= span_z - 2)
        & (column_pos >= 1)
        & (column_pos <= span_x - 2)
        & (row_pos >= 1)
        & (row_pos <= span_y - 2)
    )
    unknown = inside * interior.astype(jnp.float32)
    scaling = unknown / (diagonal + 1.0 - unknown)
    core_z = (depth_pos >= RIM) & (depth_pos < RIM + CCZ)
    core_x = (column_pos >= RIM) & (column_pos < RIM + CCX)
    core_y = (row_pos >= RIM) & (row_pos < RIM + CCY)
    face_x = (((column_pos == RIM - 1) | (column_pos == RIM + CCX - 1)) & core_z & core_y).astype(
        jnp.float32
    )
    face_y = (((row_pos == RIM - 1) | (row_pos == RIM + CCY - 1)) & core_z & core_x).astype(
        jnp.float32
    )
    face_z = (((depth_pos == RIM - 1) | (depth_pos == RIM + CCZ - 1)) & core_x & core_y).astype(
        jnp.float32
    )
    ramp_x = ((span_x - 1) / 2.0 - column_pos).astype(jnp.float32)
    ramp_y = ((span_y - 1) / 2.0 - row_pos).astype(jnp.float32)
    ramp_z = ((span_z - 1) / 2.0 - depth_pos).astype(jnp.float32)
    cheb_ratio = BOUND_MID / BOUND_HALF
    results = []
    cases = (
        (ramp_x, link_x, face_x, CCY * CCZ, 0),
        (ramp_y, link_y, face_y, CCX * CCZ, 1),
        (ramp_z, link_z, face_z, CCX * CCY, 2),
    )
    for ramp, link, face, area, direction in cases:
        ramp_full = jnp.broadcast_to(ramp, inside.shape)
        source_term = -unknown * apply_operator(ramp_full)
        update = scaling * source_term / BOUND_MID
        solution = update
        rho_old = 1.0 / cheb_ratio
        for sweep_index in range(SWEEPS - 1):
            residual = source_term - apply_operator(solution)
            rho_new = 1.0 / (2.0 * cheb_ratio - rho_old)
            update = rho_new * rho_old * update + 2.0 * rho_new / BOUND_HALF * (scaling * residual)
            solution = solution + update
            rho_old = rho_new
        pressure = ramp_full + solution
        if direction == 0:
            upper = raise_flat(pressure, span_y)
        elif direction == 1:
            upper = raise_flat(pressure, 1)
        else:
            upper = raise_depth(pressure)
        flux = link * (pressure - upper) * face
        results.append(jnp.sum(flux, axis=(1, 2)) * (0.5 / area))
    return jnp.stack(results)


LANES = 128


def window_kernel(table_ref, bounds_ref, raw_ref, o_ref, *, count_x, count_y, count):
    span_z = CCZ + 2 * RIM
    span_x = CCX + 2 * RIM
    span_y = CCY + 2 * RIM
    segments = LANES // span_y
    shape = (span_z, span_x, LANES)
    pack = pl.program_id(0)
    wide = raw_ref.shape[-1]
    depth_pos = lax.broadcasted_iota(jnp.int32, shape, 0)
    column_pos = lax.broadcasted_iota(jnp.int32, shape, 1)
    lane = lax.broadcasted_iota(jnp.int32, shape, 2)
    segment = jnp.zeros(shape, jnp.int32)
    for bound in range(1, segments + 1):
        segment = segment + (lane >= bound * span_y).astype(jnp.int32)
    row_pos = lane - span_y * segment
    noise = jnp.zeros(shape, jnp.float32)
    codes = jnp.zeros(shape, jnp.float32)
    inside = jnp.zeros(shape, jnp.float32)
    for slot in range(segments):
        window = pack * segments + slot
        valid = window < count
        window = jnp.minimum(window, count - 1)
        block_z = window // (count_x * count_y)
        block_x = (window // count_y) % count_x
        block_y = window % count_y
        shift = (slot * span_y - block_y * CCY + RIM + wide) % wide
        here = segment == slot

        def cut(field):
            slab = raw_ref[field, pl.ds(block_z * CCZ, span_z), pl.ds(block_x * CCX, span_x), :]
            return pltpu.roll(slab, shift, 2)[:, :, :LANES]

        depth_at = depth_pos + block_z * CCZ
        column_at = column_pos + block_x * CCX
        row_at = row_pos + block_y * CCY
        held = (
            (depth_at >= bounds_ref[0])
            & (depth_at < bounds_ref[1])
            & (column_at >= bounds_ref[2])
            & (column_at < bounds_ref[3])
            & (row_at >= bounds_ref[4])
            & (row_at < bounds_ref[5])
        )
        noise = jnp.where(here, cut(0), noise)
        codes = jnp.where(here, cut(1), codes)
        inside = jnp.where(here & valid & held, 1.0, inside)

    def lookup(row):
        value = jnp.zeros(shape, jnp.float32)
        for code_value in range(NFAC):
            value = jnp.where(codes == code_value, table_ref[row, code_value], value)
        return value

    log_x = noise + lookup(0)
    log_y = log_x + lookup(1)
    log_z = log_x + lookup(2)
    perm_x = jnp.exp(log_x)
    perm_y = jnp.exp(log_y)
    perm_z = jnp.exp(log_z)

    def up_x(v):
        return pltpu.roll(v, span_x - 1, 1)

    def down_x(v):
        return pltpu.roll(v, 1, 1)

    def up_y(v):
        return pltpu.roll(v, LANES - 1, 2)

    def down_y(v):
        return pltpu.roll(v, 1, 2)

    def up_z(v):
        return jnp.concatenate([v[1:], v[:1]], axis=0)

    def down_z(v):
        return jnp.concatenate([v[-1:], v[:-1]], axis=0)

    def links(perm, other_perm, other_inside, valid):
        value = inside * other_inside * 2.0 * perm * other_perm / (perm + other_perm)
        return jnp.where(valid, value, 0.0)

    link_x = links(perm_x, up_x(perm_x), up_x(inside), column_pos < span_x - 1)
    link_y = links(perm_y, up_y(perm_y), up_y(inside), row_pos < span_y - 1)
    link_z = links(perm_z, up_z(perm_z), up_z(inside), depth_pos < span_z - 1)
    diagonal = link_x + down_x(link_x) + link_y + down_y(link_y) + link_z + down_z(link_z)

    def apply_operator(field):
        beside = link_x * up_x(field) + down_x(link_x * field)
        beside = beside + link_y * up_y(field) + down_y(link_y * field)
        beside = beside + link_z * up_z(field) + down_z(link_z * field)
        return diagonal * field - beside

    interior = (
        (depth_pos >= 1)
        & (depth_pos <= span_z - 2)
        & (column_pos >= 1)
        & (column_pos <= span_x - 2)
        & (row_pos >= 1)
        & (row_pos <= span_y - 2)
    )
    unknown = jnp.where(interior, inside, 0.0)
    scaling = unknown / (diagonal + 1.0 - unknown)
    core_z = (depth_pos >= RIM) & (depth_pos < RIM + CCZ)
    core_x = (column_pos >= RIM) & (column_pos < RIM + CCX)
    core_y = (row_pos >= RIM) & (row_pos < RIM + CCY)
    face_x = ((column_pos == RIM - 1) | (column_pos == RIM + CCX - 1)) & core_z & core_y
    face_y = ((row_pos == RIM - 1) | (row_pos == RIM + CCY - 1)) & core_z & core_x
    face_z = ((depth_pos == RIM - 1) | (depth_pos == RIM + CCZ - 1)) & core_x & core_y
    ramp_x = ((span_x - 1) / 2.0 - column_pos).astype(jnp.float32)
    ramp_y = ((span_y - 1) / 2.0 - row_pos).astype(jnp.float32)
    ramp_z = ((span_z - 1) / 2.0 - depth_pos).astype(jnp.float32)
    cheb_ratio = BOUND_MID / BOUND_HALF
    cases = (
        (ramp_x, link_x, face_x, CCY * CCZ, up_x, down_x),
        (ramp_y, link_y, face_y, CCX * CCZ, up_y, down_y),
        (ramp_z, link_z, face_z, CCX * CCY, up_z, down_z),
    )
    rows = []
    for ramp, link, face, area, upper_of, lower_of in cases:
        source_term = -unknown * (link - lower_of(link))
        update = scaling * source_term / BOUND_MID
        solution = update
        rho_old = 1.0 / cheb_ratio
        for sweep_index in range(SWEEPS - 1):
            residual = source_term - apply_operator(solution)
            rho_new = 1.0 / (2.0 * cheb_ratio - rho_old)
            update = rho_new * rho_old * update + 2.0 * rho_new / BOUND_HALF * (scaling * residual)
            solution = solution + update
            rho_old = rho_new
        pressure = ramp + solution
        flux = jnp.where(face, link * (pressure - upper_of(pressure)), 0.0)
        total = jnp.sum(flux, axis=0)
        total = jnp.sum(total, axis=0, keepdims=True)
        rows.append(total * (0.5 / area))
    rows.append(jnp.zeros((8 - len(rows), LANES), jnp.float32))
    o_ref[0] = jnp.concatenate(rows, axis=0)


def upscale_windows(raw, facies_table, bounds, cols_len):
    span_y = CCY + 2 * RIM
    count_z = (raw.shape[1] - 2 * RIM) // CCZ
    count_x = (raw.shape[2] - 2 * RIM) // CCX
    count_y = cols_len // CCY
    count = count_z * count_x * count_y
    segments = LANES // span_y
    packs = -(-count // segments)
    kernel = functools.partial(window_kernel, count_x=count_x, count_y=count_y, count=count)
    sums = pl.pallas_call(
        kernel,
        grid=(packs,),
        in_specs=[
            pl.BlockSpec(memory_space=pltpu.SMEM),
            pl.BlockSpec(memory_space=pltpu.SMEM),
            pl.BlockSpec(raw.shape, lambda p: (0, 0, 0, 0)),
        ],
        out_specs=pl.BlockSpec((1, 8, LANES), lambda p: (p, 0, 0)),
        out_shape=jax.ShapeDtypeStruct((packs, 8, LANES), jnp.float32),
    )(facies_table, bounds, raw)
    sums = sums[:, :3, : segments * span_y].reshape(packs, 3, segments, span_y).sum(axis=3)
    sums = sums.transpose(1, 0, 2).reshape(3, packs * segments)[:, :count]
    return sums.reshape((3, count_z, count_x, count_y))


def coarse_sweep(perm_pad, press_pad, inside_pad, accumulation, fixed):
    centre = (slice(1, -1), slice(1, -1), slice(1, -1))
    factors = (CCY * CCZ / CCX, CCX * CCZ / CCY, CCX * CCY / CCZ)
    numer = fixed
    denom = accumulation
    for component, axis_dim in ((0, 1), (1, 2), (2, 0)):
        for offset in (-1, 1):
            window_slice = [slice(1, -1), slice(1, -1), slice(1, -1)]
            window_slice[axis_dim] = slice(1 + offset, press_pad.shape[axis_dim] - 1 + offset)
            beside = tuple(window_slice)
            link = (
                factors[component]
                * 0.5
                * (perm_pad[component][centre] + perm_pad[component][beside])
                * inside_pad[beside]
            )
            numer = numer + link * press_pad[beside]
            denom = denom + jnp.abs(link)
    return numer / denom


def span_mask(anchor, length, total, margin):
    coords = anchor - margin + jnp.arange(length + 2 * margin, dtype=jnp.int32)
    return ((coords >= 0) & (coords < total)).astype(jnp.float32)


def cut_windows(fields):
    span_z = CCZ + 2 * RIM
    span_x = CCX + 2 * RIM
    span_y = CCY + 2 * RIM
    count_z = (fields[0].shape[0] - 2 * RIM) // CCZ
    count_x = (fields[0].shape[1] - 2 * RIM) // CCX
    count_y = (fields[0].shape[2] - 2 * RIM) // CCY
    stacks = []
    for field in fields:
        pieces = []
        for block_z in range(count_z):
            for block_y in range(count_y):
                piece = field[
                    block_z * CCZ : block_z * CCZ + span_z,
                    0:span_x,
                    block_y * CCY : block_y * CCY + span_y,
                ]
                pieces.append(piece.reshape(span_z, span_x * span_y))
        stacks.append(jnp.stack(pieces))
    return (stacks, (count_z, count_x, count_y))


def faces(block, sides):
    got = []
    for axis, dim in sides:
        count = lax.axis_size(axis)
        ends = count - 1
        head = lax.slice_in_dim(block, 0, 1, axis=dim)
        tail = lax.slice_in_dim(block, block.shape[dim] - 1, block.shape[dim], axis=dim)
        lower = lax.ppermute(tail, axis, [(i, i + 1) for i in range(ends)])
        upper = lax.ppermute(head, axis, [(i + 1, i) for i in range(ends)])
        got.append((lower, upper))
    return got


def neighbour_views(block, got, dim_of):
    views = []
    for (lower, upper), dim in zip(got, dim_of):
        size = block.shape[dim]
        below = jnp.concatenate([lower, lax.slice_in_dim(block, 0, size - 1, axis=dim)], axis=dim)
        above = jnp.concatenate([lax.slice_in_dim(block, 1, size, axis=dim), upper], axis=dim)
        views.append((below, above))
    return views


def coarse_step(upscaled, views, inside_views, pressure, accumulation, fixed):
    factors = (CCY * CCZ / CCX, CCX * CCZ / CCY, CCX * CCY / CCZ)
    numer = fixed
    denom = accumulation
    for component in range(3):
        for side in range(2):
            beside = views[component][side]
            link = factors[component] * 0.5 * (upscaled[component] + beside[component]) * inside_views[component][side]
            numer = numer + link * pressure[component][side]
            denom = denom + jnp.abs(link)
    return numer / denom


def local(log_noise, facies, facies_table, pressure_old, accumulation, source):
    depth_len, rows_len, cols_len = log_noise.shape
    size_z = lax.axis_size("gz")
    size_x = lax.axis_size("gx")
    size_y = lax.axis_size("gy")
    index_z = lax.axis_index("gz")
    index_x = lax.axis_index("gx")
    index_y = lax.axis_index("gy")
    raw = jnp.stack([log_noise, facies.astype(jnp.float32)])
    wide = -(-(cols_len + 2 * RIM) // LANES) * LANES
    raw = extended(raw, (("gx", 2), ("gz", 1), ("gy", 3)), RIM, wide)
    anchor_z = index_z * depth_len
    anchor_y = index_y * cols_len
    anchor_x = index_x * rows_len
    bounds = jnp.stack(
        [
            RIM - anchor_z,
            depth_len * size_z + RIM - anchor_z,
            RIM - anchor_x,
            rows_len * size_x + RIM - anchor_x,
            RIM - anchor_y,
            cols_len * size_y + RIM - anchor_y,
        ]
    ).astype(jnp.int32)
    upscaled = upscale_windows(raw, facies_table, bounds, cols_len)
    coarse_z, coarse_x, coarse_y = pressure_old.shape
    bundle = jnp.stack([upscaled[0], upscaled[1], upscaled[2], pressure_old, accumulation, source])
    every = lax.all_gather(bundle, "gy", axis=3, tiled=True)
    every = lax.all_gather(every, "gx", axis=2, tiled=True)
    every = lax.all_gather(every, "gz", axis=1, tiled=True)
    perm_pad = jnp.pad(every[:3], ((0, 0), (1, 1), (1, 1), (1, 1)))
    old_all = every[3]
    acc_all = every[4]
    fixed_all = acc_all * old_all + every[5]
    inside_pad = jnp.pad(jnp.ones(old_all.shape, jnp.float32), 1)
    pressure = old_all
    for sweep_index in range(2):
        pressure = coarse_sweep(perm_pad, jnp.pad(pressure, 1), inside_pad, acc_all, fixed_all)
    pressure = lax.dynamic_slice(
        pressure, (index_z * coarse_z, index_x * coarse_x, index_y * coarse_y), (coarse_z, coarse_x, coarse_y)
    )
    return (pressure, upscaled)


def solution(mesh):
    placed = (
        P(("real", "gz"), "gx", "gy"),
        P(("real", "gz"), "gx", "gy"),
        P(),
        P(("real", "gz"), "gx", "gy"),
        P(("real", "gz"), "gx", "gy"),
        P(("real", "gz"), "gx", "gy"),
    )
    return jax.shard_map(
        local,
        mesh=mesh,
        in_specs=placed,
        out_specs=(P(("real", "gz"), "gx", "gy"), P(None, ("real", "gz"), "gx", "gy")),
        check_vma=False,
    )
```

```python
import functools

import jax
import jax.numpy as jnp
from jax import lax
from jax.sharding import PartitionSpec as P
from jax.experimental import pallas as pl
from jax.experimental.pallas import tpu as pltpu

NFAC = 4
CCX = 32
CCY = 32
CCZ = 8
RIM = 4
SWEEPS = 3


BOUND_MID = 1.0
BOUND_HALF = 0.9


def extended(cells, sides, width, lanes=None):
    for axis, dim in sides:
        count = lax.axis_size(axis)
        ends = count - 1
        head = lax.slice_in_dim(cells, 0, width, axis=dim)
        tail = lax.slice_in_dim(cells, cells.shape[dim] - width, cells.shape[dim], axis=dim)
        if count == 2:
            lower_side = lax.axis_index(axis) == 0
            got = lax.ppermute(jnp.where(lower_side, tail, head), axis, [(0, 1), (1, 0)])
            below = jnp.where(lower_side, 0.0, got)
            above = jnp.where(lower_side, got, 0.0)
        else:
            below = lax.ppermute(tail, axis, [(i, (i + 1) % count) for i in range(ends)])
            above = lax.ppermute(head, axis, [((i + 1) % count, i) for i in range(ends)])
        if lanes is not None and dim == cells.ndim - 1:
            extra = lanes - (cells.shape[dim] + 2 * width)
            parts = [cells, above, jnp.zeros(cells.shape[:-1] + (extra,), cells.dtype), below]
        else:
            parts = [below, cells, above]
        cells = jnp.concatenate(parts, axis=dim)
    return cells


def raise_flat(values, offset):
    zeros_block = jnp.zeros(values.shape[:-1] + (offset,), values.dtype)
    return jnp.concatenate([values[..., offset:], zeros_block], axis=-1)


def lower_flat(values, offset):
    zeros_block = jnp.zeros(values.shape[:-1] + (offset,), values.dtype)
    return jnp.concatenate([zeros_block, values[..., :-offset]], axis=-1)


def raise_depth(values):
    zeros_block = jnp.zeros(values.shape[:1] + (1,) + values.shape[2:], values.dtype)
    return jnp.concatenate([values[:, 1:], zeros_block], axis=1)


def lower_depth(values):
    zeros_block = jnp.zeros(values.shape[:1] + (1,) + values.shape[2:], values.dtype)
    return jnp.concatenate([zeros_block, values[:, :-1]], axis=1)


def log_fields(log_noise, facies, facies_table):
    base_log = log_noise
    extra_y = jnp.zeros_like(log_noise)
    extra_z = jnp.zeros_like(log_noise)
    for code_value in range(NFAC):
        matched = facies == code_value
        base_log = base_log + jnp.where(matched, facies_table[0, code_value], jnp.float32(0.0))
        extra_y = extra_y + jnp.where(matched, facies_table[1, code_value], jnp.float32(0.0))
        extra_z = extra_z + jnp.where(matched, facies_table[2, code_value], jnp.float32(0.0))
    return (base_log, base_log + extra_y, base_log + extra_z)


def upscale(perm_logs, inside):
    span_z = CCZ + 2 * RIM
    span_x = CCX + 2 * RIM
    span_y = CCY + 2 * RIM
    depth_pos = lax.broadcasted_iota(jnp.int32, (1, span_z, 1), 1)
    flat_pos = lax.broadcasted_iota(jnp.int32, (1, 1, span_x * span_y), 2)
    column_pos = flat_pos // span_y
    row_pos = flat_pos % span_y
    perm_x = jnp.exp(perm_logs[0])
    perm_y = jnp.exp(perm_logs[1])
    perm_z = jnp.exp(perm_logs[2])

    def links(perm, other_perm, other_inside):
        return inside * other_inside * 2.0 * perm * other_perm / (perm + other_perm)

    link_x = links(perm_x, raise_flat(perm_x, span_y), raise_flat(inside, span_y))
    link_y = links(perm_y, raise_flat(perm_y, 1), raise_flat(inside, 1)) * (
        row_pos < span_y - 1
    ).astype(jnp.float32)
    link_z = links(perm_z, raise_depth(perm_z), raise_depth(inside))
    diagonal = (
        link_x
        + lower_flat(link_x, span_y)
        + link_y
        + lower_flat(link_y, 1)
        + link_z
        + lower_depth(link_z)
    )

    def apply_operator(field):
        beside = link_x * raise_flat(field, span_y) + lower_flat(link_x * field, span_y)
        beside = beside + link_y * raise_flat(field, 1) + lower_flat(link_y * field, 1)
        beside = beside + link_z * raise_depth(field) + lower_depth(link_z * field)
        return diagonal * field - beside

    interior = (
        (depth_pos >= 1)
        & (depth_pos <= span_z - 2)
        & (column_pos >= 1)
        & (column_pos <= span_x - 2)
        & (row_pos >= 1)
        & (row_pos <= span_y - 2)
    )
    unknown = inside * interior.astype(jnp.float32)
    scaling = unknown / (diagonal + 1.0 - unknown)
    core_z = (depth_pos >= RIM) & (depth_pos < RIM + CCZ)
    core_x = (column_pos >= RIM) & (column_pos < RIM + CCX)
    core_y = (row_pos >= RIM) & (row_pos < RIM + CCY)
    face_x = (((column_pos == RIM - 1) | (column_pos == RIM + CCX - 1)) & core_z & core_y).astype(
        jnp.float32
    )
    face_y = (((row_pos == RIM - 1) | (row_pos == RIM + CCY - 1)) & core_z & core_x).astype(
        jnp.float32
    )
    face_z = (((depth_pos == RIM - 1) | (depth_pos == RIM + CCZ - 1)) & core_x & core_y).astype(
        jnp.float32
    )
    ramp_x = ((span_x - 1) / 2.0 - column_pos).astype(jnp.float32)
    ramp_y = ((span_y - 1) / 2.0 - row_pos).astype(jnp.float32)
    ramp_z = ((span_z - 1) / 2.0 - depth_pos).astype(jnp.float32)
    cheb_ratio = BOUND_MID / BOUND_HALF
    results = []
    cases = (
        (ramp_x, link_x, face_x, CCY * CCZ, 0),
        (ramp_y, link_y, face_y, CCX * CCZ, 1),
        (ramp_z, link_z, face_z, CCX * CCY, 2),
    )
    for ramp, link, face, area, direction in cases:
        ramp_full = jnp.broadcast_to(ramp, inside.shape)
        source_term = -unknown * apply_operator(ramp_full)
        update = scaling * source_term / BOUND_MID
        solution = update
        rho_old = 1.0 / cheb_ratio
        for sweep_index in range(SWEEPS - 1):
            residual = source_term - apply_operator(solution)
            rho_new = 1.0 / (2.0 * cheb_ratio - rho_old)
            update = rho_new * rho_old * update + 2.0 * rho_new / BOUND_HALF * (scaling * residual)
            solution = solution + update
            rho_old = rho_new
        pressure = ramp_full + solution
        if direction == 0:
            upper = raise_flat(pressure, span_y)
        elif direction == 1:
            upper = raise_flat(pressure, 1)
        else:
            upper = raise_depth(pressure)
        flux = link * (pressure - upper) * face
        results.append(jnp.sum(flux, axis=(1, 2)) * (0.5 / area))
    return jnp.stack(results)


LANES = 128


def window_kernel(table_ref, bounds_ref, raw_ref, o_ref, *, count_x, count_y, count):
    span_z = CCZ + 2 * RIM
    span_x = CCX + 2 * RIM
    span_y = CCY + 2 * RIM
    segments = LANES // span_y
    shape = (span_z, span_x, LANES)
    pack = pl.program_id(0)
    wide = raw_ref.shape[-1]
    depth_pos = lax.broadcasted_iota(jnp.int32, shape, 0)
    column_pos = lax.broadcasted_iota(jnp.int32, shape, 1)
    lane = lax.broadcasted_iota(jnp.int32, shape, 2)
    segment = jnp.zeros(shape, jnp.int32)
    for bound in range(1, segments + 1):
        segment = segment + (lane >= bound * span_y).astype(jnp.int32)
    row_pos = lane - span_y * segment
    noise = jnp.zeros(shape, jnp.float32)
    codes = jnp.zeros(shape, jnp.float32)
    inside = jnp.zeros(shape, jnp.float32)
    for slot in range(segments):
        window = pack * segments + slot
        valid = window < count
        window = jnp.minimum(window, count - 1)
        block_z = window // (count_x * count_y)
        block_x = (window // count_y) % count_x
        block_y = window % count_y
        shift = (slot * span_y - block_y * CCY + RIM + wide) % wide
        here = segment == slot

        def cut(field):
            slab = raw_ref[field, pl.ds(block_z * CCZ, span_z), pl.ds(block_x * CCX, span_x), :]
            return pltpu.roll(slab, shift, 2)[:, :, :LANES]

        depth_at = depth_pos + block_z * CCZ
        column_at = column_pos + block_x * CCX
        row_at = row_pos + block_y * CCY
        held = (
            (depth_at >= bounds_ref[0])
            & (depth_at < bounds_ref[1])
            & (column_at >= bounds_ref[2])
            & (column_at < bounds_ref[3])
            & (row_at >= bounds_ref[4])
            & (row_at < bounds_ref[5])
        )
        noise = jnp.where(here, cut(0), noise)
        codes = jnp.where(here, cut(1), codes)
        inside = jnp.where(here & valid & held, 1.0, inside)

    def lookup(row):
        value = jnp.zeros(shape, jnp.float32)
        for code_value in range(NFAC):
            value = jnp.where(codes == code_value, table_ref[row, code_value], value)
        return value

    log_x = noise + lookup(0)
    log_y = log_x + lookup(1)
    log_z = log_x + lookup(2)
    perm_x = jnp.exp(log_x)
    perm_y = jnp.exp(log_y)
    perm_z = jnp.exp(log_z)

    def up_x(v):
        return pltpu.roll(v, span_x - 1, 1)

    def down_x(v):
        return pltpu.roll(v, 1, 1)

    def up_y(v):
        return pltpu.roll(v, LANES - 1, 2)

    def down_y(v):
        return pltpu.roll(v, 1, 2)

    def up_z(v):
        return jnp.concatenate([v[1:], v[:1]], axis=0)

    def down_z(v):
        return jnp.concatenate([v[-1:], v[:-1]], axis=0)

    def links(perm, other_perm, other_inside, valid):
        value = inside * other_inside * 2.0 * perm * other_perm / (perm + other_perm)
        return jnp.where(valid, value, 0.0)

    link_x = links(perm_x, up_x(perm_x), up_x(inside), column_pos < span_x - 1)
    link_y = links(perm_y, up_y(perm_y), up_y(inside), row_pos < span_y - 1)
    link_z = links(perm_z, up_z(perm_z), up_z(inside), depth_pos < span_z - 1)
    diagonal = link_x + down_x(link_x) + link_y + down_y(link_y) + link_z + down_z(link_z)

    def apply_operator(field):
        beside = link_x * up_x(field) + down_x(link_x * field)
        beside = beside + link_y * up_y(field) + down_y(link_y * field)
        beside = beside + link_z * up_z(field) + down_z(link_z * field)
        return diagonal * field - beside

    interior = (
        (depth_pos >= 1)
        & (depth_pos <= span_z - 2)
        & (column_pos >= 1)
        & (column_pos <= span_x - 2)
        & (row_pos >= 1)
        & (row_pos <= span_y - 2)
    )
    unknown = jnp.where(interior, inside, 0.0)
    scaling = unknown / (diagonal + 1.0 - unknown)
    core_z = (depth_pos >= RIM) & (depth_pos < RIM + CCZ)
    core_x = (column_pos >= RIM) & (column_pos < RIM + CCX)
    core_y = (row_pos >= RIM) & (row_pos < RIM + CCY)
    face_x = ((column_pos == RIM - 1) | (column_pos == RIM + CCX - 1)) & core_z & core_y
    face_y = ((row_pos == RIM - 1) | (row_pos == RIM + CCY - 1)) & core_z & core_x
    face_z = ((depth_pos == RIM - 1) | (depth_pos == RIM + CCZ - 1)) & core_x & core_y
    ramp_x = ((span_x - 1) / 2.0 - column_pos).astype(jnp.float32)
    ramp_y = ((span_y - 1) / 2.0 - row_pos).astype(jnp.float32)
    ramp_z = ((span_z - 1) / 2.0 - depth_pos).astype(jnp.float32)
    cheb_ratio = BOUND_MID / BOUND_HALF
    cases = (
        (ramp_x, link_x, face_x, CCY * CCZ, up_x, down_x),
        (ramp_y, link_y, face_y, CCX * CCZ, up_y, down_y),
        (ramp_z, link_z, face_z, CCX * CCY, up_z, down_z),
    )
    rows = []
    for ramp, link, face, area, upper_of, lower_of in cases:
        source_term = -unknown * (link - lower_of(link))
        update = scaling * source_term / BOUND_MID
        solution = update
        rho_old = 1.0 / cheb_ratio
        for sweep_index in range(SWEEPS - 1):
            residual = source_term - apply_operator(solution)
            rho_new = 1.0 / (2.0 * cheb_ratio - rho_old)
            update = rho_new * rho_old * update + 2.0 * rho_new / BOUND_HALF * (scaling * residual)
            solution = solution + update
            rho_old = rho_new
        pressure = ramp + solution
        flux = jnp.where(face, link * (pressure - upper_of(pressure)), 0.0)
        total = jnp.sum(flux, axis=0)
        rows.append(jnp.sum(total, axis=0, keepdims=True) * (0.5 / area))
    out_row = lax.broadcasted_iota(jnp.int32, (8, LANES), 0)
    out_lane = lax.broadcasted_iota(jnp.int32, (8, LANES), 1)
    first_segment = segment[0, 0:1, :]
    gathered = jnp.zeros((8, LANES), jnp.float32)
    for direction in range(3):
        for slot in range(segments):
            value = jnp.sum(jnp.where(first_segment == slot, rows[direction], 0.0))
            spot = (out_row == direction) & (out_lane == pack * segments + slot)
            gathered = jnp.where(spot, value, gathered)

    @pl.when(pack == 0)
    def _():
        o_ref[...] = jnp.zeros((8, LANES), jnp.float32)

    o_ref[...] = o_ref[...] + gathered


def upscale_windows(raw, facies_table, bounds, cols_len):
    span_y = CCY + 2 * RIM
    count_z = (raw.shape[1] - 2 * RIM) // CCZ
    count_x = (raw.shape[2] - 2 * RIM) // CCX
    count_y = cols_len // CCY
    count = count_z * count_x * count_y
    segments = LANES // span_y
    packs = -(-count // segments)
    kernel = functools.partial(window_kernel, count_x=count_x, count_y=count_y, count=count)
    sums = pl.pallas_call(
        kernel,
        grid=(packs,),
        in_specs=[
            pl.BlockSpec(memory_space=pltpu.SMEM),
            pl.BlockSpec(memory_space=pltpu.SMEM),
            pl.BlockSpec(raw.shape, lambda p: (0, 0, 0, 0)),
        ],
        out_specs=pl.BlockSpec((8, LANES), lambda p: (0, 0)),
        out_shape=jax.ShapeDtypeStruct((8, LANES), jnp.float32),
    )(facies_table, bounds, raw)
    return sums[:3, :count].reshape((3, count_z, count_x, count_y))


def coarse_sweep(perm_pad, press_pad, inside_pad, accumulation, fixed):
    centre = (slice(1, -1), slice(1, -1), slice(1, -1))
    factors = (CCY * CCZ / CCX, CCX * CCZ / CCY, CCX * CCY / CCZ)
    numer = fixed
    denom = accumulation
    for component, axis_dim in ((0, 1), (1, 2), (2, 0)):
        for offset in (-1, 1):
            window_slice = [slice(1, -1), slice(1, -1), slice(1, -1)]
            window_slice[axis_dim] = slice(1 + offset, press_pad.shape[axis_dim] - 1 + offset)
            beside = tuple(window_slice)
            link = (
                factors[component]
                * 0.5
                * (perm_pad[component][centre] + perm_pad[component][beside])
                * inside_pad[beside]
            )
            numer = numer + link * press_pad[beside]
            denom = denom + jnp.abs(link)
    return numer / denom


def span_mask(anchor, length, total, margin):
    coords = anchor - margin + jnp.arange(length + 2 * margin, dtype=jnp.int32)
    return ((coords >= 0) & (coords < total)).astype(jnp.float32)


def cut_windows(fields):
    span_z = CCZ + 2 * RIM
    span_x = CCX + 2 * RIM
    span_y = CCY + 2 * RIM
    count_z = (fields[0].shape[0] - 2 * RIM) // CCZ
    count_x = (fields[0].shape[1] - 2 * RIM) // CCX
    count_y = (fields[0].shape[2] - 2 * RIM) // CCY
    stacks = []
    for field in fields:
        pieces = []
        for block_z in range(count_z):
            for block_y in range(count_y):
                piece = field[
                    block_z * CCZ : block_z * CCZ + span_z,
                    0:span_x,
                    block_y * CCY : block_y * CCY + span_y,
                ]
                pieces.append(piece.reshape(span_z, span_x * span_y))
        stacks.append(jnp.stack(pieces))
    return (stacks, (count_z, count_x, count_y))


def faces(block, sides):
    got = []
    for axis, dim in sides:
        count = lax.axis_size(axis)
        ends = count - 1
        head = lax.slice_in_dim(block, 0, 1, axis=dim)
        tail = lax.slice_in_dim(block, block.shape[dim] - 1, block.shape[dim], axis=dim)
        lower = lax.ppermute(tail, axis, [(i, i + 1) for i in range(ends)])
        upper = lax.ppermute(head, axis, [(i + 1, i) for i in range(ends)])
        got.append((lower, upper))
    return got


def neighbour_views(block, got, dim_of):
    views = []
    for (lower, upper), dim in zip(got, dim_of):
        size = block.shape[dim]
        below = jnp.concatenate([lower, lax.slice_in_dim(block, 0, size - 1, axis=dim)], axis=dim)
        above = jnp.concatenate([lax.slice_in_dim(block, 1, size, axis=dim), upper], axis=dim)
        views.append((below, above))
    return views


def coarse_step(upscaled, views, inside_views, pressure, accumulation, fixed):
    factors = (CCY * CCZ / CCX, CCX * CCZ / CCY, CCX * CCY / CCZ)
    numer = fixed
    denom = accumulation
    for component in range(3):
        for side in range(2):
            beside = views[component][side]
            link = factors[component] * 0.5 * (upscaled[component] + beside[component]) * inside_views[component][side]
            numer = numer + link * pressure[component][side]
            denom = denom + jnp.abs(link)
    return numer / denom


def local(log_noise, facies, facies_table, pressure_old, accumulation, source):
    depth_len, rows_len, cols_len = log_noise.shape
    size_z = lax.axis_size("gz")
    size_x = lax.axis_size("gx")
    size_y = lax.axis_size("gy")
    index_z = lax.axis_index("gz")
    index_x = lax.axis_index("gx")
    index_y = lax.axis_index("gy")
    raw = jnp.stack([log_noise, facies.astype(jnp.float32)])
    wide = -(-(cols_len + 2 * RIM) // LANES) * LANES
    raw = extended(raw, (("gx", 2), ("gz", 1), ("gy", 3)), RIM, wide)
    anchor_z = index_z * depth_len
    anchor_y = index_y * cols_len
    anchor_x = index_x * rows_len
    bounds = jnp.stack(
        [
            RIM - anchor_z,
            depth_len * size_z + RIM - anchor_z,
            RIM - anchor_x,
            rows_len * size_x + RIM - anchor_x,
            RIM - anchor_y,
            cols_len * size_y + RIM - anchor_y,
        ]
    ).astype(jnp.int32)
    upscaled = upscale_windows(raw, facies_table, bounds, cols_len)
    coarse_z, coarse_x, coarse_y = pressure_old.shape
    bundle = jnp.stack([upscaled[0], upscaled[1], upscaled[2], pressure_old, accumulation, source])
    every = lax.all_gather(bundle, "gy", axis=3, tiled=True)
    every = lax.all_gather(every, "gx", axis=2, tiled=True)
    every = lax.all_gather(every, "gz", axis=1, tiled=True)
    perm_pad = jnp.pad(every[:3], ((0, 0), (1, 1), (1, 1), (1, 1)))
    old_all = every[3]
    acc_all = every[4]
    fixed_all = acc_all * old_all + every[5]
    inside_pad = jnp.pad(jnp.ones(old_all.shape, jnp.float32), 1)
    pressure = old_all
    for sweep_index in range(2):
        pressure = coarse_sweep(perm_pad, jnp.pad(pressure, 1), inside_pad, acc_all, fixed_all)
    pressure = lax.dynamic_slice(
        pressure, (index_z * coarse_z, index_x * coarse_x, index_y * coarse_y), (coarse_z, coarse_x, coarse_y)
    )
    return (pressure, upscaled)


def solution(mesh):
    placed = (
        P(("real", "gz"), "gx", "gy"),
        P(("real", "gz"), "gx", "gy"),
        P(),
        P(("real", "gz"), "gx", "gy"),
        P(("real", "gz"), "gx", "gy"),
        P(("real", "gz"), "gx", "gy"),
    )
    return jax.shard_map(
        local,
        mesh=mesh,
        in_specs=placed,
        out_specs=(P(("real", "gz"), "gx", "gy"), P(None, ("real", "gz"), "gx", "gy")),
        check_vma=False,
    )
```

```python
import functools

import jax
import jax.numpy as jnp
from jax import lax
from jax.sharding import PartitionSpec as P
from jax.experimental import pallas as pl
from jax.experimental.pallas import tpu as pltpu

NFAC = 4
CCX = 32
CCY = 32
CCZ = 8
RIM = 4
SWEEPS = 3


BOUND_MID = 1.0
BOUND_HALF = 0.9


def extended(cells, sides, width, lanes=None):
    for axis, dim in sides:
        count = lax.axis_size(axis)
        ends = count - 1
        head = lax.slice_in_dim(cells, 0, width, axis=dim)
        tail = lax.slice_in_dim(cells, cells.shape[dim] - width, cells.shape[dim], axis=dim)
        if count == 2:
            lower_side = lax.axis_index(axis) == 0
            got = lax.ppermute(jnp.where(lower_side, tail, head), axis, [(0, 1), (1, 0)])
            below = jnp.where(lower_side, 0.0, got)
            above = jnp.where(lower_side, got, 0.0)
        else:
            below = lax.ppermute(tail, axis, [(i, (i + 1) % count) for i in range(ends)])
            above = lax.ppermute(head, axis, [((i + 1) % count, i) for i in range(ends)])
        if lanes is not None and dim == cells.ndim - 1:
            extra = lanes - (cells.shape[dim] + 2 * width)
            parts = [cells, above, jnp.zeros(cells.shape[:-1] + (extra,), cells.dtype), below]
        else:
            parts = [below, cells, above]
        cells = jnp.concatenate(parts, axis=dim)
    return cells


def doubling_gather(values, axis, dim):
    count = lax.axis_size(axis)
    if count & (count - 1):
        return lax.all_gather(values, axis, axis=dim, tiled=True)
    index = lax.axis_index(axis)
    step = 1
    while step < count:
        got = lax.ppermute(values, axis, [(i, i ^ step) for i in range(count)])
        lower = (index // step) % 2 == 0
        values = jnp.where(
            lower, jnp.concatenate([values, got], axis=dim), jnp.concatenate([got, values], axis=dim)
        )
        step *= 2
    return values


def raise_flat(values, offset):
    zeros_block = jnp.zeros(values.shape[:-1] + (offset,), values.dtype)
    return jnp.concatenate([values[..., offset:], zeros_block], axis=-1)


def lower_flat(values, offset):
    zeros_block = jnp.zeros(values.shape[:-1] + (offset,), values.dtype)
    return jnp.concatenate([zeros_block, values[..., :-offset]], axis=-1)


def raise_depth(values):
    zeros_block = jnp.zeros(values.shape[:1] + (1,) + values.shape[2:], values.dtype)
    return jnp.concatenate([values[:, 1:], zeros_block], axis=1)


def lower_depth(values):
    zeros_block = jnp.zeros(values.shape[:1] + (1,) + values.shape[2:], values.dtype)
    return jnp.concatenate([zeros_block, values[:, :-1]], axis=1)


def log_fields(log_noise, facies, facies_table):
    base_log = log_noise
    extra_y = jnp.zeros_like(log_noise)
    extra_z = jnp.zeros_like(log_noise)
    for code_value in range(NFAC):
        matched = facies == code_value
        base_log = base_log + jnp.where(matched, facies_table[0, code_value], jnp.float32(0.0))
        extra_y = extra_y + jnp.where(matched, facies_table[1, code_value], jnp.float32(0.0))
        extra_z = extra_z + jnp.where(matched, facies_table[2, code_value], jnp.float32(0.0))
    return (base_log, base_log + extra_y, base_log + extra_z)


def upscale(perm_logs, inside):
    span_z = CCZ + 2 * RIM
    span_x = CCX + 2 * RIM
    span_y = CCY + 2 * RIM
    depth_pos = lax.broadcasted_iota(jnp.int32, (1, span_z, 1), 1)
    flat_pos = lax.broadcasted_iota(jnp.int32, (1, 1, span_x * span_y), 2)
    column_pos = flat_pos // span_y
    row_pos = flat_pos % span_y
    perm_x = jnp.exp(perm_logs[0])
    perm_y = jnp.exp(perm_logs[1])
    perm_z = jnp.exp(perm_logs[2])

    def links(perm, other_perm, other_inside):
        return inside * other_inside * 2.0 * perm * other_perm / (perm + other_perm)

    link_x = links(perm_x, raise_flat(perm_x, span_y), raise_flat(inside, span_y))
    link_y = links(perm_y, raise_flat(perm_y, 1), raise_flat(inside, 1)) * (
        row_pos < span_y - 1
    ).astype(jnp.float32)
    link_z = links(perm_z, raise_depth(perm_z), raise_depth(inside))
    diagonal = (
        link_x
        + lower_flat(link_x, span_y)
        + link_y
        + lower_flat(link_y, 1)
        + link_z
        + lower_depth(link_z)
    )

    def apply_operator(field):
        beside = link_x * raise_flat(field, span_y) + lower_flat(link_x * field, span_y)
        beside = beside + link_y * raise_flat(field, 1) + lower_flat(link_y * field, 1)
        beside = beside + link_z * raise_depth(field) + lower_depth(link_z * field)
        return diagonal * field - beside

    interior = (
        (depth_pos >= 1)
        & (depth_pos <= span_z - 2)
        & (column_pos >= 1)
        & (column_pos <= span_x - 2)
        & (row_pos >= 1)
        & (row_pos <= span_y - 2)
    )
    unknown = inside * interior.astype(jnp.float32)
    scaling = unknown / (diagonal + 1.0 - unknown)
    core_z = (depth_pos >= RIM) & (depth_pos < RIM + CCZ)
    core_x = (column_pos >= RIM) & (column_pos < RIM + CCX)
    core_y = (row_pos >= RIM) & (row_pos < RIM + CCY)
    face_x = (((column_pos == RIM - 1) | (column_pos == RIM + CCX - 1)) & core_z & core_y).astype(
        jnp.float32
    )
    face_y = (((row_pos == RIM - 1) | (row_pos == RIM + CCY - 1)) & core_z & core_x).astype(
        jnp.float32
    )
    face_z = (((depth_pos == RIM - 1) | (depth_pos == RIM + CCZ - 1)) & core_x & core_y).astype(
        jnp.float32
    )
    ramp_x = ((span_x - 1) / 2.0 - column_pos).astype(jnp.float32)
    ramp_y = ((span_y - 1) / 2.0 - row_pos).astype(jnp.float32)
    ramp_z = ((span_z - 1) / 2.0 - depth_pos).astype(jnp.float32)
    cheb_ratio = BOUND_MID / BOUND_HALF
    results = []
    cases = (
        (ramp_x, link_x, face_x, CCY * CCZ, 0),
        (ramp_y, link_y, face_y, CCX * CCZ, 1),
        (ramp_z, link_z, face_z, CCX * CCY, 2),
    )
    for ramp, link, face, area, direction in cases:
        ramp_full = jnp.broadcast_to(ramp, inside.shape)
        source_term = -unknown * apply_operator(ramp_full)
        update = scaling * source_term / BOUND_MID
        solution = update
        rho_old = 1.0 / cheb_ratio
        for sweep_index in range(SWEEPS - 1):
            residual = source_term - apply_operator(solution)
            rho_new = 1.0 / (2.0 * cheb_ratio - rho_old)
            update = rho_new * rho_old * update + 2.0 * rho_new / BOUND_HALF * (scaling * residual)
            solution = solution + update
            rho_old = rho_new
        pressure = ramp_full + solution
        if direction == 0:
            upper = raise_flat(pressure, span_y)
        elif direction == 1:
            upper = raise_flat(pressure, 1)
        else:
            upper = raise_depth(pressure)
        flux = link * (pressure - upper) * face
        results.append(jnp.sum(flux, axis=(1, 2)) * (0.5 / area))
    return jnp.stack(results)


LANES = 128


def window_kernel(table_ref, bounds_ref, raw_ref, o_ref, *, count_x, count_y, count):
    span_z = CCZ + 2 * RIM
    span_x = CCX + 2 * RIM
    span_y = CCY + 2 * RIM
    segments = LANES // span_y
    shape = (span_z, span_x, LANES)
    pack = pl.program_id(0)
    wide = raw_ref.shape[-1]
    depth_pos = lax.broadcasted_iota(jnp.int32, shape, 0)
    column_pos = lax.broadcasted_iota(jnp.int32, shape, 1)
    lane = lax.broadcasted_iota(jnp.int32, shape, 2)
    segment = jnp.zeros(shape, jnp.int32)
    for bound in range(1, segments + 1):
        segment = segment + (lane >= bound * span_y).astype(jnp.int32)
    row_pos = lane - span_y * segment
    noise = jnp.zeros(shape, jnp.float32)
    codes = jnp.zeros(shape, jnp.float32)
    inside = jnp.zeros(shape, jnp.float32)
    for slot in range(segments):
        window = pack * segments + slot
        valid = window < count
        window = jnp.minimum(window, count - 1)
        block_z = window // (count_x * count_y)
        block_x = (window // count_y) % count_x
        block_y = window % count_y
        shift = (slot * span_y - block_y * CCY + RIM + wide) % wide
        here = segment == slot

        def cut(field):
            slab = raw_ref[field, pl.ds(block_z * CCZ, span_z), pl.ds(block_x * CCX, span_x), :]
            return pltpu.roll(slab, shift, 2)[:, :, :LANES]

        depth_at = depth_pos + block_z * CCZ
        column_at = column_pos + block_x * CCX
        row_at = row_pos + block_y * CCY
        held = (
            (depth_at >= bounds_ref[0])
            & (depth_at < bounds_ref[1])
            & (column_at >= bounds_ref[2])
            & (column_at < bounds_ref[3])
            & (row_at >= bounds_ref[4])
            & (row_at < bounds_ref[5])
        )
        noise = jnp.where(here, cut(0), noise)
        codes = jnp.where(here, cut(1), codes)
        inside = jnp.where(here & valid & held, 1.0, inside)

    def lookup(row):
        value = jnp.zeros(shape, jnp.float32)
        for code_value in range(NFAC):
            value = jnp.where(codes == code_value, table_ref[row, code_value], value)
        return value

    log_x = noise + lookup(0)
    log_y = log_x + lookup(1)
    log_z = log_x + lookup(2)
    perm_x = jnp.exp(log_x)
    perm_y = jnp.exp(log_y)
    perm_z = jnp.exp(log_z)

    def up_x(v):
        return pltpu.roll(v, span_x - 1, 1)

    def down_x(v):
        return pltpu.roll(v, 1, 1)

    def up_y(v):
        return pltpu.roll(v, LANES - 1, 2)

    def down_y(v):
        return pltpu.roll(v, 1, 2)

    def up_z(v):
        return jnp.concatenate([v[1:], v[:1]], axis=0)

    def down_z(v):
        return jnp.concatenate([v[-1:], v[:-1]], axis=0)

    def links(perm, other_perm, other_inside, valid):
        value = inside * other_inside * 2.0 * perm * other_perm / (perm + other_perm)
        return jnp.where(valid, value, 0.0)

    link_x = links(perm_x, up_x(perm_x), up_x(inside), column_pos < span_x - 1)
    link_y = links(perm_y, up_y(perm_y), up_y(inside), row_pos < span_y - 1)
    link_z = links(perm_z, up_z(perm_z), up_z(inside), depth_pos < span_z - 1)
    diagonal = link_x + down_x(link_x) + link_y + down_y(link_y) + link_z + down_z(link_z)

    def apply_operator(field):
        beside = link_x * up_x(field) + down_x(link_x * field)
        beside = beside + link_y * up_y(field) + down_y(link_y * field)
        beside = beside + link_z * up_z(field) + down_z(link_z * field)
        return diagonal * field - beside

    interior = (
        (depth_pos >= 1)
        & (depth_pos <= span_z - 2)
        & (column_pos >= 1)
        & (column_pos <= span_x - 2)
        & (row_pos >= 1)
        & (row_pos <= span_y - 2)
    )
    unknown = jnp.where(interior, inside, 0.0)
    scaling = unknown / (diagonal + 1.0 - unknown)
    core_z = (depth_pos >= RIM) & (depth_pos < RIM + CCZ)
    core_x = (column_pos >= RIM) & (column_pos < RIM + CCX)
    core_y = (row_pos >= RIM) & (row_pos < RIM + CCY)
    face_x = ((column_pos == RIM - 1) | (column_pos == RIM + CCX - 1)) & core_z & core_y
    face_y = ((row_pos == RIM - 1) | (row_pos == RIM + CCY - 1)) & core_z & core_x
    face_z = ((depth_pos == RIM - 1) | (depth_pos == RIM + CCZ - 1)) & core_x & core_y
    ramp_x = ((span_x - 1) / 2.0 - column_pos).astype(jnp.float32)
    ramp_y = ((span_y - 1) / 2.0 - row_pos).astype(jnp.float32)
    ramp_z = ((span_z - 1) / 2.0 - depth_pos).astype(jnp.float32)
    cheb_ratio = BOUND_MID / BOUND_HALF
    cases = (
        (ramp_x, link_x, face_x, CCY * CCZ, up_x, down_x),
        (ramp_y, link_y, face_y, CCX * CCZ, up_y, down_y),
        (ramp_z, link_z, face_z, CCX * CCY, up_z, down_z),
    )
    rows = []
    for ramp, link, face, area, upper_of, lower_of in cases:
        source_term = -unknown * (link - lower_of(link))
        update = scaling * source_term / BOUND_MID
        solution = update
        rho_old = 1.0 / cheb_ratio
        for sweep_index in range(SWEEPS - 1):
            residual = source_term - apply_operator(solution)
            rho_new = 1.0 / (2.0 * cheb_ratio - rho_old)
            update = rho_new * rho_old * update + 2.0 * rho_new / BOUND_HALF * (scaling * residual)
            solution = solution + update
            rho_old = rho_new
        pressure = ramp + solution
        flux = jnp.where(face, link * (pressure - upper_of(pressure)), 0.0)
        total = jnp.sum(flux, axis=0)
        total = jnp.sum(total, axis=0, keepdims=True)
        rows.append(total * (0.5 / area))
    rows.append(jnp.zeros((8 - len(rows), LANES), jnp.float32))
    o_ref[0] = jnp.concatenate(rows, axis=0)


def upscale_windows(raw, facies_table, bounds, cols_len):
    span_y = CCY + 2 * RIM
    count_z = (raw.shape[1] - 2 * RIM) // CCZ
    count_x = (raw.shape[2] - 2 * RIM) // CCX
    count_y = cols_len // CCY
    count = count_z * count_x * count_y
    segments = LANES // span_y
    packs = -(-count // segments)
    kernel = functools.partial(window_kernel, count_x=count_x, count_y=count_y, count=count)
    sums = pl.pallas_call(
        kernel,
        grid=(packs,),
        in_specs=[
            pl.BlockSpec(memory_space=pltpu.SMEM),
            pl.BlockSpec(memory_space=pltpu.SMEM),
            pl.BlockSpec(raw.shape, lambda p: (0, 0, 0, 0)),
        ],
        out_specs=pl.BlockSpec((1, 8, LANES), lambda p: (p, 0, 0)),
        out_shape=jax.ShapeDtypeStruct((packs, 8, LANES), jnp.float32),
    )(facies_table, bounds, raw)
    sums = sums[:, :3, : segments * span_y].reshape(packs, 3, segments, span_y).sum(axis=3)
    sums = sums.transpose(1, 0, 2).reshape(3, packs * segments)[:, :count]
    return sums.reshape((3, count_z, count_x, count_y))


def coarse_sweep(perm_pad, press_pad, inside_pad, accumulation, fixed):
    centre = (slice(1, -1), slice(1, -1), slice(1, -1))
    factors = (CCY * CCZ / CCX, CCX * CCZ / CCY, CCX * CCY / CCZ)
    numer = fixed
    denom = accumulation
    for component, axis_dim in ((0, 1), (1, 2), (2, 0)):
        for offset in (-1, 1):
            window_slice = [slice(1, -1), slice(1, -1), slice(1, -1)]
            window_slice[axis_dim] = slice(1 + offset, press_pad.shape[axis_dim] - 1 + offset)
            beside = tuple(window_slice)
            link = (
                factors[component]
                * 0.5
                * (perm_pad[component][centre] + perm_pad[component][beside])
                * inside_pad[beside]
            )
            numer = numer + link * press_pad[beside]
            denom = denom + jnp.abs(link)
    return numer / denom


def span_mask(anchor, length, total, margin):
    coords = anchor - margin + jnp.arange(length + 2 * margin, dtype=jnp.int32)
    return ((coords >= 0) & (coords < total)).astype(jnp.float32)


def cut_windows(fields):
    span_z = CCZ + 2 * RIM
    span_x = CCX + 2 * RIM
    span_y = CCY + 2 * RIM
    count_z = (fields[0].shape[0] - 2 * RIM) // CCZ
    count_x = (fields[0].shape[1] - 2 * RIM) // CCX
    count_y = (fields[0].shape[2] - 2 * RIM) // CCY
    stacks = []
    for field in fields:
        pieces = []
        for block_z in range(count_z):
            for block_y in range(count_y):
                piece = field[
                    block_z * CCZ : block_z * CCZ + span_z,
                    0:span_x,
                    block_y * CCY : block_y * CCY + span_y,
                ]
                pieces.append(piece.reshape(span_z, span_x * span_y))
        stacks.append(jnp.stack(pieces))
    return (stacks, (count_z, count_x, count_y))


def faces(block, sides):
    got = []
    for axis, dim in sides:
        count = lax.axis_size(axis)
        ends = count - 1
        head = lax.slice_in_dim(block, 0, 1, axis=dim)
        tail = lax.slice_in_dim(block, block.shape[dim] - 1, block.shape[dim], axis=dim)
        lower = lax.ppermute(tail, axis, [(i, i + 1) for i in range(ends)])
        upper = lax.ppermute(head, axis, [(i + 1, i) for i in range(ends)])
        got.append((lower, upper))
    return got


def neighbour_views(block, got, dim_of):
    views = []
    for (lower, upper), dim in zip(got, dim_of):
        size = block.shape[dim]
        below = jnp.concatenate([lower, lax.slice_in_dim(block, 0, size - 1, axis=dim)], axis=dim)
        above = jnp.concatenate([lax.slice_in_dim(block, 1, size, axis=dim), upper], axis=dim)
        views.append((below, above))
    return views


def coarse_step(upscaled, views, inside_views, pressure, accumulation, fixed):
    factors = (CCY * CCZ / CCX, CCX * CCZ / CCY, CCX * CCY / CCZ)
    numer = fixed
    denom = accumulation
    for component in range(3):
        for side in range(2):
            beside = views[component][side]
            link = factors[component] * 0.5 * (upscaled[component] + beside[component]) * inside_views[component][side]
            numer = numer + link * pressure[component][side]
            denom = denom + jnp.abs(link)
    return numer / denom


def local(log_noise, facies, facies_table, pressure_old, accumulation, source):
    depth_len, rows_len, cols_len = log_noise.shape
    size_z = lax.axis_size("gz")
    size_x = lax.axis_size("gx")
    size_y = lax.axis_size("gy")
    index_z = lax.axis_index("gz")
    index_x = lax.axis_index("gx")
    index_y = lax.axis_index("gy")
    raw = jnp.stack([log_noise, facies.astype(jnp.float32)])
    wide = -(-(cols_len + 2 * RIM) // LANES) * LANES
    raw = extended(raw, (("gx", 2), ("gz", 1), ("gy", 3)), RIM, wide)
    anchor_z = index_z * depth_len
    anchor_y = index_y * cols_len
    anchor_x = index_x * rows_len
    bounds = jnp.stack(
        [
            RIM - anchor_z,
            depth_len * size_z + RIM - anchor_z,
            RIM - anchor_x,
            rows_len * size_x + RIM - anchor_x,
            RIM - anchor_y,
            cols_len * size_y + RIM - anchor_y,
        ]
    ).astype(jnp.int32)
    upscaled = upscale_windows(raw, facies_table, bounds, cols_len)
    coarse_z, coarse_x, coarse_y = pressure_old.shape
    bundle = jnp.stack([upscaled[0], upscaled[1], upscaled[2], pressure_old, accumulation, source])
    every = lax.all_gather(bundle, "gy", axis=3, tiled=True)
    every = doubling_gather(every, "gx", 2)
    every = lax.all_gather(every, "gz", axis=1, tiled=True)
    perm_pad = jnp.pad(every[:3], ((0, 0), (1, 1), (1, 1), (1, 1)))
    old_all = every[3]
    acc_all = every[4]
    fixed_all = acc_all * old_all + every[5]
    inside_pad = jnp.pad(jnp.ones(old_all.shape, jnp.float32), 1)
    pressure = old_all
    for sweep_index in range(2):
        pressure = coarse_sweep(perm_pad, jnp.pad(pressure, 1), inside_pad, acc_all, fixed_all)
    pressure = lax.dynamic_slice(
        pressure, (index_z * coarse_z, index_x * coarse_x, index_y * coarse_y), (coarse_z, coarse_x, coarse_y)
    )
    return (pressure, upscaled)


def solution(mesh):
    placed = (
        P(("real", "gz"), "gx", "gy"),
        P(("real", "gz"), "gx", "gy"),
        P(),
        P(("real", "gz"), "gx", "gy"),
        P(("real", "gz"), "gx", "gy"),
        P(("real", "gz"), "gx", "gy"),
    )
    return jax.shard_map(
        local,
        mesh=mesh,
        in_specs=placed,
        out_specs=(P(("real", "gz"), "gx", "gy"), P(None, ("real", "gz"), "gx", "gy")),
        check_vma=False,
    )
```

```python
import functools

import jax
import jax.numpy as jnp
from jax import lax
from jax.sharding import PartitionSpec as P
from jax.experimental import pallas as pl
from jax.experimental.pallas import tpu as pltpu

NFAC = 4
CCX = 32
CCY = 32
CCZ = 8
RIM = 4
SWEEPS = 3


BOUND_MID = 1.0
BOUND_HALF = 0.9


def extended(cells, sides, width, lanes=None):
    for axis, dim in sides:
        count = lax.axis_size(axis)
        ends = count - 1
        head = lax.slice_in_dim(cells, 0, width, axis=dim)
        tail = lax.slice_in_dim(cells, cells.shape[dim] - width, cells.shape[dim], axis=dim)
        if count == 2:
            lower_side = lax.axis_index(axis) == 0
            got = lax.ppermute(jnp.where(lower_side, tail, head), axis, [(0, 1), (1, 0)])
            below = jnp.where(lower_side, 0.0, got)
            above = jnp.where(lower_side, got, 0.0)
        else:
            below = lax.ppermute(tail, axis, [(i, (i + 1) % count) for i in range(ends)])
            above = lax.ppermute(head, axis, [((i + 1) % count, i) for i in range(ends)])
        if lanes is not None and dim == cells.ndim - 1:
            extra = lanes - (cells.shape[dim] + 2 * width)
            parts = [cells, above, jnp.zeros(cells.shape[:-1] + (extra,), cells.dtype), below]
        else:
            parts = [below, cells, above]
        cells = jnp.concatenate(parts, axis=dim)
    return cells


def doubling_gather(values, axis, dim):
    count = lax.axis_size(axis)
    if count & (count - 1):
        return lax.all_gather(values, axis, axis=dim, tiled=True)
    index = lax.axis_index(axis)
    step = 1
    while step < count:
        got = lax.ppermute(values, axis, [(i, i ^ step) for i in range(count)])
        lower = (index // step) % 2 == 0
        values = jnp.where(
            lower, jnp.concatenate([values, got], axis=dim), jnp.concatenate([got, values], axis=dim)
        )
        step *= 2
    return values


def raise_flat(values, offset):
    zeros_block = jnp.zeros(values.shape[:-1] + (offset,), values.dtype)
    return jnp.concatenate([values[..., offset:], zeros_block], axis=-1)


def lower_flat(values, offset):
    zeros_block = jnp.zeros(values.shape[:-1] + (offset,), values.dtype)
    return jnp.concatenate([zeros_block, values[..., :-offset]], axis=-1)


def raise_depth(values):
    zeros_block = jnp.zeros(values.shape[:1] + (1,) + values.shape[2:], values.dtype)
    return jnp.concatenate([values[:, 1:], zeros_block], axis=1)


def lower_depth(values):
    zeros_block = jnp.zeros(values.shape[:1] + (1,) + values.shape[2:], values.dtype)
    return jnp.concatenate([zeros_block, values[:, :-1]], axis=1)


def log_fields(log_noise, facies, facies_table):
    base_log = log_noise
    extra_y = jnp.zeros_like(log_noise)
    extra_z = jnp.zeros_like(log_noise)
    for code_value in range(NFAC):
        matched = facies == code_value
        base_log = base_log + jnp.where(matched, facies_table[0, code_value], jnp.float32(0.0))
        extra_y = extra_y + jnp.where(matched, facies_table[1, code_value], jnp.float32(0.0))
        extra_z = extra_z + jnp.where(matched, facies_table[2, code_value], jnp.float32(0.0))
    return (base_log, base_log + extra_y, base_log + extra_z)


def upscale(perm_logs, inside):
    span_z = CCZ + 2 * RIM
    span_x = CCX + 2 * RIM
    span_y = CCY + 2 * RIM
    depth_pos = lax.broadcasted_iota(jnp.int32, (1, span_z, 1), 1)
    flat_pos = lax.broadcasted_iota(jnp.int32, (1, 1, span_x * span_y), 2)
    column_pos = flat_pos // span_y
    row_pos = flat_pos % span_y
    perm_x = jnp.exp(perm_logs[0])
    perm_y = jnp.exp(perm_logs[1])
    perm_z = jnp.exp(perm_logs[2])

    def links(perm, other_perm, other_inside):
        return inside * other_inside * 2.0 * perm * other_perm / (perm + other_perm)

    link_x = links(perm_x, raise_flat(perm_x, span_y), raise_flat(inside, span_y))
    link_y = links(perm_y, raise_flat(perm_y, 1), raise_flat(inside, 1)) * (
        row_pos < span_y - 1
    ).astype(jnp.float32)
    link_z = links(perm_z, raise_depth(perm_z), raise_depth(inside))
    diagonal = (
        link_x
        + lower_flat(link_x, span_y)
        + link_y
        + lower_flat(link_y, 1)
        + link_z
        + lower_depth(link_z)
    )

    def apply_operator(field):
        beside = link_x * raise_flat(field, span_y) + lower_flat(link_x * field, span_y)
        beside = beside + link_y * raise_flat(field, 1) + lower_flat(link_y * field, 1)
        beside = beside + link_z * raise_depth(field) + lower_depth(link_z * field)
        return diagonal * field - beside

    interior = (
        (depth_pos >= 1)
        & (depth_pos <= span_z - 2)
        & (column_pos >= 1)
        & (column_pos <= span_x - 2)
        & (row_pos >= 1)
        & (row_pos <= span_y - 2)
    )
    unknown = inside * interior.astype(jnp.float32)
    scaling = unknown / (diagonal + 1.0 - unknown)
    core_z = (depth_pos >= RIM) & (depth_pos < RIM + CCZ)
    core_x = (column_pos >= RIM) & (column_pos < RIM + CCX)
    core_y = (row_pos >= RIM) & (row_pos < RIM + CCY)
    face_x = (((column_pos == RIM - 1) | (column_pos == RIM + CCX - 1)) & core_z & core_y).astype(
        jnp.float32
    )
    face_y = (((row_pos == RIM - 1) | (row_pos == RIM + CCY - 1)) & core_z & core_x).astype(
        jnp.float32
    )
    face_z = (((depth_pos == RIM - 1) | (depth_pos == RIM + CCZ - 1)) & core_x & core_y).astype(
        jnp.float32
    )
    ramp_x = ((span_x - 1) / 2.0 - column_pos).astype(jnp.float32)
    ramp_y = ((span_y - 1) / 2.0 - row_pos).astype(jnp.float32)
    ramp_z = ((span_z - 1) / 2.0 - depth_pos).astype(jnp.float32)
    cheb_ratio = BOUND_MID / BOUND_HALF
    results = []
    cases = (
        (ramp_x, link_x, face_x, CCY * CCZ, 0),
        (ramp_y, link_y, face_y, CCX * CCZ, 1),
        (ramp_z, link_z, face_z, CCX * CCY, 2),
    )
    for ramp, link, face, area, direction in cases:
        ramp_full = jnp.broadcast_to(ramp, inside.shape)
        source_term = -unknown * apply_operator(ramp_full)
        update = scaling * source_term / BOUND_MID
        solution = update
        rho_old = 1.0 / cheb_ratio
        for sweep_index in range(SWEEPS - 1):
            residual = source_term - apply_operator(solution)
            rho_new = 1.0 / (2.0 * cheb_ratio - rho_old)
            update = rho_new * rho_old * update + 2.0 * rho_new / BOUND_HALF * (scaling * residual)
            solution = solution + update
            rho_old = rho_new
        pressure = ramp_full + solution
        if direction == 0:
            upper = raise_flat(pressure, span_y)
        elif direction == 1:
            upper = raise_flat(pressure, 1)
        else:
            upper = raise_depth(pressure)
        flux = link * (pressure - upper) * face
        results.append(jnp.sum(flux, axis=(1, 2)) * (0.5 / area))
    return jnp.stack(results)


LANES = 128


def window_kernel(table_ref, bounds_ref, raw_ref, o_ref, *, count_x, count_y, count):
    span_z = CCZ + 2 * RIM
    span_x = CCX + 2 * RIM
    span_y = CCY + 2 * RIM
    segments = LANES // span_y
    shape = (span_z, span_x, LANES)
    pack = pl.program_id(0)
    wide = raw_ref.shape[-1]
    depth_pos = lax.broadcasted_iota(jnp.int32, shape, 0)
    column_pos = lax.broadcasted_iota(jnp.int32, shape, 1)
    lane = lax.broadcasted_iota(jnp.int32, shape, 2)
    segment = jnp.zeros(shape, jnp.int32)
    for bound in range(1, segments + 1):
        segment = segment + (lane >= bound * span_y).astype(jnp.int32)
    row_pos = lane - span_y * segment
    noise = jnp.zeros(shape, jnp.float32)
    codes = jnp.zeros(shape, jnp.float32)
    inside = jnp.zeros(shape, jnp.float32)
    for slot in range(segments):
        window = pack * segments + slot
        valid = window < count
        window = jnp.minimum(window, count - 1)
        block_z = window // (count_x * count_y)
        block_x = (window // count_y) % count_x
        block_y = window % count_y
        shift = (slot * span_y - block_y * CCY + RIM + wide) % wide
        here = segment == slot

        def cut(field):
            slab = raw_ref[field, pl.ds(block_z * CCZ, span_z), pl.ds(block_x * CCX, span_x), :]
            return pltpu.roll(slab, shift, 2)[:, :, :LANES]

        depth_at = depth_pos + block_z * CCZ
        column_at = column_pos + block_x * CCX
        row_at = row_pos + block_y * CCY
        held = (
            (depth_at >= bounds_ref[0])
            & (depth_at < bounds_ref[1])
            & (column_at >= bounds_ref[2])
            & (column_at < bounds_ref[3])
            & (row_at >= bounds_ref[4])
            & (row_at < bounds_ref[5])
        )
        noise = jnp.where(here, cut(0), noise)
        codes = jnp.where(here, cut(1), codes)
        inside = jnp.where(here & valid & held, 1.0, inside)

    def lookup(row):
        value = jnp.zeros(shape, jnp.float32)
        for code_value in range(NFAC):
            value = jnp.where(codes == code_value, table_ref[row, code_value], value)
        return value

    log_x = noise + lookup(0)
    log_y = log_x + lookup(1)
    log_z = log_x + lookup(2)
    perm_x = jnp.exp(log_x)
    perm_y = jnp.exp(log_y)
    perm_z = jnp.exp(log_z)

    def up_x(v):
        return pltpu.roll(v, span_x - 1, 1)

    def down_x(v):
        return pltpu.roll(v, 1, 1)

    def up_y(v):
        return pltpu.roll(v, LANES - 1, 2)

    def down_y(v):
        return pltpu.roll(v, 1, 2)

    def up_z(v):
        return jnp.concatenate([v[1:], v[:1]], axis=0)

    def down_z(v):
        return jnp.concatenate([v[-1:], v[:-1]], axis=0)

    def links(perm, other_perm, other_inside, valid):
        value = inside * other_inside * 2.0 * perm * other_perm / (perm + other_perm)
        return jnp.where(valid, value, 0.0)

    link_x = links(perm_x, up_x(perm_x), up_x(inside), column_pos < span_x - 1)
    link_y = links(perm_y, up_y(perm_y), up_y(inside), row_pos < span_y - 1)
    link_z = links(perm_z, up_z(perm_z), up_z(inside), depth_pos < span_z - 1)
    diagonal = link_x + down_x(link_x) + link_y + down_y(link_y) + link_z + down_z(link_z)

    def apply_operator(field):
        beside = link_x * up_x(field) + down_x(link_x * field)
        beside = beside + link_y * up_y(field) + down_y(link_y * field)
        beside = beside + link_z * up_z(field) + down_z(link_z * field)
        return diagonal * field - beside

    interior = (
        (depth_pos >= 1)
        & (depth_pos <= span_z - 2)
        & (column_pos >= 1)
        & (column_pos <= span_x - 2)
        & (row_pos >= 1)
        & (row_pos <= span_y - 2)
    )
    unknown = jnp.where(interior, inside, 0.0)
    scaling = unknown / (diagonal + 1.0 - unknown)
    core_z = (depth_pos >= RIM) & (depth_pos < RIM + CCZ)
    core_x = (column_pos >= RIM) & (column_pos < RIM + CCX)
    core_y = (row_pos >= RIM) & (row_pos < RIM + CCY)
    face_x = ((column_pos == RIM - 1) | (column_pos == RIM + CCX - 1)) & core_z & core_y
    face_y = ((row_pos == RIM - 1) | (row_pos == RIM + CCY - 1)) & core_z & core_x
    face_z = ((depth_pos == RIM - 1) | (depth_pos == RIM + CCZ - 1)) & core_x & core_y
    ramp_x = ((span_x - 1) / 2.0 - column_pos).astype(jnp.float32)
    ramp_y = ((span_y - 1) / 2.0 - row_pos).astype(jnp.float32)
    ramp_z = ((span_z - 1) / 2.0 - depth_pos).astype(jnp.float32)
    cheb_ratio = BOUND_MID / BOUND_HALF
    cases = (
        (ramp_x, link_x, face_x, CCY * CCZ, up_x, down_x),
        (ramp_y, link_y, face_y, CCX * CCZ, up_y, down_y),
        (ramp_z, link_z, face_z, CCX * CCY, up_z, down_z),
    )
    rows = []
    for ramp, link, face, area, upper_of, lower_of in cases:
        source_term = -unknown * (link - lower_of(link))
        update = scaling * source_term / BOUND_MID
        solution = update
        rho_old = 1.0 / cheb_ratio
        for sweep_index in range(SWEEPS - 1):
            residual = source_term - apply_operator(solution)
            rho_new = 1.0 / (2.0 * cheb_ratio - rho_old)
            update = rho_new * rho_old * update + 2.0 * rho_new / BOUND_HALF * (scaling * residual)
            solution = solution + update
            rho_old = rho_new
        pressure = ramp + solution
        flux = jnp.where(face, link * (pressure - upper_of(pressure)), 0.0)
        total = jnp.sum(flux, axis=0)
        total = jnp.sum(total, axis=0, keepdims=True)
        rows.append(total * (0.5 / area))
    rows.append(jnp.zeros((8 - len(rows), LANES), jnp.float32))
    o_ref[0] = jnp.concatenate(rows, axis=0)


def upscale_windows(raw, facies_table, bounds, cols_len):
    span_y = CCY + 2 * RIM
    count_z = (raw.shape[1] - 2 * RIM) // CCZ
    count_x = (raw.shape[2] - 2 * RIM) // CCX
    count_y = cols_len // CCY
    count = count_z * count_x * count_y
    segments = LANES // span_y
    packs = -(-count // segments)
    kernel = functools.partial(window_kernel, count_x=count_x, count_y=count_y, count=count)
    sums = pl.pallas_call(
        kernel,
        grid=(packs,),
        in_specs=[
            pl.BlockSpec(memory_space=pltpu.SMEM),
            pl.BlockSpec(memory_space=pltpu.SMEM),
            pl.BlockSpec(raw.shape, lambda p: (0, 0, 0, 0)),
        ],
        out_specs=pl.BlockSpec((1, 8, LANES), lambda p: (p, 0, 0)),
        out_shape=jax.ShapeDtypeStruct((packs, 8, LANES), jnp.float32),
    )(facies_table, bounds, raw)
    sums = sums[:, :3, : segments * span_y].reshape(packs, 3, segments, span_y).sum(axis=3)
    sums = sums.transpose(1, 0, 2).reshape(3, packs * segments)[:, :count]
    return sums.reshape((3, count_z, count_x, count_y))


def coarse_sweep(perm_pad, press_pad, inside_pad, accumulation, fixed):
    centre = (slice(1, -1), slice(1, -1), slice(1, -1))
    factors = (CCY * CCZ / CCX, CCX * CCZ / CCY, CCX * CCY / CCZ)
    numer = fixed
    denom = accumulation
    for component, axis_dim in ((0, 1), (1, 2), (2, 0)):
        for offset in (-1, 1):
            window_slice = [slice(1, -1), slice(1, -1), slice(1, -1)]
            window_slice[axis_dim] = slice(1 + offset, press_pad.shape[axis_dim] - 1 + offset)
            beside = tuple(window_slice)
            link = (
                factors[component]
                * 0.5
                * (perm_pad[component][centre] + perm_pad[component][beside])
                * inside_pad[beside]
            )
            numer = numer + link * press_pad[beside]
            denom = denom + jnp.abs(link)
    return numer / denom


def span_mask(anchor, length, total, margin):
    coords = anchor - margin + jnp.arange(length + 2 * margin, dtype=jnp.int32)
    return ((coords >= 0) & (coords < total)).astype(jnp.float32)


def cut_windows(fields):
    span_z = CCZ + 2 * RIM
    span_x = CCX + 2 * RIM
    span_y = CCY + 2 * RIM
    count_z = (fields[0].shape[0] - 2 * RIM) // CCZ
    count_x = (fields[0].shape[1] - 2 * RIM) // CCX
    count_y = (fields[0].shape[2] - 2 * RIM) // CCY
    stacks = []
    for field in fields:
        pieces = []
        for block_z in range(count_z):
            for block_y in range(count_y):
                piece = field[
                    block_z * CCZ : block_z * CCZ + span_z,
                    0:span_x,
                    block_y * CCY : block_y * CCY + span_y,
                ]
                pieces.append(piece.reshape(span_z, span_x * span_y))
        stacks.append(jnp.stack(pieces))
    return (stacks, (count_z, count_x, count_y))


def faces(block, sides):
    got = []
    for axis, dim in sides:
        count = lax.axis_size(axis)
        ends = count - 1
        head = lax.slice_in_dim(block, 0, 1, axis=dim)
        tail = lax.slice_in_dim(block, block.shape[dim] - 1, block.shape[dim], axis=dim)
        lower = lax.ppermute(tail, axis, [(i, i + 1) for i in range(ends)])
        upper = lax.ppermute(head, axis, [(i + 1, i) for i in range(ends)])
        got.append((lower, upper))
    return got


def neighbour_views(block, got, dim_of):
    views = []
    for (lower, upper), dim in zip(got, dim_of):
        size = block.shape[dim]
        below = jnp.concatenate([lower, lax.slice_in_dim(block, 0, size - 1, axis=dim)], axis=dim)
        above = jnp.concatenate([lax.slice_in_dim(block, 1, size, axis=dim), upper], axis=dim)
        views.append((below, above))
    return views


def coarse_step(upscaled, views, inside_views, pressure, accumulation, fixed):
    factors = (CCY * CCZ / CCX, CCX * CCZ / CCY, CCX * CCY / CCZ)
    numer = fixed
    denom = accumulation
    for component in range(3):
        for side in range(2):
            beside = views[component][side]
            link = factors[component] * 0.5 * (upscaled[component] + beside[component]) * inside_views[component][side]
            numer = numer + link * pressure[component][side]
            denom = denom + jnp.abs(link)
    return numer / denom


def local(log_noise, facies, facies_table, pressure_old, accumulation, source):
    depth_len, rows_len, cols_len = log_noise.shape
    size_z = lax.axis_size("gz")
    size_x = lax.axis_size("gx")
    size_y = lax.axis_size("gy")
    index_z = lax.axis_index("gz")
    index_x = lax.axis_index("gx")
    index_y = lax.axis_index("gy")
    raw = jnp.stack([log_noise, facies.astype(jnp.float32)])
    wide = -(-(cols_len + 2 * RIM) // LANES) * LANES
    raw = extended(raw, (("gx", 2), ("gz", 1), ("gy", 3)), RIM, wide)
    anchor_z = index_z * depth_len
    anchor_y = index_y * cols_len
    anchor_x = index_x * rows_len
    bounds = jnp.stack(
        [
            RIM - anchor_z,
            depth_len * size_z + RIM - anchor_z,
            RIM - anchor_x,
            rows_len * size_x + RIM - anchor_x,
            RIM - anchor_y,
            cols_len * size_y + RIM - anchor_y,
        ]
    ).astype(jnp.int32)
    upscaled = upscale_windows(raw, facies_table, bounds, cols_len)
    coarse_z, coarse_x, coarse_y = pressure_old.shape
    bundle = jnp.stack([upscaled[0], upscaled[1], upscaled[2], pressure_old, accumulation, source])
    every = doubling_gather(bundle, "gy", 3)
    every = doubling_gather(every, "gx", 2)
    every = doubling_gather(every, "gz", 1)
    perm_pad = jnp.pad(every[:3], ((0, 0), (1, 1), (1, 1), (1, 1)))
    old_all = every[3]
    acc_all = every[4]
    fixed_all = acc_all * old_all + every[5]
    inside_pad = jnp.pad(jnp.ones(old_all.shape, jnp.float32), 1)
    pressure = old_all
    for sweep_index in range(2):
        pressure = coarse_sweep(perm_pad, jnp.pad(pressure, 1), inside_pad, acc_all, fixed_all)
    pressure = lax.dynamic_slice(
        pressure, (index_z * coarse_z, index_x * coarse_x, index_y * coarse_y), (coarse_z, coarse_x, coarse_y)
    )
    return (pressure, upscaled)


def solution(mesh):
    placed = (
        P(("real", "gz"), "gx", "gy"),
        P(("real", "gz"), "gx", "gy"),
        P(),
        P(("real", "gz"), "gx", "gy"),
        P(("real", "gz"), "gx", "gy"),
        P(("real", "gz"), "gx", "gy"),
    )
    return jax.shard_map(
        local,
        mesh=mesh,
        in_specs=placed,
        out_specs=(P(("real", "gz"), "gx", "gy"), P(None, ("real", "gz"), "gx", "gy")),
        check_vma=False,
    )
```

```python
import functools

import jax
import jax.numpy as jnp
from jax import lax
from jax.sharding import PartitionSpec as P
from jax.experimental import pallas as pl
from jax.experimental.pallas import tpu as pltpu

NFAC = 4
CCX = 32
CCY = 32
CCZ = 8
RIM = 4
SWEEPS = 3


BOUND_MID = 1.0
BOUND_HALF = 0.9


def extended(cells, sides, width, lanes=None):
    for axis, dim in sides:
        count = lax.axis_size(axis)
        ends = count - 1
        head = lax.slice_in_dim(cells, 0, width, axis=dim)
        tail = lax.slice_in_dim(cells, cells.shape[dim] - width, cells.shape[dim], axis=dim)
        if count == 2:
            lower_side = lax.axis_index(axis) == 0
            got = lax.ppermute(jnp.where(lower_side, tail, head), axis, [(0, 1), (1, 0)])
            below = got
            above = got
        else:
            below = lax.ppermute(tail, axis, [(i, (i + 1) % count) for i in range(ends)])
            above = lax.ppermute(head, axis, [((i + 1) % count, i) for i in range(ends)])
        if lanes is not None and dim == cells.ndim - 1:
            extra = lanes - (cells.shape[dim] + 2 * width)
            parts = [cells, above, jnp.zeros(cells.shape[:-1] + (extra,), cells.dtype), below]
        else:
            parts = [below, cells, above]
        cells = jnp.concatenate(parts, axis=dim)
    return cells


def doubling_gather(values, axis, dim):
    count = lax.axis_size(axis)
    if count & (count - 1):
        return lax.all_gather(values, axis, axis=dim, tiled=True)
    index = lax.axis_index(axis)
    step = 1
    while step < count:
        got = lax.ppermute(values, axis, [(i, i ^ step) for i in range(count)])
        lower = (index // step) % 2 == 0
        values = jnp.where(
            lower, jnp.concatenate([values, got], axis=dim), jnp.concatenate([got, values], axis=dim)
        )
        step *= 2
    return values


def raise_flat(values, offset):
    zeros_block = jnp.zeros(values.shape[:-1] + (offset,), values.dtype)
    return jnp.concatenate([values[..., offset:], zeros_block], axis=-1)


def lower_flat(values, offset):
    zeros_block = jnp.zeros(values.shape[:-1] + (offset,), values.dtype)
    return jnp.concatenate([zeros_block, values[..., :-offset]], axis=-1)


def raise_depth(values):
    zeros_block = jnp.zeros(values.shape[:1] + (1,) + values.shape[2:], values.dtype)
    return jnp.concatenate([values[:, 1:], zeros_block], axis=1)


def lower_depth(values):
    zeros_block = jnp.zeros(values.shape[:1] + (1,) + values.shape[2:], values.dtype)
    return jnp.concatenate([zeros_block, values[:, :-1]], axis=1)


def log_fields(log_noise, facies, facies_table):
    base_log = log_noise
    extra_y = jnp.zeros_like(log_noise)
    extra_z = jnp.zeros_like(log_noise)
    for code_value in range(NFAC):
        matched = facies == code_value
        base_log = base_log + jnp.where(matched, facies_table[0, code_value], jnp.float32(0.0))
        extra_y = extra_y + jnp.where(matched, facies_table[1, code_value], jnp.float32(0.0))
        extra_z = extra_z + jnp.where(matched, facies_table[2, code_value], jnp.float32(0.0))
    return (base_log, base_log + extra_y, base_log + extra_z)


def upscale(perm_logs, inside):
    span_z = CCZ + 2 * RIM
    span_x = CCX + 2 * RIM
    span_y = CCY + 2 * RIM
    depth_pos = lax.broadcasted_iota(jnp.int32, (1, span_z, 1), 1)
    flat_pos = lax.broadcasted_iota(jnp.int32, (1, 1, span_x * span_y), 2)
    column_pos = flat_pos // span_y
    row_pos = flat_pos % span_y
    perm_x = jnp.exp(perm_logs[0])
    perm_y = jnp.exp(perm_logs[1])
    perm_z = jnp.exp(perm_logs[2])

    def links(perm, other_perm, other_inside):
        return inside * other_inside * 2.0 * perm * other_perm / (perm + other_perm)

    link_x = links(perm_x, raise_flat(perm_x, span_y), raise_flat(inside, span_y))
    link_y = links(perm_y, raise_flat(perm_y, 1), raise_flat(inside, 1)) * (
        row_pos < span_y - 1
    ).astype(jnp.float32)
    link_z = links(perm_z, raise_depth(perm_z), raise_depth(inside))
    diagonal = (
        link_x
        + lower_flat(link_x, span_y)
        + link_y
        + lower_flat(link_y, 1)
        + link_z
        + lower_depth(link_z)
    )

    def apply_operator(field):
        beside = link_x * raise_flat(field, span_y) + lower_flat(link_x * field, span_y)
        beside = beside + link_y * raise_flat(field, 1) + lower_flat(link_y * field, 1)
        beside = beside + link_z * raise_depth(field) + lower_depth(link_z * field)
        return diagonal * field - beside

    interior = (
        (depth_pos >= 1)
        & (depth_pos <= span_z - 2)
        & (column_pos >= 1)
        & (column_pos <= span_x - 2)
        & (row_pos >= 1)
        & (row_pos <= span_y - 2)
    )
    unknown = inside * interior.astype(jnp.float32)
    scaling = unknown / (diagonal + 1.0 - unknown)
    core_z = (depth_pos >= RIM) & (depth_pos < RIM + CCZ)
    core_x = (column_pos >= RIM) & (column_pos < RIM + CCX)
    core_y = (row_pos >= RIM) & (row_pos < RIM + CCY)
    face_x = (((column_pos == RIM - 1) | (column_pos == RIM + CCX - 1)) & core_z & core_y).astype(
        jnp.float32
    )
    face_y = (((row_pos == RIM - 1) | (row_pos == RIM + CCY - 1)) & core_z & core_x).astype(
        jnp.float32
    )
    face_z = (((depth_pos == RIM - 1) | (depth_pos == RIM + CCZ - 1)) & core_x & core_y).astype(
        jnp.float32
    )
    ramp_x = ((span_x - 1) / 2.0 - column_pos).astype(jnp.float32)
    ramp_y = ((span_y - 1) / 2.0 - row_pos).astype(jnp.float32)
    ramp_z = ((span_z - 1) / 2.0 - depth_pos).astype(jnp.float32)
    cheb_ratio = BOUND_MID / BOUND_HALF
    results = []
    cases = (
        (ramp_x, link_x, face_x, CCY * CCZ, 0),
        (ramp_y, link_y, face_y, CCX * CCZ, 1),
        (ramp_z, link_z, face_z, CCX * CCY, 2),
    )
    for ramp, link, face, area, direction in cases:
        ramp_full = jnp.broadcast_to(ramp, inside.shape)
        source_term = -unknown * apply_operator(ramp_full)
        update = scaling * source_term / BOUND_MID
        solution = update
        rho_old = 1.0 / cheb_ratio
        for sweep_index in range(SWEEPS - 1):
            residual = source_term - apply_operator(solution)
            rho_new = 1.0 / (2.0 * cheb_ratio - rho_old)
            update = rho_new * rho_old * update + 2.0 * rho_new / BOUND_HALF * (scaling * residual)
            solution = solution + update
            rho_old = rho_new
        pressure = ramp_full + solution
        if direction == 0:
            upper = raise_flat(pressure, span_y)
        elif direction == 1:
            upper = raise_flat(pressure, 1)
        else:
            upper = raise_depth(pressure)
        flux = link * (pressure - upper) * face
        results.append(jnp.sum(flux, axis=(1, 2)) * (0.5 / area))
    return jnp.stack(results)


LANES = 128


def window_kernel(table_ref, bounds_ref, raw_ref, o_ref, *, count_x, count_y, count):
    span_z = CCZ + 2 * RIM
    span_x = CCX + 2 * RIM
    span_y = CCY + 2 * RIM
    segments = LANES // span_y
    shape = (span_z, span_x, LANES)
    pack = pl.program_id(0)
    wide = raw_ref.shape[-1]
    depth_pos = lax.broadcasted_iota(jnp.int32, shape, 0)
    column_pos = lax.broadcasted_iota(jnp.int32, shape, 1)
    lane = lax.broadcasted_iota(jnp.int32, shape, 2)
    segment = jnp.zeros(shape, jnp.int32)
    for bound in range(1, segments + 1):
        segment = segment + (lane >= bound * span_y).astype(jnp.int32)
    row_pos = lane - span_y * segment
    noise = jnp.zeros(shape, jnp.float32)
    codes = jnp.zeros(shape, jnp.float32)
    inside = jnp.zeros(shape, jnp.float32)
    for slot in range(segments):
        window = pack * segments + slot
        valid = window < count
        window = jnp.minimum(window, count - 1)
        block_z = window // (count_x * count_y)
        block_x = (window // count_y) % count_x
        block_y = window % count_y
        shift = (slot * span_y - block_y * CCY + RIM + wide) % wide
        here = segment == slot

        def cut(field):
            slab = raw_ref[field, pl.ds(block_z * CCZ, span_z), pl.ds(block_x * CCX, span_x), :]
            return pltpu.roll(slab, shift, 2)[:, :, :LANES]

        depth_at = depth_pos + block_z * CCZ
        column_at = column_pos + block_x * CCX
        row_at = row_pos + block_y * CCY
        held = (
            (depth_at >= bounds_ref[0])
            & (depth_at < bounds_ref[1])
            & (column_at >= bounds_ref[2])
            & (column_at < bounds_ref[3])
            & (row_at >= bounds_ref[4])
            & (row_at < bounds_ref[5])
        )
        noise = jnp.where(here, cut(0), noise)
        codes = jnp.where(here, cut(1), codes)
        inside = jnp.where(here & valid & held, 1.0, inside)

    def lookup(row):
        value = jnp.zeros(shape, jnp.float32)
        for code_value in range(NFAC):
            value = jnp.where(codes == code_value, table_ref[row, code_value], value)
        return value

    log_x = noise + lookup(0)
    log_y = log_x + lookup(1)
    log_z = log_x + lookup(2)
    perm_x = jnp.exp(log_x)
    perm_y = jnp.exp(log_y)
    perm_z = jnp.exp(log_z)

    def up_x(v):
        return pltpu.roll(v, span_x - 1, 1)

    def down_x(v):
        return pltpu.roll(v, 1, 1)

    def up_y(v):
        return pltpu.roll(v, LANES - 1, 2)

    def down_y(v):
        return pltpu.roll(v, 1, 2)

    def up_z(v):
        return jnp.concatenate([v[1:], v[:1]], axis=0)

    def down_z(v):
        return jnp.concatenate([v[-1:], v[:-1]], axis=0)

    def links(perm, other_perm, other_inside, valid):
        value = inside * other_inside * 2.0 * perm * other_perm / (perm + other_perm)
        return jnp.where(valid, value, 0.0)

    link_x = links(perm_x, up_x(perm_x), up_x(inside), column_pos < span_x - 1)
    link_y = links(perm_y, up_y(perm_y), up_y(inside), row_pos < span_y - 1)
    link_z = links(perm_z, up_z(perm_z), up_z(inside), depth_pos < span_z - 1)
    diagonal = link_x + down_x(link_x) + link_y + down_y(link_y) + link_z + down_z(link_z)

    def apply_operator(field):
        beside = link_x * up_x(field) + down_x(link_x * field)
        beside = beside + link_y * up_y(field) + down_y(link_y * field)
        beside = beside + link_z * up_z(field) + down_z(link_z * field)
        return diagonal * field - beside

    interior = (
        (depth_pos >= 1)
        & (depth_pos <= span_z - 2)
        & (column_pos >= 1)
        & (column_pos <= span_x - 2)
        & (row_pos >= 1)
        & (row_pos <= span_y - 2)
    )
    unknown = jnp.where(interior, inside, 0.0)
    scaling = unknown / (diagonal + 1.0 - unknown)
    core_z = (depth_pos >= RIM) & (depth_pos < RIM + CCZ)
    core_x = (column_pos >= RIM) & (column_pos < RIM + CCX)
    core_y = (row_pos >= RIM) & (row_pos < RIM + CCY)
    face_x = ((column_pos == RIM - 1) | (column_pos == RIM + CCX - 1)) & core_z & core_y
    face_y = ((row_pos == RIM - 1) | (row_pos == RIM + CCY - 1)) & core_z & core_x
    face_z = ((depth_pos == RIM - 1) | (depth_pos == RIM + CCZ - 1)) & core_x & core_y
    ramp_x = ((span_x - 1) / 2.0 - column_pos).astype(jnp.float32)
    ramp_y = ((span_y - 1) / 2.0 - row_pos).astype(jnp.float32)
    ramp_z = ((span_z - 1) / 2.0 - depth_pos).astype(jnp.float32)
    cheb_ratio = BOUND_MID / BOUND_HALF
    cases = (
        (ramp_x, link_x, face_x, CCY * CCZ, up_x, down_x),
        (ramp_y, link_y, face_y, CCX * CCZ, up_y, down_y),
        (ramp_z, link_z, face_z, CCX * CCY, up_z, down_z),
    )
    rows = []
    for ramp, link, face, area, upper_of, lower_of in cases:
        source_term = -unknown * (link - lower_of(link))
        update = scaling * source_term / BOUND_MID
        solution = update
        rho_old = 1.0 / cheb_ratio
        for sweep_index in range(SWEEPS - 1):
            residual = source_term - apply_operator(solution)
            rho_new = 1.0 / (2.0 * cheb_ratio - rho_old)
            update = rho_new * rho_old * update + 2.0 * rho_new / BOUND_HALF * (scaling * residual)
            solution = solution + update
            rho_old = rho_new
        pressure = ramp + solution
        flux = jnp.where(face, link * (pressure - upper_of(pressure)), 0.0)
        total = jnp.sum(flux, axis=0)
        total = jnp.sum(total, axis=0, keepdims=True)
        rows.append(total * (0.5 / area))
    rows.append(jnp.zeros((8 - len(rows), LANES), jnp.float32))
    o_ref[0] = jnp.concatenate(rows, axis=0)


def upscale_windows(raw, facies_table, bounds, cols_len):
    span_y = CCY + 2 * RIM
    count_z = (raw.shape[1] - 2 * RIM) // CCZ
    count_x = (raw.shape[2] - 2 * RIM) // CCX
    count_y = cols_len // CCY
    count = count_z * count_x * count_y
    segments = LANES // span_y
    packs = -(-count // segments)
    kernel = functools.partial(window_kernel, count_x=count_x, count_y=count_y, count=count)
    sums = pl.pallas_call(
        kernel,
        grid=(packs,),
        in_specs=[
            pl.BlockSpec(memory_space=pltpu.SMEM),
            pl.BlockSpec(memory_space=pltpu.SMEM),
            pl.BlockSpec(raw.shape, lambda p: (0, 0, 0, 0)),
        ],
        out_specs=pl.BlockSpec((1, 8, LANES), lambda p: (p, 0, 0)),
        out_shape=jax.ShapeDtypeStruct((packs, 8, LANES), jnp.float32),
    )(facies_table, bounds, raw)
    sums = sums[:, :3, : segments * span_y].reshape(packs, 3, segments, span_y).sum(axis=3)
    sums = sums.transpose(1, 0, 2).reshape(3, packs * segments)[:, :count]
    return sums.reshape((3, count_z, count_x, count_y))


def coarse_sweep(perm_pad, press_pad, inside_pad, accumulation, fixed):
    centre = (slice(1, -1), slice(1, -1), slice(1, -1))
    factors = (CCY * CCZ / CCX, CCX * CCZ / CCY, CCX * CCY / CCZ)
    numer = fixed
    denom = accumulation
    for component, axis_dim in ((0, 1), (1, 2), (2, 0)):
        for offset in (-1, 1):
            window_slice = [slice(1, -1), slice(1, -1), slice(1, -1)]
            window_slice[axis_dim] = slice(1 + offset, press_pad.shape[axis_dim] - 1 + offset)
            beside = tuple(window_slice)
            link = (
                factors[component]
                * 0.5
                * (perm_pad[component][centre] + perm_pad[component][beside])
                * inside_pad[beside]
            )
            numer = numer + link * press_pad[beside]
            denom = denom + jnp.abs(link)
    return numer / denom


def span_mask(anchor, length, total, margin):
    coords = anchor - margin + jnp.arange(length + 2 * margin, dtype=jnp.int32)
    return ((coords >= 0) & (coords < total)).astype(jnp.float32)


def cut_windows(fields):
    span_z = CCZ + 2 * RIM
    span_x = CCX + 2 * RIM
    span_y = CCY + 2 * RIM
    count_z = (fields[0].shape[0] - 2 * RIM) // CCZ
    count_x = (fields[0].shape[1] - 2 * RIM) // CCX
    count_y = (fields[0].shape[2] - 2 * RIM) // CCY
    stacks = []
    for field in fields:
        pieces = []
        for block_z in range(count_z):
            for block_y in range(count_y):
                piece = field[
                    block_z * CCZ : block_z * CCZ + span_z,
                    0:span_x,
                    block_y * CCY : block_y * CCY + span_y,
                ]
                pieces.append(piece.reshape(span_z, span_x * span_y))
        stacks.append(jnp.stack(pieces))
    return (stacks, (count_z, count_x, count_y))


def faces(block, sides):
    got = []
    for axis, dim in sides:
        count = lax.axis_size(axis)
        ends = count - 1
        head = lax.slice_in_dim(block, 0, 1, axis=dim)
        tail = lax.slice_in_dim(block, block.shape[dim] - 1, block.shape[dim], axis=dim)
        lower = lax.ppermute(tail, axis, [(i, i + 1) for i in range(ends)])
        upper = lax.ppermute(head, axis, [(i + 1, i) for i in range(ends)])
        got.append((lower, upper))
    return got


def neighbour_views(block, got, dim_of):
    views = []
    for (lower, upper), dim in zip(got, dim_of):
        size = block.shape[dim]
        below = jnp.concatenate([lower, lax.slice_in_dim(block, 0, size - 1, axis=dim)], axis=dim)
        above = jnp.concatenate([lax.slice_in_dim(block, 1, size, axis=dim), upper], axis=dim)
        views.append((below, above))
    return views


def coarse_step(upscaled, views, inside_views, pressure, accumulation, fixed):
    factors = (CCY * CCZ / CCX, CCX * CCZ / CCY, CCX * CCY / CCZ)
    numer = fixed
    denom = accumulation
    for component in range(3):
        for side in range(2):
            beside = views[component][side]
            link = factors[component] * 0.5 * (upscaled[component] + beside[component]) * inside_views[component][side]
            numer = numer + link * pressure[component][side]
            denom = denom + jnp.abs(link)
    return numer / denom


def local(log_noise, facies, facies_table, pressure_old, accumulation, source):
    depth_len, rows_len, cols_len = log_noise.shape
    size_z = lax.axis_size("gz")
    size_x = lax.axis_size("gx")
    size_y = lax.axis_size("gy")
    index_z = lax.axis_index("gz")
    index_x = lax.axis_index("gx")
    index_y = lax.axis_index("gy")
    raw = jnp.stack([log_noise, facies.astype(jnp.float32)])
    wide = -(-(cols_len + 2 * RIM) // LANES) * LANES
    raw = extended(raw, (("gx", 2), ("gz", 1), ("gy", 3)), RIM, wide)
    anchor_z = index_z * depth_len
    anchor_y = index_y * cols_len
    anchor_x = index_x * rows_len
    bounds = jnp.stack(
        [
            RIM - anchor_z,
            depth_len * size_z + RIM - anchor_z,
            RIM - anchor_x,
            rows_len * size_x + RIM - anchor_x,
            RIM - anchor_y,
            cols_len * size_y + RIM - anchor_y,
        ]
    ).astype(jnp.int32)
    upscaled = upscale_windows(raw, facies_table, bounds, cols_len)
    coarse_z, coarse_x, coarse_y = pressure_old.shape
    bundle = jnp.stack([upscaled[0], upscaled[1], upscaled[2], pressure_old, accumulation, source])
    every = doubling_gather(bundle, "gy", 3)
    every = doubling_gather(every, "gx", 2)
    every = doubling_gather(every, "gz", 1)
    perm_pad = jnp.pad(every[:3], ((0, 0), (1, 1), (1, 1), (1, 1)))
    old_all = every[3]
    acc_all = every[4]
    fixed_all = acc_all * old_all + every[5]
    inside_pad = jnp.pad(jnp.ones(old_all.shape, jnp.float32), 1)
    pressure = old_all
    for sweep_index in range(2):
        pressure = coarse_sweep(perm_pad, jnp.pad(pressure, 1), inside_pad, acc_all, fixed_all)
    pressure = lax.dynamic_slice(
        pressure, (index_z * coarse_z, index_x * coarse_x, index_y * coarse_y), (coarse_z, coarse_x, coarse_y)
    )
    return (pressure, upscaled)


def solution(mesh):
    placed = (
        P(("real", "gz"), "gx", "gy"),
        P(("real", "gz"), "gx", "gy"),
        P(),
        P(("real", "gz"), "gx", "gy"),
        P(("real", "gz"), "gx", "gy"),
        P(("real", "gz"), "gx", "gy"),
    )
    return jax.shard_map(
        local,
        mesh=mesh,
        in_specs=placed,
        out_specs=(P(("real", "gz"), "gx", "gy"), P(None, ("real", "gz"), "gx", "gy")),
        check_vma=False,
    )
```

```python
import functools

import jax
import jax.numpy as jnp
from jax import lax
from jax.sharding import PartitionSpec as P
from jax.experimental import pallas as pl
from jax.experimental.pallas import tpu as pltpu

NFAC = 4
CCX = 32
CCY = 32
CCZ = 8
RIM = 4
SWEEPS = 3


BOUND_MID = 1.0
BOUND_HALF = 0.9


def extended(cells, sides, width, lanes=None):
    for axis, dim in sides:
        count = lax.axis_size(axis)
        ends = count - 1
        head = lax.slice_in_dim(cells, 0, width, axis=dim)
        tail = lax.slice_in_dim(cells, cells.shape[dim] - width, cells.shape[dim], axis=dim)
        if count == 2:
            lower_side = lax.axis_index(axis) == 0
            got = lax.ppermute(jnp.where(lower_side, tail, head), axis, [(0, 1), (1, 0)])
            below = got
            above = got
        else:
            below = lax.ppermute(tail, axis, [(i, (i + 1) % count) for i in range(ends)])
            above = lax.ppermute(head, axis, [((i + 1) % count, i) for i in range(ends)])
        if lanes is not None and dim == cells.ndim - 1:
            extra = lanes - (cells.shape[dim] + 2 * width)
            parts = [cells, above, jnp.zeros(cells.shape[:-1] + (extra,), cells.dtype), below]
        else:
            parts = [below, cells, above]
        cells = jnp.concatenate(parts, axis=dim)
    return cells


def doubling_gather(values, axis, dim):
    count = lax.axis_size(axis)
    if count & (count - 1):
        return lax.all_gather(values, axis, axis=dim, tiled=True)
    index = lax.axis_index(axis)
    step = 1
    while step < count:
        got = lax.ppermute(values, axis, [(i, i ^ step) for i in range(count)])
        lower = (index // step) % 2 == 0
        values = jnp.where(
            lower, jnp.concatenate([values, got], axis=dim), jnp.concatenate([got, values], axis=dim)
        )
        step *= 2
    return values


def raise_flat(values, offset):
    zeros_block = jnp.zeros(values.shape[:-1] + (offset,), values.dtype)
    return jnp.concatenate([values[..., offset:], zeros_block], axis=-1)


def lower_flat(values, offset):
    zeros_block = jnp.zeros(values.shape[:-1] + (offset,), values.dtype)
    return jnp.concatenate([zeros_block, values[..., :-offset]], axis=-1)


def raise_depth(values):
    zeros_block = jnp.zeros(values.shape[:1] + (1,) + values.shape[2:], values.dtype)
    return jnp.concatenate([values[:, 1:], zeros_block], axis=1)


def lower_depth(values):
    zeros_block = jnp.zeros(values.shape[:1] + (1,) + values.shape[2:], values.dtype)
    return jnp.concatenate([zeros_block, values[:, :-1]], axis=1)


def log_fields(log_noise, facies, facies_table):
    base_log = log_noise
    extra_y = jnp.zeros_like(log_noise)
    extra_z = jnp.zeros_like(log_noise)
    for code_value in range(NFAC):
        matched = facies == code_value
        base_log = base_log + jnp.where(matched, facies_table[0, code_value], jnp.float32(0.0))
        extra_y = extra_y + jnp.where(matched, facies_table[1, code_value], jnp.float32(0.0))
        extra_z = extra_z + jnp.where(matched, facies_table[2, code_value], jnp.float32(0.0))
    return (base_log, base_log + extra_y, base_log + extra_z)


def upscale(perm_logs, inside):
    span_z = CCZ + 2 * RIM
    span_x = CCX + 2 * RIM
    span_y = CCY + 2 * RIM
    depth_pos = lax.broadcasted_iota(jnp.int32, (1, span_z, 1), 1)
    flat_pos = lax.broadcasted_iota(jnp.int32, (1, 1, span_x * span_y), 2)
    column_pos = flat_pos // span_y
    row_pos = flat_pos % span_y
    perm_x = jnp.exp(perm_logs[0])
    perm_y = jnp.exp(perm_logs[1])
    perm_z = jnp.exp(perm_logs[2])

    def links(perm, other_perm, other_inside):
        return inside * other_inside * 2.0 * perm * other_perm / (perm + other_perm)

    link_x = links(perm_x, raise_flat(perm_x, span_y), raise_flat(inside, span_y))
    link_y = links(perm_y, raise_flat(perm_y, 1), raise_flat(inside, 1)) * (
        row_pos < span_y - 1
    ).astype(jnp.float32)
    link_z = links(perm_z, raise_depth(perm_z), raise_depth(inside))
    diagonal = (
        link_x
        + lower_flat(link_x, span_y)
        + link_y
        + lower_flat(link_y, 1)
        + link_z
        + lower_depth(link_z)
    )

    def apply_operator(field):
        beside = link_x * raise_flat(field, span_y) + lower_flat(link_x * field, span_y)
        beside = beside + link_y * raise_flat(field, 1) + lower_flat(link_y * field, 1)
        beside = beside + link_z * raise_depth(field) + lower_depth(link_z * field)
        return diagonal * field - beside

    interior = (
        (depth_pos >= 1)
        & (depth_pos <= span_z - 2)
        & (column_pos >= 1)
        & (column_pos <= span_x - 2)
        & (row_pos >= 1)
        & (row_pos <= span_y - 2)
    )
    unknown = inside * interior.astype(jnp.float32)
    scaling = unknown / (diagonal + 1.0 - unknown)
    core_z = (depth_pos >= RIM) & (depth_pos < RIM + CCZ)
    core_x = (column_pos >= RIM) & (column_pos < RIM + CCX)
    core_y = (row_pos >= RIM) & (row_pos < RIM + CCY)
    face_x = (((column_pos == RIM - 1) | (column_pos == RIM + CCX - 1)) & core_z & core_y).astype(
        jnp.float32
    )
    face_y = (((row_pos == RIM - 1) | (row_pos == RIM + CCY - 1)) & core_z & core_x).astype(
        jnp.float32
    )
    face_z = (((depth_pos == RIM - 1) | (depth_pos == RIM + CCZ - 1)) & core_x & core_y).astype(
        jnp.float32
    )
    ramp_x = ((span_x - 1) / 2.0 - column_pos).astype(jnp.float32)
    ramp_y = ((span_y - 1) / 2.0 - row_pos).astype(jnp.float32)
    ramp_z = ((span_z - 1) / 2.0 - depth_pos).astype(jnp.float32)
    cheb_ratio = BOUND_MID / BOUND_HALF
    results = []
    cases = (
        (ramp_x, link_x, face_x, CCY * CCZ, 0),
        (ramp_y, link_y, face_y, CCX * CCZ, 1),
        (ramp_z, link_z, face_z, CCX * CCY, 2),
    )
    for ramp, link, face, area, direction in cases:
        ramp_full = jnp.broadcast_to(ramp, inside.shape)
        source_term = -unknown * apply_operator(ramp_full)
        update = scaling * source_term / BOUND_MID
        solution = update
        rho_old = 1.0 / cheb_ratio
        for sweep_index in range(SWEEPS - 1):
            residual = source_term - apply_operator(solution)
            rho_new = 1.0 / (2.0 * cheb_ratio - rho_old)
            update = rho_new * rho_old * update + 2.0 * rho_new / BOUND_HALF * (scaling * residual)
            solution = solution + update
            rho_old = rho_new
        pressure = ramp_full + solution
        if direction == 0:
            upper = raise_flat(pressure, span_y)
        elif direction == 1:
            upper = raise_flat(pressure, 1)
        else:
            upper = raise_depth(pressure)
        flux = link * (pressure - upper) * face
        results.append(jnp.sum(flux, axis=(1, 2)) * (0.5 / area))
    return jnp.stack(results)


LANES = 128


def window_kernel(table_ref, bounds_ref, raw_ref, o_ref, *, count_x, count_y, count):
    span_z = CCZ + 2 * RIM
    span_x = CCX + 2 * RIM
    span_y = CCY + 2 * RIM
    segments = LANES // span_y
    shape = (span_z, span_x, LANES)
    pack = pl.program_id(0)
    wide = raw_ref.shape[-1]
    depth_pos = lax.broadcasted_iota(jnp.int32, shape, 0)
    column_pos = lax.broadcasted_iota(jnp.int32, shape, 1)
    lane = lax.broadcasted_iota(jnp.int32, shape, 2)
    segment = jnp.zeros(shape, jnp.int32)
    for bound in range(1, segments + 1):
        segment = segment + (lane >= bound * span_y).astype(jnp.int32)
    row_pos = lane - span_y * segment
    noise = jnp.zeros(shape, jnp.float32)
    codes = jnp.zeros(shape, jnp.float32)
    inside = jnp.zeros(shape, jnp.float32)
    for slot in range(segments):
        window = pack * segments + slot
        valid = window < count
        window = jnp.minimum(window, count - 1)
        block_z = window // (count_x * count_y)
        block_x = (window // count_y) % count_x
        block_y = window % count_y
        shift = (slot * span_y - block_y * CCY + RIM + wide) % wide
        here = segment == slot

        def cut(field):
            slab = raw_ref[field, pl.ds(block_z * CCZ, span_z), pl.ds(block_x * CCX, span_x), :]
            return pltpu.roll(slab, shift, 2)[:, :, :LANES]

        depth_at = depth_pos + block_z * CCZ
        column_at = column_pos + block_x * CCX
        row_at = row_pos + block_y * CCY
        held = (
            (depth_at >= bounds_ref[0])
            & (depth_at < bounds_ref[1])
            & (column_at >= bounds_ref[2])
            & (column_at < bounds_ref[3])
            & (row_at >= bounds_ref[4])
            & (row_at < bounds_ref[5])
        )
        noise = jnp.where(here, cut(0), noise)
        codes = jnp.where(here, cut(1), codes)
        inside = jnp.where(here & valid & held, 1.0, inside)

    def lookup(row):
        value = jnp.zeros(shape, jnp.float32)
        for code_value in range(NFAC):
            value = jnp.where(codes == code_value, table_ref[row, code_value], value)
        return value

    log_x = noise + lookup(0)
    log_y = log_x + lookup(1)
    log_z = log_x + lookup(2)
    perm_x = jnp.exp(log_x)
    perm_y = jnp.exp(log_y)
    perm_z = jnp.exp(log_z)

    def up_x(v):
        return pltpu.roll(v, span_x - 1, 1)

    def down_x(v):
        return pltpu.roll(v, 1, 1)

    def up_y(v):
        return pltpu.roll(v, LANES - 1, 2)

    def down_y(v):
        return pltpu.roll(v, 1, 2)

    def up_z(v):
        return jnp.concatenate([v[1:], v[:1]], axis=0)

    def down_z(v):
        return jnp.concatenate([v[-1:], v[:-1]], axis=0)

    def links(perm, other_perm, other_inside, valid):
        value = inside * other_inside * 2.0 * perm * other_perm / (perm + other_perm)
        return jnp.where(valid, value, 0.0)

    link_x = links(perm_x, up_x(perm_x), up_x(inside), column_pos < span_x - 1)
    link_y = links(perm_y, up_y(perm_y), up_y(inside), row_pos < span_y - 1)
    link_z = links(perm_z, up_z(perm_z), up_z(inside), depth_pos < span_z - 1)
    diagonal = link_x + down_x(link_x) + link_y + down_y(link_y) + link_z + down_z(link_z)

    def apply_operator(field):
        beside = link_x * up_x(field) + down_x(link_x * field)
        beside = beside + link_y * up_y(field) + down_y(link_y * field)
        beside = beside + link_z * up_z(field) + down_z(link_z * field)
        return diagonal * field - beside

    interior = (
        (depth_pos >= 1)
        & (depth_pos <= span_z - 2)
        & (column_pos >= 1)
        & (column_pos <= span_x - 2)
        & (row_pos >= 1)
        & (row_pos <= span_y - 2)
    )
    unknown = jnp.where(interior, inside, 0.0)
    scaling = unknown / (diagonal + 1.0 - unknown)
    core_z = (depth_pos >= RIM) & (depth_pos < RIM + CCZ)
    core_x = (column_pos >= RIM) & (column_pos < RIM + CCX)
    core_y = (row_pos >= RIM) & (row_pos < RIM + CCY)
    face_x = ((column_pos == RIM - 1) | (column_pos == RIM + CCX - 1)) & core_z & core_y
    face_y = ((row_pos == RIM - 1) | (row_pos == RIM + CCY - 1)) & core_z & core_x
    face_z = ((depth_pos == RIM - 1) | (depth_pos == RIM + CCZ - 1)) & core_x & core_y
    ramp_x = ((span_x - 1) / 2.0 - column_pos).astype(jnp.float32)
    ramp_y = ((span_y - 1) / 2.0 - row_pos).astype(jnp.float32)
    ramp_z = ((span_z - 1) / 2.0 - depth_pos).astype(jnp.float32)
    cheb_ratio = BOUND_MID / BOUND_HALF
    cases = (
        (ramp_x, link_x, face_x, CCY * CCZ, up_x, down_x),
        (ramp_y, link_y, face_y, CCX * CCZ, up_y, down_y),
        (ramp_z, link_z, face_z, CCX * CCY, up_z, down_z),
    )
    rows = []
    for ramp, link, face, area, upper_of, lower_of in cases:
        source_term = -unknown * (link - lower_of(link))
        update = scaling * source_term / BOUND_MID
        solution = update
        rho_old = 1.0 / cheb_ratio
        for sweep_index in range(SWEEPS - 1):
            residual = source_term - apply_operator(solution)
            rho_new = 1.0 / (2.0 * cheb_ratio - rho_old)
            update = rho_new * rho_old * update + 2.0 * rho_new / BOUND_HALF * (scaling * residual)
            solution = solution + update
            rho_old = rho_new
        pressure = ramp + solution
        flux = jnp.where(face, link * (pressure - upper_of(pressure)), 0.0)
        total = jnp.sum(flux, axis=0)
        total = jnp.sum(total, axis=0, keepdims=True)
        rows.append(total * (0.5 / area))
    rows.append(jnp.zeros((8 - len(rows), LANES), jnp.float32))
    o_ref[0] = jnp.concatenate(rows, axis=0)


def upscale_windows(raw, facies_table, bounds, cols_len):
    span_y = CCY + 2 * RIM
    count_z = (raw.shape[1] - 2 * RIM) // CCZ
    count_x = (raw.shape[2] - 2 * RIM) // CCX
    count_y = cols_len // CCY
    count = count_z * count_x * count_y
    segments = LANES // span_y
    packs = -(-count // segments)
    kernel = functools.partial(window_kernel, count_x=count_x, count_y=count_y, count=count)
    sums = pl.pallas_call(
        kernel,
        grid=(packs,),
        in_specs=[
            pl.BlockSpec(memory_space=pltpu.SMEM),
            pl.BlockSpec(memory_space=pltpu.SMEM),
            pl.BlockSpec(raw.shape, lambda p: (0, 0, 0, 0)),
        ],
        out_specs=pl.BlockSpec((1, 8, LANES), lambda p: (p, 0, 0)),
        out_shape=jax.ShapeDtypeStruct((packs, 8, LANES), jnp.float32),
    )(facies_table, bounds, raw)
    sums = sums[:, :3, : segments * span_y].reshape(packs, 3, segments, span_y).sum(axis=3)
    sums = sums.transpose(1, 0, 2).reshape(3, packs * segments)[:, :count]
    return sums.reshape((3, count_z, count_x, count_y))


def coarse_sweep(perm_pad, press_pad, inside_pad, accumulation, fixed):
    centre = (slice(1, -1), slice(1, -1), slice(1, -1))
    factors = (CCY * CCZ / CCX, CCX * CCZ / CCY, CCX * CCY / CCZ)
    numer = fixed
    denom = accumulation
    for component, axis_dim in ((0, 1), (1, 2), (2, 0)):
        for offset in (-1, 1):
            window_slice = [slice(1, -1), slice(1, -1), slice(1, -1)]
            window_slice[axis_dim] = slice(1 + offset, press_pad.shape[axis_dim] - 1 + offset)
            beside = tuple(window_slice)
            link = (
                factors[component]
                * 0.5
                * (perm_pad[component][centre] + perm_pad[component][beside])
                * inside_pad[beside]
            )
            numer = numer + link * press_pad[beside]
            denom = denom + jnp.abs(link)
    return numer / denom


def span_mask(anchor, length, total, margin):
    coords = anchor - margin + jnp.arange(length + 2 * margin, dtype=jnp.int32)
    return ((coords >= 0) & (coords < total)).astype(jnp.float32)


def cut_windows(fields):
    span_z = CCZ + 2 * RIM
    span_x = CCX + 2 * RIM
    span_y = CCY + 2 * RIM
    count_z = (fields[0].shape[0] - 2 * RIM) // CCZ
    count_x = (fields[0].shape[1] - 2 * RIM) // CCX
    count_y = (fields[0].shape[2] - 2 * RIM) // CCY
    stacks = []
    for field in fields:
        pieces = []
        for block_z in range(count_z):
            for block_y in range(count_y):
                piece = field[
                    block_z * CCZ : block_z * CCZ + span_z,
                    0:span_x,
                    block_y * CCY : block_y * CCY + span_y,
                ]
                pieces.append(piece.reshape(span_z, span_x * span_y))
        stacks.append(jnp.stack(pieces))
    return (stacks, (count_z, count_x, count_y))


def faces(block, sides):
    got = []
    for axis, dim in sides:
        count = lax.axis_size(axis)
        ends = count - 1
        head = lax.slice_in_dim(block, 0, 1, axis=dim)
        tail = lax.slice_in_dim(block, block.shape[dim] - 1, block.shape[dim], axis=dim)
        lower = lax.ppermute(tail, axis, [(i, i + 1) for i in range(ends)])
        upper = lax.ppermute(head, axis, [(i + 1, i) for i in range(ends)])
        got.append((lower, upper))
    return got


def neighbour_views(block, got, dim_of):
    views = []
    for (lower, upper), dim in zip(got, dim_of):
        size = block.shape[dim]
        below = jnp.concatenate([lower, lax.slice_in_dim(block, 0, size - 1, axis=dim)], axis=dim)
        above = jnp.concatenate([lax.slice_in_dim(block, 1, size, axis=dim), upper], axis=dim)
        views.append((below, above))
    return views


def coarse_step(upscaled, views, inside_views, pressure, accumulation, fixed):
    factors = (CCY * CCZ / CCX, CCX * CCZ / CCY, CCX * CCY / CCZ)
    numer = fixed
    denom = accumulation
    for component in range(3):
        for side in range(2):
            beside = views[component][side]
            link = factors[component] * 0.5 * (upscaled[component] + beside[component]) * inside_views[component][side]
            numer = numer + link * pressure[component][side]
            denom = denom + jnp.abs(link)
    return numer / denom


def local(log_noise, facies, facies_table, pressure_old, accumulation, source):
    depth_len, rows_len, cols_len = log_noise.shape
    size_z = lax.axis_size("gz")
    size_x = lax.axis_size("gx")
    size_y = lax.axis_size("gy")
    index_z = lax.axis_index("gz")
    index_x = lax.axis_index("gx")
    index_y = lax.axis_index("gy")
    raw = jnp.stack([log_noise, facies.astype(jnp.float32)])
    wide = -(-(cols_len + 2 * RIM) // LANES) * LANES
    raw = extended(raw, (("gz", 1), ("gx", 2), ("gy", 3)), RIM, wide)
    anchor_z = index_z * depth_len
    anchor_y = index_y * cols_len
    anchor_x = index_x * rows_len
    bounds = jnp.stack(
        [
            RIM - anchor_z,
            depth_len * size_z + RIM - anchor_z,
            RIM - anchor_x,
            rows_len * size_x + RIM - anchor_x,
            RIM - anchor_y,
            cols_len * size_y + RIM - anchor_y,
        ]
    ).astype(jnp.int32)
    upscaled = upscale_windows(raw, facies_table, bounds, cols_len)
    coarse_z, coarse_x, coarse_y = pressure_old.shape
    bundle = jnp.stack([upscaled[0], upscaled[1], upscaled[2], pressure_old, accumulation, source])
    every = doubling_gather(bundle, "gy", 3)
    every = doubling_gather(every, "gx", 2)
    every = doubling_gather(every, "gz", 1)
    perm_pad = jnp.pad(every[:3], ((0, 0), (1, 1), (1, 1), (1, 1)))
    old_all = every[3]
    acc_all = every[4]
    fixed_all = acc_all * old_all + every[5]
    inside_pad = jnp.pad(jnp.ones(old_all.shape, jnp.float32), 1)
    pressure = old_all
    for sweep_index in range(2):
        pressure = coarse_sweep(perm_pad, jnp.pad(pressure, 1), inside_pad, acc_all, fixed_all)
    pressure = lax.dynamic_slice(
        pressure, (index_z * coarse_z, index_x * coarse_x, index_y * coarse_y), (coarse_z, coarse_x, coarse_y)
    )
    return (pressure, upscaled)


def solution(mesh):
    placed = (
        P(("real", "gz"), "gx", "gy"),
        P(("real", "gz"), "gx", "gy"),
        P(),
        P(("real", "gz"), "gx", "gy"),
        P(("real", "gz"), "gx", "gy"),
        P(("real", "gz"), "gx", "gy"),
    )
    return jax.shard_map(
        local,
        mesh=mesh,
        in_specs=placed,
        out_specs=(P(("real", "gz"), "gx", "gy"), P(None, ("real", "gz"), "gx", "gy")),
        check_vma=False,
    )
```

```python
import functools

import jax
import jax.numpy as jnp
from jax import lax
from jax.sharding import PartitionSpec as P
from jax.experimental import pallas as pl
from jax.experimental.pallas import tpu as pltpu

NFAC = 4
CCX = 32
CCY = 32
CCZ = 8
RIM = 4
SWEEPS = 3


BOUND_MID = 1.0
BOUND_HALF = 0.9


def extended(cells, sides, width, lanes=None):
    for axis, dim in sides:
        count = lax.axis_size(axis)
        ends = count - 1
        head = lax.slice_in_dim(cells, 0, width, axis=dim)
        tail = lax.slice_in_dim(cells, cells.shape[dim] - width, cells.shape[dim], axis=dim)
        if count == 2:
            lower_side = lax.axis_index(axis) == 0
            got = lax.ppermute(jnp.where(lower_side, tail, head), axis, [(0, 1), (1, 0)])
            below = got
            above = got
        elif count % 2 == 0:
            even = lax.axis_index(axis) % 2 == 0
            first = [(i, i ^ 1) for i in range(count)]
            second = [(i, i + 1 if i % 2 else i - 1) for i in range(1, count - 1)]
            got_first = lax.ppermute(jnp.where(even, tail, head), axis, first)
            got_second = lax.ppermute(jnp.where(even, head, tail), axis, second)
            below = jnp.where(even, got_second, got_first)
            above = jnp.where(even, got_first, got_second)
        else:
            below = lax.ppermute(tail, axis, [(i, (i + 1) % count) for i in range(ends)])
            above = lax.ppermute(head, axis, [((i + 1) % count, i) for i in range(ends)])
        if lanes is not None and dim == cells.ndim - 1:
            extra = lanes - (cells.shape[dim] + 2 * width)
            parts = [cells, above, jnp.zeros(cells.shape[:-1] + (extra,), cells.dtype), below]
        else:
            parts = [below, cells, above]
        cells = jnp.concatenate(parts, axis=dim)
    return cells


def doubling_gather(values, axis, dim):
    count = lax.axis_size(axis)
    if count & (count - 1):
        return lax.all_gather(values, axis, axis=dim, tiled=True)
    index = lax.axis_index(axis)
    step = 1
    while step < count:
        got = lax.ppermute(values, axis, [(i, i ^ step) for i in range(count)])
        lower = (index // step) % 2 == 0
        values = jnp.where(
            lower, jnp.concatenate([values, got], axis=dim), jnp.concatenate([got, values], axis=dim)
        )
        step *= 2
    return values


def raise_flat(values, offset):
    zeros_block = jnp.zeros(values.shape[:-1] + (offset,), values.dtype)
    return jnp.concatenate([values[..., offset:], zeros_block], axis=-1)


def lower_flat(values, offset):
    zeros_block = jnp.zeros(values.shape[:-1] + (offset,), values.dtype)
    return jnp.concatenate([zeros_block, values[..., :-offset]], axis=-1)


def raise_depth(values):
    zeros_block = jnp.zeros(values.shape[:1] + (1,) + values.shape[2:], values.dtype)
    return jnp.concatenate([values[:, 1:], zeros_block], axis=1)


def lower_depth(values):
    zeros_block = jnp.zeros(values.shape[:1] + (1,) + values.shape[2:], values.dtype)
    return jnp.concatenate([zeros_block, values[:, :-1]], axis=1)


def log_fields(log_noise, facies, facies_table):
    base_log = log_noise
    extra_y = jnp.zeros_like(log_noise)
    extra_z = jnp.zeros_like(log_noise)
    for code_value in range(NFAC):
        matched = facies == code_value
        base_log = base_log + jnp.where(matched, facies_table[0, code_value], jnp.float32(0.0))
        extra_y = extra_y + jnp.where(matched, facies_table[1, code_value], jnp.float32(0.0))
        extra_z = extra_z + jnp.where(matched, facies_table[2, code_value], jnp.float32(0.0))
    return (base_log, base_log + extra_y, base_log + extra_z)


def upscale(perm_logs, inside):
    span_z = CCZ + 2 * RIM
    span_x = CCX + 2 * RIM
    span_y = CCY + 2 * RIM
    depth_pos = lax.broadcasted_iota(jnp.int32, (1, span_z, 1), 1)
    flat_pos = lax.broadcasted_iota(jnp.int32, (1, 1, span_x * span_y), 2)
    column_pos = flat_pos // span_y
    row_pos = flat_pos % span_y
    perm_x = jnp.exp(perm_logs[0])
    perm_y = jnp.exp(perm_logs[1])
    perm_z = jnp.exp(perm_logs[2])

    def links(perm, other_perm, other_inside):
        return inside * other_inside * 2.0 * perm * other_perm / (perm + other_perm)

    link_x = links(perm_x, raise_flat(perm_x, span_y), raise_flat(inside, span_y))
    link_y = links(perm_y, raise_flat(perm_y, 1), raise_flat(inside, 1)) * (
        row_pos < span_y - 1
    ).astype(jnp.float32)
    link_z = links(perm_z, raise_depth(perm_z), raise_depth(inside))
    diagonal = (
        link_x
        + lower_flat(link_x, span_y)
        + link_y
        + lower_flat(link_y, 1)
        + link_z
        + lower_depth(link_z)
    )

    def apply_operator(field):
        beside = link_x * raise_flat(field, span_y) + lower_flat(link_x * field, span_y)
        beside = beside + link_y * raise_flat(field, 1) + lower_flat(link_y * field, 1)
        beside = beside + link_z * raise_depth(field) + lower_depth(link_z * field)
        return diagonal * field - beside

    interior = (
        (depth_pos >= 1)
        & (depth_pos <= span_z - 2)
        & (column_pos >= 1)
        & (column_pos <= span_x - 2)
        & (row_pos >= 1)
        & (row_pos <= span_y - 2)
    )
    unknown = inside * interior.astype(jnp.float32)
    scaling = unknown / (diagonal + 1.0 - unknown)
    core_z = (depth_pos >= RIM) & (depth_pos < RIM + CCZ)
    core_x = (column_pos >= RIM) & (column_pos < RIM + CCX)
    core_y = (row_pos >= RIM) & (row_pos < RIM + CCY)
    face_x = (((column_pos == RIM - 1) | (column_pos == RIM + CCX - 1)) & core_z & core_y).astype(
        jnp.float32
    )
    face_y = (((row_pos == RIM - 1) | (row_pos == RIM + CCY - 1)) & core_z & core_x).astype(
        jnp.float32
    )
    face_z = (((depth_pos == RIM - 1) | (depth_pos == RIM + CCZ - 1)) & core_x & core_y).astype(
        jnp.float32
    )
    ramp_x = ((span_x - 1) / 2.0 - column_pos).astype(jnp.float32)
    ramp_y = ((span_y - 1) / 2.0 - row_pos).astype(jnp.float32)
    ramp_z = ((span_z - 1) / 2.0 - depth_pos).astype(jnp.float32)
    cheb_ratio = BOUND_MID / BOUND_HALF
    results = []
    cases = (
        (ramp_x, link_x, face_x, CCY * CCZ, 0),
        (ramp_y, link_y, face_y, CCX * CCZ, 1),
        (ramp_z, link_z, face_z, CCX * CCY, 2),
    )
    for ramp, link, face, area, direction in cases:
        ramp_full = jnp.broadcast_to(ramp, inside.shape)
        source_term = -unknown * apply_operator(ramp_full)
        update = scaling * source_term / BOUND_MID
        solution = update
        rho_old = 1.0 / cheb_ratio
        for sweep_index in range(SWEEPS - 1):
            residual = source_term - apply_operator(solution)
            rho_new = 1.0 / (2.0 * cheb_ratio - rho_old)
            update = rho_new * rho_old * update + 2.0 * rho_new / BOUND_HALF * (scaling * residual)
            solution = solution + update
            rho_old = rho_new
        pressure = ramp_full + solution
        if direction == 0:
            upper = raise_flat(pressure, span_y)
        elif direction == 1:
            upper = raise_flat(pressure, 1)
        else:
            upper = raise_depth(pressure)
        flux = link * (pressure - upper) * face
        results.append(jnp.sum(flux, axis=(1, 2)) * (0.5 / area))
    return jnp.stack(results)


LANES = 128


def window_kernel(table_ref, bounds_ref, raw_ref, o_ref, *, count_x, count_y, count):
    span_z = CCZ + 2 * RIM
    span_x = CCX + 2 * RIM
    span_y = CCY + 2 * RIM
    segments = LANES // span_y
    shape = (span_z, span_x, LANES)
    pack = pl.program_id(0)
    wide = raw_ref.shape[-1]
    depth_pos = lax.broadcasted_iota(jnp.int32, shape, 0)
    column_pos = lax.broadcasted_iota(jnp.int32, shape, 1)
    lane = lax.broadcasted_iota(jnp.int32, shape, 2)
    segment = jnp.zeros(shape, jnp.int32)
    for bound in range(1, segments + 1):
        segment = segment + (lane >= bound * span_y).astype(jnp.int32)
    row_pos = lane - span_y * segment
    noise = jnp.zeros(shape, jnp.float32)
    codes = jnp.zeros(shape, jnp.float32)
    inside = jnp.zeros(shape, jnp.float32)
    for slot in range(segments):
        window = pack * segments + slot
        valid = window < count
        window = jnp.minimum(window, count - 1)
        block_z = window // (count_x * count_y)
        block_x = (window // count_y) % count_x
        block_y = window % count_y
        shift = (slot * span_y - block_y * CCY + RIM + wide) % wide
        here = segment == slot

        def cut(field):
            slab = raw_ref[field, pl.ds(block_z * CCZ, span_z), pl.ds(block_x * CCX, span_x), :]
            return pltpu.roll(slab, shift, 2)[:, :, :LANES]

        depth_at = depth_pos + block_z * CCZ
        column_at = column_pos + block_x * CCX
        row_at = row_pos + block_y * CCY
        held = (
            (depth_at >= bounds_ref[0])
            & (depth_at < bounds_ref[1])
            & (column_at >= bounds_ref[2])
            & (column_at < bounds_ref[3])
            & (row_at >= bounds_ref[4])
            & (row_at < bounds_ref[5])
        )
        noise = jnp.where(here, cut(0), noise)
        codes = jnp.where(here, cut(1), codes)
        inside = jnp.where(here & valid & held, 1.0, inside)

    def lookup(row):
        value = jnp.zeros(shape, jnp.float32)
        for code_value in range(NFAC):
            value = jnp.where(codes == code_value, table_ref[row, code_value], value)
        return value

    log_x = noise + lookup(0)
    log_y = log_x + lookup(1)
    log_z = log_x + lookup(2)
    perm_x = jnp.exp(log_x)
    perm_y = jnp.exp(log_y)
    perm_z = jnp.exp(log_z)

    def up_x(v):
        return pltpu.roll(v, span_x - 1, 1)

    def down_x(v):
        return pltpu.roll(v, 1, 1)

    def up_y(v):
        return pltpu.roll(v, LANES - 1, 2)

    def down_y(v):
        return pltpu.roll(v, 1, 2)

    def up_z(v):
        return jnp.concatenate([v[1:], v[:1]], axis=0)

    def down_z(v):
        return jnp.concatenate([v[-1:], v[:-1]], axis=0)

    def links(perm, other_perm, other_inside, valid):
        value = inside * other_inside * 2.0 * perm * other_perm / (perm + other_perm)
        return jnp.where(valid, value, 0.0)

    link_x = links(perm_x, up_x(perm_x), up_x(inside), column_pos < span_x - 1)
    link_y = links(perm_y, up_y(perm_y), up_y(inside), row_pos < span_y - 1)
    link_z = links(perm_z, up_z(perm_z), up_z(inside), depth_pos < span_z - 1)
    diagonal = link_x + down_x(link_x) + link_y + down_y(link_y) + link_z + down_z(link_z)

    def apply_operator(field):
        beside = link_x * up_x(field) + down_x(link_x * field)
        beside = beside + link_y * up_y(field) + down_y(link_y * field)
        beside = beside + link_z * up_z(field) + down_z(link_z * field)
        return diagonal * field - beside

    interior = (
        (depth_pos >= 1)
        & (depth_pos <= span_z - 2)
        & (column_pos >= 1)
        & (column_pos <= span_x - 2)
        & (row_pos >= 1)
        & (row_pos <= span_y - 2)
    )
    unknown = jnp.where(interior, inside, 0.0)
    scaling = unknown / (diagonal + 1.0 - unknown)
    core_z = (depth_pos >= RIM) & (depth_pos < RIM + CCZ)
    core_x = (column_pos >= RIM) & (column_pos < RIM + CCX)
    core_y = (row_pos >= RIM) & (row_pos < RIM + CCY)
    face_x = ((column_pos == RIM - 1) | (column_pos == RIM + CCX - 1)) & core_z & core_y
    face_y = ((row_pos == RIM - 1) | (row_pos == RIM + CCY - 1)) & core_z & core_x
    face_z = ((depth_pos == RIM - 1) | (depth_pos == RIM + CCZ - 1)) & core_x & core_y
    ramp_x = ((span_x - 1) / 2.0 - column_pos).astype(jnp.float32)
    ramp_y = ((span_y - 1) / 2.0 - row_pos).astype(jnp.float32)
    ramp_z = ((span_z - 1) / 2.0 - depth_pos).astype(jnp.float32)
    cheb_ratio = BOUND_MID / BOUND_HALF
    cases = (
        (ramp_x, link_x, face_x, CCY * CCZ, up_x, down_x),
        (ramp_y, link_y, face_y, CCX * CCZ, up_y, down_y),
        (ramp_z, link_z, face_z, CCX * CCY, up_z, down_z),
    )
    rows = []
    for ramp, link, face, area, upper_of, lower_of in cases:
        source_term = -unknown * (link - lower_of(link))
        update = scaling * source_term / BOUND_MID
        solution = update
        rho_old = 1.0 / cheb_ratio
        for sweep_index in range(SWEEPS - 1):
            residual = source_term - apply_operator(solution)
            rho_new = 1.0 / (2.0 * cheb_ratio - rho_old)
            update = rho_new * rho_old * update + 2.0 * rho_new / BOUND_HALF * (scaling * residual)
            solution = solution + update
            rho_old = rho_new
        pressure = ramp + solution
        flux = jnp.where(face, link * (pressure - upper_of(pressure)), 0.0)
        total = jnp.sum(flux, axis=0)
        total = jnp.sum(total, axis=0, keepdims=True)
        rows.append(total * (0.5 / area))
    rows.append(jnp.zeros((8 - len(rows), LANES), jnp.float32))
    o_ref[0] = jnp.concatenate(rows, axis=0)


def upscale_windows(raw, facies_table, bounds, cols_len):
    span_y = CCY + 2 * RIM
    count_z = (raw.shape[1] - 2 * RIM) // CCZ
    count_x = (raw.shape[2] - 2 * RIM) // CCX
    count_y = cols_len // CCY
    count = count_z * count_x * count_y
    segments = LANES // span_y
    packs = -(-count // segments)
    kernel = functools.partial(window_kernel, count_x=count_x, count_y=count_y, count=count)
    sums = pl.pallas_call(
        kernel,
        grid=(packs,),
        in_specs=[
            pl.BlockSpec(memory_space=pltpu.SMEM),
            pl.BlockSpec(memory_space=pltpu.SMEM),
            pl.BlockSpec(raw.shape, lambda p: (0, 0, 0, 0)),
        ],
        out_specs=pl.BlockSpec((1, 8, LANES), lambda p: (p, 0, 0)),
        out_shape=jax.ShapeDtypeStruct((packs, 8, LANES), jnp.float32),
    )(facies_table, bounds, raw)
    sums = sums[:, :3, : segments * span_y].reshape(packs, 3, segments, span_y).sum(axis=3)
    sums = sums.transpose(1, 0, 2).reshape(3, packs * segments)[:, :count]
    return sums.reshape((3, count_z, count_x, count_y))


def coarse_sweep(perm_pad, press_pad, inside_pad, accumulation, fixed):
    centre = (slice(1, -1), slice(1, -1), slice(1, -1))
    factors = (CCY * CCZ / CCX, CCX * CCZ / CCY, CCX * CCY / CCZ)
    numer = fixed
    denom = accumulation
    for component, axis_dim in ((0, 1), (1, 2), (2, 0)):
        for offset in (-1, 1):
            window_slice = [slice(1, -1), slice(1, -1), slice(1, -1)]
            window_slice[axis_dim] = slice(1 + offset, press_pad.shape[axis_dim] - 1 + offset)
            beside = tuple(window_slice)
            link = (
                factors[component]
                * 0.5
                * (perm_pad[component][centre] + perm_pad[component][beside])
                * inside_pad[beside]
            )
            numer = numer + link * press_pad[beside]
            denom = denom + jnp.abs(link)
    return numer / denom


def span_mask(anchor, length, total, margin):
    coords = anchor - margin + jnp.arange(length + 2 * margin, dtype=jnp.int32)
    return ((coords >= 0) & (coords < total)).astype(jnp.float32)


def cut_windows(fields):
    span_z = CCZ + 2 * RIM
    span_x = CCX + 2 * RIM
    span_y = CCY + 2 * RIM
    count_z = (fields[0].shape[0] - 2 * RIM) // CCZ
    count_x = (fields[0].shape[1] - 2 * RIM) // CCX
    count_y = (fields[0].shape[2] - 2 * RIM) // CCY
    stacks = []
    for field in fields:
        pieces = []
        for block_z in range(count_z):
            for block_y in range(count_y):
                piece = field[
                    block_z * CCZ : block_z * CCZ + span_z,
                    0:span_x,
                    block_y * CCY : block_y * CCY + span_y,
                ]
                pieces.append(piece.reshape(span_z, span_x * span_y))
        stacks.append(jnp.stack(pieces))
    return (stacks, (count_z, count_x, count_y))


def faces(block, sides):
    got = []
    for axis, dim in sides:
        count = lax.axis_size(axis)
        ends = count - 1
        head = lax.slice_in_dim(block, 0, 1, axis=dim)
        tail = lax.slice_in_dim(block, block.shape[dim] - 1, block.shape[dim], axis=dim)
        lower = lax.ppermute(tail, axis, [(i, i + 1) for i in range(ends)])
        upper = lax.ppermute(head, axis, [(i + 1, i) for i in range(ends)])
        got.append((lower, upper))
    return got


def neighbour_views(block, got, dim_of):
    views = []
    for (lower, upper), dim in zip(got, dim_of):
        size = block.shape[dim]
        below = jnp.concatenate([lower, lax.slice_in_dim(block, 0, size - 1, axis=dim)], axis=dim)
        above = jnp.concatenate([lax.slice_in_dim(block, 1, size, axis=dim), upper], axis=dim)
        views.append((below, above))
    return views


def coarse_step(upscaled, views, inside_views, pressure, accumulation, fixed):
    factors = (CCY * CCZ / CCX, CCX * CCZ / CCY, CCX * CCY / CCZ)
    numer = fixed
    denom = accumulation
    for component in range(3):
        for side in range(2):
            beside = views[component][side]
            link = factors[component] * 0.5 * (upscaled[component] + beside[component]) * inside_views[component][side]
            numer = numer + link * pressure[component][side]
            denom = denom + jnp.abs(link)
    return numer / denom


def local(log_noise, facies, facies_table, pressure_old, accumulation, source):
    depth_len, rows_len, cols_len = log_noise.shape
    size_z = lax.axis_size("gz")
    size_x = lax.axis_size("gx")
    size_y = lax.axis_size("gy")
    index_z = lax.axis_index("gz")
    index_x = lax.axis_index("gx")
    index_y = lax.axis_index("gy")
    raw = jnp.stack([log_noise, facies.astype(jnp.float32)])
    wide = -(-(cols_len + 2 * RIM) // LANES) * LANES
    raw = extended(raw, (("gx", 2), ("gz", 1), ("gy", 3)), RIM, wide)
    anchor_z = index_z * depth_len
    anchor_y = index_y * cols_len
    anchor_x = index_x * rows_len
    bounds = jnp.stack(
        [
            RIM - anchor_z,
            depth_len * size_z + RIM - anchor_z,
            RIM - anchor_x,
            rows_len * size_x + RIM - anchor_x,
            RIM - anchor_y,
            cols_len * size_y + RIM - anchor_y,
        ]
    ).astype(jnp.int32)
    upscaled = upscale_windows(raw, facies_table, bounds, cols_len)
    coarse_z, coarse_x, coarse_y = pressure_old.shape
    bundle = jnp.stack([upscaled[0], upscaled[1], upscaled[2], pressure_old, accumulation, source])
    every = doubling_gather(bundle, "gy", 3)
    every = doubling_gather(every, "gx", 2)
    every = doubling_gather(every, "gz", 1)
    perm_pad = jnp.pad(every[:3], ((0, 0), (1, 1), (1, 1), (1, 1)))
    old_all = every[3]
    acc_all = every[4]
    fixed_all = acc_all * old_all + every[5]
    inside_pad = jnp.pad(jnp.ones(old_all.shape, jnp.float32), 1)
    pressure = old_all
    for sweep_index in range(2):
        pressure = coarse_sweep(perm_pad, jnp.pad(pressure, 1), inside_pad, acc_all, fixed_all)
    pressure = lax.dynamic_slice(
        pressure, (index_z * coarse_z, index_x * coarse_x, index_y * coarse_y), (coarse_z, coarse_x, coarse_y)
    )
    return (pressure, upscaled)


def solution(mesh):
    placed = (
        P(("real", "gz"), "gx", "gy"),
        P(("real", "gz"), "gx", "gy"),
        P(),
        P(("real", "gz"), "gx", "gy"),
        P(("real", "gz"), "gx", "gy"),
        P(("real", "gz"), "gx", "gy"),
    )
    return jax.shard_map(
        local,
        mesh=mesh,
        in_specs=placed,
        out_specs=(P(("real", "gz"), "gx", "gy"), P(None, ("real", "gz"), "gx", "gy")),
        check_vma=False,
    )
```

```python
import functools

import jax
import jax.numpy as jnp
from jax import lax
from jax.sharding import PartitionSpec as P
from jax.experimental import pallas as pl
from jax.experimental.pallas import tpu as pltpu

NFAC = 4
CCX = 32
CCY = 32
CCZ = 8
RIM = 4
SWEEPS = 3


BOUND_MID = 1.0
BOUND_HALF = 0.9


def extended(cells, sides, width, lanes=None):
    for axis, dim in sides:
        count = lax.axis_size(axis)
        ends = count - 1
        head = lax.slice_in_dim(cells, 0, width, axis=dim)
        tail = lax.slice_in_dim(cells, cells.shape[dim] - width, cells.shape[dim], axis=dim)
        if count == 2:
            lower_side = lax.axis_index(axis) == 0
            got = lax.ppermute(jnp.where(lower_side, tail, head), axis, [(0, 1), (1, 0)])
            below = got
            above = got
        elif count % 2 == 0:
            even = lax.axis_index(axis) % 2 == 0
            first = [(i, i ^ 1) for i in range(count)]
            second = [(i, i + 1 if i % 2 else i - 1) for i in range(1, count - 1)]
            got_first = lax.ppermute(jnp.where(even, tail, head), axis, first)
            got_second = lax.ppermute(jnp.where(even, head, tail), axis, second)
            below = jnp.where(even, got_second, got_first)
            above = jnp.where(even, got_first, got_second)
        else:
            below = lax.ppermute(tail, axis, [(i, (i + 1) % count) for i in range(ends)])
            above = lax.ppermute(head, axis, [((i + 1) % count, i) for i in range(ends)])
        if lanes is not None and dim == cells.ndim - 1:
            extra = lanes - (cells.shape[dim] + 2 * width)
            parts = [cells, above, jnp.zeros(cells.shape[:-1] + (extra,), cells.dtype), below]
        else:
            parts = [below, cells, above]
        cells = jnp.concatenate(parts, axis=dim)
    return cells


def halo_xy_then_z(block, width, lanes):
    size_x = lax.axis_size("gx")
    size_y = lax.axis_size("gy")
    if size_y != 2 or size_x % 2:
        return extended(block, (("gx", 2), ("gz", 1), ("gy", 3)), width, lanes)
    even = lax.axis_index("gx") % 2 == 0
    low_y = lax.axis_index("gy") == 0

    def edge(values, dim, upper):
        length = values.shape[dim]
        start = length - width if upper else 0
        return lax.slice_in_dim(values, start, start + width, axis=dim)

    def y_side(values):
        return jnp.where(low_y, edge(values, 3, True), edge(values, 3, False))

    def partner(i):
        return i + 1 if i % 2 else i - 1

    first = [(i, i ^ 1) for i in range(size_x)]
    second = [(i, partner(i)) for i in range(1, size_x - 1)]
    send_first = jnp.where(even, edge(block, 2, True), edge(block, 2, False))
    send_second = jnp.where(even, edge(block, 2, False), edge(block, 2, True))
    got_first = lax.ppermute(send_first, "gx", first)
    got_second = lax.ppermute(send_second, "gx", second)
    got_y = lax.ppermute(y_side(block), "gy", [(0, 1), (1, 0)])
    names = ("gx", "gy")
    corner_first = [(i * 2 + j, (i ^ 1) * 2 + 1 - j) for i in range(size_x) for j in range(2)]
    corner_second = [(i * 2 + j, partner(i) * 2 + 1 - j) for i in range(1, size_x - 1) for j in range(2)]
    got_corner_first = lax.ppermute(y_side(send_first), names, corner_first)
    got_corner_second = lax.ppermute(y_side(send_second), names, corner_second)
    below_x = jnp.where(even, got_second, got_first)
    above_x = jnp.where(even, got_first, got_second)
    below_corner = jnp.where(even, got_corner_second, got_corner_first)
    above_corner = jnp.where(even, got_corner_first, got_corner_second)
    centre = jnp.concatenate([below_x, block, above_x], axis=2)
    rim = jnp.concatenate([below_corner, got_y, above_corner], axis=2)
    extra = lanes - (block.shape[3] + 2 * width)
    zeros = jnp.zeros(centre.shape[:3] + (extra,), centre.dtype)
    cells = jnp.concatenate([centre, rim, zeros, rim], axis=3)
    return extended(cells, (("gz", 1),), width)


def doubling_gather(values, axis, dim):
    count = lax.axis_size(axis)
    if count & (count - 1):
        return lax.all_gather(values, axis, axis=dim, tiled=True)
    index = lax.axis_index(axis)
    step = 1
    while step < count:
        got = lax.ppermute(values, axis, [(i, i ^ step) for i in range(count)])
        lower = (index // step) % 2 == 0
        values = jnp.where(
            lower, jnp.concatenate([values, got], axis=dim), jnp.concatenate([got, values], axis=dim)
        )
        step *= 2
    return values


def raise_flat(values, offset):
    zeros_block = jnp.zeros(values.shape[:-1] + (offset,), values.dtype)
    return jnp.concatenate([values[..., offset:], zeros_block], axis=-1)


def lower_flat(values, offset):
    zeros_block = jnp.zeros(values.shape[:-1] + (offset,), values.dtype)
    return jnp.concatenate([zeros_block, values[..., :-offset]], axis=-1)


def raise_depth(values):
    zeros_block = jnp.zeros(values.shape[:1] + (1,) + values.shape[2:], values.dtype)
    return jnp.concatenate([values[:, 1:], zeros_block], axis=1)


def lower_depth(values):
    zeros_block = jnp.zeros(values.shape[:1] + (1,) + values.shape[2:], values.dtype)
    return jnp.concatenate([zeros_block, values[:, :-1]], axis=1)


def log_fields(log_noise, facies, facies_table):
    base_log = log_noise
    extra_y = jnp.zeros_like(log_noise)
    extra_z = jnp.zeros_like(log_noise)
    for code_value in range(NFAC):
        matched = facies == code_value
        base_log = base_log + jnp.where(matched, facies_table[0, code_value], jnp.float32(0.0))
        extra_y = extra_y + jnp.where(matched, facies_table[1, code_value], jnp.float32(0.0))
        extra_z = extra_z + jnp.where(matched, facies_table[2, code_value], jnp.float32(0.0))
    return (base_log, base_log + extra_y, base_log + extra_z)


def upscale(perm_logs, inside):
    span_z = CCZ + 2 * RIM
    span_x = CCX + 2 * RIM
    span_y = CCY + 2 * RIM
    depth_pos = lax.broadcasted_iota(jnp.int32, (1, span_z, 1), 1)
    flat_pos = lax.broadcasted_iota(jnp.int32, (1, 1, span_x * span_y), 2)
    column_pos = flat_pos // span_y
    row_pos = flat_pos % span_y
    perm_x = jnp.exp(perm_logs[0])
    perm_y = jnp.exp(perm_logs[1])
    perm_z = jnp.exp(perm_logs[2])

    def links(perm, other_perm, other_inside):
        return inside * other_inside * 2.0 * perm * other_perm / (perm + other_perm)

    link_x = links(perm_x, raise_flat(perm_x, span_y), raise_flat(inside, span_y))
    link_y = links(perm_y, raise_flat(perm_y, 1), raise_flat(inside, 1)) * (
        row_pos < span_y - 1
    ).astype(jnp.float32)
    link_z = links(perm_z, raise_depth(perm_z), raise_depth(inside))
    diagonal = (
        link_x
        + lower_flat(link_x, span_y)
        + link_y
        + lower_flat(link_y, 1)
        + link_z
        + lower_depth(link_z)
    )

    def apply_operator(field):
        beside = link_x * raise_flat(field, span_y) + lower_flat(link_x * field, span_y)
        beside = beside + link_y * raise_flat(field, 1) + lower_flat(link_y * field, 1)
        beside = beside + link_z * raise_depth(field) + lower_depth(link_z * field)
        return diagonal * field - beside

    interior = (
        (depth_pos >= 1)
        & (depth_pos <= span_z - 2)
        & (column_pos >= 1)
        & (column_pos <= span_x - 2)
        & (row_pos >= 1)
        & (row_pos <= span_y - 2)
    )
    unknown = inside * interior.astype(jnp.float32)
    scaling = unknown / (diagonal + 1.0 - unknown)
    core_z = (depth_pos >= RIM) & (depth_pos < RIM + CCZ)
    core_x = (column_pos >= RIM) & (column_pos < RIM + CCX)
    core_y = (row_pos >= RIM) & (row_pos < RIM + CCY)
    face_x = (((column_pos == RIM - 1) | (column_pos == RIM + CCX - 1)) & core_z & core_y).astype(
        jnp.float32
    )
    face_y = (((row_pos == RIM - 1) | (row_pos == RIM + CCY - 1)) & core_z & core_x).astype(
        jnp.float32
    )
    face_z = (((depth_pos == RIM - 1) | (depth_pos == RIM + CCZ - 1)) & core_x & core_y).astype(
        jnp.float32
    )
    ramp_x = ((span_x - 1) / 2.0 - column_pos).astype(jnp.float32)
    ramp_y = ((span_y - 1) / 2.0 - row_pos).astype(jnp.float32)
    ramp_z = ((span_z - 1) / 2.0 - depth_pos).astype(jnp.float32)
    cheb_ratio = BOUND_MID / BOUND_HALF
    results = []
    cases = (
        (ramp_x, link_x, face_x, CCY * CCZ, 0),
        (ramp_y, link_y, face_y, CCX * CCZ, 1),
        (ramp_z, link_z, face_z, CCX * CCY, 2),
    )
    for ramp, link, face, area, direction in cases:
        ramp_full = jnp.broadcast_to(ramp, inside.shape)
        source_term = -unknown * apply_operator(ramp_full)
        update = scaling * source_term / BOUND_MID
        solution = update
        rho_old = 1.0 / cheb_ratio
        for sweep_index in range(SWEEPS - 1):
            residual = source_term - apply_operator(solution)
            rho_new = 1.0 / (2.0 * cheb_ratio - rho_old)
            update = rho_new * rho_old * update + 2.0 * rho_new / BOUND_HALF * (scaling * residual)
            solution = solution + update
            rho_old = rho_new
        pressure = ramp_full + solution
        if direction == 0:
            upper = raise_flat(pressure, span_y)
        elif direction == 1:
            upper = raise_flat(pressure, 1)
        else:
            upper = raise_depth(pressure)
        flux = link * (pressure - upper) * face
        results.append(jnp.sum(flux, axis=(1, 2)) * (0.5 / area))
    return jnp.stack(results)


LANES = 128


def window_kernel(table_ref, bounds_ref, raw_ref, o_ref, *, count_x, count_y, count):
    span_z = CCZ + 2 * RIM
    span_x = CCX + 2 * RIM
    span_y = CCY + 2 * RIM
    segments = LANES // span_y
    shape = (span_z, span_x, LANES)
    pack = pl.program_id(0)
    wide = raw_ref.shape[-1]
    depth_pos = lax.broadcasted_iota(jnp.int32, shape, 0)
    column_pos = lax.broadcasted_iota(jnp.int32, shape, 1)
    lane = lax.broadcasted_iota(jnp.int32, shape, 2)
    segment = jnp.zeros(shape, jnp.int32)
    for bound in range(1, segments + 1):
        segment = segment + (lane >= bound * span_y).astype(jnp.int32)
    row_pos = lane - span_y * segment
    noise = jnp.zeros(shape, jnp.float32)
    codes = jnp.zeros(shape, jnp.float32)
    inside = jnp.zeros(shape, jnp.float32)
    for slot in range(segments):
        window = pack * segments + slot
        valid = window < count
        window = jnp.minimum(window, count - 1)
        block_z = window // (count_x * count_y)
        block_x = (window // count_y) % count_x
        block_y = window % count_y
        shift = (slot * span_y - block_y * CCY + RIM + wide) % wide
        here = segment == slot

        def cut(field):
            slab = raw_ref[field, pl.ds(block_z * CCZ, span_z), pl.ds(block_x * CCX, span_x), :]
            return pltpu.roll(slab, shift, 2)[:, :, :LANES]

        depth_at = depth_pos + block_z * CCZ
        column_at = column_pos + block_x * CCX
        row_at = row_pos + block_y * CCY
        held = (
            (depth_at >= bounds_ref[0])
            & (depth_at < bounds_ref[1])
            & (column_at >= bounds_ref[2])
            & (column_at < bounds_ref[3])
            & (row_at >= bounds_ref[4])
            & (row_at < bounds_ref[5])
        )
        noise = jnp.where(here, cut(0), noise)
        codes = jnp.where(here, cut(1), codes)
        inside = jnp.where(here & valid & held, 1.0, inside)

    def lookup(row):
        value = jnp.zeros(shape, jnp.float32)
        for code_value in range(NFAC):
            value = jnp.where(codes == code_value, table_ref[row, code_value], value)
        return value

    log_x = noise + lookup(0)
    log_y = log_x + lookup(1)
    log_z = log_x + lookup(2)
    perm_x = jnp.exp(log_x)
    perm_y = jnp.exp(log_y)
    perm_z = jnp.exp(log_z)

    def up_x(v):
        return pltpu.roll(v, span_x - 1, 1)

    def down_x(v):
        return pltpu.roll(v, 1, 1)

    def up_y(v):
        return pltpu.roll(v, LANES - 1, 2)

    def down_y(v):
        return pltpu.roll(v, 1, 2)

    def up_z(v):
        return jnp.concatenate([v[1:], v[:1]], axis=0)

    def down_z(v):
        return jnp.concatenate([v[-1:], v[:-1]], axis=0)

    def links(perm, other_perm, other_inside, valid):
        value = inside * other_inside * 2.0 * perm * other_perm / (perm + other_perm)
        return jnp.where(valid, value, 0.0)

    link_x = links(perm_x, up_x(perm_x), up_x(inside), column_pos < span_x - 1)
    link_y = links(perm_y, up_y(perm_y), up_y(inside), row_pos < span_y - 1)
    link_z = links(perm_z, up_z(perm_z), up_z(inside), depth_pos < span_z - 1)
    diagonal = link_x + down_x(link_x) + link_y + down_y(link_y) + link_z + down_z(link_z)

    def apply_operator(field):
        beside = link_x * up_x(field) + down_x(link_x * field)
        beside = beside + link_y * up_y(field) + down_y(link_y * field)
        beside = beside + link_z * up_z(field) + down_z(link_z * field)
        return diagonal * field - beside

    interior = (
        (depth_pos >= 1)
        & (depth_pos <= span_z - 2)
        & (column_pos >= 1)
        & (column_pos <= span_x - 2)
        & (row_pos >= 1)
        & (row_pos <= span_y - 2)
    )
    unknown = jnp.where(interior, inside, 0.0)
    scaling = unknown / (diagonal + 1.0 - unknown)
    core_z = (depth_pos >= RIM) & (depth_pos < RIM + CCZ)
    core_x = (column_pos >= RIM) & (column_pos < RIM + CCX)
    core_y = (row_pos >= RIM) & (row_pos < RIM + CCY)
    face_x = ((column_pos == RIM - 1) | (column_pos == RIM + CCX - 1)) & core_z & core_y
    face_y = ((row_pos == RIM - 1) | (row_pos == RIM + CCY - 1)) & core_z & core_x
    face_z = ((depth_pos == RIM - 1) | (depth_pos == RIM + CCZ - 1)) & core_x & core_y
    ramp_x = ((span_x - 1) / 2.0 - column_pos).astype(jnp.float32)
    ramp_y = ((span_y - 1) / 2.0 - row_pos).astype(jnp.float32)
    ramp_z = ((span_z - 1) / 2.0 - depth_pos).astype(jnp.float32)
    cheb_ratio = BOUND_MID / BOUND_HALF
    cases = (
        (ramp_x, link_x, face_x, CCY * CCZ, up_x, down_x),
        (ramp_y, link_y, face_y, CCX * CCZ, up_y, down_y),
        (ramp_z, link_z, face_z, CCX * CCY, up_z, down_z),
    )
    rows = []
    for ramp, link, face, area, upper_of, lower_of in cases:
        source_term = -unknown * (link - lower_of(link))
        update = scaling * source_term / BOUND_MID
        solution = update
        rho_old = 1.0 / cheb_ratio
        for sweep_index in range(SWEEPS - 1):
            residual = source_term - apply_operator(solution)
            rho_new = 1.0 / (2.0 * cheb_ratio - rho_old)
            update = rho_new * rho_old * update + 2.0 * rho_new / BOUND_HALF * (scaling * residual)
            solution = solution + update
            rho_old = rho_new
        pressure = ramp + solution
        flux = jnp.where(face, link * (pressure - upper_of(pressure)), 0.0)
        total = jnp.sum(flux, axis=0)
        total = jnp.sum(total, axis=0, keepdims=True)
        rows.append(total * (0.5 / area))
    rows.append(jnp.zeros((8 - len(rows), LANES), jnp.float32))
    o_ref[0] = jnp.concatenate(rows, axis=0)


def upscale_windows(raw, facies_table, bounds, cols_len):
    span_y = CCY + 2 * RIM
    count_z = (raw.shape[1] - 2 * RIM) // CCZ
    count_x = (raw.shape[2] - 2 * RIM) // CCX
    count_y = cols_len // CCY
    count = count_z * count_x * count_y
    segments = LANES // span_y
    packs = -(-count // segments)
    kernel = functools.partial(window_kernel, count_x=count_x, count_y=count_y, count=count)
    sums = pl.pallas_call(
        kernel,
        grid=(packs,),
        in_specs=[
            pl.BlockSpec(memory_space=pltpu.SMEM),
            pl.BlockSpec(memory_space=pltpu.SMEM),
            pl.BlockSpec(raw.shape, lambda p: (0, 0, 0, 0)),
        ],
        out_specs=pl.BlockSpec((1, 8, LANES), lambda p: (p, 0, 0)),
        out_shape=jax.ShapeDtypeStruct((packs, 8, LANES), jnp.float32),
    )(facies_table, bounds, raw)
    sums = sums[:, :3, : segments * span_y].reshape(packs, 3, segments, span_y).sum(axis=3)
    sums = sums.transpose(1, 0, 2).reshape(3, packs * segments)[:, :count]
    return sums.reshape((3, count_z, count_x, count_y))


def coarse_sweep(perm_pad, press_pad, inside_pad, accumulation, fixed):
    centre = (slice(1, -1), slice(1, -1), slice(1, -1))
    factors = (CCY * CCZ / CCX, CCX * CCZ / CCY, CCX * CCY / CCZ)
    numer = fixed
    denom = accumulation
    for component, axis_dim in ((0, 1), (1, 2), (2, 0)):
        for offset in (-1, 1):
            window_slice = [slice(1, -1), slice(1, -1), slice(1, -1)]
            window_slice[axis_dim] = slice(1 + offset, press_pad.shape[axis_dim] - 1 + offset)
            beside = tuple(window_slice)
            link = (
                factors[component]
                * 0.5
                * (perm_pad[component][centre] + perm_pad[component][beside])
                * inside_pad[beside]
            )
            numer = numer + link * press_pad[beside]
            denom = denom + jnp.abs(link)
    return numer / denom


def span_mask(anchor, length, total, margin):
    coords = anchor - margin + jnp.arange(length + 2 * margin, dtype=jnp.int32)
    return ((coords >= 0) & (coords < total)).astype(jnp.float32)


def cut_windows(fields):
    span_z = CCZ + 2 * RIM
    span_x = CCX + 2 * RIM
    span_y = CCY + 2 * RIM
    count_z = (fields[0].shape[0] - 2 * RIM) // CCZ
    count_x = (fields[0].shape[1] - 2 * RIM) // CCX
    count_y = (fields[0].shape[2] - 2 * RIM) // CCY
    stacks = []
    for field in fields:
        pieces = []
        for block_z in range(count_z):
            for block_y in range(count_y):
                piece = field[
                    block_z * CCZ : block_z * CCZ + span_z,
                    0:span_x,
                    block_y * CCY : block_y * CCY + span_y,
                ]
                pieces.append(piece.reshape(span_z, span_x * span_y))
        stacks.append(jnp.stack(pieces))
    return (stacks, (count_z, count_x, count_y))


def faces(block, sides):
    got = []
    for axis, dim in sides:
        count = lax.axis_size(axis)
        ends = count - 1
        head = lax.slice_in_dim(block, 0, 1, axis=dim)
        tail = lax.slice_in_dim(block, block.shape[dim] - 1, block.shape[dim], axis=dim)
        lower = lax.ppermute(tail, axis, [(i, i + 1) for i in range(ends)])
        upper = lax.ppermute(head, axis, [(i + 1, i) for i in range(ends)])
        got.append((lower, upper))
    return got


def neighbour_views(block, got, dim_of):
    views = []
    for (lower, upper), dim in zip(got, dim_of):
        size = block.shape[dim]
        below = jnp.concatenate([lower, lax.slice_in_dim(block, 0, size - 1, axis=dim)], axis=dim)
        above = jnp.concatenate([lax.slice_in_dim(block, 1, size, axis=dim), upper], axis=dim)
        views.append((below, above))
    return views


def coarse_step(upscaled, views, inside_views, pressure, accumulation, fixed):
    factors = (CCY * CCZ / CCX, CCX * CCZ / CCY, CCX * CCY / CCZ)
    numer = fixed
    denom = accumulation
    for component in range(3):
        for side in range(2):
            beside = views[component][side]
            link = factors[component] * 0.5 * (upscaled[component] + beside[component]) * inside_views[component][side]
            numer = numer + link * pressure[component][side]
            denom = denom + jnp.abs(link)
    return numer / denom


def local(log_noise, facies, facies_table, pressure_old, accumulation, source):
    depth_len, rows_len, cols_len = log_noise.shape
    size_z = lax.axis_size("gz")
    size_x = lax.axis_size("gx")
    size_y = lax.axis_size("gy")
    index_z = lax.axis_index("gz")
    index_x = lax.axis_index("gx")
    index_y = lax.axis_index("gy")
    raw = jnp.stack([log_noise, facies.astype(jnp.float32)])
    wide = -(-(cols_len + 2 * RIM) // LANES) * LANES
    raw = halo_xy_then_z(raw, RIM, wide)
    anchor_z = index_z * depth_len
    anchor_y = index_y * cols_len
    anchor_x = index_x * rows_len
    bounds = jnp.stack(
        [
            RIM - anchor_z,
            depth_len * size_z + RIM - anchor_z,
            RIM - anchor_x,
            rows_len * size_x + RIM - anchor_x,
            RIM - anchor_y,
            cols_len * size_y + RIM - anchor_y,
        ]
    ).astype(jnp.int32)
    upscaled = upscale_windows(raw, facies_table, bounds, cols_len)
    coarse_z, coarse_x, coarse_y = pressure_old.shape
    bundle = jnp.stack([upscaled[0], upscaled[1], upscaled[2], pressure_old, accumulation, source])
    every = doubling_gather(bundle, "gy", 3)
    every = doubling_gather(every, "gx", 2)
    every = doubling_gather(every, "gz", 1)
    perm_pad = jnp.pad(every[:3], ((0, 0), (1, 1), (1, 1), (1, 1)))
    old_all = every[3]
    acc_all = every[4]
    fixed_all = acc_all * old_all + every[5]
    inside_pad = jnp.pad(jnp.ones(old_all.shape, jnp.float32), 1)
    pressure = old_all
    for sweep_index in range(2):
        pressure = coarse_sweep(perm_pad, jnp.pad(pressure, 1), inside_pad, acc_all, fixed_all)
    pressure = lax.dynamic_slice(
        pressure, (index_z * coarse_z, index_x * coarse_x, index_y * coarse_y), (coarse_z, coarse_x, coarse_y)
    )
    return (pressure, upscaled)


def solution(mesh):
    placed = (
        P(("real", "gz"), "gx", "gy"),
        P(("real", "gz"), "gx", "gy"),
        P(),
        P(("real", "gz"), "gx", "gy"),
        P(("real", "gz"), "gx", "gy"),
        P(("real", "gz"), "gx", "gy"),
    )
    return jax.shard_map(
        local,
        mesh=mesh,
        in_specs=placed,
        out_specs=(P(("real", "gz"), "gx", "gy"), P(None, ("real", "gz"), "gx", "gy")),
        check_vma=False,
    )
```

```python
import functools

import jax
import jax.numpy as jnp
from jax import lax
from jax.sharding import PartitionSpec as P
from jax.experimental import pallas as pl
from jax.experimental.pallas import tpu as pltpu

NFAC = 4
CCX = 32
CCY = 32
CCZ = 8
RIM = 4
SWEEPS = 3


BOUND_MID = 1.0
BOUND_HALF = 0.9


def extended(cells, sides, width, lanes=None):
    for axis, dim in sides:
        count = lax.axis_size(axis)
        ends = count - 1
        head = lax.slice_in_dim(cells, 0, width, axis=dim)
        tail = lax.slice_in_dim(cells, cells.shape[dim] - width, cells.shape[dim], axis=dim)
        if count == 2:
            lower_side = lax.axis_index(axis) == 0
            got = lax.ppermute(jnp.where(lower_side, tail, head), axis, [(0, 1), (1, 0)])
            below = got
            above = got
        elif count % 2 == 0:
            even = lax.axis_index(axis) % 2 == 0
            first = [(i, i ^ 1) for i in range(count)]
            second = [(i, i + 1 if i % 2 else i - 1) for i in range(1, count - 1)]
            got_first = lax.ppermute(jnp.where(even, tail, head), axis, first)
            got_second = lax.ppermute(jnp.where(even, head, tail), axis, second)
            below = jnp.where(even, got_second, got_first)
            above = jnp.where(even, got_first, got_second)
        else:
            below = lax.ppermute(tail, axis, [(i, (i + 1) % count) for i in range(ends)])
            above = lax.ppermute(head, axis, [((i + 1) % count, i) for i in range(ends)])
        if lanes is not None and dim == cells.ndim - 1:
            extra = lanes - (cells.shape[dim] + 2 * width)
            parts = [cells, above, jnp.zeros(cells.shape[:-1] + (extra,), cells.dtype), below]
        else:
            parts = [below, cells, above]
        cells = jnp.concatenate(parts, axis=dim)
    return cells


def face_slabs(block, axis, dim):
    count = lax.axis_size(axis)
    head = lax.slice_in_dim(block, 0, 1, axis=dim)
    tail = lax.slice_in_dim(block, block.shape[dim] - 1, block.shape[dim], axis=dim)
    index = lax.axis_index(axis)
    if count == 1:
        return jnp.zeros_like(tail), jnp.zeros_like(head)
    if count == 2:
        lower_side = index == 0
        got = lax.ppermute(jnp.where(lower_side, tail, head), axis, [(0, 1), (1, 0)])
        return jnp.where(lower_side, 0.0, got), jnp.where(lower_side, got, 0.0)
    if count % 2 == 0:
        even = index % 2 == 0
        first = [(i, i ^ 1) for i in range(count)]
        second = [(i, i + 1 if i % 2 else i - 1) for i in range(1, count - 1)]
        got_first = lax.ppermute(jnp.where(even, tail, head), axis, first)
        got_second = lax.ppermute(jnp.where(even, head, tail), axis, second)
        return jnp.where(even, got_second, got_first), jnp.where(even, got_first, got_second)
    lower = lax.ppermute(tail, axis, [(i, i + 1) for i in range(count - 1)])
    upper = lax.ppermute(head, axis, [(i + 1, i) for i in range(count - 1)])
    return lower, upper


def faces(block, sides):
    return [face_slabs(block, axis, dim) for axis, dim in sides]


def neighbour_views(block, got, dim_of):
    views = []
    for (lower, upper), dim in zip(got, dim_of):
        size = block.shape[dim]
        below = jnp.concatenate([lower, lax.slice_in_dim(block, 0, size - 1, axis=dim)], axis=dim)
        above = jnp.concatenate([lax.slice_in_dim(block, 1, size, axis=dim), upper], axis=dim)
        views.append((below, above))
    return views


def coarse_step(upscaled, views, inside_views, pressure, accumulation, fixed):
    factors = (CCY * CCZ / CCX, CCX * CCZ / CCY, CCX * CCY / CCZ)
    numer = fixed
    denom = accumulation
    for component in range(3):
        for side in range(2):
            beside = views[component][side]
            link = factors[component] * 0.5 * (upscaled[component] + beside[component]) * inside_views[component][side]
            numer = numer + link * pressure[component][side]
            denom = denom + jnp.abs(link)
    return numer / denom


def doubling_gather(values, axis, dim):
    count = lax.axis_size(axis)
    if count & (count - 1):
        return lax.all_gather(values, axis, axis=dim, tiled=True)
    index = lax.axis_index(axis)
    step = 1
    while step < count:
        got = lax.ppermute(values, axis, [(i, i ^ step) for i in range(count)])
        lower = (index // step) % 2 == 0
        values = jnp.where(
            lower, jnp.concatenate([values, got], axis=dim), jnp.concatenate([got, values], axis=dim)
        )
        step *= 2
    return values


def raise_flat(values, offset):
    zeros_block = jnp.zeros(values.shape[:-1] + (offset,), values.dtype)
    return jnp.concatenate([values[..., offset:], zeros_block], axis=-1)


def lower_flat(values, offset):
    zeros_block = jnp.zeros(values.shape[:-1] + (offset,), values.dtype)
    return jnp.concatenate([zeros_block, values[..., :-offset]], axis=-1)


def raise_depth(values):
    zeros_block = jnp.zeros(values.shape[:1] + (1,) + values.shape[2:], values.dtype)
    return jnp.concatenate([values[:, 1:], zeros_block], axis=1)


def lower_depth(values):
    zeros_block = jnp.zeros(values.shape[:1] + (1,) + values.shape[2:], values.dtype)
    return jnp.concatenate([zeros_block, values[:, :-1]], axis=1)


def log_fields(log_noise, facies, facies_table):
    base_log = log_noise
    extra_y = jnp.zeros_like(log_noise)
    extra_z = jnp.zeros_like(log_noise)
    for code_value in range(NFAC):
        matched = facies == code_value
        base_log = base_log + jnp.where(matched, facies_table[0, code_value], jnp.float32(0.0))
        extra_y = extra_y + jnp.where(matched, facies_table[1, code_value], jnp.float32(0.0))
        extra_z = extra_z + jnp.where(matched, facies_table[2, code_value], jnp.float32(0.0))
    return (base_log, base_log + extra_y, base_log + extra_z)


def upscale(perm_logs, inside):
    span_z = CCZ + 2 * RIM
    span_x = CCX + 2 * RIM
    span_y = CCY + 2 * RIM
    depth_pos = lax.broadcasted_iota(jnp.int32, (1, span_z, 1), 1)
    flat_pos = lax.broadcasted_iota(jnp.int32, (1, 1, span_x * span_y), 2)
    column_pos = flat_pos // span_y
    row_pos = flat_pos % span_y
    perm_x = jnp.exp(perm_logs[0])
    perm_y = jnp.exp(perm_logs[1])
    perm_z = jnp.exp(perm_logs[2])

    def links(perm, other_perm, other_inside):
        return inside * other_inside * 2.0 * perm * other_perm / (perm + other_perm)

    link_x = links(perm_x, raise_flat(perm_x, span_y), raise_flat(inside, span_y))
    link_y = links(perm_y, raise_flat(perm_y, 1), raise_flat(inside, 1)) * (
        row_pos < span_y - 1
    ).astype(jnp.float32)
    link_z = links(perm_z, raise_depth(perm_z), raise_depth(inside))
    diagonal = (
        link_x
        + lower_flat(link_x, span_y)
        + link_y
        + lower_flat(link_y, 1)
        + link_z
        + lower_depth(link_z)
    )

    def apply_operator(field):
        beside = link_x * raise_flat(field, span_y) + lower_flat(link_x * field, span_y)
        beside = beside + link_y * raise_flat(field, 1) + lower_flat(link_y * field, 1)
        beside = beside + link_z * raise_depth(field) + lower_depth(link_z * field)
        return diagonal * field - beside

    interior = (
        (depth_pos >= 1)
        & (depth_pos <= span_z - 2)
        & (column_pos >= 1)
        & (column_pos <= span_x - 2)
        & (row_pos >= 1)
        & (row_pos <= span_y - 2)
    )
    unknown = inside * interior.astype(jnp.float32)
    scaling = unknown / (diagonal + 1.0 - unknown)
    core_z = (depth_pos >= RIM) & (depth_pos < RIM + CCZ)
    core_x = (column_pos >= RIM) & (column_pos < RIM + CCX)
    core_y = (row_pos >= RIM) & (row_pos < RIM + CCY)
    face_x = (((column_pos == RIM - 1) | (column_pos == RIM + CCX - 1)) & core_z & core_y).astype(
        jnp.float32
    )
    face_y = (((row_pos == RIM - 1) | (row_pos == RIM + CCY - 1)) & core_z & core_x).astype(
        jnp.float32
    )
    face_z = (((depth_pos == RIM - 1) | (depth_pos == RIM + CCZ - 1)) & core_x & core_y).astype(
        jnp.float32
    )
    ramp_x = ((span_x - 1) / 2.0 - column_pos).astype(jnp.float32)
    ramp_y = ((span_y - 1) / 2.0 - row_pos).astype(jnp.float32)
    ramp_z = ((span_z - 1) / 2.0 - depth_pos).astype(jnp.float32)
    cheb_ratio = BOUND_MID / BOUND_HALF
    results = []
    cases = (
        (ramp_x, link_x, face_x, CCY * CCZ, 0),
        (ramp_y, link_y, face_y, CCX * CCZ, 1),
        (ramp_z, link_z, face_z, CCX * CCY, 2),
    )
    for ramp, link, face, area, direction in cases:
        ramp_full = jnp.broadcast_to(ramp, inside.shape)
        source_term = -unknown * apply_operator(ramp_full)
        update = scaling * source_term / BOUND_MID
        solution = update
        rho_old = 1.0 / cheb_ratio
        for sweep_index in range(SWEEPS - 1):
            residual = source_term - apply_operator(solution)
            rho_new = 1.0 / (2.0 * cheb_ratio - rho_old)
            update = rho_new * rho_old * update + 2.0 * rho_new / BOUND_HALF * (scaling * residual)
            solution = solution + update
            rho_old = rho_new
        pressure = ramp_full + solution
        if direction == 0:
            upper = raise_flat(pressure, span_y)
        elif direction == 1:
            upper = raise_flat(pressure, 1)
        else:
            upper = raise_depth(pressure)
        flux = link * (pressure - upper) * face
        results.append(jnp.sum(flux, axis=(1, 2)) * (0.5 / area))
    return jnp.stack(results)


LANES = 128


def window_kernel(table_ref, bounds_ref, raw_ref, o_ref, *, count_x, count_y, count):
    span_z = CCZ + 2 * RIM
    span_x = CCX + 2 * RIM
    span_y = CCY + 2 * RIM
    segments = LANES // span_y
    shape = (span_z, span_x, LANES)
    pack = pl.program_id(0)
    wide = raw_ref.shape[-1]
    depth_pos = lax.broadcasted_iota(jnp.int32, shape, 0)
    column_pos = lax.broadcasted_iota(jnp.int32, shape, 1)
    lane = lax.broadcasted_iota(jnp.int32, shape, 2)
    segment = jnp.zeros(shape, jnp.int32)
    for bound in range(1, segments + 1):
        segment = segment + (lane >= bound * span_y).astype(jnp.int32)
    row_pos = lane - span_y * segment
    noise = jnp.zeros(shape, jnp.float32)
    codes = jnp.zeros(shape, jnp.float32)
    inside = jnp.zeros(shape, jnp.float32)
    for slot in range(segments):
        window = pack * segments + slot
        valid = window < count
        window = jnp.minimum(window, count - 1)
        block_z = window // (count_x * count_y)
        block_x = (window // count_y) % count_x
        block_y = window % count_y
        shift = (slot * span_y - block_y * CCY + RIM + wide) % wide
        here = segment == slot

        def cut(field):
            slab = raw_ref[field, pl.ds(block_z * CCZ, span_z), pl.ds(block_x * CCX, span_x), :]
            return pltpu.roll(slab, shift, 2)[:, :, :LANES]

        depth_at = depth_pos + block_z * CCZ
        column_at = column_pos + block_x * CCX
        row_at = row_pos + block_y * CCY
        held = (
            (depth_at >= bounds_ref[0])
            & (depth_at < bounds_ref[1])
            & (column_at >= bounds_ref[2])
            & (column_at < bounds_ref[3])
            & (row_at >= bounds_ref[4])
            & (row_at < bounds_ref[5])
        )
        noise = jnp.where(here, cut(0), noise)
        codes = jnp.where(here, cut(1), codes)
        inside = jnp.where(here & valid & held, 1.0, inside)

    def lookup(row):
        value = jnp.zeros(shape, jnp.float32)
        for code_value in range(NFAC):
            value = jnp.where(codes == code_value, table_ref[row, code_value], value)
        return value

    log_x = noise + lookup(0)
    log_y = log_x + lookup(1)
    log_z = log_x + lookup(2)
    perm_x = jnp.exp(log_x)
    perm_y = jnp.exp(log_y)
    perm_z = jnp.exp(log_z)

    def up_x(v):
        return pltpu.roll(v, span_x - 1, 1)

    def down_x(v):
        return pltpu.roll(v, 1, 1)

    def up_y(v):
        return pltpu.roll(v, LANES - 1, 2)

    def down_y(v):
        return pltpu.roll(v, 1, 2)

    def up_z(v):
        return jnp.concatenate([v[1:], v[:1]], axis=0)

    def down_z(v):
        return jnp.concatenate([v[-1:], v[:-1]], axis=0)

    def links(perm, other_perm, other_inside, valid):
        value = inside * other_inside * 2.0 * perm * other_perm / (perm + other_perm)
        return jnp.where(valid, value, 0.0)

    link_x = links(perm_x, up_x(perm_x), up_x(inside), column_pos < span_x - 1)
    link_y = links(perm_y, up_y(perm_y), up_y(inside), row_pos < span_y - 1)
    link_z = links(perm_z, up_z(perm_z), up_z(inside), depth_pos < span_z - 1)
    diagonal = link_x + down_x(link_x) + link_y + down_y(link_y) + link_z + down_z(link_z)

    def apply_operator(field):
        beside = link_x * up_x(field) + down_x(link_x * field)
        beside = beside + link_y * up_y(field) + down_y(link_y * field)
        beside = beside + link_z * up_z(field) + down_z(link_z * field)
        return diagonal * field - beside

    interior = (
        (depth_pos >= 1)
        & (depth_pos <= span_z - 2)
        & (column_pos >= 1)
        & (column_pos <= span_x - 2)
        & (row_pos >= 1)
        & (row_pos <= span_y - 2)
    )
    unknown = jnp.where(interior, inside, 0.0)
    scaling = unknown / (diagonal + 1.0 - unknown)
    core_z = (depth_pos >= RIM) & (depth_pos < RIM + CCZ)
    core_x = (column_pos >= RIM) & (column_pos < RIM + CCX)
    core_y = (row_pos >= RIM) & (row_pos < RIM + CCY)
    face_x = ((column_pos == RIM - 1) | (column_pos == RIM + CCX - 1)) & core_z & core_y
    face_y = ((row_pos == RIM - 1) | (row_pos == RIM + CCY - 1)) & core_z & core_x
    face_z = ((depth_pos == RIM - 1) | (depth_pos == RIM + CCZ - 1)) & core_x & core_y
    ramp_x = ((span_x - 1) / 2.0 - column_pos).astype(jnp.float32)
    ramp_y = ((span_y - 1) / 2.0 - row_pos).astype(jnp.float32)
    ramp_z = ((span_z - 1) / 2.0 - depth_pos).astype(jnp.float32)
    cheb_ratio = BOUND_MID / BOUND_HALF
    cases = (
        (ramp_x, link_x, face_x, CCY * CCZ, up_x, down_x),
        (ramp_y, link_y, face_y, CCX * CCZ, up_y, down_y),
        (ramp_z, link_z, face_z, CCX * CCY, up_z, down_z),
    )
    rows = []
    for ramp, link, face, area, upper_of, lower_of in cases:
        source_term = -unknown * (link - lower_of(link))
        update = scaling * source_term / BOUND_MID
        solution = update
        rho_old = 1.0 / cheb_ratio
        for sweep_index in range(SWEEPS - 1):
            residual = source_term - apply_operator(solution)
            rho_new = 1.0 / (2.0 * cheb_ratio - rho_old)
            update = rho_new * rho_old * update + 2.0 * rho_new / BOUND_HALF * (scaling * residual)
            solution = solution + update
            rho_old = rho_new
        pressure = ramp + solution
        flux = jnp.where(face, link * (pressure - upper_of(pressure)), 0.0)
        total = jnp.sum(flux, axis=0)
        total = jnp.sum(total, axis=0, keepdims=True)
        rows.append(total * (0.5 / area))
    rows.append(jnp.zeros((8 - len(rows), LANES), jnp.float32))
    o_ref[0] = jnp.concatenate(rows, axis=0)


def upscale_windows(raw, facies_table, bounds, cols_len):
    span_y = CCY + 2 * RIM
    count_z = (raw.shape[1] - 2 * RIM) // CCZ
    count_x = (raw.shape[2] - 2 * RIM) // CCX
    count_y = cols_len // CCY
    count = count_z * count_x * count_y
    segments = LANES // span_y
    packs = -(-count // segments)
    kernel = functools.partial(window_kernel, count_x=count_x, count_y=count_y, count=count)
    sums = pl.pallas_call(
        kernel,
        grid=(packs,),
        in_specs=[
            pl.BlockSpec(memory_space=pltpu.SMEM),
            pl.BlockSpec(memory_space=pltpu.SMEM),
            pl.BlockSpec(raw.shape, lambda p: (0, 0, 0, 0)),
        ],
        out_specs=pl.BlockSpec((1, 8, LANES), lambda p: (p, 0, 0)),
        out_shape=jax.ShapeDtypeStruct((packs, 8, LANES), jnp.float32),
    )(facies_table, bounds, raw)
    sums = sums[:, :3, : segments * span_y].reshape(packs, 3, segments, span_y).sum(axis=3)
    sums = sums.transpose(1, 0, 2).reshape(3, packs * segments)[:, :count]
    return sums.reshape((3, count_z, count_x, count_y))


def coarse_sweep(perm_pad, press_pad, inside_pad, accumulation, fixed):
    centre = (slice(1, -1), slice(1, -1), slice(1, -1))
    factors = (CCY * CCZ / CCX, CCX * CCZ / CCY, CCX * CCY / CCZ)
    numer = fixed
    denom = accumulation
    for component, axis_dim in ((0, 1), (1, 2), (2, 0)):
        for offset in (-1, 1):
            window_slice = [slice(1, -1), slice(1, -1), slice(1, -1)]
            window_slice[axis_dim] = slice(1 + offset, press_pad.shape[axis_dim] - 1 + offset)
            beside = tuple(window_slice)
            link = (
                factors[component]
                * 0.5
                * (perm_pad[component][centre] + perm_pad[component][beside])
                * inside_pad[beside]
            )
            numer = numer + link * press_pad[beside]
            denom = denom + jnp.abs(link)
    return numer / denom


def span_mask(anchor, length, total, margin):
    coords = anchor - margin + jnp.arange(length + 2 * margin, dtype=jnp.int32)
    return ((coords >= 0) & (coords < total)).astype(jnp.float32)


def cut_windows(fields):
    span_z = CCZ + 2 * RIM
    span_x = CCX + 2 * RIM
    span_y = CCY + 2 * RIM
    count_z = (fields[0].shape[0] - 2 * RIM) // CCZ
    count_x = (fields[0].shape[1] - 2 * RIM) // CCX
    count_y = (fields[0].shape[2] - 2 * RIM) // CCY
    stacks = []
    for field in fields:
        pieces = []
        for block_z in range(count_z):
            for block_y in range(count_y):
                piece = field[
                    block_z * CCZ : block_z * CCZ + span_z,
                    0:span_x,
                    block_y * CCY : block_y * CCY + span_y,
                ]
                pieces.append(piece.reshape(span_z, span_x * span_y))
        stacks.append(jnp.stack(pieces))
    return (stacks, (count_z, count_x, count_y))


def faces(block, sides):
    got = []
    for axis, dim in sides:
        count = lax.axis_size(axis)
        ends = count - 1
        head = lax.slice_in_dim(block, 0, 1, axis=dim)
        tail = lax.slice_in_dim(block, block.shape[dim] - 1, block.shape[dim], axis=dim)
        lower = lax.ppermute(tail, axis, [(i, i + 1) for i in range(ends)])
        upper = lax.ppermute(head, axis, [(i + 1, i) for i in range(ends)])
        got.append((lower, upper))
    return got


def neighbour_views(block, got, dim_of):
    views = []
    for (lower, upper), dim in zip(got, dim_of):
        size = block.shape[dim]
        below = jnp.concatenate([lower, lax.slice_in_dim(block, 0, size - 1, axis=dim)], axis=dim)
        above = jnp.concatenate([lax.slice_in_dim(block, 1, size, axis=dim), upper], axis=dim)
        views.append((below, above))
    return views


def coarse_step(upscaled, views, inside_views, pressure, accumulation, fixed):
    factors = (CCY * CCZ / CCX, CCX * CCZ / CCY, CCX * CCY / CCZ)
    numer = fixed
    denom = accumulation
    for component in range(3):
        for side in range(2):
            beside = views[component][side]
            link = factors[component] * 0.5 * (upscaled[component] + beside[component]) * inside_views[component][side]
            numer = numer + link * pressure[component][side]
            denom = denom + jnp.abs(link)
    return numer / denom


def local(log_noise, facies, facies_table, pressure_old, accumulation, source):
    depth_len, rows_len, cols_len = log_noise.shape
    size_z = lax.axis_size("gz")
    size_x = lax.axis_size("gx")
    size_y = lax.axis_size("gy")
    index_z = lax.axis_index("gz")
    index_x = lax.axis_index("gx")
    index_y = lax.axis_index("gy")
    raw = jnp.stack([log_noise, facies.astype(jnp.float32)])
    wide = -(-(cols_len + 2 * RIM) // LANES) * LANES
    raw = extended(raw, (("gx", 2), ("gz", 1), ("gy", 3)), RIM, wide)
    anchor_z = index_z * depth_len
    anchor_y = index_y * cols_len
    anchor_x = index_x * rows_len
    bounds = jnp.stack(
        [
            RIM - anchor_z,
            depth_len * size_z + RIM - anchor_z,
            RIM - anchor_x,
            rows_len * size_x + RIM - anchor_x,
            RIM - anchor_y,
            cols_len * size_y + RIM - anchor_y,
        ]
    ).astype(jnp.int32)
    upscaled = upscale_windows(raw, facies_table, bounds, cols_len)
    fixed = accumulation * pressure_old + source
    ones = jnp.ones_like(pressure_old)
    bundle = jnp.stack([upscaled[0], upscaled[1], upscaled[2], pressure_old, ones])
    sides = (("gx", 2), ("gy", 3), ("gz", 1))
    dim_of = (2, 3, 1)
    views = neighbour_views(bundle, faces(bundle, sides), dim_of)
    inside_views = [(below[4], above[4]) for below, above in views]
    perm_views = [(below[:3], above[:3]) for below, above in views]
    press_views = [(below[3], above[3]) for below, above in views]
    pressure = coarse_step(upscaled, perm_views, inside_views, press_views, accumulation, fixed)
    got = faces(pressure, (("gx", 1), ("gy", 2), ("gz", 0)))
    press_views = neighbour_views(pressure, got, (1, 2, 0))
    pressure = coarse_step(upscaled, perm_views, inside_views, press_views, accumulation, fixed)
    return (pressure, upscaled)


def solution(mesh):
    placed = (
        P(("real", "gz"), "gx", "gy"),
        P(("real", "gz"), "gx", "gy"),
        P(),
        P(("real", "gz"), "gx", "gy"),
        P(("real", "gz"), "gx", "gy"),
        P(("real", "gz"), "gx", "gy"),
    )
    return jax.shard_map(
        local,
        mesh=mesh,
        in_specs=placed,
        out_specs=(P(("real", "gz"), "gx", "gy"), P(None, ("real", "gz"), "gx", "gy")),
        check_vma=False,
    )
```

```python
import functools

import jax
import jax.numpy as jnp
from jax import lax
from jax.sharding import PartitionSpec as P
from jax.experimental import pallas as pl
from jax.experimental.pallas import tpu as pltpu

NFAC = 4
CCX = 32
CCY = 32
CCZ = 8
RIM = 4
SWEEPS = 3


BOUND_MID = 1.0
BOUND_HALF = 0.9


def extended(cells, sides, width, lanes=None):
    for axis, dim in sides:
        count = lax.axis_size(axis)
        ends = count - 1
        head = lax.slice_in_dim(cells, 0, width, axis=dim)
        tail = lax.slice_in_dim(cells, cells.shape[dim] - width, cells.shape[dim], axis=dim)
        both = jnp.concatenate([tail, head], axis=dim)

        def lower_half(values):
            return lax.slice_in_dim(values, 0, width, axis=dim)

        def upper_half(values):
            return lax.slice_in_dim(values, width, 2 * width, axis=dim)

        if count == 2:
            got = lax.ppermute(both, axis, [(0, 1), (1, 0)])
            below = lower_half(got)
            above = upper_half(got)
        elif count % 2 == 0:
            even = lax.axis_index(axis) % 2 == 0
            first = [(i, i ^ 1) for i in range(count)]
            second = [(i, i + 1 if i % 2 else i - 1) for i in range(1, count - 1)]
            got_first = lax.ppermute(both, axis, first)
            got_second = lax.ppermute(both, axis, second)
            below = jnp.where(even, lower_half(got_second), lower_half(got_first))
            above = jnp.where(even, upper_half(got_first), upper_half(got_second))
        else:
            below = lax.ppermute(tail, axis, [(i, (i + 1) % count) for i in range(ends)])
            above = lax.ppermute(head, axis, [((i + 1) % count, i) for i in range(ends)])
        if lanes is not None and dim == cells.ndim - 1:
            extra = lanes - (cells.shape[dim] + 2 * width)
            parts = [cells, above, jnp.zeros(cells.shape[:-1] + (extra,), cells.dtype), below]
        else:
            parts = [below, cells, above]
        cells = jnp.concatenate(parts, axis=dim)
    return cells


def doubling_gather(values, axis, dim):
    count = lax.axis_size(axis)
    if count & (count - 1):
        return lax.all_gather(values, axis, axis=dim, tiled=True)
    index = lax.axis_index(axis)
    step = 1
    while step < count:
        got = lax.ppermute(values, axis, [(i, i ^ step) for i in range(count)])
        lower = (index // step) % 2 == 0
        values = jnp.where(
            lower, jnp.concatenate([values, got], axis=dim), jnp.concatenate([got, values], axis=dim)
        )
        step *= 2
    return values


def raise_flat(values, offset):
    zeros_block = jnp.zeros(values.shape[:-1] + (offset,), values.dtype)
    return jnp.concatenate([values[..., offset:], zeros_block], axis=-1)


def lower_flat(values, offset):
    zeros_block = jnp.zeros(values.shape[:-1] + (offset,), values.dtype)
    return jnp.concatenate([zeros_block, values[..., :-offset]], axis=-1)


def raise_depth(values):
    zeros_block = jnp.zeros(values.shape[:1] + (1,) + values.shape[2:], values.dtype)
    return jnp.concatenate([values[:, 1:], zeros_block], axis=1)


def lower_depth(values):
    zeros_block = jnp.zeros(values.shape[:1] + (1,) + values.shape[2:], values.dtype)
    return jnp.concatenate([zeros_block, values[:, :-1]], axis=1)


def log_fields(log_noise, facies, facies_table):
    base_log = log_noise
    extra_y = jnp.zeros_like(log_noise)
    extra_z = jnp.zeros_like(log_noise)
    for code_value in range(NFAC):
        matched = facies == code_value
        base_log = base_log + jnp.where(matched, facies_table[0, code_value], jnp.float32(0.0))
        extra_y = extra_y + jnp.where(matched, facies_table[1, code_value], jnp.float32(0.0))
        extra_z = extra_z + jnp.where(matched, facies_table[2, code_value], jnp.float32(0.0))
    return (base_log, base_log + extra_y, base_log + extra_z)


def upscale(perm_logs, inside):
    span_z = CCZ + 2 * RIM
    span_x = CCX + 2 * RIM
    span_y = CCY + 2 * RIM
    depth_pos = lax.broadcasted_iota(jnp.int32, (1, span_z, 1), 1)
    flat_pos = lax.broadcasted_iota(jnp.int32, (1, 1, span_x * span_y), 2)
    column_pos = flat_pos // span_y
    row_pos = flat_pos % span_y
    perm_x = jnp.exp(perm_logs[0])
    perm_y = jnp.exp(perm_logs[1])
    perm_z = jnp.exp(perm_logs[2])

    def links(perm, other_perm, other_inside):
        return inside * other_inside * 2.0 * perm * other_perm / (perm + other_perm)

    link_x = links(perm_x, raise_flat(perm_x, span_y), raise_flat(inside, span_y))
    link_y = links(perm_y, raise_flat(perm_y, 1), raise_flat(inside, 1)) * (
        row_pos < span_y - 1
    ).astype(jnp.float32)
    link_z = links(perm_z, raise_depth(perm_z), raise_depth(inside))
    diagonal = (
        link_x
        + lower_flat(link_x, span_y)
        + link_y
        + lower_flat(link_y, 1)
        + link_z
        + lower_depth(link_z)
    )

    def apply_operator(field):
        beside = link_x * raise_flat(field, span_y) + lower_flat(link_x * field, span_y)
        beside = beside + link_y * raise_flat(field, 1) + lower_flat(link_y * field, 1)
        beside = beside + link_z * raise_depth(field) + lower_depth(link_z * field)
        return diagonal * field - beside

    interior = (
        (depth_pos >= 1)
        & (depth_pos <= span_z - 2)
        & (column_pos >= 1)
        & (column_pos <= span_x - 2)
        & (row_pos >= 1)
        & (row_pos <= span_y - 2)
    )
    unknown = inside * interior.astype(jnp.float32)
    scaling = unknown / (diagonal + 1.0 - unknown)
    core_z = (depth_pos >= RIM) & (depth_pos < RIM + CCZ)
    core_x = (column_pos >= RIM) & (column_pos < RIM + CCX)
    core_y = (row_pos >= RIM) & (row_pos < RIM + CCY)
    face_x = (((column_pos == RIM - 1) | (column_pos == RIM + CCX - 1)) & core_z & core_y).astype(
        jnp.float32
    )
    face_y = (((row_pos == RIM - 1) | (row_pos == RIM + CCY - 1)) & core_z & core_x).astype(
        jnp.float32
    )
    face_z = (((depth_pos == RIM - 1) | (depth_pos == RIM + CCZ - 1)) & core_x & core_y).astype(
        jnp.float32
    )
    ramp_x = ((span_x - 1) / 2.0 - column_pos).astype(jnp.float32)
    ramp_y = ((span_y - 1) / 2.0 - row_pos).astype(jnp.float32)
    ramp_z = ((span_z - 1) / 2.0 - depth_pos).astype(jnp.float32)
    cheb_ratio = BOUND_MID / BOUND_HALF
    results = []
    cases = (
        (ramp_x, link_x, face_x, CCY * CCZ, 0),
        (ramp_y, link_y, face_y, CCX * CCZ, 1),
        (ramp_z, link_z, face_z, CCX * CCY, 2),
    )
    for ramp, link, face, area, direction in cases:
        ramp_full = jnp.broadcast_to(ramp, inside.shape)
        source_term = -unknown * apply_operator(ramp_full)
        update = scaling * source_term / BOUND_MID
        solution = update
        rho_old = 1.0 / cheb_ratio
        for sweep_index in range(SWEEPS - 1):
            residual = source_term - apply_operator(solution)
            rho_new = 1.0 / (2.0 * cheb_ratio - rho_old)
            update = rho_new * rho_old * update + 2.0 * rho_new / BOUND_HALF * (scaling * residual)
            solution = solution + update
            rho_old = rho_new
        pressure = ramp_full + solution
        if direction == 0:
            upper = raise_flat(pressure, span_y)
        elif direction == 1:
            upper = raise_flat(pressure, 1)
        else:
            upper = raise_depth(pressure)
        flux = link * (pressure - upper) * face
        results.append(jnp.sum(flux, axis=(1, 2)) * (0.5 / area))
    return jnp.stack(results)


LANES = 128


def window_kernel(table_ref, bounds_ref, raw_ref, o_ref, *, count_x, count_y, count):
    span_z = CCZ + 2 * RIM
    span_x = CCX + 2 * RIM
    span_y = CCY + 2 * RIM
    segments = LANES // span_y
    shape = (span_z, span_x, LANES)
    pack = pl.program_id(0)
    wide = raw_ref.shape[-1]
    depth_pos = lax.broadcasted_iota(jnp.int32, shape, 0)
    column_pos = lax.broadcasted_iota(jnp.int32, shape, 1)
    lane = lax.broadcasted_iota(jnp.int32, shape, 2)
    segment = jnp.zeros(shape, jnp.int32)
    for bound in range(1, segments + 1):
        segment = segment + (lane >= bound * span_y).astype(jnp.int32)
    row_pos = lane - span_y * segment
    noise = jnp.zeros(shape, jnp.float32)
    codes = jnp.zeros(shape, jnp.float32)
    inside = jnp.zeros(shape, jnp.float32)
    for slot in range(segments):
        window = pack * segments + slot
        valid = window < count
        window = jnp.minimum(window, count - 1)
        block_z = window // (count_x * count_y)
        block_x = (window // count_y) % count_x
        block_y = window % count_y
        shift = (slot * span_y - block_y * CCY + RIM + wide) % wide
        here = segment == slot

        def cut(field):
            slab = raw_ref[field, pl.ds(block_z * CCZ, span_z), pl.ds(block_x * CCX, span_x), :]
            return pltpu.roll(slab, shift, 2)[:, :, :LANES]

        depth_at = depth_pos + block_z * CCZ
        column_at = column_pos + block_x * CCX
        row_at = row_pos + block_y * CCY
        held = (
            (depth_at >= bounds_ref[0])
            & (depth_at < bounds_ref[1])
            & (column_at >= bounds_ref[2])
            & (column_at < bounds_ref[3])
            & (row_at >= bounds_ref[4])
            & (row_at < bounds_ref[5])
        )
        noise = jnp.where(here, cut(0), noise)
        codes = jnp.where(here, cut(1), codes)
        inside = jnp.where(here & valid & held, 1.0, inside)

    def lookup(row):
        value = jnp.zeros(shape, jnp.float32)
        for code_value in range(NFAC):
            value = jnp.where(codes == code_value, table_ref[row, code_value], value)
        return value

    log_x = noise + lookup(0)
    log_y = log_x + lookup(1)
    log_z = log_x + lookup(2)
    perm_x = jnp.exp(log_x)
    perm_y = jnp.exp(log_y)
    perm_z = jnp.exp(log_z)

    def up_x(v):
        return pltpu.roll(v, span_x - 1, 1)

    def down_x(v):
        return pltpu.roll(v, 1, 1)

    def up_y(v):
        return pltpu.roll(v, LANES - 1, 2)

    def down_y(v):
        return pltpu.roll(v, 1, 2)

    def up_z(v):
        return jnp.concatenate([v[1:], v[:1]], axis=0)

    def down_z(v):
        return jnp.concatenate([v[-1:], v[:-1]], axis=0)

    def links(perm, other_perm, other_inside, valid):
        value = inside * other_inside * 2.0 * perm * other_perm / (perm + other_perm)
        return jnp.where(valid, value, 0.0)

    link_x = links(perm_x, up_x(perm_x), up_x(inside), column_pos < span_x - 1)
    link_y = links(perm_y, up_y(perm_y), up_y(inside), row_pos < span_y - 1)
    link_z = links(perm_z, up_z(perm_z), up_z(inside), depth_pos < span_z - 1)
    diagonal = link_x + down_x(link_x) + link_y + down_y(link_y) + link_z + down_z(link_z)

    def apply_operator(field):
        beside = link_x * up_x(field) + down_x(link_x * field)
        beside = beside + link_y * up_y(field) + down_y(link_y * field)
        beside = beside + link_z * up_z(field) + down_z(link_z * field)
        return diagonal * field - beside

    interior = (
        (depth_pos >= 1)
        & (depth_pos <= span_z - 2)
        & (column_pos >= 1)
        & (column_pos <= span_x - 2)
        & (row_pos >= 1)
        & (row_pos <= span_y - 2)
    )
    unknown = jnp.where(interior, inside, 0.0)
    scaling = unknown / (diagonal + 1.0 - unknown)
    core_z = (depth_pos >= RIM) & (depth_pos < RIM + CCZ)
    core_x = (column_pos >= RIM) & (column_pos < RIM + CCX)
    core_y = (row_pos >= RIM) & (row_pos < RIM + CCY)
    face_x = ((column_pos == RIM - 1) | (column_pos == RIM + CCX - 1)) & core_z & core_y
    face_y = ((row_pos == RIM - 1) | (row_pos == RIM + CCY - 1)) & core_z & core_x
    face_z = ((depth_pos == RIM - 1) | (depth_pos == RIM + CCZ - 1)) & core_x & core_y
    ramp_x = ((span_x - 1) / 2.0 - column_pos).astype(jnp.float32)
    ramp_y = ((span_y - 1) / 2.0 - row_pos).astype(jnp.float32)
    ramp_z = ((span_z - 1) / 2.0 - depth_pos).astype(jnp.float32)
    cheb_ratio = BOUND_MID / BOUND_HALF
    cases = (
        (ramp_x, link_x, face_x, CCY * CCZ, up_x, down_x),
        (ramp_y, link_y, face_y, CCX * CCZ, up_y, down_y),
        (ramp_z, link_z, face_z, CCX * CCY, up_z, down_z),
    )
    rows = []
    for ramp, link, face, area, upper_of, lower_of in cases:
        source_term = -unknown * (link - lower_of(link))
        update = scaling * source_term / BOUND_MID
        solution = update
        rho_old = 1.0 / cheb_ratio
        for sweep_index in range(SWEEPS - 1):
            residual = source_term - apply_operator(solution)
            rho_new = 1.0 / (2.0 * cheb_ratio - rho_old)
            update = rho_new * rho_old * update + 2.0 * rho_new / BOUND_HALF * (scaling * residual)
            solution = solution + update
            rho_old = rho_new
        pressure = ramp + solution
        flux = jnp.where(face, link * (pressure - upper_of(pressure)), 0.0)
        total = jnp.sum(flux, axis=0)
        total = jnp.sum(total, axis=0, keepdims=True)
        rows.append(total * (0.5 / area))
    rows.append(jnp.zeros((8 - len(rows), LANES), jnp.float32))
    o_ref[0] = jnp.concatenate(rows, axis=0)


def upscale_windows(raw, facies_table, bounds, cols_len):
    span_y = CCY + 2 * RIM
    count_z = (raw.shape[1] - 2 * RIM) // CCZ
    count_x = (raw.shape[2] - 2 * RIM) // CCX
    count_y = cols_len // CCY
    count = count_z * count_x * count_y
    segments = LANES // span_y
    packs = -(-count // segments)
    kernel = functools.partial(window_kernel, count_x=count_x, count_y=count_y, count=count)
    sums = pl.pallas_call(
        kernel,
        grid=(packs,),
        in_specs=[
            pl.BlockSpec(memory_space=pltpu.SMEM),
            pl.BlockSpec(memory_space=pltpu.SMEM),
            pl.BlockSpec(raw.shape, lambda p: (0, 0, 0, 0)),
        ],
        out_specs=pl.BlockSpec((1, 8, LANES), lambda p: (p, 0, 0)),
        out_shape=jax.ShapeDtypeStruct((packs, 8, LANES), jnp.float32),
    )(facies_table, bounds, raw)
    sums = sums[:, :3, : segments * span_y].reshape(packs, 3, segments, span_y).sum(axis=3)
    sums = sums.transpose(1, 0, 2).reshape(3, packs * segments)[:, :count]
    return sums.reshape((3, count_z, count_x, count_y))


def coarse_sweep(perm_pad, press_pad, inside_pad, accumulation, fixed):
    centre = (slice(1, -1), slice(1, -1), slice(1, -1))
    factors = (CCY * CCZ / CCX, CCX * CCZ / CCY, CCX * CCY / CCZ)
    numer = fixed
    denom = accumulation
    for component, axis_dim in ((0, 1), (1, 2), (2, 0)):
        for offset in (-1, 1):
            window_slice = [slice(1, -1), slice(1, -1), slice(1, -1)]
            window_slice[axis_dim] = slice(1 + offset, press_pad.shape[axis_dim] - 1 + offset)
            beside = tuple(window_slice)
            link = (
                factors[component]
                * 0.5
                * (perm_pad[component][centre] + perm_pad[component][beside])
                * inside_pad[beside]
            )
            numer = numer + link * press_pad[beside]
            denom = denom + jnp.abs(link)
    return numer / denom


def span_mask(anchor, length, total, margin):
    coords = anchor - margin + jnp.arange(length + 2 * margin, dtype=jnp.int32)
    return ((coords >= 0) & (coords < total)).astype(jnp.float32)


def cut_windows(fields):
    span_z = CCZ + 2 * RIM
    span_x = CCX + 2 * RIM
    span_y = CCY + 2 * RIM
    count_z = (fields[0].shape[0] - 2 * RIM) // CCZ
    count_x = (fields[0].shape[1] - 2 * RIM) // CCX
    count_y = (fields[0].shape[2] - 2 * RIM) // CCY
    stacks = []
    for field in fields:
        pieces = []
        for block_z in range(count_z):
            for block_y in range(count_y):
                piece = field[
                    block_z * CCZ : block_z * CCZ + span_z,
                    0:span_x,
                    block_y * CCY : block_y * CCY + span_y,
                ]
                pieces.append(piece.reshape(span_z, span_x * span_y))
        stacks.append(jnp.stack(pieces))
    return (stacks, (count_z, count_x, count_y))


def faces(block, sides):
    got = []
    for axis, dim in sides:
        count = lax.axis_size(axis)
        ends = count - 1
        head = lax.slice_in_dim(block, 0, 1, axis=dim)
        tail = lax.slice_in_dim(block, block.shape[dim] - 1, block.shape[dim], axis=dim)
        lower = lax.ppermute(tail, axis, [(i, i + 1) for i in range(ends)])
        upper = lax.ppermute(head, axis, [(i + 1, i) for i in range(ends)])
        got.append((lower, upper))
    return got


def neighbour_views(block, got, dim_of):
    views = []
    for (lower, upper), dim in zip(got, dim_of):
        size = block.shape[dim]
        below = jnp.concatenate([lower, lax.slice_in_dim(block, 0, size - 1, axis=dim)], axis=dim)
        above = jnp.concatenate([lax.slice_in_dim(block, 1, size, axis=dim), upper], axis=dim)
        views.append((below, above))
    return views


def coarse_step(upscaled, views, inside_views, pressure, accumulation, fixed):
    factors = (CCY * CCZ / CCX, CCX * CCZ / CCY, CCX * CCY / CCZ)
    numer = fixed
    denom = accumulation
    for component in range(3):
        for side in range(2):
            beside = views[component][side]
            link = factors[component] * 0.5 * (upscaled[component] + beside[component]) * inside_views[component][side]
            numer = numer + link * pressure[component][side]
            denom = denom + jnp.abs(link)
    return numer / denom


def local(log_noise, facies, facies_table, pressure_old, accumulation, source):
    depth_len, rows_len, cols_len = log_noise.shape
    size_z = lax.axis_size("gz")
    size_x = lax.axis_size("gx")
    size_y = lax.axis_size("gy")
    index_z = lax.axis_index("gz")
    index_x = lax.axis_index("gx")
    index_y = lax.axis_index("gy")
    raw = jnp.stack([log_noise, facies.astype(jnp.float32)])
    wide = -(-(cols_len + 2 * RIM) // LANES) * LANES
    raw = extended(raw, (("gx", 2), ("gz", 1), ("gy", 3)), RIM, wide)
    anchor_z = index_z * depth_len
    anchor_y = index_y * cols_len
    anchor_x = index_x * rows_len
    bounds = jnp.stack(
        [
            RIM - anchor_z,
            depth_len * size_z + RIM - anchor_z,
            RIM - anchor_x,
            rows_len * size_x + RIM - anchor_x,
            RIM - anchor_y,
            cols_len * size_y + RIM - anchor_y,
        ]
    ).astype(jnp.int32)
    upscaled = upscale_windows(raw, facies_table, bounds, cols_len)
    coarse_z, coarse_x, coarse_y = pressure_old.shape
    bundle = jnp.stack([upscaled[0], upscaled[1], upscaled[2], pressure_old, accumulation, source])
    every = doubling_gather(bundle, "gy", 3)
    every = doubling_gather(every, "gx", 2)
    every = doubling_gather(every, "gz", 1)
    perm_pad = jnp.pad(every[:3], ((0, 0), (1, 1), (1, 1), (1, 1)))
    old_all = every[3]
    acc_all = every[4]
    fixed_all = acc_all * old_all + every[5]
    inside_pad = jnp.pad(jnp.ones(old_all.shape, jnp.float32), 1)
    pressure = old_all
    for sweep_index in range(2):
        pressure = coarse_sweep(perm_pad, jnp.pad(pressure, 1), inside_pad, acc_all, fixed_all)
    pressure = lax.dynamic_slice(
        pressure, (index_z * coarse_z, index_x * coarse_x, index_y * coarse_y), (coarse_z, coarse_x, coarse_y)
    )
    return (pressure, upscaled)


def solution(mesh):
    placed = (
        P(("real", "gz"), "gx", "gy"),
        P(("real", "gz"), "gx", "gy"),
        P(),
        P(("real", "gz"), "gx", "gy"),
        P(("real", "gz"), "gx", "gy"),
        P(("real", "gz"), "gx", "gy"),
    )
    return jax.shard_map(
        local,
        mesh=mesh,
        in_specs=placed,
        out_specs=(P(("real", "gz"), "gx", "gy"), P(None, ("real", "gz"), "gx", "gy")),
        check_vma=False,
    )
```

```python
import functools

import jax
import jax.numpy as jnp
from jax import lax
from jax.sharding import PartitionSpec as P
from jax.experimental import pallas as pl
from jax.experimental.pallas import tpu as pltpu

NFAC = 4
CCX = 32
CCY = 32
CCZ = 8
RIM = 4
SWEEPS = 3


BOUND_MID = 1.0
BOUND_HALF = 0.9


def extended(cells, sides, width, lanes=None):
    for axis, dim in sides:
        count = lax.axis_size(axis)
        ends = count - 1
        head = lax.slice_in_dim(cells, 0, width, axis=dim)
        tail = lax.slice_in_dim(cells, cells.shape[dim] - width, cells.shape[dim], axis=dim)
        if count == 2:
            lower_side = lax.axis_index(axis) == 0
            got = lax.ppermute(jnp.where(lower_side, tail, head), axis, [(0, 1), (1, 0)])
            below = got
            above = got
        elif count % 2 == 0:
            even = lax.axis_index(axis) % 2 == 0
            first = [(i, i ^ 1) for i in range(count)]
            second = [(i, i + 1 if i % 2 else i - 1) for i in range(1, count - 1)]
            got_first = lax.ppermute(jnp.where(even, tail, head), axis, first)
            got_second = lax.ppermute(jnp.where(even, head, tail), axis, second)
            below = jnp.where(even, got_second, got_first)
            above = jnp.where(even, got_first, got_second)
        else:
            below = lax.ppermute(tail, axis, [(i, (i + 1) % count) for i in range(ends)])
            above = lax.ppermute(head, axis, [((i + 1) % count, i) for i in range(ends)])
        if lanes is not None and dim == cells.ndim - 1:
            extra = lanes - (cells.shape[dim] + 2 * width)
            parts = [cells, above, jnp.zeros(cells.shape[:-1] + (extra,), cells.dtype), below]
        else:
            parts = [below, cells, above]
        cells = jnp.concatenate(parts, axis=dim)
    return cells


def doubling_gather(values, axis, dim):
    count = lax.axis_size(axis)
    if count & (count - 1):
        return lax.all_gather(values, axis, axis=dim, tiled=True)
    index = lax.axis_index(axis)
    step = 1
    while step < count:
        got = lax.ppermute(values, axis, [(i, i ^ step) for i in range(count)])
        lower = (index // step) % 2 == 0
        values = jnp.where(
            lower, jnp.concatenate([values, got], axis=dim), jnp.concatenate([got, values], axis=dim)
        )
        step *= 2
    return values


def raise_flat(values, offset):
    zeros_block = jnp.zeros(values.shape[:-1] + (offset,), values.dtype)
    return jnp.concatenate([values[..., offset:], zeros_block], axis=-1)


def lower_flat(values, offset):
    zeros_block = jnp.zeros(values.shape[:-1] + (offset,), values.dtype)
    return jnp.concatenate([zeros_block, values[..., :-offset]], axis=-1)


def raise_depth(values):
    zeros_block = jnp.zeros(values.shape[:1] + (1,) + values.shape[2:], values.dtype)
    return jnp.concatenate([values[:, 1:], zeros_block], axis=1)


def lower_depth(values):
    zeros_block = jnp.zeros(values.shape[:1] + (1,) + values.shape[2:], values.dtype)
    return jnp.concatenate([zeros_block, values[:, :-1]], axis=1)


def log_fields(log_noise, facies, facies_table):
    base_log = log_noise
    extra_y = jnp.zeros_like(log_noise)
    extra_z = jnp.zeros_like(log_noise)
    for code_value in range(NFAC):
        matched = facies == code_value
        base_log = base_log + jnp.where(matched, facies_table[0, code_value], jnp.float32(0.0))
        extra_y = extra_y + jnp.where(matched, facies_table[1, code_value], jnp.float32(0.0))
        extra_z = extra_z + jnp.where(matched, facies_table[2, code_value], jnp.float32(0.0))
    return (base_log, base_log + extra_y, base_log + extra_z)


def upscale(perm_logs, inside):
    span_z = CCZ + 2 * RIM
    span_x = CCX + 2 * RIM
    span_y = CCY + 2 * RIM
    depth_pos = lax.broadcasted_iota(jnp.int32, (1, span_z, 1), 1)
    flat_pos = lax.broadcasted_iota(jnp.int32, (1, 1, span_x * span_y), 2)
    column_pos = flat_pos // span_y
    row_pos = flat_pos % span_y
    perm_x = jnp.exp(perm_logs[0])
    perm_y = jnp.exp(perm_logs[1])
    perm_z = jnp.exp(perm_logs[2])

    def links(perm, other_perm, other_inside):
        return inside * other_inside * 2.0 * perm * other_perm / (perm + other_perm)

    link_x = links(perm_x, raise_flat(perm_x, span_y), raise_flat(inside, span_y))
    link_y = links(perm_y, raise_flat(perm_y, 1), raise_flat(inside, 1)) * (
        row_pos < span_y - 1
    ).astype(jnp.float32)
    link_z = links(perm_z, raise_depth(perm_z), raise_depth(inside))
    diagonal = (
        link_x
        + lower_flat(link_x, span_y)
        + link_y
        + lower_flat(link_y, 1)
        + link_z
        + lower_depth(link_z)
    )

    def apply_operator(field):
        beside = link_x * raise_flat(field, span_y) + lower_flat(link_x * field, span_y)
        beside = beside + link_y * raise_flat(field, 1) + lower_flat(link_y * field, 1)
        beside = beside + link_z * raise_depth(field) + lower_depth(link_z * field)
        return diagonal * field - beside

    interior = (
        (depth_pos >= 1)
        & (depth_pos <= span_z - 2)
        & (column_pos >= 1)
        & (column_pos <= span_x - 2)
        & (row_pos >= 1)
        & (row_pos <= span_y - 2)
    )
    unknown = inside * interior.astype(jnp.float32)
    scaling = unknown / (diagonal + 1.0 - unknown)
    core_z = (depth_pos >= RIM) & (depth_pos < RIM + CCZ)
    core_x = (column_pos >= RIM) & (column_pos < RIM + CCX)
    core_y = (row_pos >= RIM) & (row_pos < RIM + CCY)
    face_x = (((column_pos == RIM - 1) | (column_pos == RIM + CCX - 1)) & core_z & core_y).astype(
        jnp.float32
    )
    face_y = (((row_pos == RIM - 1) | (row_pos == RIM + CCY - 1)) & core_z & core_x).astype(
        jnp.float32
    )
    face_z = (((depth_pos == RIM - 1) | (depth_pos == RIM + CCZ - 1)) & core_x & core_y).astype(
        jnp.float32
    )
    ramp_x = ((span_x - 1) / 2.0 - column_pos).astype(jnp.float32)
    ramp_y = ((span_y - 1) / 2.0 - row_pos).astype(jnp.float32)
    ramp_z = ((span_z - 1) / 2.0 - depth_pos).astype(jnp.float32)
    cheb_ratio = BOUND_MID / BOUND_HALF
    results = []
    cases = (
        (ramp_x, link_x, face_x, CCY * CCZ, 0),
        (ramp_y, link_y, face_y, CCX * CCZ, 1),
        (ramp_z, link_z, face_z, CCX * CCY, 2),
    )
    for ramp, link, face, area, direction in cases:
        ramp_full = jnp.broadcast_to(ramp, inside.shape)
        source_term = -unknown * apply_operator(ramp_full)
        update = scaling * source_term / BOUND_MID
        solution = update
        rho_old = 1.0 / cheb_ratio
        for sweep_index in range(SWEEPS - 1):
            residual = source_term - apply_operator(solution)
            rho_new = 1.0 / (2.0 * cheb_ratio - rho_old)
            update = rho_new * rho_old * update + 2.0 * rho_new / BOUND_HALF * (scaling * residual)
            solution = solution + update
            rho_old = rho_new
        pressure = ramp_full + solution
        if direction == 0:
            upper = raise_flat(pressure, span_y)
        elif direction == 1:
            upper = raise_flat(pressure, 1)
        else:
            upper = raise_depth(pressure)
        flux = link * (pressure - upper) * face
        results.append(jnp.sum(flux, axis=(1, 2)) * (0.5 / area))
    return jnp.stack(results)


LANES = 128


def window_kernel(table_ref, bounds_ref, raw_ref, o_ref, *, count_x, count_y, count):
    span_z = CCZ + 2 * RIM
    span_x = CCX + 2 * RIM
    span_y = CCY + 2 * RIM
    segments = LANES // span_y
    shape = (span_z, span_x, LANES)
    pack = pl.program_id(0)
    wide = raw_ref.shape[-1]
    depth_pos = lax.broadcasted_iota(jnp.int32, shape, 0)
    column_pos = lax.broadcasted_iota(jnp.int32, shape, 1)
    lane = lax.broadcasted_iota(jnp.int32, shape, 2)
    segment = jnp.zeros(shape, jnp.int32)
    for bound in range(1, segments + 1):
        segment = segment + (lane >= bound * span_y).astype(jnp.int32)
    row_pos = lane - span_y * segment
    noise = jnp.zeros(shape, jnp.float32)
    codes = jnp.zeros(shape, jnp.float32)
    inside = jnp.zeros(shape, jnp.float32)
    for slot in range(segments):
        window = pack * segments + slot
        valid = window < count
        window = jnp.minimum(window, count - 1)
        block_z = window // (count_x * count_y)
        block_x = (window // count_y) % count_x
        block_y = window % count_y
        shift = (slot * span_y - block_y * CCY + RIM + wide) % wide
        here = segment == slot

        def cut(field):
            slab = raw_ref[field, pl.ds(block_z * CCZ, span_z), pl.ds(block_x * CCX, span_x), :]
            return pltpu.roll(slab, shift, 2)[:, :, :LANES]

        depth_at = depth_pos + block_z * CCZ
        column_at = column_pos + block_x * CCX
        row_at = row_pos + block_y * CCY
        held = (
            (depth_at >= bounds_ref[0])
            & (depth_at < bounds_ref[1])
            & (column_at >= bounds_ref[2])
            & (column_at < bounds_ref[3])
            & (row_at >= bounds_ref[4])
            & (row_at < bounds_ref[5])
        )
        noise = jnp.where(here, cut(0), noise)
        codes = jnp.where(here, cut(1), codes)
        inside = jnp.where(here & valid & held, 1.0, inside)

    def lookup(row):
        value = jnp.zeros(shape, jnp.float32)
        for code_value in range(NFAC):
            value = jnp.where(codes == code_value, table_ref[row, code_value], value)
        return value

    log_x = noise + lookup(0)
    log_y = log_x + lookup(1)
    log_z = log_x + lookup(2)
    perm_x = jnp.exp(log_x)
    perm_y = jnp.exp(log_y)
    perm_z = jnp.exp(log_z)

    def up_x(v):
        return pltpu.roll(v, span_x - 1, 1)

    def down_x(v):
        return pltpu.roll(v, 1, 1)

    def up_y(v):
        return pltpu.roll(v, LANES - 1, 2)

    def down_y(v):
        return pltpu.roll(v, 1, 2)

    def up_z(v):
        return jnp.concatenate([v[1:], v[:1]], axis=0)

    def down_z(v):
        return jnp.concatenate([v[-1:], v[:-1]], axis=0)

    def links(perm, other_perm, other_inside, valid):
        value = inside * other_inside * 2.0 * perm * other_perm / (perm + other_perm)
        return jnp.where(valid, value, 0.0)

    link_x = links(perm_x, up_x(perm_x), up_x(inside), column_pos < span_x - 1)
    link_y = links(perm_y, up_y(perm_y), up_y(inside), row_pos < span_y - 1)
    link_z = links(perm_z, up_z(perm_z), up_z(inside), depth_pos < span_z - 1)
    diagonal = link_x + down_x(link_x) + link_y + down_y(link_y) + link_z + down_z(link_z)

    def apply_operator(field):
        beside = link_x * up_x(field) + down_x(link_x * field)
        beside = beside + link_y * up_y(field) + down_y(link_y * field)
        beside = beside + link_z * up_z(field) + down_z(link_z * field)
        return diagonal * field - beside

    interior = (
        (depth_pos >= 1)
        & (depth_pos <= span_z - 2)
        & (column_pos >= 1)
        & (column_pos <= span_x - 2)
        & (row_pos >= 1)
        & (row_pos <= span_y - 2)
    )
    unknown = jnp.where(interior, inside, 0.0)
    scaling = unknown / (diagonal + 1.0 - unknown)
    core_z = (depth_pos >= RIM) & (depth_pos < RIM + CCZ)
    core_x = (column_pos >= RIM) & (column_pos < RIM + CCX)
    core_y = (row_pos >= RIM) & (row_pos < RIM + CCY)
    face_x = ((column_pos == RIM - 1) | (column_pos == RIM + CCX - 1)) & core_z & core_y
    face_y = ((row_pos == RIM - 1) | (row_pos == RIM + CCY - 1)) & core_z & core_x
    face_z = ((depth_pos == RIM - 1) | (depth_pos == RIM + CCZ - 1)) & core_x & core_y
    ramp_x = ((span_x - 1) / 2.0 - column_pos).astype(jnp.float32)
    ramp_y = ((span_y - 1) / 2.0 - row_pos).astype(jnp.float32)
    ramp_z = ((span_z - 1) / 2.0 - depth_pos).astype(jnp.float32)
    cheb_ratio = BOUND_MID / BOUND_HALF
    cases = (
        (ramp_x, link_x, face_x, CCY * CCZ, up_x, down_x),
        (ramp_y, link_y, face_y, CCX * CCZ, up_y, down_y),
        (ramp_z, link_z, face_z, CCX * CCY, up_z, down_z),
    )
    rows = []
    for ramp, link, face, area, upper_of, lower_of in cases:
        source_term = -unknown * (link - lower_of(link))
        update = scaling * source_term / BOUND_MID
        solution = update
        rho_old = 1.0 / cheb_ratio
        for sweep_index in range(SWEEPS - 1):
            residual = source_term - apply_operator(solution)
            rho_new = 1.0 / (2.0 * cheb_ratio - rho_old)
            update = rho_new * rho_old * update + 2.0 * rho_new / BOUND_HALF * (scaling * residual)
            solution = solution + update
            rho_old = rho_new
        pressure = ramp + solution
        flux = jnp.where(face, link * (pressure - upper_of(pressure)), 0.0)
        total = jnp.sum(flux, axis=0)
        total = jnp.sum(total, axis=0, keepdims=True)
        rows.append(total * (0.5 / area))
    rows.append(jnp.zeros((8 - len(rows), LANES), jnp.float32))
    o_ref[0] = jnp.concatenate(rows, axis=0)


def upscale_windows(raw, facies_table, bounds, cols_len):
    span_y = CCY + 2 * RIM
    count_z = (raw.shape[1] - 2 * RIM) // CCZ
    count_x = (raw.shape[2] - 2 * RIM) // CCX
    count_y = cols_len // CCY
    count = count_z * count_x * count_y
    segments = LANES // span_y
    packs = -(-count // segments)
    kernel = functools.partial(window_kernel, count_x=count_x, count_y=count_y, count=count)
    sums = pl.pallas_call(
        kernel,
        grid=(packs,),
        in_specs=[
            pl.BlockSpec(memory_space=pltpu.SMEM),
            pl.BlockSpec(memory_space=pltpu.SMEM),
            pl.BlockSpec(raw.shape, lambda p: (0, 0, 0, 0)),
        ],
        out_specs=pl.BlockSpec((1, 8, LANES), lambda p: (p, 0, 0)),
        out_shape=jax.ShapeDtypeStruct((packs, 8, LANES), jnp.float32),
    )(facies_table, bounds, raw)
    sums = sums[:, :3, : segments * span_y].reshape(packs, 3, segments, span_y).sum(axis=3)
    sums = sums.transpose(1, 0, 2).reshape(3, packs * segments)[:, :count]
    return sums.reshape((3, count_z, count_x, count_y))


def coarse_sweep(perm_pad, press_pad, inside_pad, accumulation, fixed):
    centre = (slice(1, -1), slice(1, -1), slice(1, -1))
    factors = (CCY * CCZ / CCX, CCX * CCZ / CCY, CCX * CCY / CCZ)
    numer = fixed
    denom = accumulation
    for component, axis_dim in ((0, 1), (1, 2), (2, 0)):
        for offset in (-1, 1):
            window_slice = [slice(1, -1), slice(1, -1), slice(1, -1)]
            window_slice[axis_dim] = slice(1 + offset, press_pad.shape[axis_dim] - 1 + offset)
            beside = tuple(window_slice)
            link = (
                factors[component]
                * 0.5
                * (perm_pad[component][centre] + perm_pad[component][beside])
                * inside_pad[beside]
            )
            numer = numer + link * press_pad[beside]
            denom = denom + jnp.abs(link)
    return numer / denom


def span_mask(anchor, length, total, margin):
    coords = anchor - margin + jnp.arange(length + 2 * margin, dtype=jnp.int32)
    return ((coords >= 0) & (coords < total)).astype(jnp.float32)


def cut_windows(fields):
    span_z = CCZ + 2 * RIM
    span_x = CCX + 2 * RIM
    span_y = CCY + 2 * RIM
    count_z = (fields[0].shape[0] - 2 * RIM) // CCZ
    count_x = (fields[0].shape[1] - 2 * RIM) // CCX
    count_y = (fields[0].shape[2] - 2 * RIM) // CCY
    stacks = []
    for field in fields:
        pieces = []
        for block_z in range(count_z):
            for block_y in range(count_y):
                piece = field[
                    block_z * CCZ : block_z * CCZ + span_z,
                    0:span_x,
                    block_y * CCY : block_y * CCY + span_y,
                ]
                pieces.append(piece.reshape(span_z, span_x * span_y))
        stacks.append(jnp.stack(pieces))
    return (stacks, (count_z, count_x, count_y))


def faces(block, sides):
    got = []
    for axis, dim in sides:
        count = lax.axis_size(axis)
        ends = count - 1
        head = lax.slice_in_dim(block, 0, 1, axis=dim)
        tail = lax.slice_in_dim(block, block.shape[dim] - 1, block.shape[dim], axis=dim)
        lower = lax.ppermute(tail, axis, [(i, i + 1) for i in range(ends)])
        upper = lax.ppermute(head, axis, [(i + 1, i) for i in range(ends)])
        got.append((lower, upper))
    return got


def neighbour_views(block, got, dim_of):
    views = []
    for (lower, upper), dim in zip(got, dim_of):
        size = block.shape[dim]
        below = jnp.concatenate([lower, lax.slice_in_dim(block, 0, size - 1, axis=dim)], axis=dim)
        above = jnp.concatenate([lax.slice_in_dim(block, 1, size, axis=dim), upper], axis=dim)
        views.append((below, above))
    return views


def coarse_step(upscaled, views, inside_views, pressure, accumulation, fixed):
    factors = (CCY * CCZ / CCX, CCX * CCZ / CCY, CCX * CCY / CCZ)
    numer = fixed
    denom = accumulation
    for component in range(3):
        for side in range(2):
            beside = views[component][side]
            link = factors[component] * 0.5 * (upscaled[component] + beside[component]) * inside_views[component][side]
            numer = numer + link * pressure[component][side]
            denom = denom + jnp.abs(link)
    return numer / denom


def local(log_noise, facies, facies_table, pressure_old, accumulation, source):
    depth_len, rows_len, cols_len = log_noise.shape
    size_z = lax.axis_size("gz")
    size_x = lax.axis_size("gx")
    size_y = lax.axis_size("gy")
    index_z = lax.axis_index("gz")
    index_x = lax.axis_index("gx")
    index_y = lax.axis_index("gy")
    raw = jnp.stack([log_noise, facies.astype(jnp.float32)])
    wide = -(-(cols_len + 2 * RIM) // LANES) * LANES
    raw = extended(raw, (("gx", 2), ("gz", 1), ("gy", 3)), RIM, wide)
    anchor_z = index_z * depth_len
    anchor_y = index_y * cols_len
    anchor_x = index_x * rows_len
    bounds = jnp.stack(
        [
            RIM - anchor_z,
            depth_len * size_z + RIM - anchor_z,
            RIM - anchor_x,
            rows_len * size_x + RIM - anchor_x,
            RIM - anchor_y,
            cols_len * size_y + RIM - anchor_y,
        ]
    ).astype(jnp.int32)
    upscaled = upscale_windows(raw, facies_table, bounds, cols_len)
    coarse_z, coarse_x, coarse_y = pressure_old.shape
    bundle = jnp.stack([upscaled[0], upscaled[1], upscaled[2], pressure_old, accumulation, source])
    every = doubling_gather(bundle, "gx", 2)
    every = doubling_gather(every, "gy", 3)
    every = doubling_gather(every, "gz", 1)
    perm_pad = jnp.pad(every[:3], ((0, 0), (1, 1), (1, 1), (1, 1)))
    old_all = every[3]
    acc_all = every[4]
    fixed_all = acc_all * old_all + every[5]
    inside_pad = jnp.pad(jnp.ones(old_all.shape, jnp.float32), 1)
    pressure = old_all
    for sweep_index in range(2):
        pressure = coarse_sweep(perm_pad, jnp.pad(pressure, 1), inside_pad, acc_all, fixed_all)
    pressure = lax.dynamic_slice(
        pressure, (index_z * coarse_z, index_x * coarse_x, index_y * coarse_y), (coarse_z, coarse_x, coarse_y)
    )
    return (pressure, upscaled)


def solution(mesh):
    placed = (
        P(("real", "gz"), "gx", "gy"),
        P(("real", "gz"), "gx", "gy"),
        P(),
        P(("real", "gz"), "gx", "gy"),
        P(("real", "gz"), "gx", "gy"),
        P(("real", "gz"), "gx", "gy"),
    )
    return jax.shard_map(
        local,
        mesh=mesh,
        in_specs=placed,
        out_specs=(P(("real", "gz"), "gx", "gy"), P(None, ("real", "gz"), "gx", "gy")),
        check_vma=False,
    )
```

```python
import functools

import jax
import jax.numpy as jnp
from jax import lax
from jax.sharding import PartitionSpec as P
from jax.experimental import pallas as pl
from jax.experimental.pallas import tpu as pltpu

NFAC = 4
CCX = 32
CCY = 32
CCZ = 8
RIM = 4
SWEEPS = 3


BOUND_MID = 1.0
BOUND_HALF = 0.9


def extended(cells, sides, width, lanes=None):
    for axis, dim in sides:
        count = lax.axis_size(axis)
        ends = count - 1
        head = lax.slice_in_dim(cells, 0, width, axis=dim)
        tail = lax.slice_in_dim(cells, cells.shape[dim] - width, cells.shape[dim], axis=dim)
        if count == 2:
            lower_side = lax.axis_index(axis) == 0
            got = lax.ppermute(jnp.where(lower_side, tail, head), axis, [(0, 1), (1, 0)])
            below = got
            above = got
        elif count % 2 == 0:
            even = lax.axis_index(axis) % 2 == 0
            first = [(i, i ^ 1) for i in range(count)]
            second = [(i, i + 1 if i % 2 else i - 1) for i in range(1, count - 1)]
            got_first = lax.ppermute(jnp.where(even, tail, head), axis, first)
            got_second = lax.ppermute(jnp.where(even, head, tail), axis, second)
            below = jnp.where(even, got_second, got_first)
            above = jnp.where(even, got_first, got_second)
        else:
            below = lax.ppermute(tail, axis, [(i, (i + 1) % count) for i in range(ends)])
            above = lax.ppermute(head, axis, [((i + 1) % count, i) for i in range(ends)])
        if lanes is not None and dim == cells.ndim - 1:
            extra = lanes - (cells.shape[dim] + 2 * width)
            parts = [cells, above, jnp.zeros(cells.shape[:-1] + (extra,), cells.dtype), below]
        else:
            parts = [below, cells, above]
        cells = jnp.concatenate(parts, axis=dim)
    return cells


def halo_xz_then_y(block, width, lanes):
    size_x = lax.axis_size("gx")
    size_z = lax.axis_size("gz")
    if size_z != 2 or size_x % 2:
        return extended(block, (("gx", 2), ("gz", 1), ("gy", 3)), width, lanes)
    even = lax.axis_index("gx") % 2 == 0
    low_z = lax.axis_index("gz") == 0

    def edge(values, dim, upper):
        length = values.shape[dim]
        start = length - width if upper else 0
        return lax.slice_in_dim(values, start, start + width, axis=dim)

    def z_side(values):
        return jnp.where(low_z, edge(values, 1, True), edge(values, 1, False))

    def partner(i):
        return i + 1 if i % 2 else i - 1

    first = [(i, i ^ 1) for i in range(size_x)]
    second = [(i, partner(i)) for i in range(1, size_x - 1)]
    send_first = jnp.where(even, edge(block, 2, True), edge(block, 2, False))
    send_second = jnp.where(even, edge(block, 2, False), edge(block, 2, True))
    got_first = lax.ppermute(send_first, "gx", first)
    got_second = lax.ppermute(send_second, "gx", second)
    got_z = lax.ppermute(z_side(block), "gz", [(0, 1), (1, 0)])
    names = ("gx", "gz")
    corner_first = [(i * 2 + j, (i ^ 1) * 2 + 1 - j) for i in range(size_x) for j in range(2)]
    corner_second = [(i * 2 + j, partner(i) * 2 + 1 - j) for i in range(1, size_x - 1) for j in range(2)]
    got_corner_first = lax.ppermute(z_side(send_first), names, corner_first)
    got_corner_second = lax.ppermute(z_side(send_second), names, corner_second)
    below_x = jnp.where(even, got_second, got_first)
    above_x = jnp.where(even, got_first, got_second)
    below_corner = jnp.where(even, got_corner_second, got_corner_first)
    above_corner = jnp.where(even, got_corner_first, got_corner_second)
    centre = jnp.concatenate([below_x, block, above_x], axis=2)
    rim = jnp.concatenate([below_corner, got_z, above_corner], axis=2)
    cells = jnp.concatenate([rim, centre, rim], axis=1)
    return extended(cells, (("gy", 3),), width, lanes)


def doubling_gather(values, axis, dim):
    count = lax.axis_size(axis)
    if count & (count - 1):
        return lax.all_gather(values, axis, axis=dim, tiled=True)
    index = lax.axis_index(axis)
    step = 1
    while step < count:
        got = lax.ppermute(values, axis, [(i, i ^ step) for i in range(count)])
        lower = (index // step) % 2 == 0
        values = jnp.where(
            lower, jnp.concatenate([values, got], axis=dim), jnp.concatenate([got, values], axis=dim)
        )
        step *= 2
    return values


def raise_flat(values, offset):
    zeros_block = jnp.zeros(values.shape[:-1] + (offset,), values.dtype)
    return jnp.concatenate([values[..., offset:], zeros_block], axis=-1)


def lower_flat(values, offset):
    zeros_block = jnp.zeros(values.shape[:-1] + (offset,), values.dtype)
    return jnp.concatenate([zeros_block, values[..., :-offset]], axis=-1)


def raise_depth(values):
    zeros_block = jnp.zeros(values.shape[:1] + (1,) + values.shape[2:], values.dtype)
    return jnp.concatenate([values[:, 1:], zeros_block], axis=1)


def lower_depth(values):
    zeros_block = jnp.zeros(values.shape[:1] + (1,) + values.shape[2:], values.dtype)
    return jnp.concatenate([zeros_block, values[:, :-1]], axis=1)


def log_fields(log_noise, facies, facies_table):
    base_log = log_noise
    extra_y = jnp.zeros_like(log_noise)
    extra_z = jnp.zeros_like(log_noise)
    for code_value in range(NFAC):
        matched = facies == code_value
        base_log = base_log + jnp.where(matched, facies_table[0, code_value], jnp.float32(0.0))
        extra_y = extra_y + jnp.where(matched, facies_table[1, code_value], jnp.float32(0.0))
        extra_z = extra_z + jnp.where(matched, facies_table[2, code_value], jnp.float32(0.0))
    return (base_log, base_log + extra_y, base_log + extra_z)


def upscale(perm_logs, inside):
    span_z = CCZ + 2 * RIM
    span_x = CCX + 2 * RIM
    span_y = CCY + 2 * RIM
    depth_pos = lax.broadcasted_iota(jnp.int32, (1, span_z, 1), 1)
    flat_pos = lax.broadcasted_iota(jnp.int32, (1, 1, span_x * span_y), 2)
    column_pos = flat_pos // span_y
    row_pos = flat_pos % span_y
    perm_x = jnp.exp(perm_logs[0])
    perm_y = jnp.exp(perm_logs[1])
    perm_z = jnp.exp(perm_logs[2])

    def links(perm, other_perm, other_inside):
        return inside * other_inside * 2.0 * perm * other_perm / (perm + other_perm)

    link_x = links(perm_x, raise_flat(perm_x, span_y), raise_flat(inside, span_y))
    link_y = links(perm_y, raise_flat(perm_y, 1), raise_flat(inside, 1)) * (
        row_pos < span_y - 1
    ).astype(jnp.float32)
    link_z = links(perm_z, raise_depth(perm_z), raise_depth(inside))
    diagonal = (
        link_x
        + lower_flat(link_x, span_y)
        + link_y
        + lower_flat(link_y, 1)
        + link_z
        + lower_depth(link_z)
    )

    def apply_operator(field):
        beside = link_x * raise_flat(field, span_y) + lower_flat(link_x * field, span_y)
        beside = beside + link_y * raise_flat(field, 1) + lower_flat(link_y * field, 1)
        beside = beside + link_z * raise_depth(field) + lower_depth(link_z * field)
        return diagonal * field - beside

    interior = (
        (depth_pos >= 1)
        & (depth_pos <= span_z - 2)
        & (column_pos >= 1)
        & (column_pos <= span_x - 2)
        & (row_pos >= 1)
        & (row_pos <= span_y - 2)
    )
    unknown = inside * interior.astype(jnp.float32)
    scaling = unknown / (diagonal + 1.0 - unknown)
    core_z = (depth_pos >= RIM) & (depth_pos < RIM + CCZ)
    core_x = (column_pos >= RIM) & (column_pos < RIM + CCX)
    core_y = (row_pos >= RIM) & (row_pos < RIM + CCY)
    face_x = (((column_pos == RIM - 1) | (column_pos == RIM + CCX - 1)) & core_z & core_y).astype(
        jnp.float32
    )
    face_y = (((row_pos == RIM - 1) | (row_pos == RIM + CCY - 1)) & core_z & core_x).astype(
        jnp.float32
    )
    face_z = (((depth_pos == RIM - 1) | (depth_pos == RIM + CCZ - 1)) & core_x & core_y).astype(
        jnp.float32
    )
    ramp_x = ((span_x - 1) / 2.0 - column_pos).astype(jnp.float32)
    ramp_y = ((span_y - 1) / 2.0 - row_pos).astype(jnp.float32)
    ramp_z = ((span_z - 1) / 2.0 - depth_pos).astype(jnp.float32)
    cheb_ratio = BOUND_MID / BOUND_HALF
    results = []
    cases = (
        (ramp_x, link_x, face_x, CCY * CCZ, 0),
        (ramp_y, link_y, face_y, CCX * CCZ, 1),
        (ramp_z, link_z, face_z, CCX * CCY, 2),
    )
    for ramp, link, face, area, direction in cases:
        ramp_full = jnp.broadcast_to(ramp, inside.shape)
        source_term = -unknown * apply_operator(ramp_full)
        update = scaling * source_term / BOUND_MID
        solution = update
        rho_old = 1.0 / cheb_ratio
        for sweep_index in range(SWEEPS - 1):
            residual = source_term - apply_operator(solution)
            rho_new = 1.0 / (2.0 * cheb_ratio - rho_old)
            update = rho_new * rho_old * update + 2.0 * rho_new / BOUND_HALF * (scaling * residual)
            solution = solution + update
            rho_old = rho_new
        pressure = ramp_full + solution
        if direction == 0:
            upper = raise_flat(pressure, span_y)
        elif direction == 1:
            upper = raise_flat(pressure, 1)
        else:
            upper = raise_depth(pressure)
        flux = link * (pressure - upper) * face
        results.append(jnp.sum(flux, axis=(1, 2)) * (0.5 / area))
    return jnp.stack(results)


LANES = 128


def window_kernel(table_ref, bounds_ref, raw_ref, o_ref, *, count_x, count_y, count):
    span_z = CCZ + 2 * RIM
    span_x = CCX + 2 * RIM
    span_y = CCY + 2 * RIM
    segments = LANES // span_y
    shape = (span_z, span_x, LANES)
    pack = pl.program_id(0)
    wide = raw_ref.shape[-1]
    depth_pos = lax.broadcasted_iota(jnp.int32, shape, 0)
    column_pos = lax.broadcasted_iota(jnp.int32, shape, 1)
    lane = lax.broadcasted_iota(jnp.int32, shape, 2)
    segment = jnp.zeros(shape, jnp.int32)
    for bound in range(1, segments + 1):
        segment = segment + (lane >= bound * span_y).astype(jnp.int32)
    row_pos = lane - span_y * segment
    noise = jnp.zeros(shape, jnp.float32)
    codes = jnp.zeros(shape, jnp.float32)
    inside = jnp.zeros(shape, jnp.float32)
    for slot in range(segments):
        window = pack * segments + slot
        valid = window < count
        window = jnp.minimum(window, count - 1)
        block_z = window // (count_x * count_y)
        block_x = (window // count_y) % count_x
        block_y = window % count_y
        shift = (slot * span_y - block_y * CCY + RIM + wide) % wide
        here = segment == slot

        def cut(field):
            slab = raw_ref[field, pl.ds(block_z * CCZ, span_z), pl.ds(block_x * CCX, span_x), :]
            return pltpu.roll(slab, shift, 2)[:, :, :LANES]

        depth_at = depth_pos + block_z * CCZ
        column_at = column_pos + block_x * CCX
        row_at = row_pos + block_y * CCY
        held = (
            (depth_at >= bounds_ref[0])
            & (depth_at < bounds_ref[1])
            & (column_at >= bounds_ref[2])
            & (column_at < bounds_ref[3])
            & (row_at >= bounds_ref[4])
            & (row_at < bounds_ref[5])
        )
        noise = jnp.where(here, cut(0), noise)
        codes = jnp.where(here, cut(1), codes)
        inside = jnp.where(here & valid & held, 1.0, inside)

    def lookup(row):
        value = jnp.zeros(shape, jnp.float32)
        for code_value in range(NFAC):
            value = jnp.where(codes == code_value, table_ref[row, code_value], value)
        return value

    log_x = noise + lookup(0)
    log_y = log_x + lookup(1)
    log_z = log_x + lookup(2)
    perm_x = jnp.exp(log_x)
    perm_y = jnp.exp(log_y)
    perm_z = jnp.exp(log_z)

    def up_x(v):
        return pltpu.roll(v, span_x - 1, 1)

    def down_x(v):
        return pltpu.roll(v, 1, 1)

    def up_y(v):
        return pltpu.roll(v, LANES - 1, 2)

    def down_y(v):
        return pltpu.roll(v, 1, 2)

    def up_z(v):
        return jnp.concatenate([v[1:], v[:1]], axis=0)

    def down_z(v):
        return jnp.concatenate([v[-1:], v[:-1]], axis=0)

    def links(perm, other_perm, other_inside, valid):
        value = inside * other_inside * 2.0 * perm * other_perm / (perm + other_perm)
        return jnp.where(valid, value, 0.0)

    link_x = links(perm_x, up_x(perm_x), up_x(inside), column_pos < span_x - 1)
    link_y = links(perm_y, up_y(perm_y), up_y(inside), row_pos < span_y - 1)
    link_z = links(perm_z, up_z(perm_z), up_z(inside), depth_pos < span_z - 1)
    diagonal = link_x + down_x(link_x) + link_y + down_y(link_y) + link_z + down_z(link_z)

    def apply_operator(field):
        beside = link_x * up_x(field) + down_x(link_x * field)
        beside = beside + link_y * up_y(field) + down_y(link_y * field)
        beside = beside + link_z * up_z(field) + down_z(link_z * field)
        return diagonal * field - beside

    interior = (
        (depth_pos >= 1)
        & (depth_pos <= span_z - 2)
        & (column_pos >= 1)
        & (column_pos <= span_x - 2)
        & (row_pos >= 1)
        & (row_pos <= span_y - 2)
    )
    unknown = jnp.where(interior, inside, 0.0)
    scaling = unknown / (diagonal + 1.0 - unknown)
    core_z = (depth_pos >= RIM) & (depth_pos < RIM + CCZ)
    core_x = (column_pos >= RIM) & (column_pos < RIM + CCX)
    core_y = (row_pos >= RIM) & (row_pos < RIM + CCY)
    face_x = ((column_pos == RIM - 1) | (column_pos == RIM + CCX - 1)) & core_z & core_y
    face_y = ((row_pos == RIM - 1) | (row_pos == RIM + CCY - 1)) & core_z & core_x
    face_z = ((depth_pos == RIM - 1) | (depth_pos == RIM + CCZ - 1)) & core_x & core_y
    ramp_x = ((span_x - 1) / 2.0 - column_pos).astype(jnp.float32)
    ramp_y = ((span_y - 1) / 2.0 - row_pos).astype(jnp.float32)
    ramp_z = ((span_z - 1) / 2.0 - depth_pos).astype(jnp.float32)
    cheb_ratio = BOUND_MID / BOUND_HALF
    cases = (
        (ramp_x, link_x, face_x, CCY * CCZ, up_x, down_x),
        (ramp_y, link_y, face_y, CCX * CCZ, up_y, down_y),
        (ramp_z, link_z, face_z, CCX * CCY, up_z, down_z),
    )
    rows = []
    for ramp, link, face, area, upper_of, lower_of in cases:
        source_term = -unknown * (link - lower_of(link))
        update = scaling * source_term / BOUND_MID
        solution = update
        rho_old = 1.0 / cheb_ratio
        for sweep_index in range(SWEEPS - 1):
            residual = source_term - apply_operator(solution)
            rho_new = 1.0 / (2.0 * cheb_ratio - rho_old)
            update = rho_new * rho_old * update + 2.0 * rho_new / BOUND_HALF * (scaling * residual)
            solution = solution + update
            rho_old = rho_new
        pressure = ramp + solution
        flux = jnp.where(face, link * (pressure - upper_of(pressure)), 0.0)
        total = jnp.sum(flux, axis=0)
        total = jnp.sum(total, axis=0, keepdims=True)
        rows.append(total * (0.5 / area))
    rows.append(jnp.zeros((8 - len(rows), LANES), jnp.float32))
    o_ref[0] = jnp.concatenate(rows, axis=0)


def upscale_windows(raw, facies_table, bounds, cols_len):
    span_y = CCY + 2 * RIM
    count_z = (raw.shape[1] - 2 * RIM) // CCZ
    count_x = (raw.shape[2] - 2 * RIM) // CCX
    count_y = cols_len // CCY
    count = count_z * count_x * count_y
    segments = LANES // span_y
    packs = -(-count // segments)
    kernel = functools.partial(window_kernel, count_x=count_x, count_y=count_y, count=count)
    sums = pl.pallas_call(
        kernel,
        grid=(packs,),
        in_specs=[
            pl.BlockSpec(memory_space=pltpu.SMEM),
            pl.BlockSpec(memory_space=pltpu.SMEM),
            pl.BlockSpec(raw.shape, lambda p: (0, 0, 0, 0)),
        ],
        out_specs=pl.BlockSpec((1, 8, LANES), lambda p: (p, 0, 0)),
        out_shape=jax.ShapeDtypeStruct((packs, 8, LANES), jnp.float32),
    )(facies_table, bounds, raw)
    sums = sums[:, :3, : segments * span_y].reshape(packs, 3, segments, span_y).sum(axis=3)
    sums = sums.transpose(1, 0, 2).reshape(3, packs * segments)[:, :count]
    return sums.reshape((3, count_z, count_x, count_y))


def coarse_sweep(perm_pad, press_pad, inside_pad, accumulation, fixed):
    centre = (slice(1, -1), slice(1, -1), slice(1, -1))
    factors = (CCY * CCZ / CCX, CCX * CCZ / CCY, CCX * CCY / CCZ)
    numer = fixed
    denom = accumulation
    for component, axis_dim in ((0, 1), (1, 2), (2, 0)):
        for offset in (-1, 1):
            window_slice = [slice(1, -1), slice(1, -1), slice(1, -1)]
            window_slice[axis_dim] = slice(1 + offset, press_pad.shape[axis_dim] - 1 + offset)
            beside = tuple(window_slice)
            link = (
                factors[component]
                * 0.5
                * (perm_pad[component][centre] + perm_pad[component][beside])
                * inside_pad[beside]
            )
            numer = numer + link * press_pad[beside]
            denom = denom + jnp.abs(link)
    return numer / denom


def span_mask(anchor, length, total, margin):
    coords = anchor - margin + jnp.arange(length + 2 * margin, dtype=jnp.int32)
    return ((coords >= 0) & (coords < total)).astype(jnp.float32)


def cut_windows(fields):
    span_z = CCZ + 2 * RIM
    span_x = CCX + 2 * RIM
    span_y = CCY + 2 * RIM
    count_z = (fields[0].shape[0] - 2 * RIM) // CCZ
    count_x = (fields[0].shape[1] - 2 * RIM) // CCX
    count_y = (fields[0].shape[2] - 2 * RIM) // CCY
    stacks = []
    for field in fields:
        pieces = []
        for block_z in range(count_z):
            for block_y in range(count_y):
                piece = field[
                    block_z * CCZ : block_z * CCZ + span_z,
                    0:span_x,
                    block_y * CCY : block_y * CCY + span_y,
                ]
                pieces.append(piece.reshape(span_z, span_x * span_y))
        stacks.append(jnp.stack(pieces))
    return (stacks, (count_z, count_x, count_y))


def faces(block, sides):
    got = []
    for axis, dim in sides:
        count = lax.axis_size(axis)
        ends = count - 1
        head = lax.slice_in_dim(block, 0, 1, axis=dim)
        tail = lax.slice_in_dim(block, block.shape[dim] - 1, block.shape[dim], axis=dim)
        lower = lax.ppermute(tail, axis, [(i, i + 1) for i in range(ends)])
        upper = lax.ppermute(head, axis, [(i + 1, i) for i in range(ends)])
        got.append((lower, upper))
    return got


def neighbour_views(block, got, dim_of):
    views = []
    for (lower, upper), dim in zip(got, dim_of):
        size = block.shape[dim]
        below = jnp.concatenate([lower, lax.slice_in_dim(block, 0, size - 1, axis=dim)], axis=dim)
        above = jnp.concatenate([lax.slice_in_dim(block, 1, size, axis=dim), upper], axis=dim)
        views.append((below, above))
    return views


def coarse_step(upscaled, views, inside_views, pressure, accumulation, fixed):
    factors = (CCY * CCZ / CCX, CCX * CCZ / CCY, CCX * CCY / CCZ)
    numer = fixed
    denom = accumulation
    for component in range(3):
        for side in range(2):
            beside = views[component][side]
            link = factors[component] * 0.5 * (upscaled[component] + beside[component]) * inside_views[component][side]
            numer = numer + link * pressure[component][side]
            denom = denom + jnp.abs(link)
    return numer / denom


def local(log_noise, facies, facies_table, pressure_old, accumulation, source):
    depth_len, rows_len, cols_len = log_noise.shape
    size_z = lax.axis_size("gz")
    size_x = lax.axis_size("gx")
    size_y = lax.axis_size("gy")
    index_z = lax.axis_index("gz")
    index_x = lax.axis_index("gx")
    index_y = lax.axis_index("gy")
    raw = jnp.stack([log_noise, facies.astype(jnp.float32)])
    wide = -(-(cols_len + 2 * RIM) // LANES) * LANES
    raw = halo_xz_then_y(raw, RIM, wide)
    anchor_z = index_z * depth_len
    anchor_y = index_y * cols_len
    anchor_x = index_x * rows_len
    bounds = jnp.stack(
        [
            RIM - anchor_z,
            depth_len * size_z + RIM - anchor_z,
            RIM - anchor_x,
            rows_len * size_x + RIM - anchor_x,
            RIM - anchor_y,
            cols_len * size_y + RIM - anchor_y,
        ]
    ).astype(jnp.int32)
    upscaled = upscale_windows(raw, facies_table, bounds, cols_len)
    coarse_z, coarse_x, coarse_y = pressure_old.shape
    bundle = jnp.stack([upscaled[0], upscaled[1], upscaled[2], pressure_old, accumulation, source])
    every = doubling_gather(bundle, "gy", 3)
    every = doubling_gather(every, "gx", 2)
    every = doubling_gather(every, "gz", 1)
    perm_pad = jnp.pad(every[:3], ((0, 0), (1, 1), (1, 1), (1, 1)))
    old_all = every[3]
    acc_all = every[4]
    fixed_all = acc_all * old_all + every[5]
    inside_pad = jnp.pad(jnp.ones(old_all.shape, jnp.float32), 1)
    pressure = old_all
    for sweep_index in range(2):
        pressure = coarse_sweep(perm_pad, jnp.pad(pressure, 1), inside_pad, acc_all, fixed_all)
    pressure = lax.dynamic_slice(
        pressure, (index_z * coarse_z, index_x * coarse_x, index_y * coarse_y), (coarse_z, coarse_x, coarse_y)
    )
    return (pressure, upscaled)


def solution(mesh):
    placed = (
        P(("real", "gz"), "gx", "gy"),
        P(("real", "gz"), "gx", "gy"),
        P(),
        P(("real", "gz"), "gx", "gy"),
        P(("real", "gz"), "gx", "gy"),
        P(("real", "gz"), "gx", "gy"),
    )
    return jax.shard_map(
        local,
        mesh=mesh,
        in_specs=placed,
        out_specs=(P(("real", "gz"), "gx", "gy"), P(None, ("real", "gz"), "gx", "gy")),
        check_vma=False,
    )
```

```python
import functools

import jax
import jax.numpy as jnp
from jax import lax
from jax.sharding import PartitionSpec as P
from jax.experimental import pallas as pl
from jax.experimental.pallas import tpu as pltpu

NFAC = 4
CCX = 32
CCY = 32
CCZ = 8
RIM = 4
SWEEPS = 3


BOUND_MID = 1.0
BOUND_HALF = 0.9


def extended(cells, sides, width, lanes=None):
    for axis, dim in sides:
        count = lax.axis_size(axis)
        ends = count - 1
        head = lax.slice_in_dim(cells, 0, width, axis=dim)
        tail = lax.slice_in_dim(cells, cells.shape[dim] - width, cells.shape[dim], axis=dim)
        if count == 2 and dim == cells.ndim - 1:
            got = lax.ppermute(jnp.concatenate([tail, head], axis=dim), axis, [(0, 1), (1, 0)])
            below = lax.slice_in_dim(got, 0, width, axis=dim)
            above = lax.slice_in_dim(got, width, 2 * width, axis=dim)
        elif count == 2:
            lower_side = lax.axis_index(axis) == 0
            got = lax.ppermute(jnp.where(lower_side, tail, head), axis, [(0, 1), (1, 0)])
            below = got
            above = got
        elif count % 2 == 0:
            even = lax.axis_index(axis) % 2 == 0
            first = [(i, i ^ 1) for i in range(count)]
            second = [(i, i + 1 if i % 2 else i - 1) for i in range(1, count - 1)]
            got_first = lax.ppermute(jnp.where(even, tail, head), axis, first)
            got_second = lax.ppermute(jnp.where(even, head, tail), axis, second)
            below = jnp.where(even, got_second, got_first)
            above = jnp.where(even, got_first, got_second)
        else:
            below = lax.ppermute(tail, axis, [(i, (i + 1) % count) for i in range(ends)])
            above = lax.ppermute(head, axis, [((i + 1) % count, i) for i in range(ends)])
        if lanes is not None and dim == cells.ndim - 1:
            extra = lanes - (cells.shape[dim] + 2 * width)
            parts = [cells, above, jnp.zeros(cells.shape[:-1] + (extra,), cells.dtype), below]
        else:
            parts = [below, cells, above]
        cells = jnp.concatenate(parts, axis=dim)
    return cells


def doubling_gather(values, axis, dim):
    count = lax.axis_size(axis)
    if count & (count - 1):
        return lax.all_gather(values, axis, axis=dim, tiled=True)
    index = lax.axis_index(axis)
    step = 1
    while step < count:
        got = lax.ppermute(values, axis, [(i, i ^ step) for i in range(count)])
        lower = (index // step) % 2 == 0
        values = jnp.where(
            lower, jnp.concatenate([values, got], axis=dim), jnp.concatenate([got, values], axis=dim)
        )
        step *= 2
    return values


def raise_flat(values, offset):
    zeros_block = jnp.zeros(values.shape[:-1] + (offset,), values.dtype)
    return jnp.concatenate([values[..., offset:], zeros_block], axis=-1)


def lower_flat(values, offset):
    zeros_block = jnp.zeros(values.shape[:-1] + (offset,), values.dtype)
    return jnp.concatenate([zeros_block, values[..., :-offset]], axis=-1)


def raise_depth(values):
    zeros_block = jnp.zeros(values.shape[:1] + (1,) + values.shape[2:], values.dtype)
    return jnp.concatenate([values[:, 1:], zeros_block], axis=1)


def lower_depth(values):
    zeros_block = jnp.zeros(values.shape[:1] + (1,) + values.shape[2:], values.dtype)
    return jnp.concatenate([zeros_block, values[:, :-1]], axis=1)


def log_fields(log_noise, facies, facies_table):
    base_log = log_noise
    extra_y = jnp.zeros_like(log_noise)
    extra_z = jnp.zeros_like(log_noise)
    for code_value in range(NFAC):
        matched = facies == code_value
        base_log = base_log + jnp.where(matched, facies_table[0, code_value], jnp.float32(0.0))
        extra_y = extra_y + jnp.where(matched, facies_table[1, code_value], jnp.float32(0.0))
        extra_z = extra_z + jnp.where(matched, facies_table[2, code_value], jnp.float32(0.0))
    return (base_log, base_log + extra_y, base_log + extra_z)


def upscale(perm_logs, inside):
    span_z = CCZ + 2 * RIM
    span_x = CCX + 2 * RIM
    span_y = CCY + 2 * RIM
    depth_pos = lax.broadcasted_iota(jnp.int32, (1, span_z, 1), 1)
    flat_pos = lax.broadcasted_iota(jnp.int32, (1, 1, span_x * span_y), 2)
    column_pos = flat_pos // span_y
    row_pos = flat_pos % span_y
    perm_x = jnp.exp(perm_logs[0])
    perm_y = jnp.exp(perm_logs[1])
    perm_z = jnp.exp(perm_logs[2])

    def links(perm, other_perm, other_inside):
        return inside * other_inside * 2.0 * perm * other_perm / (perm + other_perm)

    link_x = links(perm_x, raise_flat(perm_x, span_y), raise_flat(inside, span_y))
    link_y = links(perm_y, raise_flat(perm_y, 1), raise_flat(inside, 1)) * (
        row_pos < span_y - 1
    ).astype(jnp.float32)
    link_z = links(perm_z, raise_depth(perm_z), raise_depth(inside))
    diagonal = (
        link_x
        + lower_flat(link_x, span_y)
        + link_y
        + lower_flat(link_y, 1)
        + link_z
        + lower_depth(link_z)
    )

    def apply_operator(field):
        beside = link_x * raise_flat(field, span_y) + lower_flat(link_x * field, span_y)
        beside = beside + link_y * raise_flat(field, 1) + lower_flat(link_y * field, 1)
        beside = beside + link_z * raise_depth(field) + lower_depth(link_z * field)
        return diagonal * field - beside

    interior = (
        (depth_pos >= 1)
        & (depth_pos <= span_z - 2)
        & (column_pos >= 1)
        & (column_pos <= span_x - 2)
        & (row_pos >= 1)
        & (row_pos <= span_y - 2)
    )
    unknown = inside * interior.astype(jnp.float32)
    scaling = unknown / (diagonal + 1.0 - unknown)
    core_z = (depth_pos >= RIM) & (depth_pos < RIM + CCZ)
    core_x = (column_pos >= RIM) & (column_pos < RIM + CCX)
    core_y = (row_pos >= RIM) & (row_pos < RIM + CCY)
    face_x = (((column_pos == RIM - 1) | (column_pos == RIM + CCX - 1)) & core_z & core_y).astype(
        jnp.float32
    )
    face_y = (((row_pos == RIM - 1) | (row_pos == RIM + CCY - 1)) & core_z & core_x).astype(
        jnp.float32
    )
    face_z = (((depth_pos == RIM - 1) | (depth_pos == RIM + CCZ - 1)) & core_x & core_y).astype(
        jnp.float32
    )
    ramp_x = ((span_x - 1) / 2.0 - column_pos).astype(jnp.float32)
    ramp_y = ((span_y - 1) / 2.0 - row_pos).astype(jnp.float32)
    ramp_z = ((span_z - 1) / 2.0 - depth_pos).astype(jnp.float32)
    cheb_ratio = BOUND_MID / BOUND_HALF
    results = []
    cases = (
        (ramp_x, link_x, face_x, CCY * CCZ, 0),
        (ramp_y, link_y, face_y, CCX * CCZ, 1),
        (ramp_z, link_z, face_z, CCX * CCY, 2),
    )
    for ramp, link, face, area, direction in cases:
        ramp_full = jnp.broadcast_to(ramp, inside.shape)
        source_term = -unknown * apply_operator(ramp_full)
        update = scaling * source_term / BOUND_MID
        solution = update
        rho_old = 1.0 / cheb_ratio
        for sweep_index in range(SWEEPS - 1):
            residual = source_term - apply_operator(solution)
            rho_new = 1.0 / (2.0 * cheb_ratio - rho_old)
            update = rho_new * rho_old * update + 2.0 * rho_new / BOUND_HALF * (scaling * residual)
            solution = solution + update
            rho_old = rho_new
        pressure = ramp_full + solution
        if direction == 0:
            upper = raise_flat(pressure, span_y)
        elif direction == 1:
            upper = raise_flat(pressure, 1)
        else:
            upper = raise_depth(pressure)
        flux = link * (pressure - upper) * face
        results.append(jnp.sum(flux, axis=(1, 2)) * (0.5 / area))
    return jnp.stack(results)


LANES = 128


def window_kernel(table_ref, bounds_ref, raw_ref, o_ref, *, count_x, count_y, count):
    span_z = CCZ + 2 * RIM
    span_x = CCX + 2 * RIM
    span_y = CCY + 2 * RIM
    segments = LANES // span_y
    shape = (span_z, span_x, LANES)
    pack = pl.program_id(0)
    wide = raw_ref.shape[-1]
    depth_pos = lax.broadcasted_iota(jnp.int32, shape, 0)
    column_pos = lax.broadcasted_iota(jnp.int32, shape, 1)
    lane = lax.broadcasted_iota(jnp.int32, shape, 2)
    segment = jnp.zeros(shape, jnp.int32)
    for bound in range(1, segments + 1):
        segment = segment + (lane >= bound * span_y).astype(jnp.int32)
    row_pos = lane - span_y * segment
    noise = jnp.zeros(shape, jnp.float32)
    codes = jnp.zeros(shape, jnp.float32)
    inside = jnp.zeros(shape, jnp.float32)
    for slot in range(segments):
        window = pack * segments + slot
        valid = window < count
        window = jnp.minimum(window, count - 1)
        block_z = window // (count_x * count_y)
        block_x = (window // count_y) % count_x
        block_y = window % count_y
        shift = (slot * span_y - block_y * CCY + RIM + wide) % wide
        here = segment == slot

        def cut(field):
            slab = raw_ref[field, pl.ds(block_z * CCZ, span_z), pl.ds(block_x * CCX, span_x), :]
            return pltpu.roll(slab, shift, 2)[:, :, :LANES]

        depth_at = depth_pos + block_z * CCZ
        column_at = column_pos + block_x * CCX
        row_at = row_pos + block_y * CCY
        held = (
            (depth_at >= bounds_ref[0])
            & (depth_at < bounds_ref[1])
            & (column_at >= bounds_ref[2])
            & (column_at < bounds_ref[3])
            & (row_at >= bounds_ref[4])
            & (row_at < bounds_ref[5])
        )
        noise = jnp.where(here, cut(0), noise)
        codes = jnp.where(here, cut(1), codes)
        inside = jnp.where(here & valid & held, 1.0, inside)

    def lookup(row):
        value = jnp.zeros(shape, jnp.float32)
        for code_value in range(NFAC):
            value = jnp.where(codes == code_value, table_ref[row, code_value], value)
        return value

    log_x = noise + lookup(0)
    log_y = log_x + lookup(1)
    log_z = log_x + lookup(2)
    perm_x = jnp.exp(log_x)
    perm_y = jnp.exp(log_y)
    perm_z = jnp.exp(log_z)

    def up_x(v):
        return pltpu.roll(v, span_x - 1, 1)

    def down_x(v):
        return pltpu.roll(v, 1, 1)

    def up_y(v):
        return pltpu.roll(v, LANES - 1, 2)

    def down_y(v):
        return pltpu.roll(v, 1, 2)

    def up_z(v):
        return jnp.concatenate([v[1:], v[:1]], axis=0)

    def down_z(v):
        return jnp.concatenate([v[-1:], v[:-1]], axis=0)

    def links(perm, other_perm, other_inside, valid):
        value = inside * other_inside * 2.0 * perm * other_perm / (perm + other_perm)
        return jnp.where(valid, value, 0.0)

    link_x = links(perm_x, up_x(perm_x), up_x(inside), column_pos < span_x - 1)
    link_y = links(perm_y, up_y(perm_y), up_y(inside), row_pos < span_y - 1)
    link_z = links(perm_z, up_z(perm_z), up_z(inside), depth_pos < span_z - 1)
    diagonal = link_x + down_x(link_x) + link_y + down_y(link_y) + link_z + down_z(link_z)

    def apply_operator(field):
        beside = link_x * up_x(field) + down_x(link_x * field)
        beside = beside + link_y * up_y(field) + down_y(link_y * field)
        beside = beside + link_z * up_z(field) + down_z(link_z * field)
        return diagonal * field - beside

    interior = (
        (depth_pos >= 1)
        & (depth_pos <= span_z - 2)
        & (column_pos >= 1)
        & (column_pos <= span_x - 2)
        & (row_pos >= 1)
        & (row_pos <= span_y - 2)
    )
    unknown = jnp.where(interior, inside, 0.0)
    scaling = unknown / (diagonal + 1.0 - unknown)
    core_z = (depth_pos >= RIM) & (depth_pos < RIM + CCZ)
    core_x = (column_pos >= RIM) & (column_pos < RIM + CCX)
    core_y = (row_pos >= RIM) & (row_pos < RIM + CCY)
    face_x = ((column_pos == RIM - 1) | (column_pos == RIM + CCX - 1)) & core_z & core_y
    face_y = ((row_pos == RIM - 1) | (row_pos == RIM + CCY - 1)) & core_z & core_x
    face_z = ((depth_pos == RIM - 1) | (depth_pos == RIM + CCZ - 1)) & core_x & core_y
    ramp_x = ((span_x - 1) / 2.0 - column_pos).astype(jnp.float32)
    ramp_y = ((span_y - 1) / 2.0 - row_pos).astype(jnp.float32)
    ramp_z = ((span_z - 1) / 2.0 - depth_pos).astype(jnp.float32)
    cheb_ratio = BOUND_MID / BOUND_HALF
    cases = (
        (ramp_x, link_x, face_x, CCY * CCZ, up_x, down_x),
        (ramp_y, link_y, face_y, CCX * CCZ, up_y, down_y),
        (ramp_z, link_z, face_z, CCX * CCY, up_z, down_z),
    )
    rows = []
    for ramp, link, face, area, upper_of, lower_of in cases:
        source_term = -unknown * (link - lower_of(link))
        update = scaling * source_term / BOUND_MID
        solution = update
        rho_old = 1.0 / cheb_ratio
        for sweep_index in range(SWEEPS - 1):
            residual = source_term - apply_operator(solution)
            rho_new = 1.0 / (2.0 * cheb_ratio - rho_old)
            update = rho_new * rho_old * update + 2.0 * rho_new / BOUND_HALF * (scaling * residual)
            solution = solution + update
            rho_old = rho_new
        pressure = ramp + solution
        flux = jnp.where(face, link * (pressure - upper_of(pressure)), 0.0)
        total = jnp.sum(flux, axis=0)
        total = jnp.sum(total, axis=0, keepdims=True)
        rows.append(total * (0.5 / area))
    rows.append(jnp.zeros((8 - len(rows), LANES), jnp.float32))
    o_ref[0] = jnp.concatenate(rows, axis=0)


def upscale_windows(raw, facies_table, bounds, cols_len):
    span_y = CCY + 2 * RIM
    count_z = (raw.shape[1] - 2 * RIM) // CCZ
    count_x = (raw.shape[2] - 2 * RIM) // CCX
    count_y = cols_len // CCY
    count = count_z * count_x * count_y
    segments = LANES // span_y
    packs = -(-count // segments)
    kernel = functools.partial(window_kernel, count_x=count_x, count_y=count_y, count=count)
    sums = pl.pallas_call(
        kernel,
        grid=(packs,),
        in_specs=[
            pl.BlockSpec(memory_space=pltpu.SMEM),
            pl.BlockSpec(memory_space=pltpu.SMEM),
            pl.BlockSpec(raw.shape, lambda p: (0, 0, 0, 0)),
        ],
        out_specs=pl.BlockSpec((1, 8, LANES), lambda p: (p, 0, 0)),
        out_shape=jax.ShapeDtypeStruct((packs, 8, LANES), jnp.float32),
    )(facies_table, bounds, raw)
    sums = sums[:, :3, : segments * span_y].reshape(packs, 3, segments, span_y).sum(axis=3)
    sums = sums.transpose(1, 0, 2).reshape(3, packs * segments)[:, :count]
    return sums.reshape((3, count_z, count_x, count_y))


def coarse_sweep(perm_pad, press_pad, inside_pad, accumulation, fixed):
    centre = (slice(1, -1), slice(1, -1), slice(1, -1))
    factors = (CCY * CCZ / CCX, CCX * CCZ / CCY, CCX * CCY / CCZ)
    numer = fixed
    denom = accumulation
    for component, axis_dim in ((0, 1), (1, 2), (2, 0)):
        for offset in (-1, 1):
            window_slice = [slice(1, -1), slice(1, -1), slice(1, -1)]
            window_slice[axis_dim] = slice(1 + offset, press_pad.shape[axis_dim] - 1 + offset)
            beside = tuple(window_slice)
            link = (
                factors[component]
                * 0.5
                * (perm_pad[component][centre] + perm_pad[component][beside])
                * inside_pad[beside]
            )
            numer = numer + link * press_pad[beside]
            denom = denom + jnp.abs(link)
    return numer / denom


def span_mask(anchor, length, total, margin):
    coords = anchor - margin + jnp.arange(length + 2 * margin, dtype=jnp.int32)
    return ((coords >= 0) & (coords < total)).astype(jnp.float32)


def cut_windows(fields):
    span_z = CCZ + 2 * RIM
    span_x = CCX + 2 * RIM
    span_y = CCY + 2 * RIM
    count_z = (fields[0].shape[0] - 2 * RIM) // CCZ
    count_x = (fields[0].shape[1] - 2 * RIM) // CCX
    count_y = (fields[0].shape[2] - 2 * RIM) // CCY
    stacks = []
    for field in fields:
        pieces = []
        for block_z in range(count_z):
            for block_y in range(count_y):
                piece = field[
                    block_z * CCZ : block_z * CCZ + span_z,
                    0:span_x,
                    block_y * CCY : block_y * CCY + span_y,
                ]
                pieces.append(piece.reshape(span_z, span_x * span_y))
        stacks.append(jnp.stack(pieces))
    return (stacks, (count_z, count_x, count_y))


def faces(block, sides):
    got = []
    for axis, dim in sides:
        count = lax.axis_size(axis)
        ends = count - 1
        head = lax.slice_in_dim(block, 0, 1, axis=dim)
        tail = lax.slice_in_dim(block, block.shape[dim] - 1, block.shape[dim], axis=dim)
        lower = lax.ppermute(tail, axis, [(i, i + 1) for i in range(ends)])
        upper = lax.ppermute(head, axis, [(i + 1, i) for i in range(ends)])
        got.append((lower, upper))
    return got


def neighbour_views(block, got, dim_of):
    views = []
    for (lower, upper), dim in zip(got, dim_of):
        size = block.shape[dim]
        below = jnp.concatenate([lower, lax.slice_in_dim(block, 0, size - 1, axis=dim)], axis=dim)
        above = jnp.concatenate([lax.slice_in_dim(block, 1, size, axis=dim), upper], axis=dim)
        views.append((below, above))
    return views


def coarse_step(upscaled, views, inside_views, pressure, accumulation, fixed):
    factors = (CCY * CCZ / CCX, CCX * CCZ / CCY, CCX * CCY / CCZ)
    numer = fixed
    denom = accumulation
    for component in range(3):
        for side in range(2):
            beside = views[component][side]
            link = factors[component] * 0.5 * (upscaled[component] + beside[component]) * inside_views[component][side]
            numer = numer + link * pressure[component][side]
            denom = denom + jnp.abs(link)
    return numer / denom


def local(log_noise, facies, facies_table, pressure_old, accumulation, source):
    depth_len, rows_len, cols_len = log_noise.shape
    size_z = lax.axis_size("gz")
    size_x = lax.axis_size("gx")
    size_y = lax.axis_size("gy")
    index_z = lax.axis_index("gz")
    index_x = lax.axis_index("gx")
    index_y = lax.axis_index("gy")
    raw = jnp.stack([log_noise, facies.astype(jnp.float32)])
    wide = -(-(cols_len + 2 * RIM) // LANES) * LANES
    raw = extended(raw, (("gx", 2), ("gz", 1), ("gy", 3)), RIM, wide)
    anchor_z = index_z * depth_len
    anchor_y = index_y * cols_len
    anchor_x = index_x * rows_len
    bounds = jnp.stack(
        [
            RIM - anchor_z,
            depth_len * size_z + RIM - anchor_z,
            RIM - anchor_x,
            rows_len * size_x + RIM - anchor_x,
            RIM - anchor_y,
            cols_len * size_y + RIM - anchor_y,
        ]
    ).astype(jnp.int32)
    upscaled = upscale_windows(raw, facies_table, bounds, cols_len)
    coarse_z, coarse_x, coarse_y = pressure_old.shape
    bundle = jnp.stack([upscaled[0], upscaled[1], upscaled[2], pressure_old, accumulation, source])
    every = doubling_gather(bundle, "gy", 3)
    every = doubling_gather(every, "gx", 2)
    every = doubling_gather(every, "gz", 1)
    perm_pad = jnp.pad(every[:3], ((0, 0), (1, 1), (1, 1), (1, 1)))
    old_all = every[3]
    acc_all = every[4]
    fixed_all = acc_all * old_all + every[5]
    inside_pad = jnp.pad(jnp.ones(old_all.shape, jnp.float32), 1)
    pressure = old_all
    for sweep_index in range(2):
        pressure = coarse_sweep(perm_pad, jnp.pad(pressure, 1), inside_pad, acc_all, fixed_all)
    pressure = lax.dynamic_slice(
        pressure, (index_z * coarse_z, index_x * coarse_x, index_y * coarse_y), (coarse_z, coarse_x, coarse_y)
    )
    return (pressure, upscaled)


def solution(mesh):
    placed = (
        P(("real", "gz"), "gx", "gy"),
        P(("real", "gz"), "gx", "gy"),
        P(),
        P(("real", "gz"), "gx", "gy"),
        P(("real", "gz"), "gx", "gy"),
        P(("real", "gz"), "gx", "gy"),
    )
    return jax.shard_map(
        local,
        mesh=mesh,
        in_specs=placed,
        out_specs=(P(("real", "gz"), "gx", "gy"), P(None, ("real", "gz"), "gx", "gy")),
        check_vma=False,
    )
```

```python
import functools

import jax
import jax.numpy as jnp
from jax import lax
from jax.sharding import PartitionSpec as P
from jax.experimental import pallas as pl
from jax.experimental.pallas import tpu as pltpu

NFAC = 4
CCX = 32
CCY = 32
CCZ = 8
RIM = 4
SWEEPS = 3


BOUND_MID = 1.0
BOUND_HALF = 0.9


def extended(cells, sides, width, lanes=None):
    for axis, dim in sides:
        count = lax.axis_size(axis)
        ends = count - 1
        head = lax.slice_in_dim(cells, 0, width, axis=dim)
        tail = lax.slice_in_dim(cells, cells.shape[dim] - width, cells.shape[dim], axis=dim)
        if count == 2:
            lower_side = lax.axis_index(axis) == 0
            got = lax.ppermute(jnp.where(lower_side, tail, head), axis, [(0, 1), (1, 0)])
            below = got
            above = got
        elif count % 2 == 0:
            even = lax.axis_index(axis) % 2 == 0
            first = [(i, i ^ 1) for i in range(count)]
            second = [(i, i + 1 if i % 2 else i - 1) for i in range(1, count - 1)]
            got_first = lax.ppermute(jnp.where(even, tail, head), axis, first)
            got_second = lax.ppermute(jnp.where(even, head, tail), axis, second)
            below = jnp.where(even, got_second, got_first)
            above = jnp.where(even, got_first, got_second)
        else:
            below = lax.ppermute(tail, axis, [(i, (i + 1) % count) for i in range(ends)])
            above = lax.ppermute(head, axis, [((i + 1) % count, i) for i in range(ends)])
        if lanes is not None and dim == cells.ndim - 1:
            extra = lanes - (cells.shape[dim] + 2 * width)
            parts = [cells, above, jnp.zeros(cells.shape[:-1] + (extra,), cells.dtype), below]
        else:
            parts = [below, cells, above]
        cells = jnp.concatenate(parts, axis=dim)
    return cells


def doubling_gather(values, axis, dim):
    count = lax.axis_size(axis)
    if count & (count - 1):
        return lax.all_gather(values, axis, axis=dim, tiled=True)
    index = lax.axis_index(axis)
    step = 1
    while step < count:
        got = lax.ppermute(values, axis, [(i, i ^ step) for i in range(count)])
        lower = (index // step) % 2 == 0
        values = jnp.where(
            lower, jnp.concatenate([values, got], axis=dim), jnp.concatenate([got, values], axis=dim)
        )
        step *= 2
    return values


def raise_flat(values, offset):
    zeros_block = jnp.zeros(values.shape[:-1] + (offset,), values.dtype)
    return jnp.concatenate([values[..., offset:], zeros_block], axis=-1)


def lower_flat(values, offset):
    zeros_block = jnp.zeros(values.shape[:-1] + (offset,), values.dtype)
    return jnp.concatenate([zeros_block, values[..., :-offset]], axis=-1)


def raise_depth(values):
    zeros_block = jnp.zeros(values.shape[:1] + (1,) + values.shape[2:], values.dtype)
    return jnp.concatenate([values[:, 1:], zeros_block], axis=1)


def lower_depth(values):
    zeros_block = jnp.zeros(values.shape[:1] + (1,) + values.shape[2:], values.dtype)
    return jnp.concatenate([zeros_block, values[:, :-1]], axis=1)


def log_fields(log_noise, facies, facies_table):
    base_log = log_noise
    extra_y = jnp.zeros_like(log_noise)
    extra_z = jnp.zeros_like(log_noise)
    for code_value in range(NFAC):
        matched = facies == code_value
        base_log = base_log + jnp.where(matched, facies_table[0, code_value], jnp.float32(0.0))
        extra_y = extra_y + jnp.where(matched, facies_table[1, code_value], jnp.float32(0.0))
        extra_z = extra_z + jnp.where(matched, facies_table[2, code_value], jnp.float32(0.0))
    return (base_log, base_log + extra_y, base_log + extra_z)


def upscale(perm_logs, inside):
    span_z = CCZ + 2 * RIM
    span_x = CCX + 2 * RIM
    span_y = CCY + 2 * RIM
    depth_pos = lax.broadcasted_iota(jnp.int32, (1, span_z, 1), 1)
    flat_pos = lax.broadcasted_iota(jnp.int32, (1, 1, span_x * span_y), 2)
    column_pos = flat_pos // span_y
    row_pos = flat_pos % span_y
    perm_x = jnp.exp(perm_logs[0])
    perm_y = jnp.exp(perm_logs[1])
    perm_z = jnp.exp(perm_logs[2])

    def links(perm, other_perm, other_inside):
        return inside * other_inside * 2.0 * perm * other_perm / (perm + other_perm)

    link_x = links(perm_x, raise_flat(perm_x, span_y), raise_flat(inside, span_y))
    link_y = links(perm_y, raise_flat(perm_y, 1), raise_flat(inside, 1)) * (
        row_pos < span_y - 1
    ).astype(jnp.float32)
    link_z = links(perm_z, raise_depth(perm_z), raise_depth(inside))
    diagonal = (
        link_x
        + lower_flat(link_x, span_y)
        + link_y
        + lower_flat(link_y, 1)
        + link_z
        + lower_depth(link_z)
    )

    def apply_operator(field):
        beside = link_x * raise_flat(field, span_y) + lower_flat(link_x * field, span_y)
        beside = beside + link_y * raise_flat(field, 1) + lower_flat(link_y * field, 1)
        beside = beside + link_z * raise_depth(field) + lower_depth(link_z * field)
        return diagonal * field - beside

    interior = (
        (depth_pos >= 1)
        & (depth_pos <= span_z - 2)
        & (column_pos >= 1)
        & (column_pos <= span_x - 2)
        & (row_pos >= 1)
        & (row_pos <= span_y - 2)
    )
    unknown = inside * interior.astype(jnp.float32)
    scaling = unknown / (diagonal + 1.0 - unknown)
    core_z = (depth_pos >= RIM) & (depth_pos < RIM + CCZ)
    core_x = (column_pos >= RIM) & (column_pos < RIM + CCX)
    core_y = (row_pos >= RIM) & (row_pos < RIM + CCY)
    face_x = (((column_pos == RIM - 1) | (column_pos == RIM + CCX - 1)) & core_z & core_y).astype(
        jnp.float32
    )
    face_y = (((row_pos == RIM - 1) | (row_pos == RIM + CCY - 1)) & core_z & core_x).astype(
        jnp.float32
    )
    face_z = (((depth_pos == RIM - 1) | (depth_pos == RIM + CCZ - 1)) & core_x & core_y).astype(
        jnp.float32
    )
    ramp_x = ((span_x - 1) / 2.0 - column_pos).astype(jnp.float32)
    ramp_y = ((span_y - 1) / 2.0 - row_pos).astype(jnp.float32)
    ramp_z = ((span_z - 1) / 2.0 - depth_pos).astype(jnp.float32)
    cheb_ratio = BOUND_MID / BOUND_HALF
    results = []
    cases = (
        (ramp_x, link_x, face_x, CCY * CCZ, 0),
        (ramp_y, link_y, face_y, CCX * CCZ, 1),
        (ramp_z, link_z, face_z, CCX * CCY, 2),
    )
    for ramp, link, face, area, direction in cases:
        ramp_full = jnp.broadcast_to(ramp, inside.shape)
        source_term = -unknown * apply_operator(ramp_full)
        update = scaling * source_term / BOUND_MID
        solution = update
        rho_old = 1.0 / cheb_ratio
        for sweep_index in range(SWEEPS - 1):
            residual = source_term - apply_operator(solution)
            rho_new = 1.0 / (2.0 * cheb_ratio - rho_old)
            update = rho_new * rho_old * update + 2.0 * rho_new / BOUND_HALF * (scaling * residual)
            solution = solution + update
            rho_old = rho_new
        pressure = ramp_full + solution
        if direction == 0:
            upper = raise_flat(pressure, span_y)
        elif direction == 1:
            upper = raise_flat(pressure, 1)
        else:
            upper = raise_depth(pressure)
        flux = link * (pressure - upper) * face
        results.append(jnp.sum(flux, axis=(1, 2)) * (0.5 / area))
    return jnp.stack(results)


LANES = 128


def window_kernel(table_ref, bounds_ref, raw_ref, o_ref, *, count_x, count_y, count):
    span_z = CCZ + 2 * RIM
    span_x = CCX + 2 * RIM
    span_y = CCY + 2 * RIM
    segments = LANES // span_y
    shape = (span_z, span_x, LANES)
    pack = pl.program_id(0)
    wide = raw_ref.shape[-1]
    depth_pos = lax.broadcasted_iota(jnp.int32, shape, 0)
    column_pos = lax.broadcasted_iota(jnp.int32, shape, 1)
    lane = lax.broadcasted_iota(jnp.int32, shape, 2)
    segment = jnp.zeros(shape, jnp.int32)
    for bound in range(1, segments + 1):
        segment = segment + (lane >= bound * span_y).astype(jnp.int32)
    row_pos = lane - span_y * segment
    noise = jnp.zeros(shape, jnp.float32)
    codes = jnp.zeros(shape, jnp.float32)
    inside = jnp.zeros(shape, jnp.float32)
    for slot in range(segments):
        window = pack * segments + slot
        valid = window < count
        window = jnp.minimum(window, count - 1)
        block_z = window // (count_x * count_y)
        block_x = (window // count_y) % count_x
        block_y = window % count_y
        shift = (slot * span_y - block_y * CCY + RIM + wide) % wide
        here = segment == slot

        def cut(field):
            slab = raw_ref[field, pl.ds(block_z * CCZ, span_z), pl.ds(block_x * CCX, span_x), :]
            return pltpu.roll(slab, shift, 2)[:, :, :LANES]

        depth_at = block_z * CCZ
        column_at = block_x * CCX
        row_at = block_y * CCY
        held = (
            (depth_pos >= bounds_ref[0] - depth_at)
            & (depth_pos < bounds_ref[1] - depth_at)
            & (column_pos >= bounds_ref[2] - column_at)
            & (column_pos < bounds_ref[3] - column_at)
            & (row_pos >= bounds_ref[4] - row_at)
            & (row_pos < bounds_ref[5] - row_at)
        )
        noise = jnp.where(here, cut(0), noise)
        codes = jnp.where(here, cut(1), codes)
        inside = jnp.where(here & valid & held, 1.0, inside)

    def lookup(row):
        value = jnp.zeros(shape, jnp.float32)
        for code_value in range(NFAC):
            value = jnp.where(codes == code_value, table_ref[row, code_value], value)
        return value

    log_x = noise + lookup(0)
    log_y = log_x + lookup(1)
    log_z = log_x + lookup(2)
    perm_x = jnp.exp(log_x)
    perm_y = jnp.exp(log_y)
    perm_z = jnp.exp(log_z)

    def up_x(v):
        return pltpu.roll(v, span_x - 1, 1)

    def down_x(v):
        return pltpu.roll(v, 1, 1)

    def up_y(v):
        return pltpu.roll(v, LANES - 1, 2)

    def down_y(v):
        return pltpu.roll(v, 1, 2)

    def up_z(v):
        return jnp.concatenate([v[1:], v[:1]], axis=0)

    def down_z(v):
        return jnp.concatenate([v[-1:], v[:-1]], axis=0)

    def links(perm, other_perm, other_inside, valid):
        value = inside * other_inside * 2.0 * perm * other_perm / (perm + other_perm)
        return jnp.where(valid, value, 0.0)

    link_x = links(perm_x, up_x(perm_x), up_x(inside), column_pos < span_x - 1)
    link_y = links(perm_y, up_y(perm_y), up_y(inside), row_pos < span_y - 1)
    link_z = links(perm_z, up_z(perm_z), up_z(inside), depth_pos < span_z - 1)
    diagonal = link_x + down_x(link_x) + link_y + down_y(link_y) + link_z + down_z(link_z)

    def apply_operator(field):
        beside = link_x * up_x(field) + down_x(link_x * field)
        beside = beside + link_y * up_y(field) + down_y(link_y * field)
        beside = beside + link_z * up_z(field) + down_z(link_z * field)
        return diagonal * field - beside

    interior = (
        (depth_pos >= 1)
        & (depth_pos <= span_z - 2)
        & (column_pos >= 1)
        & (column_pos <= span_x - 2)
        & (row_pos >= 1)
        & (row_pos <= span_y - 2)
    )
    unknown = jnp.where(interior, inside, 0.0)
    scaling = unknown / (diagonal + 1.0 - unknown)
    core_z = (depth_pos >= RIM) & (depth_pos < RIM + CCZ)
    core_x = (column_pos >= RIM) & (column_pos < RIM + CCX)
    core_y = (row_pos >= RIM) & (row_pos < RIM + CCY)
    face_x = ((column_pos == RIM - 1) | (column_pos == RIM + CCX - 1)) & core_z & core_y
    face_y = ((row_pos == RIM - 1) | (row_pos == RIM + CCY - 1)) & core_z & core_x
    face_z = ((depth_pos == RIM - 1) | (depth_pos == RIM + CCZ - 1)) & core_x & core_y
    ramp_x = ((span_x - 1) / 2.0 - column_pos).astype(jnp.float32)
    ramp_y = ((span_y - 1) / 2.0 - row_pos).astype(jnp.float32)
    ramp_z = ((span_z - 1) / 2.0 - depth_pos).astype(jnp.float32)
    cheb_ratio = BOUND_MID / BOUND_HALF
    cases = (
        (ramp_x, link_x, face_x, CCY * CCZ, up_x, down_x),
        (ramp_y, link_y, face_y, CCX * CCZ, up_y, down_y),
        (ramp_z, link_z, face_z, CCX * CCY, up_z, down_z),
    )
    rows = []
    for ramp, link, face, area, upper_of, lower_of in cases:
        source_term = -unknown * (link - lower_of(link))
        update = scaling * source_term / BOUND_MID
        solution = update
        rho_old = 1.0 / cheb_ratio
        for sweep_index in range(SWEEPS - 1):
            residual = source_term - apply_operator(solution)
            rho_new = 1.0 / (2.0 * cheb_ratio - rho_old)
            update = rho_new * rho_old * update + 2.0 * rho_new / BOUND_HALF * (scaling * residual)
            solution = solution + update
            rho_old = rho_new
        pressure = ramp + solution
        flux = jnp.where(face, link * (pressure - upper_of(pressure)), 0.0)
        total = jnp.sum(flux, axis=0)
        total = jnp.sum(total, axis=0, keepdims=True)
        rows.append(total * (0.5 / area))
    rows.append(jnp.zeros((8 - len(rows), LANES), jnp.float32))
    o_ref[0] = jnp.concatenate(rows, axis=0)


def upscale_windows(raw, facies_table, bounds, cols_len):
    span_y = CCY + 2 * RIM
    count_z = (raw.shape[1] - 2 * RIM) // CCZ
    count_x = (raw.shape[2] - 2 * RIM) // CCX
    count_y = cols_len // CCY
    count = count_z * count_x * count_y
    segments = LANES // span_y
    packs = -(-count // segments)
    kernel = functools.partial(window_kernel, count_x=count_x, count_y=count_y, count=count)
    sums = pl.pallas_call(
        kernel,
        grid=(packs,),
        in_specs=[
            pl.BlockSpec(memory_space=pltpu.SMEM),
            pl.BlockSpec(memory_space=pltpu.SMEM),
            pl.BlockSpec(raw.shape, lambda p: (0, 0, 0, 0)),
        ],
        out_specs=pl.BlockSpec((1, 8, LANES), lambda p: (p, 0, 0)),
        out_shape=jax.ShapeDtypeStruct((packs, 8, LANES), jnp.float32),
    )(facies_table, bounds, raw)
    sums = sums[:, :3, : segments * span_y].reshape(packs, 3, segments, span_y).sum(axis=3)
    sums = sums.transpose(1, 0, 2).reshape(3, packs * segments)[:, :count]
    return sums.reshape((3, count_z, count_x, count_y))


def coarse_sweep(perm_pad, press_pad, inside_pad, accumulation, fixed):
    centre = (slice(1, -1), slice(1, -1), slice(1, -1))
    factors = (CCY * CCZ / CCX, CCX * CCZ / CCY, CCX * CCY / CCZ)
    numer = fixed
    denom = accumulation
    for component, axis_dim in ((0, 1), (1, 2), (2, 0)):
        for offset in (-1, 1):
            window_slice = [slice(1, -1), slice(1, -1), slice(1, -1)]
            window_slice[axis_dim] = slice(1 + offset, press_pad.shape[axis_dim] - 1 + offset)
            beside = tuple(window_slice)
            link = (
                factors[component]
                * 0.5
                * (perm_pad[component][centre] + perm_pad[component][beside])
                * inside_pad[beside]
            )
            numer = numer + link * press_pad[beside]
            denom = denom + jnp.abs(link)
    return numer / denom


def span_mask(anchor, length, total, margin):
    coords = anchor - margin + jnp.arange(length + 2 * margin, dtype=jnp.int32)
    return ((coords >= 0) & (coords < total)).astype(jnp.float32)


def cut_windows(fields):
    span_z = CCZ + 2 * RIM
    span_x = CCX + 2 * RIM
    span_y = CCY + 2 * RIM
    count_z = (fields[0].shape[0] - 2 * RIM) // CCZ
    count_x = (fields[0].shape[1] - 2 * RIM) // CCX
    count_y = (fields[0].shape[2] - 2 * RIM) // CCY
    stacks = []
    for field in fields:
        pieces = []
        for block_z in range(count_z):
            for block_y in range(count_y):
                piece = field[
                    block_z * CCZ : block_z * CCZ + span_z,
                    0:span_x,
                    block_y * CCY : block_y * CCY + span_y,
                ]
                pieces.append(piece.reshape(span_z, span_x * span_y))
        stacks.append(jnp.stack(pieces))
    return (stacks, (count_z, count_x, count_y))


def faces(block, sides):
    got = []
    for axis, dim in sides:
        count = lax.axis_size(axis)
        ends = count - 1
        head = lax.slice_in_dim(block, 0, 1, axis=dim)
        tail = lax.slice_in_dim(block, block.shape[dim] - 1, block.shape[dim], axis=dim)
        lower = lax.ppermute(tail, axis, [(i, i + 1) for i in range(ends)])
        upper = lax.ppermute(head, axis, [(i + 1, i) for i in range(ends)])
        got.append((lower, upper))
    return got


def neighbour_views(block, got, dim_of):
    views = []
    for (lower, upper), dim in zip(got, dim_of):
        size = block.shape[dim]
        below = jnp.concatenate([lower, lax.slice_in_dim(block, 0, size - 1, axis=dim)], axis=dim)
        above = jnp.concatenate([lax.slice_in_dim(block, 1, size, axis=dim), upper], axis=dim)
        views.append((below, above))
    return views


def coarse_step(upscaled, views, inside_views, pressure, accumulation, fixed):
    factors = (CCY * CCZ / CCX, CCX * CCZ / CCY, CCX * CCY / CCZ)
    numer = fixed
    denom = accumulation
    for component in range(3):
        for side in range(2):
            beside = views[component][side]
            link = factors[component] * 0.5 * (upscaled[component] + beside[component]) * inside_views[component][side]
            numer = numer + link * pressure[component][side]
            denom = denom + jnp.abs(link)
    return numer / denom


def local(log_noise, facies, facies_table, pressure_old, accumulation, source):
    depth_len, rows_len, cols_len = log_noise.shape
    size_z = lax.axis_size("gz")
    size_x = lax.axis_size("gx")
    size_y = lax.axis_size("gy")
    index_z = lax.axis_index("gz")
    index_x = lax.axis_index("gx")
    index_y = lax.axis_index("gy")
    raw = jnp.stack([log_noise, facies.astype(jnp.float32)])
    wide = -(-(cols_len + 2 * RIM) // LANES) * LANES
    raw = extended(raw, (("gx", 2), ("gz", 1), ("gy", 3)), RIM, wide)
    anchor_z = index_z * depth_len
    anchor_y = index_y * cols_len
    anchor_x = index_x * rows_len
    bounds = jnp.stack(
        [
            RIM - anchor_z,
            depth_len * size_z + RIM - anchor_z,
            RIM - anchor_x,
            rows_len * size_x + RIM - anchor_x,
            RIM - anchor_y,
            cols_len * size_y + RIM - anchor_y,
        ]
    ).astype(jnp.int32)
    upscaled = upscale_windows(raw, facies_table, bounds, cols_len)
    coarse_z, coarse_x, coarse_y = pressure_old.shape
    bundle = jnp.stack([upscaled[0], upscaled[1], upscaled[2], pressure_old, accumulation, source])
    every = doubling_gather(bundle, "gy", 3)
    every = doubling_gather(every, "gx", 2)
    every = doubling_gather(every, "gz", 1)
    perm_pad = jnp.pad(every[:3], ((0, 0), (1, 1), (1, 1), (1, 1)))
    old_all = every[3]
    acc_all = every[4]
    fixed_all = acc_all * old_all + every[5]
    inside_pad = jnp.pad(jnp.ones(old_all.shape, jnp.float32), 1)
    pressure = old_all
    for sweep_index in range(2):
        pressure = coarse_sweep(perm_pad, jnp.pad(pressure, 1), inside_pad, acc_all, fixed_all)
    pressure = lax.dynamic_slice(
        pressure, (index_z * coarse_z, index_x * coarse_x, index_y * coarse_y), (coarse_z, coarse_x, coarse_y)
    )
    return (pressure, upscaled)


def solution(mesh):
    placed = (
        P(("real", "gz"), "gx", "gy"),
        P(("real", "gz"), "gx", "gy"),
        P(),
        P(("real", "gz"), "gx", "gy"),
        P(("real", "gz"), "gx", "gy"),
        P(("real", "gz"), "gx", "gy"),
    )
    return jax.shard_map(
        local,
        mesh=mesh,
        in_specs=placed,
        out_specs=(P(("real", "gz"), "gx", "gy"), P(None, ("real", "gz"), "gx", "gy")),
        check_vma=False,
    )
```

```python
import functools

import jax
import jax.numpy as jnp
from jax import lax
from jax.sharding import PartitionSpec as P
from jax.experimental import pallas as pl
from jax.experimental.pallas import tpu as pltpu

NFAC = 4
CCX = 32
CCY = 32
CCZ = 8
RIM = 4
SWEEPS = 3


BOUND_MID = 1.0
BOUND_HALF = 0.9


def extended(cells, sides, width, lanes=None):
    for axis, dim in sides:
        count = lax.axis_size(axis)
        ends = count - 1
        head = lax.slice_in_dim(cells, 0, width, axis=dim)
        tail = lax.slice_in_dim(cells, cells.shape[dim] - width, cells.shape[dim], axis=dim)
        if count == 2:
            lower_side = lax.axis_index(axis) == 0
            got = lax.ppermute(jnp.where(lower_side, tail, head), axis, [(0, 1), (1, 0)])
            below = got
            above = got
        elif count % 2 == 0:
            even = lax.axis_index(axis) % 2 == 0
            first = [(i, i ^ 1) for i in range(count)]
            second = [(i, i + 1 if i % 2 else i - 1) for i in range(1, count - 1)]
            got_first = lax.ppermute(jnp.where(even, tail, head), axis, first)
            got_second = lax.ppermute(jnp.where(even, head, tail), axis, second)
            below = jnp.where(even, got_second, got_first)
            above = jnp.where(even, got_first, got_second)
        else:
            below = lax.ppermute(tail, axis, [(i, (i + 1) % count) for i in range(ends)])
            above = lax.ppermute(head, axis, [((i + 1) % count, i) for i in range(ends)])
        if lanes is not None and dim == cells.ndim - 1:
            extra = lanes - (cells.shape[dim] + 2 * width)
            parts = [cells, above, jnp.zeros(cells.shape[:-1] + (extra,), cells.dtype), below]
        else:
            parts = [below, cells, above]
        cells = jnp.concatenate(parts, axis=dim)
    return cells


def doubling_gather(values, axis, dim):
    count = lax.axis_size(axis)
    if count & (count - 1):
        return lax.all_gather(values, axis, axis=dim, tiled=True)
    index = lax.axis_index(axis)
    step = 1
    while step < count:
        got = lax.ppermute(values, axis, [(i, i ^ step) for i in range(count)])
        lower = (index // step) % 2 == 0
        values = jnp.where(
            lower, jnp.concatenate([values, got], axis=dim), jnp.concatenate([got, values], axis=dim)
        )
        step *= 2
    return values


def raise_flat(values, offset):
    zeros_block = jnp.zeros(values.shape[:-1] + (offset,), values.dtype)
    return jnp.concatenate([values[..., offset:], zeros_block], axis=-1)


def lower_flat(values, offset):
    zeros_block = jnp.zeros(values.shape[:-1] + (offset,), values.dtype)
    return jnp.concatenate([zeros_block, values[..., :-offset]], axis=-1)


def raise_depth(values):
    zeros_block = jnp.zeros(values.shape[:1] + (1,) + values.shape[2:], values.dtype)
    return jnp.concatenate([values[:, 1:], zeros_block], axis=1)


def lower_depth(values):
    zeros_block = jnp.zeros(values.shape[:1] + (1,) + values.shape[2:], values.dtype)
    return jnp.concatenate([zeros_block, values[:, :-1]], axis=1)


def log_fields(log_noise, facies, facies_table):
    base_log = log_noise
    extra_y = jnp.zeros_like(log_noise)
    extra_z = jnp.zeros_like(log_noise)
    for code_value in range(NFAC):
        matched = facies == code_value
        base_log = base_log + jnp.where(matched, facies_table[0, code_value], jnp.float32(0.0))
        extra_y = extra_y + jnp.where(matched, facies_table[1, code_value], jnp.float32(0.0))
        extra_z = extra_z + jnp.where(matched, facies_table[2, code_value], jnp.float32(0.0))
    return (base_log, base_log + extra_y, base_log + extra_z)


def upscale(perm_logs, inside):
    span_z = CCZ + 2 * RIM
    span_x = CCX + 2 * RIM
    span_y = CCY + 2 * RIM
    depth_pos = lax.broadcasted_iota(jnp.int32, (1, span_z, 1), 1)
    flat_pos = lax.broadcasted_iota(jnp.int32, (1, 1, span_x * span_y), 2)
    column_pos = flat_pos // span_y
    row_pos = flat_pos % span_y
    perm_x = jnp.exp(perm_logs[0])
    perm_y = jnp.exp(perm_logs[1])
    perm_z = jnp.exp(perm_logs[2])

    def links(perm, other_perm, other_inside):
        return inside * other_inside * 2.0 * perm * other_perm / (perm + other_perm)

    link_x = links(perm_x, raise_flat(perm_x, span_y), raise_flat(inside, span_y))
    link_y = links(perm_y, raise_flat(perm_y, 1), raise_flat(inside, 1)) * (
        row_pos < span_y - 1
    ).astype(jnp.float32)
    link_z = links(perm_z, raise_depth(perm_z), raise_depth(inside))
    diagonal = (
        link_x
        + lower_flat(link_x, span_y)
        + link_y
        + lower_flat(link_y, 1)
        + link_z
        + lower_depth(link_z)
    )

    def apply_operator(field):
        beside = link_x * raise_flat(field, span_y) + lower_flat(link_x * field, span_y)
        beside = beside + link_y * raise_flat(field, 1) + lower_flat(link_y * field, 1)
        beside = beside + link_z * raise_depth(field) + lower_depth(link_z * field)
        return diagonal * field - beside

    interior = (
        (depth_pos >= 1)
        & (depth_pos <= span_z - 2)
        & (column_pos >= 1)
        & (column_pos <= span_x - 2)
        & (row_pos >= 1)
        & (row_pos <= span_y - 2)
    )
    unknown = inside * interior.astype(jnp.float32)
    scaling = unknown / (diagonal + 1.0 - unknown)
    core_z = (depth_pos >= RIM) & (depth_pos < RIM + CCZ)
    core_x = (column_pos >= RIM) & (column_pos < RIM + CCX)
    core_y = (row_pos >= RIM) & (row_pos < RIM + CCY)
    face_x = (((column_pos == RIM - 1) | (column_pos == RIM + CCX - 1)) & core_z & core_y).astype(
        jnp.float32
    )
    face_y = (((row_pos == RIM - 1) | (row_pos == RIM + CCY - 1)) & core_z & core_x).astype(
        jnp.float32
    )
    face_z = (((depth_pos == RIM - 1) | (depth_pos == RIM + CCZ - 1)) & core_x & core_y).astype(
        jnp.float32
    )
    ramp_x = ((span_x - 1) / 2.0 - column_pos).astype(jnp.float32)
    ramp_y = ((span_y - 1) / 2.0 - row_pos).astype(jnp.float32)
    ramp_z = ((span_z - 1) / 2.0 - depth_pos).astype(jnp.float32)
    cheb_ratio = BOUND_MID / BOUND_HALF
    results = []
    cases = (
        (ramp_x, link_x, face_x, CCY * CCZ, 0),
        (ramp_y, link_y, face_y, CCX * CCZ, 1),
        (ramp_z, link_z, face_z, CCX * CCY, 2),
    )
    for ramp, link, face, area, direction in cases:
        ramp_full = jnp.broadcast_to(ramp, inside.shape)
        source_term = -unknown * apply_operator(ramp_full)
        update = scaling * source_term / BOUND_MID
        solution = update
        rho_old = 1.0 / cheb_ratio
        for sweep_index in range(SWEEPS - 1):
            residual = source_term - apply_operator(solution)
            rho_new = 1.0 / (2.0 * cheb_ratio - rho_old)
            update = rho_new * rho_old * update + 2.0 * rho_new / BOUND_HALF * (scaling * residual)
            solution = solution + update
            rho_old = rho_new
        pressure = ramp_full + solution
        if direction == 0:
            upper = raise_flat(pressure, span_y)
        elif direction == 1:
            upper = raise_flat(pressure, 1)
        else:
            upper = raise_depth(pressure)
        flux = link * (pressure - upper) * face
        results.append(jnp.sum(flux, axis=(1, 2)) * (0.5 / area))
    return jnp.stack(results)


LANES = 128


def window_kernel(table_ref, bounds_ref, raw_ref, o_ref, *, count_x, count_y, count):
    span_z = CCZ + 2 * RIM
    span_x = CCX + 2 * RIM
    span_y = CCY + 2 * RIM
    segments = LANES // span_y
    shape = (span_z, span_x, LANES)
    pack = pl.program_id(0)
    wide = raw_ref.shape[-1]
    depth_pos = lax.broadcasted_iota(jnp.int32, shape, 0)
    column_pos = lax.broadcasted_iota(jnp.int32, shape, 1)
    lane = lax.broadcasted_iota(jnp.int32, shape, 2)
    segment = jnp.zeros(shape, jnp.int32)
    for bound in range(1, segments + 1):
        segment = segment + (lane >= bound * span_y).astype(jnp.int32)
    row_pos = lane - span_y * segment
    noise = jnp.zeros(shape, jnp.float32)
    codes = jnp.zeros(shape, jnp.float32)
    inside = jnp.zeros(shape, jnp.float32)
    for slot in range(segments):
        window = pack * segments + slot
        valid = window < count
        window = jnp.minimum(window, count - 1)
        block_z = window // (count_x * count_y)
        block_x = (window // count_y) % count_x
        block_y = window % count_y
        shift = (slot * span_y - block_y * CCY + RIM + wide) % wide
        here = segment == slot

        def cut(field):
            slab = raw_ref[field, pl.ds(block_z * CCZ, span_z), pl.ds(block_x * CCX, span_x), :]
            return pltpu.roll(slab, shift, 2)[:, :, :LANES]

        depth_at = depth_pos + block_z * CCZ
        column_at = column_pos + block_x * CCX
        row_at = row_pos + block_y * CCY
        held = (
            (depth_at >= bounds_ref[0])
            & (depth_at < bounds_ref[1])
            & (column_at >= bounds_ref[2])
            & (column_at < bounds_ref[3])
            & (row_at >= bounds_ref[4])
            & (row_at < bounds_ref[5])
        )
        noise = jnp.where(here, cut(0), noise)
        codes = jnp.where(here, cut(1), codes)
        inside = jnp.where(here & valid & held, 1.0, inside)

    def lookup(row):
        value = jnp.zeros(shape, jnp.float32)
        for code_value in range(NFAC):
            value = jnp.where(codes == code_value, table_ref[row, code_value], value)
        return value

    log_x = noise + lookup(0)
    log_y = log_x + lookup(1)
    log_z = log_x + lookup(2)
    perm_x = jnp.exp(log_x)
    perm_y = jnp.exp(log_y)
    perm_z = jnp.exp(log_z)

    def up_x(v):
        return pltpu.roll(v, span_x - 1, 1)

    def down_x(v):
        return pltpu.roll(v, 1, 1)

    def up_y(v):
        return pltpu.roll(v, LANES - 1, 2)

    def down_y(v):
        return pltpu.roll(v, 1, 2)

    def up_z(v):
        return jnp.concatenate([v[1:], v[:1]], axis=0)

    def down_z(v):
        return jnp.concatenate([v[-1:], v[:-1]], axis=0)

    def links(perm, other_perm, other_inside, valid):
        value = inside * other_inside * 2.0 * perm * other_perm / (perm + other_perm)
        return jnp.where(valid, value, 0.0)

    link_x = links(perm_x, up_x(perm_x), up_x(inside), column_pos < span_x - 1)
    link_y = links(perm_y, up_y(perm_y), up_y(inside), row_pos < span_y - 1)
    link_z = links(perm_z, up_z(perm_z), up_z(inside), depth_pos < span_z - 1)
    diagonal = link_x + down_x(link_x) + link_y + down_y(link_y) + link_z + down_z(link_z)

    def apply_operator(field):
        beside = link_x * up_x(field) + down_x(link_x * field)
        beside = beside + link_y * up_y(field) + down_y(link_y * field)
        beside = beside + link_z * up_z(field) + down_z(link_z * field)
        return diagonal * field - beside

    interior = (
        (depth_pos >= 1)
        & (depth_pos <= span_z - 2)
        & (column_pos >= 1)
        & (column_pos <= span_x - 2)
        & (row_pos >= 1)
        & (row_pos <= span_y - 2)
    )
    unknown = jnp.where(interior, inside, 0.0)
    scaling = unknown / (diagonal + 1.0 - unknown)
    core_z = (depth_pos >= RIM) & (depth_pos < RIM + CCZ)
    core_x = (column_pos >= RIM) & (column_pos < RIM + CCX)
    core_y = (row_pos >= RIM) & (row_pos < RIM + CCY)
    face_x = ((column_pos == RIM - 1) | (column_pos == RIM + CCX - 1)) & core_z & core_y
    face_y = ((row_pos == RIM - 1) | (row_pos == RIM + CCY - 1)) & core_z & core_x
    face_z = ((depth_pos == RIM - 1) | (depth_pos == RIM + CCZ - 1)) & core_x & core_y
    ramp_x = ((span_x - 1) / 2.0 - column_pos).astype(jnp.float32)
    ramp_y = ((span_y - 1) / 2.0 - row_pos).astype(jnp.float32)
    ramp_z = ((span_z - 1) / 2.0 - depth_pos).astype(jnp.float32)
    cheb_ratio = BOUND_MID / BOUND_HALF
    cases = (
        (ramp_x, link_x, face_x, CCY * CCZ, up_x, down_x),
        (ramp_y, link_y, face_y, CCX * CCZ, up_y, down_y),
        (ramp_z, link_z, face_z, CCX * CCY, up_z, down_z),
    )
    rows = []
    for ramp, link, face, area, upper_of, lower_of in cases:
        source_term = -unknown * (link - lower_of(link))
        update = scaling * source_term / BOUND_MID
        solution = update
        rho_old = 1.0 / cheb_ratio
        for sweep_index in range(SWEEPS - 1):
            residual = source_term - apply_operator(solution)
            rho_new = 1.0 / (2.0 * cheb_ratio - rho_old)
            update = rho_new * rho_old * update + 2.0 * rho_new / BOUND_HALF * (scaling * residual)
            solution = solution + update
            rho_old = rho_new
        pressure = ramp + solution
        flux = jnp.where(face, link * (pressure - upper_of(pressure)), 0.0)
        total = jnp.sum(flux, axis=0)
        total = jnp.sum(total, axis=0, keepdims=True)
        rows.append(total * (0.5 / area))
    rows.append(jnp.zeros((8 - len(rows), LANES), jnp.float32))
    o_ref[0] = jnp.concatenate(rows, axis=0)


def upscale_windows(raw, facies_table, bounds, cols_len):
    span_y = CCY + 2 * RIM
    count_z = (raw.shape[1] - 2 * RIM) // CCZ
    count_x = (raw.shape[2] - 2 * RIM) // CCX
    count_y = cols_len // CCY
    count = count_z * count_x * count_y
    segments = LANES // span_y
    packs = -(-count // segments)
    kernel = functools.partial(window_kernel, count_x=count_x, count_y=count_y, count=count)
    sums = pl.pallas_call(
        kernel,
        grid=(packs,),
        in_specs=[
            pl.BlockSpec(memory_space=pltpu.SMEM),
            pl.BlockSpec(memory_space=pltpu.SMEM),
            pl.BlockSpec(raw.shape, lambda p: (0, 0, 0, 0)),
        ],
        out_specs=pl.BlockSpec((1, 8, LANES), lambda p: (p, 0, 0)),
        out_shape=jax.ShapeDtypeStruct((packs, 8, LANES), jnp.float32),
    )(facies_table, bounds, raw)
    sums = sums[:, :3, : segments * span_y].reshape(packs, 3, segments, span_y).sum(axis=3)
    sums = sums.transpose(1, 0, 2).reshape(3, packs * segments)[:, :count]
    return sums.reshape((3, count_z, count_x, count_y))


def coarse_sweep(perm_pad, press_pad, inside_pad, accumulation, fixed):
    centre = (slice(1, -1), slice(1, -1), slice(1, -1))
    factors = (CCY * CCZ / CCX, CCX * CCZ / CCY, CCX * CCY / CCZ)
    numer = fixed
    denom = accumulation
    for component, axis_dim in ((0, 1), (1, 2), (2, 0)):
        for offset in (-1, 1):
            window_slice = [slice(1, -1), slice(1, -1), slice(1, -1)]
            window_slice[axis_dim] = slice(1 + offset, press_pad.shape[axis_dim] - 1 + offset)
            beside = tuple(window_slice)
            link = (
                factors[component]
                * 0.5
                * (perm_pad[component][centre] + perm_pad[component][beside])
                * inside_pad[beside]
            )
            numer = numer + link * press_pad[beside]
            denom = denom + jnp.abs(link)
    return numer / denom


def span_mask(anchor, length, total, margin):
    coords = anchor - margin + jnp.arange(length + 2 * margin, dtype=jnp.int32)
    return ((coords >= 0) & (coords < total)).astype(jnp.float32)


def cut_windows(fields):
    span_z = CCZ + 2 * RIM
    span_x = CCX + 2 * RIM
    span_y = CCY + 2 * RIM
    count_z = (fields[0].shape[0] - 2 * RIM) // CCZ
    count_x = (fields[0].shape[1] - 2 * RIM) // CCX
    count_y = (fields[0].shape[2] - 2 * RIM) // CCY
    stacks = []
    for field in fields:
        pieces = []
        for block_z in range(count_z):
            for block_y in range(count_y):
                piece = field[
                    block_z * CCZ : block_z * CCZ + span_z,
                    0:span_x,
                    block_y * CCY : block_y * CCY + span_y,
                ]
                pieces.append(piece.reshape(span_z, span_x * span_y))
        stacks.append(jnp.stack(pieces))
    return (stacks, (count_z, count_x, count_y))


def faces(block, sides):
    got = []
    for axis, dim in sides:
        count = lax.axis_size(axis)
        ends = count - 1
        head = lax.slice_in_dim(block, 0, 1, axis=dim)
        tail = lax.slice_in_dim(block, block.shape[dim] - 1, block.shape[dim], axis=dim)
        lower = lax.ppermute(tail, axis, [(i, i + 1) for i in range(ends)])
        upper = lax.ppermute(head, axis, [(i + 1, i) for i in range(ends)])
        got.append((lower, upper))
    return got


def neighbour_views(block, got, dim_of):
    views = []
    for (lower, upper), dim in zip(got, dim_of):
        size = block.shape[dim]
        below = jnp.concatenate([lower, lax.slice_in_dim(block, 0, size - 1, axis=dim)], axis=dim)
        above = jnp.concatenate([lax.slice_in_dim(block, 1, size, axis=dim), upper], axis=dim)
        views.append((below, above))
    return views


def coarse_step(upscaled, views, inside_views, pressure, accumulation, fixed):
    factors = (CCY * CCZ / CCX, CCX * CCZ / CCY, CCX * CCY / CCZ)
    numer = fixed
    denom = accumulation
    for component in range(3):
        for side in range(2):
            beside = views[component][side]
            link = factors[component] * 0.5 * (upscaled[component] + beside[component]) * inside_views[component][side]
            numer = numer + link * pressure[component][side]
            denom = denom + jnp.abs(link)
    return numer / denom


def local(log_noise, facies, facies_table, pressure_old, accumulation, source):
    depth_len, rows_len, cols_len = log_noise.shape
    size_z = lax.axis_size("gz")
    size_x = lax.axis_size("gx")
    size_y = lax.axis_size("gy")
    index_z = lax.axis_index("gz")
    index_x = lax.axis_index("gx")
    index_y = lax.axis_index("gy")
    raw = jnp.stack([log_noise, facies.astype(jnp.float32)])
    wide = -(-(cols_len + 2 * RIM) // LANES) * LANES
    raw = extended(raw, (("gx", 2), ("gy", 3), ("gz", 1)), RIM, wide)
    anchor_z = index_z * depth_len
    anchor_y = index_y * cols_len
    anchor_x = index_x * rows_len
    bounds = jnp.stack(
        [
            RIM - anchor_z,
            depth_len * size_z + RIM - anchor_z,
            RIM - anchor_x,
            rows_len * size_x + RIM - anchor_x,
            RIM - anchor_y,
            cols_len * size_y + RIM - anchor_y,
        ]
    ).astype(jnp.int32)
    upscaled = upscale_windows(raw, facies_table, bounds, cols_len)
    coarse_z, coarse_x, coarse_y = pressure_old.shape
    bundle = jnp.stack([upscaled[0], upscaled[1], upscaled[2], pressure_old, accumulation, source])
    every = doubling_gather(bundle, "gy", 3)
    every = doubling_gather(every, "gx", 2)
    every = doubling_gather(every, "gz", 1)
    perm_pad = jnp.pad(every[:3], ((0, 0), (1, 1), (1, 1), (1, 1)))
    old_all = every[3]
    acc_all = every[4]
    fixed_all = acc_all * old_all + every[5]
    inside_pad = jnp.pad(jnp.ones(old_all.shape, jnp.float32), 1)
    pressure = old_all
    for sweep_index in range(2):
        pressure = coarse_sweep(perm_pad, jnp.pad(pressure, 1), inside_pad, acc_all, fixed_all)
    pressure = lax.dynamic_slice(
        pressure, (index_z * coarse_z, index_x * coarse_x, index_y * coarse_y), (coarse_z, coarse_x, coarse_y)
    )
    return (pressure, upscaled)


def solution(mesh):
    placed = (
        P(("real", "gz"), "gx", "gy"),
        P(("real", "gz"), "gx", "gy"),
        P(),
        P(("real", "gz"), "gx", "gy"),
        P(("real", "gz"), "gx", "gy"),
        P(("real", "gz"), "gx", "gy"),
    )
    return jax.shard_map(
        local,
        mesh=mesh,
        in_specs=placed,
        out_specs=(P(("real", "gz"), "gx", "gy"), P(None, ("real", "gz"), "gx", "gy")),
        check_vma=False,
    )
```

```python
import functools

import jax
import jax.numpy as jnp
from jax import lax
from jax.sharding import PartitionSpec as P
from jax.experimental import pallas as pl
from jax.experimental.pallas import tpu as pltpu

NFAC = 4
CCX = 32
CCY = 32
CCZ = 8
RIM = 4
SWEEPS = 3


BOUND_MID = 1.0
BOUND_HALF = 0.9


def extended(cells, sides, width, lanes=None):
    for axis, dim in sides:
        count = lax.axis_size(axis)
        ends = count - 1
        head = lax.slice_in_dim(cells, 0, width, axis=dim)
        tail = lax.slice_in_dim(cells, cells.shape[dim] - width, cells.shape[dim], axis=dim)
        if count == 2:
            lower_side = lax.axis_index(axis) == 0
            got = lax.ppermute(jnp.where(lower_side, tail, head), axis, [(0, 1), (1, 0)])
            below = got
            above = got
        elif count % 2 == 0:
            even = lax.axis_index(axis) % 2 == 0
            first = [(i, i ^ 1) for i in range(count)]
            second = [(i, i + 1 if i % 2 else i - 1) for i in range(1, count - 1)]
            got_first = lax.ppermute(jnp.where(even, tail, head), axis, first)
            got_second = lax.ppermute(jnp.where(even, head, tail), axis, second)
            below = jnp.where(even, got_second, got_first)
            above = jnp.where(even, got_first, got_second)
        else:
            below = lax.ppermute(tail, axis, [(i, (i + 1) % count) for i in range(ends)])
            above = lax.ppermute(head, axis, [((i + 1) % count, i) for i in range(ends)])
        if lanes is not None and dim == cells.ndim - 1:
            extra = lanes - (cells.shape[dim] + 2 * width)
            parts = [cells, above, jnp.zeros(cells.shape[:-1] + (extra,), cells.dtype), below]
        else:
            parts = [below, cells, above]
        cells = jnp.concatenate(parts, axis=dim)
    return cells


def doubling_gather(values, axis, dim):
    count = lax.axis_size(axis)
    if count & (count - 1):
        return lax.all_gather(values, axis, axis=dim, tiled=True)
    index = lax.axis_index(axis)
    step = 1
    while step < count:
        got = lax.ppermute(values, axis, [(i, i ^ step) for i in range(count)])
        lower = (index // step) % 2 == 0
        values = jnp.where(
            lower, jnp.concatenate([values, got], axis=dim), jnp.concatenate([got, values], axis=dim)
        )
        step *= 2
    return values


def raise_flat(values, offset):
    zeros_block = jnp.zeros(values.shape[:-1] + (offset,), values.dtype)
    return jnp.concatenate([values[..., offset:], zeros_block], axis=-1)


def lower_flat(values, offset):
    zeros_block = jnp.zeros(values.shape[:-1] + (offset,), values.dtype)
    return jnp.concatenate([zeros_block, values[..., :-offset]], axis=-1)


def raise_depth(values):
    zeros_block = jnp.zeros(values.shape[:1] + (1,) + values.shape[2:], values.dtype)
    return jnp.concatenate([values[:, 1:], zeros_block], axis=1)


def lower_depth(values):
    zeros_block = jnp.zeros(values.shape[:1] + (1,) + values.shape[2:], values.dtype)
    return jnp.concatenate([zeros_block, values[:, :-1]], axis=1)


def log_fields(log_noise, facies, facies_table):
    base_log = log_noise
    extra_y = jnp.zeros_like(log_noise)
    extra_z = jnp.zeros_like(log_noise)
    for code_value in range(NFAC):
        matched = facies == code_value
        base_log = base_log + jnp.where(matched, facies_table[0, code_value], jnp.float32(0.0))
        extra_y = extra_y + jnp.where(matched, facies_table[1, code_value], jnp.float32(0.0))
        extra_z = extra_z + jnp.where(matched, facies_table[2, code_value], jnp.float32(0.0))
    return (base_log, base_log + extra_y, base_log + extra_z)


def upscale(perm_logs, inside):
    span_z = CCZ + 2 * RIM
    span_x = CCX + 2 * RIM
    span_y = CCY + 2 * RIM
    depth_pos = lax.broadcasted_iota(jnp.int32, (1, span_z, 1), 1)
    flat_pos = lax.broadcasted_iota(jnp.int32, (1, 1, span_x * span_y), 2)
    column_pos = flat_pos // span_y
    row_pos = flat_pos % span_y
    perm_x = jnp.exp(perm_logs[0])
    perm_y = jnp.exp(perm_logs[1])
    perm_z = jnp.exp(perm_logs[2])

    def links(perm, other_perm, other_inside):
        return inside * other_inside * 2.0 * perm * other_perm / (perm + other_perm)

    link_x = links(perm_x, raise_flat(perm_x, span_y), raise_flat(inside, span_y))
    link_y = links(perm_y, raise_flat(perm_y, 1), raise_flat(inside, 1)) * (
        row_pos < span_y - 1
    ).astype(jnp.float32)
    link_z = links(perm_z, raise_depth(perm_z), raise_depth(inside))
    diagonal = (
        link_x
        + lower_flat(link_x, span_y)
        + link_y
        + lower_flat(link_y, 1)
        + link_z
        + lower_depth(link_z)
    )

    def apply_operator(field):
        beside = link_x * raise_flat(field, span_y) + lower_flat(link_x * field, span_y)
        beside = beside + link_y * raise_flat(field, 1) + lower_flat(link_y * field, 1)
        beside = beside + link_z * raise_depth(field) + lower_depth(link_z * field)
        return diagonal * field - beside

    interior = (
        (depth_pos >= 1)
        & (depth_pos <= span_z - 2)
        & (column_pos >= 1)
        & (column_pos <= span_x - 2)
        & (row_pos >= 1)
        & (row_pos <= span_y - 2)
    )
    unknown = inside * interior.astype(jnp.float32)
    scaling = unknown / (diagonal + 1.0 - unknown)
    core_z = (depth_pos >= RIM) & (depth_pos < RIM + CCZ)
    core_x = (column_pos >= RIM) & (column_pos < RIM + CCX)
    core_y = (row_pos >= RIM) & (row_pos < RIM + CCY)
    face_x = (((column_pos == RIM - 1) | (column_pos == RIM + CCX - 1)) & core_z & core_y).astype(
        jnp.float32
    )
    face_y = (((row_pos == RIM - 1) | (row_pos == RIM + CCY - 1)) & core_z & core_x).astype(
        jnp.float32
    )
    face_z = (((depth_pos == RIM - 1) | (depth_pos == RIM + CCZ - 1)) & core_x & core_y).astype(
        jnp.float32
    )
    ramp_x = ((span_x - 1) / 2.0 - column_pos).astype(jnp.float32)
    ramp_y = ((span_y - 1) / 2.0 - row_pos).astype(jnp.float32)
    ramp_z = ((span_z - 1) / 2.0 - depth_pos).astype(jnp.float32)
    cheb_ratio = BOUND_MID / BOUND_HALF
    results = []
    cases = (
        (ramp_x, link_x, face_x, CCY * CCZ, 0),
        (ramp_y, link_y, face_y, CCX * CCZ, 1),
        (ramp_z, link_z, face_z, CCX * CCY, 2),
    )
    for ramp, link, face, area, direction in cases:
        ramp_full = jnp.broadcast_to(ramp, inside.shape)
        source_term = -unknown * apply_operator(ramp_full)
        update = scaling * source_term / BOUND_MID
        solution = update
        rho_old = 1.0 / cheb_ratio
        for sweep_index in range(SWEEPS - 1):
            residual = source_term - apply_operator(solution)
            rho_new = 1.0 / (2.0 * cheb_ratio - rho_old)
            update = rho_new * rho_old * update + 2.0 * rho_new / BOUND_HALF * (scaling * residual)
            solution = solution + update
            rho_old = rho_new
        pressure = ramp_full + solution
        if direction == 0:
            upper = raise_flat(pressure, span_y)
        elif direction == 1:
            upper = raise_flat(pressure, 1)
        else:
            upper = raise_depth(pressure)
        flux = link * (pressure - upper) * face
        results.append(jnp.sum(flux, axis=(1, 2)) * (0.5 / area))
    return jnp.stack(results)


LANES = 128


def window_kernel(table_ref, bounds_ref, raw_ref, o_ref, *, count_x, count_y, count):
    span_z = CCZ + 2 * RIM
    span_x = CCX + 2 * RIM
    span_y = CCY + 2 * RIM
    segments = LANES // span_y
    shape = (span_z, span_x, LANES)
    pack = pl.program_id(0)
    wide = raw_ref.shape[-1]
    depth_pos = lax.broadcasted_iota(jnp.int32, shape, 0)
    column_pos = lax.broadcasted_iota(jnp.int32, shape, 1)
    lane = lax.broadcasted_iota(jnp.int32, shape, 2)
    segment = jnp.zeros(shape, jnp.int32)
    for bound in range(1, segments + 1):
        segment = segment + (lane >= bound * span_y).astype(jnp.int32)
    row_pos = lane - span_y * segment
    noise = jnp.zeros(shape, jnp.float32)
    codes = jnp.zeros(shape, jnp.float32)
    inside = jnp.zeros(shape, jnp.float32)
    for slot in range(segments):
        window = pack * segments + slot
        valid = window < count
        window = jnp.minimum(window, count - 1)
        block_z = window // (count_x * count_y)
        block_x = (window // count_y) % count_x
        block_y = window % count_y
        shift = (slot * span_y - block_y * CCY + RIM + wide) % wide
        here = segment == slot

        def cut(field):
            slab = raw_ref[field, pl.ds(block_z * CCZ, span_z), pl.ds(block_x * CCX, span_x), :]
            return pltpu.roll(slab, shift, 2)[:, :, :LANES]

        depth_at = depth_pos + block_z * CCZ
        column_at = column_pos + block_x * CCX
        row_at = row_pos + block_y * CCY
        held = (
            (depth_at >= bounds_ref[0])
            & (depth_at < bounds_ref[1])
            & (column_at >= bounds_ref[2])
            & (column_at < bounds_ref[3])
            & (row_at >= bounds_ref[4])
            & (row_at < bounds_ref[5])
        )
        noise = jnp.where(here, cut(0), noise)
        codes = jnp.where(here, cut(1), codes)
        inside = jnp.where(here & valid & held, 1.0, inside)

    def lookup(row):
        value = jnp.zeros(shape, jnp.float32)
        for code_value in range(NFAC):
            value = jnp.where(codes == code_value, table_ref[row, code_value], value)
        return value

    log_x = noise + lookup(0)
    log_y = log_x + lookup(1)
    log_z = log_x + lookup(2)
    perm_x = jnp.exp(log_x)
    perm_y = jnp.exp(log_y)
    perm_z = jnp.exp(log_z)

    def up_x(v):
        return pltpu.roll(v, span_x - 1, 1)

    def down_x(v):
        return pltpu.roll(v, 1, 1)

    def up_y(v):
        return pltpu.roll(v, LANES - 1, 2)

    def down_y(v):
        return pltpu.roll(v, 1, 2)

    def up_z(v):
        return jnp.concatenate([v[1:], v[:1]], axis=0)

    def down_z(v):
        return jnp.concatenate([v[-1:], v[:-1]], axis=0)

    def links(perm, other_perm, other_inside, valid):
        value = inside * other_inside * 2.0 * perm * other_perm / (perm + other_perm)
        return jnp.where(valid, value, 0.0)

    link_x = links(perm_x, up_x(perm_x), up_x(inside), column_pos < span_x - 1)
    link_y = links(perm_y, up_y(perm_y), up_y(inside), row_pos < span_y - 1)
    link_z = links(perm_z, up_z(perm_z), up_z(inside), depth_pos < span_z - 1)
    diagonal = link_x + down_x(link_x) + link_y + down_y(link_y) + link_z + down_z(link_z)

    def apply_operator(field):
        beside = link_x * up_x(field) + down_x(link_x * field)
        beside = beside + link_y * up_y(field) + down_y(link_y * field)
        beside = beside + link_z * up_z(field) + down_z(link_z * field)
        return diagonal * field - beside

    interior = (
        (depth_pos >= 1)
        & (depth_pos <= span_z - 2)
        & (column_pos >= 1)
        & (column_pos <= span_x - 2)
        & (row_pos >= 1)
        & (row_pos <= span_y - 2)
    )
    unknown = jnp.where(interior, inside, 0.0)
    scaling = unknown / (diagonal + 1.0 - unknown)
    core_z = (depth_pos >= RIM) & (depth_pos < RIM + CCZ)
    core_x = (column_pos >= RIM) & (column_pos < RIM + CCX)
    core_y = (row_pos >= RIM) & (row_pos < RIM + CCY)
    face_x = ((column_pos == RIM - 1) | (column_pos == RIM + CCX - 1)) & core_z & core_y
    face_y = ((row_pos == RIM - 1) | (row_pos == RIM + CCY - 1)) & core_z & core_x
    face_z = ((depth_pos == RIM - 1) | (depth_pos == RIM + CCZ - 1)) & core_x & core_y
    ramp_x = ((span_x - 1) / 2.0 - column_pos).astype(jnp.float32)
    ramp_y = ((span_y - 1) / 2.0 - row_pos).astype(jnp.float32)
    ramp_z = ((span_z - 1) / 2.0 - depth_pos).astype(jnp.float32)
    cheb_ratio = BOUND_MID / BOUND_HALF
    cases = (
        (ramp_x, link_x, face_x, CCY * CCZ, up_x, down_x),
        (ramp_y, link_y, face_y, CCX * CCZ, up_y, down_y),
        (ramp_z, link_z, face_z, CCX * CCY, up_z, down_z),
    )
    rows = []
    for ramp, link, face, area, upper_of, lower_of in cases:
        source_term = -unknown * (link - lower_of(link))
        update = scaling * source_term / BOUND_MID
        solution = update
        rho_old = 1.0 / cheb_ratio
        for sweep_index in range(SWEEPS - 1):
            residual = source_term - apply_operator(solution)
            rho_new = 1.0 / (2.0 * cheb_ratio - rho_old)
            update = rho_new * rho_old * update + 2.0 * rho_new / BOUND_HALF * (scaling * residual)
            solution = solution + update
            rho_old = rho_new
        pressure = ramp + solution
        flux = jnp.where(face, link * (pressure - upper_of(pressure)), 0.0)
        total = jnp.sum(flux, axis=0)
        total = jnp.sum(total, axis=0, keepdims=True)
        rows.append(total * (0.5 / area))
    o_ref[0] = jnp.concatenate(rows, axis=0)


def upscale_windows(raw, facies_table, bounds, cols_len):
    span_y = CCY + 2 * RIM
    count_z = (raw.shape[1] - 2 * RIM) // CCZ
    count_x = (raw.shape[2] - 2 * RIM) // CCX
    count_y = cols_len // CCY
    count = count_z * count_x * count_y
    segments = LANES // span_y
    packs = -(-count // segments)
    kernel = functools.partial(window_kernel, count_x=count_x, count_y=count_y, count=count)
    sums = pl.pallas_call(
        kernel,
        grid=(packs,),
        in_specs=[
            pl.BlockSpec(memory_space=pltpu.SMEM),
            pl.BlockSpec(memory_space=pltpu.SMEM),
            pl.BlockSpec(raw.shape, lambda p: (0, 0, 0, 0)),
        ],
        out_specs=pl.BlockSpec((1, 3, LANES), lambda p: (p, 0, 0)),
        out_shape=jax.ShapeDtypeStruct((packs, 3, LANES), jnp.float32),
    )(facies_table, bounds, raw)
    sums = sums[:, :, : segments * span_y].reshape(packs, 3, segments, span_y).sum(axis=3)
    sums = sums.transpose(1, 0, 2).reshape(3, packs * segments)[:, :count]
    return sums.reshape((3, count_z, count_x, count_y))


def coarse_sweep(perm_pad, press_pad, inside_pad, accumulation, fixed):
    centre = (slice(1, -1), slice(1, -1), slice(1, -1))
    factors = (CCY * CCZ / CCX, CCX * CCZ / CCY, CCX * CCY / CCZ)
    numer = fixed
    denom = accumulation
    for component, axis_dim in ((0, 1), (1, 2), (2, 0)):
        for offset in (-1, 1):
            window_slice = [slice(1, -1), slice(1, -1), slice(1, -1)]
            window_slice[axis_dim] = slice(1 + offset, press_pad.shape[axis_dim] - 1 + offset)
            beside = tuple(window_slice)
            link = (
                factors[component]
                * 0.5
                * (perm_pad[component][centre] + perm_pad[component][beside])
                * inside_pad[beside]
            )
            numer = numer + link * press_pad[beside]
            denom = denom + jnp.abs(link)
    return numer / denom


def span_mask(anchor, length, total, margin):
    coords = anchor - margin + jnp.arange(length + 2 * margin, dtype=jnp.int32)
    return ((coords >= 0) & (coords < total)).astype(jnp.float32)


def cut_windows(fields):
    span_z = CCZ + 2 * RIM
    span_x = CCX + 2 * RIM
    span_y = CCY + 2 * RIM
    count_z = (fields[0].shape[0] - 2 * RIM) // CCZ
    count_x = (fields[0].shape[1] - 2 * RIM) // CCX
    count_y = (fields[0].shape[2] - 2 * RIM) // CCY
    stacks = []
    for field in fields:
        pieces = []
        for block_z in range(count_z):
            for block_y in range(count_y):
                piece = field[
                    block_z * CCZ : block_z * CCZ + span_z,
                    0:span_x,
                    block_y * CCY : block_y * CCY + span_y,
                ]
                pieces.append(piece.reshape(span_z, span_x * span_y))
        stacks.append(jnp.stack(pieces))
    return (stacks, (count_z, count_x, count_y))


def faces(block, sides):
    got = []
    for axis, dim in sides:
        count = lax.axis_size(axis)
        ends = count - 1
        head = lax.slice_in_dim(block, 0, 1, axis=dim)
        tail = lax.slice_in_dim(block, block.shape[dim] - 1, block.shape[dim], axis=dim)
        lower = lax.ppermute(tail, axis, [(i, i + 1) for i in range(ends)])
        upper = lax.ppermute(head, axis, [(i + 1, i) for i in range(ends)])
        got.append((lower, upper))
    return got


def neighbour_views(block, got, dim_of):
    views = []
    for (lower, upper), dim in zip(got, dim_of):
        size = block.shape[dim]
        below = jnp.concatenate([lower, lax.slice_in_dim(block, 0, size - 1, axis=dim)], axis=dim)
        above = jnp.concatenate([lax.slice_in_dim(block, 1, size, axis=dim), upper], axis=dim)
        views.append((below, above))
    return views


def coarse_step(upscaled, views, inside_views, pressure, accumulation, fixed):
    factors = (CCY * CCZ / CCX, CCX * CCZ / CCY, CCX * CCY / CCZ)
    numer = fixed
    denom = accumulation
    for component in range(3):
        for side in range(2):
            beside = views[component][side]
            link = factors[component] * 0.5 * (upscaled[component] + beside[component]) * inside_views[component][side]
            numer = numer + link * pressure[component][side]
            denom = denom + jnp.abs(link)
    return numer / denom


def local(log_noise, facies, facies_table, pressure_old, accumulation, source):
    depth_len, rows_len, cols_len = log_noise.shape
    size_z = lax.axis_size("gz")
    size_x = lax.axis_size("gx")
    size_y = lax.axis_size("gy")
    index_z = lax.axis_index("gz")
    index_x = lax.axis_index("gx")
    index_y = lax.axis_index("gy")
    raw = jnp.stack([log_noise, facies.astype(jnp.float32)])
    wide = -(-(cols_len + 2 * RIM) // LANES) * LANES
    raw = extended(raw, (("gx", 2), ("gz", 1), ("gy", 3)), RIM, wide)
    anchor_z = index_z * depth_len
    anchor_y = index_y * cols_len
    anchor_x = index_x * rows_len
    bounds = jnp.stack(
        [
            RIM - anchor_z,
            depth_len * size_z + RIM - anchor_z,
            RIM - anchor_x,
            rows_len * size_x + RIM - anchor_x,
            RIM - anchor_y,
            cols_len * size_y + RIM - anchor_y,
        ]
    ).astype(jnp.int32)
    upscaled = upscale_windows(raw, facies_table, bounds, cols_len)
    coarse_z, coarse_x, coarse_y = pressure_old.shape
    bundle = jnp.stack([upscaled[0], upscaled[1], upscaled[2], pressure_old, accumulation, source])
    every = doubling_gather(bundle, "gy", 3)
    every = doubling_gather(every, "gx", 2)
    every = doubling_gather(every, "gz", 1)
    perm_pad = jnp.pad(every[:3], ((0, 0), (1, 1), (1, 1), (1, 1)))
    old_all = every[3]
    acc_all = every[4]
    fixed_all = acc_all * old_all + every[5]
    inside_pad = jnp.pad(jnp.ones(old_all.shape, jnp.float32), 1)
    pressure = old_all
    for sweep_index in range(2):
        pressure = coarse_sweep(perm_pad, jnp.pad(pressure, 1), inside_pad, acc_all, fixed_all)
    pressure = lax.dynamic_slice(
        pressure, (index_z * coarse_z, index_x * coarse_x, index_y * coarse_y), (coarse_z, coarse_x, coarse_y)
    )
    return (pressure, upscaled)


def solution(mesh):
    placed = (
        P(("real", "gz"), "gx", "gy"),
        P(("real", "gz"), "gx", "gy"),
        P(),
        P(("real", "gz"), "gx", "gy"),
        P(("real", "gz"), "gx", "gy"),
        P(("real", "gz"), "gx", "gy"),
    )
    return jax.shard_map(
        local,
        mesh=mesh,
        in_specs=placed,
        out_specs=(P(("real", "gz"), "gx", "gy"), P(None, ("real", "gz"), "gx", "gy")),
        check_vma=False,
    )
```
